128 devices in a mesh: dom: 16 (over y, z), face: 8 (over x, core).
Axes of the slice: x: 4, y: 4, z: 4, core: 2. Of those that a mesh axis runs over, the one named last changes fastest.
Arguments:
- coefficients: float32 [8192, 4096], P(('dom', 'face')), may hold values from -6 to 6
- diffusion: float32 [8192, 3], P(('dom', 'face')), may hold values from 0.05 to 0.5
- velocity: float32 [8192, 3], P(('dom', 'face')), may hold values from -1 to 1
- orders: int32 [8192], P(('dom', 'face')), may hold values from 4 to 15, as said below
- target: int32 [8192], P(('dom', 'face')), may hold values from 0 to 8191, as said below
- local_faces: int32 [128, 4, 64], P(('dom', 'face')), may hold values from 0 to 63, each once within a row
- partner_faces: int32 [128, 2, 64], P(('dom', 'face')), may hold values from -1 to 63, as said below
- partner_turns: int32 [128, 2, 64], P(('dom', 'face')), may hold values from 0 to 7
Outputs:
- advanced: float32 [8192, 4096], P(('dom', 'face'))
The draws below stay inside these ranges and needn't reach their ends.
Inputs may be any that keep to these rules, and one draw needn't show every extreme that they name: `target`: a permutation of the new slots; slot s lies in block s // 64; an element of block b has its new slot in block b - 1, b, b + 1 or b + 128 // 2 (taken mod 128), and exactly 4 elements of each block move to each of the blocks b - 1, b + 1 and b + 64. `orders`: an element whose new slot s has s mod 64 < 32 has order below 8; every other element has order 16 // 2 or more. Entries are -1 exactly for face 0 in the blocks of the first partition and for face 1 in the blocks of the last; every other row partner_faces[b, r, :] is a permutation of 0 to 63.
All inputs are finite; a program needn't handle non-finite values.
Results may differ from the reference program's by a relative error of at most 0.0001.
Values sent between devices are 32-bit elements; how exact they have to be, the bound alone decides.
No kernel may reach another device: no remote copies, remote signals or barrier semaphores. Data moves between devices by JAX's collectives and lax.ppermute only.
A program may use at most 128 MiB of HBM per device.

```python
import math
import jax
import jax.numpy as jnp
import numpy as np
from jax import lax

P_SIZE = 16
CO = 4096
E_DEV = 64
LOW_DEV = 32
GROUPS = 8
BLOCKS = 128
ELEMS = 8192


def migration_plan(key):
    block_count = BLOCKS
    moving = E_DEV // 16
    base_key = jax.random.fold_in(key, 11)
    key_flip, key_rank, key_low, key_high = jax.random.split(base_key, 4)
    flip = jax.random.randint(key_flip, (), 0, 2)
    ranking = jax.vmap(lambda sub_key: jax.random.permutation(sub_key, E_DEV))(jax.random.split(key_rank, block_count))
    low_slots = jax.vmap(lambda sub_key: jax.random.permutation(sub_key, LOW_DEV))(jax.random.split(key_low, block_count))
    high_slots = LOW_DEV + jax.vmap(lambda sub_key: jax.random.permutation(sub_key, E_DEV - LOW_DEV))(jax.random.split(key_high, block_count))
    block_ids = jnp.arange(block_count, dtype=jnp.int32)
    heavy = block_ids % 2 == flip
    slot_list = jnp.where(heavy[:, None], jnp.concatenate([low_slots, high_slots], axis=1), jnp.concatenate([high_slots, low_slots], axis=1))
    source_block = block_ids[:, None]
    receiver = jnp.where(ranking < moving, (source_block + 1) % block_count, jnp.where(ranking < 2 * moving, (source_block + block_count - 1) % block_count, jnp.where(ranking < 3 * moving, (source_block + block_count // 2) % block_count, source_block)))
    new_slot = slot_list[receiver, ranking]
    return ((receiver * E_DEV + new_slot).reshape(-1).astype(jnp.int32), new_slot.reshape(-1).astype(jnp.int32))


def draw_target(key, part):
    placed, new_slot = migration_plan(key)
    return placed


def draw_orders(key, part):
    placed, new_slot = migration_plan(key)
    order_key = jax.random.fold_in(key, 23)
    key_low, key_high = jax.random.split(order_key, 2)
    low_orders = jax.random.randint(key_low, new_slot.shape, P_SIZE // 4, P_SIZE // 2)
    high_orders = jax.random.randint(key_high, new_slot.shape, P_SIZE // 2, P_SIZE)
    chosen = jnp.where(new_slot < LOW_DEV, low_orders, high_orders)
    chosen = jnp.where(new_slot == 0, P_SIZE // 4, chosen)
    chosen = jnp.where(new_slot == LOW_DEV, P_SIZE - 1, chosen)
    return chosen.astype(jnp.int32)


def draw_partner_faces(key, part):
    face_key = jax.random.fold_in(key, 37)
    shuffled = jax.vmap(lambda sub_key: jax.random.permutation(sub_key, E_DEV))(jax.random.split(face_key, BLOCKS * 2))
    shuffled = shuffled.reshape(BLOCKS, 2, E_DEV).astype(jnp.int32)
    block_ids = jnp.arange(BLOCKS, dtype=jnp.int32)[:, None, None]
    face_side = jnp.arange(2, dtype=jnp.int32)[None, :, None]
    boundary = (face_side == 0) & (block_ids < GROUPS) | (face_side == 1) & (block_ids >= BLOCKS - GROUPS)
    return jnp.where(boundary, -1, shuffled).astype(jnp.int32)


def set_ends(array, own_key, low, largest):
    longest = array.shape.index(max(array.shape))
    spots = []
    for shift in (0, 1):
        where = [jax.random.randint(jax.random.fold_in(own_key, axis), (), 0, length) for axis, length in enumerate(array.shape)]
        where[longest] = (where[longest] + shift) % array.shape[longest]
        spots.append(tuple(where))
    return array.at[spots[0]].set(low).at[spots[1]].set(largest)


def shard_levels(stream_key, dims, cuts, least, top_value):
    def one(axis_at, parts):
        heights = jax.random.uniform(jax.random.fold_in(jax.random.fold_in(stream_key, 6), axis_at), (parts,), jnp.float32, least / len(cuts), top_value / len(cuts))
        return jnp.repeat(jnp.exp(heights), dims[axis_at] // parts).reshape((-1,) + (1,) * (len(dims) - axis_at - 1))

    factor_of = one(*cuts[0])
    for cut in cuts[1:]:
        factor_of = factor_of * one(*cut)
    return factor_of


def scatter_about(rng, dims, width, most, cuts=(), kind=jnp.bfloat16):
    entries = width * jax.random.normal(rng, dims, jnp.float32)
    if cuts:
        entries = entries * shard_levels(rng, dims, cuts, -0.22, 0.18)
    return jnp.clip(entries, -most, most).astype(kind)


def setup_inputs(seed: int = 0) -> dict:
    key_of = jax.random.split(jax.random.key(seed), 9)
    coefficients = scatter_about(key_of[0], (ELEMS, CO), 1.0, 6.0, ((0, 128),), jnp.float32)
    diffusion = jnp.clip(jnp.exp(math.log(0.5) - 2.3025851 * jax.random.uniform(key_of[1], (ELEMS, 3), jnp.float32) ** shard_levels(key_of[1], (ELEMS, 3), ((0, 128),), -0.2, 0.2)), 0.05, 0.5)
    velocity = jnp.clip(jax.random.uniform(key_of[2], (ELEMS, 3), jnp.float32, -1.0, 1.0) * shard_levels(key_of[2], (ELEMS, 3), ((0, 128),), -0.4, 0.0), -1.0, 1.0)
    orders = draw_orders(jax.random.fold_in(key_of[8], 71), 0)
    target = draw_target(jax.random.fold_in(key_of[8], 71), 0)
    local_faces = jax.vmap(lambda own: jax.random.permutation(own, E_DEV))(jax.random.split(key_of[5], BLOCKS * 4)).reshape((BLOCKS, 4, E_DEV)).astype(jnp.int32)
    partner_faces = draw_partner_faces(jax.random.fold_in(key_of[8], 71), 0)
    partner_turns = set_ends(jax.random.randint(key_of[7], (BLOCKS, 2, E_DEV), 0, 8), jax.random.fold_in(key_of[7], 1), 0, 7).astype(jnp.int32)
    return dict(coefficients=coefficients, diffusion=diffusion, velocity=velocity, orders=orders, target=target, local_faces=local_faces, partner_faces=partner_faces, partner_turns=partner_turns)


EXACT_DOT = lax.Precision.HIGHEST
TIME_STEP = 0.25
DIRECTION_FORMS = ["kn,snbc->skbc", "kn,sanc->sakc", "kn,sabn->sabk"]
TRACE_FORMS = ["n,snbc->sbc", "n,sanc->sac", "n,sabn->sab"]
LIFT_FORMS = ["n,sbc->snbc", "n,sac->sanc", "n,sab->sabn"]


def mode_tables():
    ladder = np.arange(P_SIZE)
    spacing = ladder[None, :] - ladder[:, None]
    derivative = np.where((spacing > 0) & (spacing % 2 == 1), (2.0 * ladder[:, None] + 1.0) / P_SIZE, 0.0)
    second = derivative @ derivative / P_SIZE
    side_signs = np.stack([(-1.0) ** ladder, np.ones(P_SIZE)])
    weights = (2.0 * ladder + 1.0) / (2.0 * P_SIZE)
    return derivative, second, side_signs, weights


def top_mode():
    ladder = np.arange(P_SIZE)
    first_idx, second_idx, third_idx = np.meshgrid(ladder, ladder, ladder, indexing="ij")
    return jnp.asarray(np.maximum(np.maximum(first_idx, second_idx), third_idx).reshape(-1), jnp.int32)


def block_terms(inputs):
    solution, diffusion_block, velocity_block = inputs
    derivative, second, side_signs, weights = mode_tables()
    derivative = jnp.asarray(derivative, jnp.float32)
    second = jnp.asarray(second, jnp.float32)
    side_signs = jnp.asarray(side_signs, jnp.float32)
    cube_view = solution.reshape(-1, P_SIZE, P_SIZE, P_SIZE)
    summed = jnp.zeros_like(cube_view)
    trace_list = []
    for direction in range(3):
        summed = summed + diffusion_block[:, direction, None, None, None] * jnp.einsum(DIRECTION_FORMS[direction], second, cube_view, precision=EXACT_DOT)
        summed = summed - velocity_block[:, direction, None, None, None] * jnp.einsum(DIRECTION_FORMS[direction], derivative, cube_view, precision=EXACT_DOT)
        for face_side in range(2):
            trace_list.append(jnp.einsum(TRACE_FORMS[direction], side_signs[face_side], cube_view, precision=EXACT_DOT))
    return summed.reshape(-1, CO), jnp.stack(trace_list, axis=1)


def block_lift(jump_block):
    derivative, second, side_signs, weights = mode_tables()
    lift_signs = jnp.asarray(side_signs * weights[None, :], jnp.float32)
    summed = jnp.zeros((jump_block.shape[0], P_SIZE, P_SIZE, P_SIZE), jnp.float32)
    for direction in range(3):
        for face_side in range(2):
            summed = summed + jnp.einsum(LIFT_FORMS[direction], lift_signs[face_side], jump_block[:, 2 * direction + face_side], precision=EXACT_DOT)
    return summed.reshape(-1, CO)


def reorient(trace_rows, turn_codes):
    alternating = jnp.asarray((-1.0) ** np.arange(P_SIZE), jnp.float32)
    flipped = jnp.where((turn_codes % 2 == 1)[:, None, None], jnp.swapaxes(trace_rows, 1, 2), trace_rows)
    row_signs = jnp.where(((turn_codes // 2) % 2 == 1)[:, None, None], alternating[None, :, None], 1.0)
    col_signs = jnp.where(((turn_codes // 4) % 2 == 1)[:, None, None], alternating[None, None, :], 1.0)
    return flipped * row_signs * col_signs


def apply_operator(solution, live_rows, diffusion, velocity, local_faces, partner_faces, partner_turns):
    volume, traces = lax.map(block_terms, (solution.reshape(BLOCKS, E_DEV, CO), diffusion.reshape(BLOCKS, E_DEV, 3), velocity.reshape(BLOCKS, E_DEV, 3)))
    volume = volume.reshape(ELEMS, CO)
    traces = traces.reshape(ELEMS, 6, P_SIZE, P_SIZE)
    slot_ids = jnp.arange(ELEMS, dtype=jnp.int32)
    block_ids = slot_ids // E_DEV
    within = slot_ids % E_DEV
    partner_lower = partner_faces[block_ids, 0, within]
    lower_source = jnp.clip((block_ids - GROUPS) * E_DEV + jnp.maximum(partner_lower, 0), 0, ELEMS - 1)
    lower_trace = jnp.where((partner_lower >= 0)[:, None, None], reorient(traces[lower_source, 1], partner_turns[block_ids, 0, within]), 0.0)
    partner_upper = partner_faces[block_ids, 1, within]
    upper_source = jnp.clip((block_ids + GROUPS) * E_DEV + jnp.maximum(partner_upper, 0), 0, ELEMS - 1)
    upper_trace = jnp.where((partner_upper >= 0)[:, None, None], reorient(traces[upper_source, 0], partner_turns[block_ids, 1, within]), 0.0)
    neighbour_list = [lower_trace, upper_trace]
    for offset_face, opposite in zip(range(4), (3, 2, 5, 4)):
        neighbour_list.append(traces[block_ids * E_DEV + local_faces[block_ids, offset_face, within], opposite])
    jump_rows = traces - jnp.stack(neighbour_list, axis=1)
    lifted = lax.map(block_lift, jump_rows.reshape(BLOCKS, E_DEV, 6, P_SIZE, P_SIZE)).reshape(ELEMS, CO)
    return live_rows * (volume - lifted)


def reference(coefficients, diffusion, velocity, orders, target, local_faces, partner_faces, partner_turns):
    placed_coefficients = jnp.zeros((ELEMS, CO), jnp.float32).at[target].set(coefficients)
    placed_diffusion = jnp.zeros((ELEMS, 3), jnp.float32).at[target].set(diffusion)
    placed_velocity = jnp.zeros((ELEMS, 3), jnp.float32).at[target].set(velocity)
    placed_orders = jnp.zeros((ELEMS,), jnp.int32).at[target].set(orders)
    live_rows = (top_mode()[None, :] <= placed_orders[:, None]).astype(jnp.float32)
    solution = live_rows * placed_coefficients
    half_field = solution + 0.5 * TIME_STEP * apply_operator(solution, live_rows, placed_diffusion, placed_velocity, local_faces, partner_faces, partner_turns)
    return solution + TIME_STEP * apply_operator(half_field, live_rows, placed_diffusion, placed_velocity, local_faces, partner_faces, partner_turns)
```

```python
import jax
import jax.numpy as jnp
import numpy as np
from jax import lax
from jax.sharding import PartitionSpec as P

P_SIZE = 16


EXACT_DOT = lax.Precision.HIGHEST
TIME_STEP = 0.25


def with_halo(shard, sides, width):
    for axis, dim in sides:
        size, length = (lax.axis_size(axis), shard.shape[dim])
        up = [(i, (i + 1) % size) for i in range(size - 1)]
        down = [(j, i) for i, j in up]
        last = lax.slice_in_dim(shard, length - width, length, axis=dim)
        first = lax.slice_in_dim(shard, 0, width, axis=dim)
        before = lax.ppermute(last, axis, up)
        after = lax.ppermute(first, axis, down)
        shard = jnp.concatenate([before, shard, after], axis=dim)
    return shard


def mode_tables():
    ladder = np.arange(P_SIZE)
    spacing = ladder[None, :] - ladder[:, None]
    derivative = np.where(
        (spacing > 0) & (spacing % 2 == 1), (2.0 * ladder[:, None] + 1.0) / P_SIZE, 0.0
    )
    second = derivative @ derivative / P_SIZE
    side_signs = np.stack([(-1.0) ** ladder, np.ones(P_SIZE)])
    weights = (2.0 * ladder + 1.0) / (2.0 * P_SIZE)
    return (derivative, second, side_signs, weights)


def live_modes(order_values):
    ladder = np.arange(P_SIZE)
    first_idx, second_idx, third_idx = np.meshgrid(ladder, ladder, ladder, indexing="ij")
    top_mode = jnp.asarray(
        np.maximum(np.maximum(first_idx, second_idx), third_idx).reshape(-1), jnp.int32
    )
    return (top_mode <= order_values[..., None]).astype(jnp.float32)


def kron_tables(extent):
    derivative, second, side_signs, weights = mode_tables()
    derivative = derivative[:extent, :extent]
    second = second[:extent, :extent]
    identity = np.eye(extent)
    first_axis = np.concatenate([second, derivative], axis=0)
    spread_diff = np.concatenate([np.kron(identity, second.T), np.kron(second.T, identity)], axis=1)
    spread_adv = np.concatenate(
        [np.kron(identity, derivative.T), np.kron(derivative.T, identity)], axis=1
    )
    return (
        jnp.asarray(first_axis, jnp.float32),
        jnp.asarray(spread_diff, jnp.float32),
        jnp.asarray(spread_adv, jnp.float32),
    )


def volume_terms(solution, diffusion, velocity, extent):
    item_count = solution.shape[0]
    plane = extent * extent
    first_axis, spread_diff, spread_adv = kron_tables(extent)
    cube_view = solution.reshape(item_count, extent, plane)
    leading = jnp.einsum("kn,mnq->mkq", first_axis, cube_view, precision=EXACT_DOT)
    summed = (
        diffusion[:, 0, None, None] * leading[:, :extent]
        - velocity[:, 0, None, None] * leading[:, extent:]
    )
    flat_rows = solution.reshape(item_count * extent, plane)
    diff_part = jnp.dot(flat_rows, spread_diff, precision=EXACT_DOT).reshape(
        item_count, extent, 2, plane
    )
    summed = (
        summed
        + diffusion[:, 2, None, None] * diff_part[:, :, 0]
        + diffusion[:, 1, None, None] * diff_part[:, :, 1]
    )
    adv_part = jnp.dot(flat_rows, spread_adv, precision=EXACT_DOT).reshape(
        item_count, extent, 2, plane
    )
    summed = (
        summed
        - velocity[:, 2, None, None] * adv_part[:, :, 0]
        - velocity[:, 1, None, None] * adv_part[:, :, 1]
    )
    return summed.reshape(item_count, extent * plane)


def local_volume(solution, diffusion, velocity):
    return volume_terms(solution, diffusion, velocity, P_SIZE)


def side_table(values_pair):
    identity = np.eye(P_SIZE)
    return np.concatenate(
        [
            np.kron(values_pair[0][:, None], identity),
            np.kron(values_pair[1][:, None], identity),
            np.kron(identity, values_pair[0][:, None]),
            np.kron(identity, values_pair[1][:, None]),
        ],
        axis=1,
    )


def face_traces(solution):
    item_count = solution.shape[0]
    derivative, second, side_signs, weights = mode_tables()
    leading = jnp.einsum(
        "fn,mnq->mfq",
        jnp.asarray(side_signs, jnp.float32),
        solution.reshape(item_count, P_SIZE, P_SIZE * P_SIZE),
        precision=EXACT_DOT,
    )
    others = jnp.dot(
        solution.reshape(item_count * P_SIZE, P_SIZE * P_SIZE),
        jnp.asarray(side_table(side_signs), jnp.float32),
        precision=EXACT_DOT,
    )
    others = (
        others.reshape(item_count, P_SIZE, 4, P_SIZE)
        .transpose(0, 2, 1, 3)
        .reshape(item_count, 4, P_SIZE * P_SIZE)
    )
    return jnp.concatenate([leading, others], axis=1)


def lift_terms(jump_rows):
    item_count = jump_rows.shape[0]
    derivative, second, side_signs, weights = mode_tables()
    lift_signs = side_signs * weights[None, :]
    leading = jnp.einsum(
        "fn,mfq->mnq", jnp.asarray(lift_signs, jnp.float32), jump_rows[:, :2], precision=EXACT_DOT
    )
    others = (
        jump_rows[:, 2:]
        .reshape(item_count, 4, P_SIZE, P_SIZE)
        .transpose(0, 2, 1, 3)
        .reshape(item_count * P_SIZE, 4 * P_SIZE)
    )
    spread = jnp.dot(
        others, jnp.asarray(side_table(lift_signs).T, jnp.float32), precision=EXACT_DOT
    )
    return leading.reshape(item_count, P_SIZE**3) + spread.reshape(item_count, P_SIZE**3)


def reorient(trace_rows, turn_codes):
    item_count = trace_rows.shape[0]
    alternating = jnp.asarray((-1.0) ** np.arange(P_SIZE), jnp.float32)
    square = trace_rows.reshape(item_count, P_SIZE, P_SIZE)
    flipped = jnp.where((turn_codes % 2 == 1)[:, None, None], jnp.swapaxes(square, 1, 2), square)
    row_signs = jnp.where(
        (turn_codes // 2 % 2 == 1)[:, None, None], alternating[None, :, None], 1.0
    )
    col_signs = jnp.where(
        (turn_codes // 4 % 2 == 1)[:, None, None], alternating[None, None, :], 1.0
    )
    return (flipped * row_signs * col_signs).reshape(item_count, P_SIZE * P_SIZE)


def apply_operator(solution, live_rows, volume, local_faces, partner_faces, partner_turns):
    traces = face_traces(solution)
    ends = jnp.stack([traces[:, 0], traces[:, 1]])
    bordered = with_halo(ends, (("dom", 0),), 1)
    from_below = bordered[0]
    from_above = bordered[3]
    lower_choice = partner_faces[0, 0]
    upper_choice = partner_faces[0, 1]
    lower_trace = jnp.where(
        (lower_choice >= 0)[:, None],
        reorient(from_below[jnp.maximum(lower_choice, 0)], partner_turns[0, 0]),
        0.0,
    )
    upper_trace = jnp.where(
        (upper_choice >= 0)[:, None],
        reorient(from_above[jnp.maximum(upper_choice, 0)], partner_turns[0, 1]),
        0.0,
    )
    neighbour_list = [lower_trace, upper_trace]
    for offset_face, opposite in zip(range(4), (3, 2, 5, 4)):
        neighbour_list.append(traces[local_faces[0, offset_face], opposite])
    jump_rows = traces - jnp.stack(neighbour_list, axis=1)
    return live_rows * (volume - lift_terms(jump_rows))


def pick_rows(chosen, count):
    rank = jnp.cumsum(chosen.astype(jnp.int32)) - 1
    hit = chosen[None, :] & (rank[None, :] == jnp.arange(count, dtype=jnp.int32)[:, None])
    rows = jnp.arange(chosen.shape[0], dtype=jnp.int32)
    return jnp.sum(jnp.where(hit, rows[None, :], 0), axis=1)


def pick_rows_inverse(slots, count):
    hit = slots[None, :] == jnp.arange(count, dtype=jnp.int32)[:, None]
    rows = jnp.arange(slots.shape[0], dtype=jnp.int32)
    return jnp.sum(jnp.where(hit, rows[None, :], 0), axis=1)


def shards(
    coefficients, diffusion, velocity, orders, target, local_faces, partner_faces, partner_turns
):
    element_count = coefficients.shape[0]
    blocks_all = lax.axis_size(("dom", "face"))
    moving = element_count // 16
    destination = target // element_count
    new_slot = target % element_count
    here = lax.axis_index(("dom", "face"))
    side_info = jnp.concatenate(
        [
            diffusion,
            velocity,
            new_slot[:, None].astype(jnp.float32),
            orders[:, None].astype(jnp.float32),
        ],
        axis=1,
    )
    side_width = side_info.shape[1]
    got_coef = [coefficients]
    got_side = [side_info]
    got_slot = [jnp.where(destination == here, new_slot, element_count)]
    for shift in (1, blocks_all - 1, blocks_all // 2):
        picked = pick_rows(destination == (here + shift) % blocks_all, moving)
        side_row = jnp.zeros((1, P_SIZE**3), jnp.float32)
        side_row = side_row.at[0, : moving * side_width].set(side_info[picked].reshape(-1))
        parcel = jnp.concatenate([coefficients[picked], side_row], axis=0)
        pairs = [(i, (i + shift) % blocks_all) for i in range(blocks_all)]
        arrived = lax.ppermute(parcel, ("dom", "face"), pairs)
        arrived_side = arrived[moving, : moving * side_width].reshape(moving, side_width)
        got_coef.append(arrived[:moving])
        got_side.append(arrived_side)
        got_slot.append(arrived_side[:, 6].astype(jnp.int32))
    got_coef = jnp.concatenate(got_coef, axis=0)
    got_side = jnp.concatenate(got_side, axis=0)
    got_slot = jnp.concatenate(got_slot, axis=0)
    source = pick_rows_inverse(got_slot, element_count)
    placed_side = got_side[source]
    diffusion_here = placed_side[:, 0:3]
    velocity_here = placed_side[:, 3:6]
    live_rows = live_modes(placed_side[:, 7].astype(jnp.int32))
    solution = live_rows * got_coef[source]
    first_volume = local_volume(solution, diffusion_here, velocity_here)
    half_field = solution + 0.5 * TIME_STEP * apply_operator(
        solution, live_rows, first_volume, local_faces, partner_faces, partner_turns
    )
    second_volume = local_volume(half_field, diffusion_here, velocity_here)
    return solution + TIME_STEP * apply_operator(
        half_field, live_rows, second_volume, local_faces, partner_faces, partner_turns
    )


def solution(mesh):
    in_specs = (
        P(("dom", "face"), None),
        P(("dom", "face"), None),
        P(("dom", "face"), None),
        P(("dom", "face")),
        P(("dom", "face")),
        P(("dom", "face"), None, None),
        P(("dom", "face"), None, None),
        P(("dom", "face"), None, None),
    )
    out_specs = P(("dom", "face"), None)
    return jax.shard_map(shards, mesh=mesh, in_specs=in_specs, out_specs=out_specs, check_vma=False)
```

```python
import functools
import jax
import jax.numpy as jnp
import numpy as np
from jax import lax
from jax.experimental import pallas as pl
from jax.experimental.pallas import tpu as pltpu
from jax.sharding import PartitionSpec as P

P_SIZE = 16
PLANE = P_SIZE * P_SIZE
TIME_STEP = 0.25


def mode_tables():
    ladder = np.arange(P_SIZE)
    spacing = ladder[None, :] - ladder[:, None]
    derivative = np.where(
        (spacing > 0) & (spacing % 2 == 1), (2.0 * ladder[:, None] + 1.0) / P_SIZE, 0.0
    )
    second = derivative @ derivative / P_SIZE
    side_signs = np.stack([(-1.0) ** ladder, np.ones(P_SIZE)])
    weights = (2.0 * ladder + 1.0) / (2.0 * P_SIZE)
    return (derivative, second, side_signs, weights)


def side_table(values_pair):
    identity = np.eye(P_SIZE)
    return np.concatenate(
        [
            np.kron(values_pair[0][:, None], identity),
            np.kron(values_pair[1][:, None], identity),
            np.kron(identity, values_pair[0][:, None]),
            np.kron(identity, values_pair[1][:, None]),
        ],
        axis=1,
    )


def kernel_tables():
    derivative, second, side_signs, weights = mode_tables()
    derivative = derivative.astype(np.float32).astype(np.float64)
    second = second.astype(np.float32).astype(np.float64)
    identity = np.eye(P_SIZE)
    traces = side_table(side_signs)
    swapped = traces[:, [16 * g + j for g in (1, 0, 3, 2) for j in range(P_SIZE)]]
    pad = np.zeros((PLANE, 64))
    spread = np.concatenate(
        [
            np.kron(identity, second.T),
            np.kron(second.T, identity),
            np.kron(identity, derivative.T),
            np.kron(derivative.T, identity),
            traces, pad, swapped, pad,
        ],
        axis=1,
    ).astype(np.float32)
    spread_hi = spread.astype(jnp.bfloat16)
    spread_lo = (spread[:, : 2 * PLANE] - spread_hi[:, : 2 * PLANE].astype(np.float32)).astype(jnp.bfloat16)
    lift_signs = side_signs * weights[None, :]
    lift = np.concatenate([side_table(lift_signs).T, np.zeros((64, PLANE))], axis=0)
    lanes = np.arange(PLANE)
    flip = np.zeros((PLANE, PLANE))
    flip[lanes, (lanes % P_SIZE) * P_SIZE + lanes // P_SIZE] = 1.0
    return (
        jnp.asarray(spread_hi),
        jnp.asarray(spread_lo),
        jnp.asarray(lift, jnp.bfloat16),
        jnp.asarray(flip, jnp.bfloat16),
    )


def top_modes():
    ladder = np.arange(P_SIZE)
    first_idx, second_idx, third_idx = np.meshgrid(ladder, ladder, ladder, indexing="ij")
    return np.maximum(np.maximum(first_idx, second_idx), third_idx).reshape(1, -1).astype(np.int32)


def split_two(x):
    hi = x.astype(jnp.bfloat16)
    lo = (x - hi.astype(jnp.float32)).astype(jnp.bfloat16)
    return hi, lo


def mxu(a, b):
    return jnp.dot(a, b, preferred_element_type=jnp.float32)


def exact_pick(onehot, x):
    hi = x.astype(jnp.bfloat16)
    rest = x - hi.astype(jnp.float32)
    mid = rest.astype(jnp.bfloat16)
    lo = (rest - mid.astype(jnp.float32)).astype(jnp.bfloat16)
    return mxu(onehot, hi) + mxu(onehot, mid) + mxu(onehot, lo)


def end_traces(slabs):
    total = slabs[0] + slabs[1]
    even = slabs[0] - slabs[1]
    for a in range(2, P_SIZE):
        total = total + slabs[a]
        even = even + slabs[a] if a % 2 == 0 else even - slabs[a]
    return even, total


def turn(rows, codes, flip):
    lane = lax.broadcasted_iota(jnp.int32, (1, PLANE), 1)
    swapped = exact_pick_right(rows, flip)
    rows = jnp.where(codes % 2 == 1, swapped, rows)
    row_odd = (lane // P_SIZE) % 2 == 1
    col_odd = lane % 2 == 1
    negate = ((codes // 2) % 2 == 1) & row_odd
    negate = negate != (((codes // 4) % 2 == 1) & col_odd)
    return jnp.where(negate, -rows, rows)


def exact_pick_right(x, onehot):
    hi = x.astype(jnp.bfloat16)
    rest = x - hi.astype(jnp.float32)
    mid = rest.astype(jnp.bfloat16)
    lo = (rest - mid.astype(jnp.float32)).astype(jnp.bfloat16)
    return mxu(hi, onehot) + mxu(mid, onehot) + mxu(lo, onehot)


def section_body(
    v_ref, base_ref, top_ref, order_ref, weight_ref, lower_ref, upper_ref, pick_ref, turn_ref,
    spread_hi_ref, spread_lo_ref, lift_ref, flip_ref, out_ref, ends_ref, *, scale
):
    count = v_ref.shape[0]
    derivative, second, side_signs, weights = mode_tables()
    second = second.astype(np.float32)
    derivative = derivative.astype(np.float32)
    lift_signs = (side_signs * weights[None, :]).astype(np.float32)
    slabs = [v_ref[:, a * PLANE : (a + 1) * PLANE] for a in range(P_SIZE)]
    weight = weight_ref[...]
    diff0 = jnp.broadcast_to(weight[:, 0:1], (count, PLANE))
    vel0 = jnp.broadcast_to(weight[:, 3:4], (count, PLANE))
    first = []
    for k in range(P_SIZE):
        acc_s = None
        acc_d = None
        for n in range(k + 1, P_SIZE):
            if second[k, n] != 0.0:
                term = float(second[k, n]) * slabs[n]
                acc_s = term if acc_s is None else acc_s + term
            if derivative[k, n] != 0.0:
                term = float(derivative[k, n]) * slabs[n]
                acc_d = term if acc_d is None else acc_d + term
        part = jnp.zeros((count, PLANE), jnp.float32)
        if acc_s is not None:
            part = part + diff0 * acc_s
        if acc_d is not None:
            part = part - vel0 * acc_d
        first.append(part)
    stacked = jnp.concatenate(slabs, axis=0)
    hi, lo = split_two(stacked)
    spread_hi = spread_hi_ref[...]
    wide = mxu(hi, spread_hi) + mxu(lo, spread_hi)
    fine = mxu(hi, spread_lo_ref[...])
    weight_rows = jnp.concatenate([weight] * P_SIZE, axis=0)
    inner = (
        weight_rows[:, 2:3] * (wide[:, 0:PLANE] + fine[:, 0:PLANE])
        + weight_rows[:, 1:2] * (wide[:, PLANE : 2 * PLANE] + fine[:, PLANE : 2 * PLANE])
        - weight_rows[:, 5:6] * wide[:, 2 * PLANE : 3 * PLANE]
        - weight_rows[:, 4:5] * wide[:, 3 * PLANE : 4 * PLANE]
    )
    own = jnp.concatenate(
        [wide[a * count : (a + 1) * count, 4 * PLANE : 4 * PLANE + 128] for a in range(P_SIZE)], axis=1
    )
    other = jnp.concatenate(
        [wide[a * count : (a + 1) * count, 4 * PLANE + 128 : 4 * PLANE + 256] for a in range(P_SIZE)], axis=1
    )
    lane = lax.broadcasted_iota(jnp.int32, (1, P_SIZE * 128), 1) % 128
    across = jnp.zeros_like(own)
    for face in range(4):
        gathered = exact_pick(pick_ref[face], other)
        across = jnp.where(lane // P_SIZE == face, gathered, across)
    jump = own - across
    jump_rows = jnp.concatenate([jump[:, a * 128 : (a + 1) * 128] for a in range(P_SIZE)], axis=0)
    jhi, jlo = split_two(jump_rows)
    lift_mat = lift_ref[...]
    lifted = mxu(jhi, lift_mat) + mxu(jlo, lift_mat)
    even, total = end_traces(slabs)
    codes = turn_ref[...]
    flip = flip_ref[...]
    below = turn(exact_pick(pick_ref[4], lower_ref[...]), codes[:, 0:1], flip)
    above = turn(exact_pick(pick_ref[5], upper_ref[...]), codes[:, 1:2], flip)
    jump0 = even - below
    jump1 = total - above
    top = top_ref[...]
    order = order_ref[...]
    news = []
    for a in range(P_SIZE):
        rows = slice(a * count, (a + 1) * count)
        volume = first[a] + inner[rows]
        lift = lifted[rows] + float(lift_signs[0, a]) * jump0 + float(lift_signs[1, a]) * jump1
        live = top[:, a * PLANE : (a + 1) * PLANE] <= order
        update = jnp.where(live, volume - lift, 0.0)
        new = base_ref[:, a * PLANE : (a + 1) * PLANE] + scale * update
        out_ref[:, a * PLANE : (a + 1) * PLANE] = new
        news.append(new)
    even, total = end_traces(news)
    ends_ref[0] = even
    ends_ref[1] = total


def section(v, base, top, order, weight, lower, upper, picks, codes, tables, scale):
    count = v.shape[0]
    spec = pl.BlockSpec(memory_space=pltpu.VMEM)
    return pl.pallas_call(
        functools.partial(section_body, scale=scale),
        out_shape=(
            jax.ShapeDtypeStruct(v.shape, jnp.float32),
            jax.ShapeDtypeStruct((2, count, PLANE), jnp.float32),
        ),
        in_specs=[spec] * 13,
        out_specs=(spec, spec),
        compiler_params=pltpu.CompilerParams(vmem_limit_bytes=60 * 1024 * 1024),
    )(v, base, top, order, weight, lower, upper, picks, codes, *tables)


def prep_body(placed_ref, top_ref, order_ref, field_ref, ends_ref):
    news = []
    for a in range(P_SIZE):
        lanes = slice(a * PLANE, (a + 1) * PLANE)
        live = top_ref[:, lanes] <= order_ref[...]
        new = jnp.where(live, placed_ref[:, lanes], 0.0)
        field_ref[:, lanes] = new
        news.append(new)
    even, total = end_traces(news)
    ends_ref[0] = even
    ends_ref[1] = total


def prep(placed, top, order):
    count = placed.shape[0]
    spec = pl.BlockSpec(memory_space=pltpu.VMEM)
    return pl.pallas_call(
        prep_body,
        out_shape=(
            jax.ShapeDtypeStruct(placed.shape, jnp.float32),
            jax.ShapeDtypeStruct((2, count, PLANE), jnp.float32),
        ),
        in_specs=[spec] * 3,
        out_specs=(spec, spec),
    )(placed, top, order)


def exchange(ends):
    size = lax.axis_size("dom")
    up = [(i, i + 1) for i in range(size - 1)]
    down = [(i + 1, i) for i in range(size - 1)]
    return lax.ppermute(ends[1], "dom", up), lax.ppermute(ends[0], "dom", down)


def pick_rows(chosen, count):
    rank = jnp.cumsum(chosen.astype(jnp.int32)) - 1
    hit = chosen[None, :] & (rank[None, :] == jnp.arange(count, dtype=jnp.int32)[:, None])
    rows = jnp.arange(chosen.shape[0], dtype=jnp.int32)
    return jnp.sum(jnp.where(hit, rows[None, :], 0), axis=1)


def pick_rows_inverse(slots, count):
    hit = slots[None, :] == jnp.arange(count, dtype=jnp.int32)[:, None]
    rows = jnp.arange(slots.shape[0], dtype=jnp.int32)
    return jnp.sum(jnp.where(hit, rows[None, :], 0), axis=1)


def shards(
    coefficients, diffusion, velocity, orders, target, local_faces, partner_faces, partner_turns
):
    element_count = coefficients.shape[0]
    blocks_all = lax.axis_size(("dom", "face"))
    moving = element_count // 16
    destination = target // element_count
    new_slot = target % element_count
    here = lax.axis_index(("dom", "face"))
    side_info = jnp.concatenate(
        [
            diffusion,
            velocity,
            new_slot[:, None].astype(jnp.float32),
            orders[:, None].astype(jnp.float32),
        ],
        axis=1,
    )
    side_width = side_info.shape[1]
    got_coef = [coefficients]
    got_side = [side_info]
    got_slot = [jnp.where(destination == here, new_slot, element_count)]
    for shift in (1, blocks_all - 1, blocks_all // 2):
        picked = pick_rows(destination == (here + shift) % blocks_all, moving)
        side_row = jnp.zeros((1, P_SIZE**3), jnp.float32)
        side_row = side_row.at[0, : moving * side_width].set(side_info[picked].reshape(-1))
        parcel = jnp.concatenate([coefficients[picked], side_row], axis=0)
        pairs = [(i, (i + shift) % blocks_all) for i in range(blocks_all)]
        arrived = lax.ppermute(parcel, ("dom", "face"), pairs)
        arrived_side = arrived[moving, : moving * side_width].reshape(moving, side_width)
        got_coef.append(arrived[:moving])
        got_side.append(arrived_side)
        got_slot.append(arrived_side[:, 6].astype(jnp.int32))
    got_coef = jnp.concatenate(got_coef, axis=0)
    got_side = jnp.concatenate(got_side, axis=0)
    got_slot = jnp.concatenate(got_slot, axis=0)
    source = pick_rows_inverse(got_slot, element_count)
    placed_side = got_side[source]
    weight = jnp.concatenate(
        [placed_side[:, 0:6], jnp.zeros((element_count, 2), jnp.float32)], axis=1
    )
    order = placed_side[:, 7:8].astype(jnp.int32)
    top = jnp.asarray(top_modes())
    tables = kernel_tables()
    neighbours = jnp.concatenate([local_faces[0], partner_faces[0]], axis=0)
    picks = (
        neighbours[:, :, None] == jnp.arange(element_count, dtype=jnp.int32)[None, None, :]
    ).astype(jnp.bfloat16)
    codes = partner_turns[0].T
    field, ends = prep(got_coef[source], top, order)
    lower, upper = exchange(ends)
    half, ends = section(
        field, field, top, order, weight, lower, upper, picks, codes, tables, 0.5 * TIME_STEP
    )
    lower, upper = exchange(ends)
    advanced, _ = section(
        half, field, top, order, weight, lower, upper, picks, codes, tables, TIME_STEP
    )
    return advanced


def solution(mesh):
    in_specs = (
        P(("dom", "face"), None),
        P(("dom", "face"), None),
        P(("dom", "face"), None),
        P(("dom", "face")),
        P(("dom", "face")),
        P(("dom", "face"), None, None),
        P(("dom", "face"), None, None),
        P(("dom", "face"), None, None),
    )
    out_specs = P(("dom", "face"), None)
    return jax.shard_map(shards, mesh=mesh, in_specs=in_specs, out_specs=out_specs, check_vma=False)
```

```python
import functools
import jax
import jax.numpy as jnp
import numpy as np
from jax import lax
from jax.experimental import pallas as pl
from jax.experimental.pallas import tpu as pltpu
from jax.sharding import PartitionSpec as P

P_SIZE = 16
PLANE = P_SIZE * P_SIZE
TIME_STEP = 0.25


def mode_tables():
    ladder = np.arange(P_SIZE)
    spacing = ladder[None, :] - ladder[:, None]
    derivative = np.where(
        (spacing > 0) & (spacing % 2 == 1), (2.0 * ladder[:, None] + 1.0) / P_SIZE, 0.0
    )
    second = derivative @ derivative / P_SIZE
    side_signs = np.stack([(-1.0) ** ladder, np.ones(P_SIZE)])
    weights = (2.0 * ladder + 1.0) / (2.0 * P_SIZE)
    return (derivative, second, side_signs, weights)


def side_table(values_pair):
    identity = np.eye(P_SIZE)
    return np.concatenate(
        [
            np.kron(values_pair[0][:, None], identity),
            np.kron(values_pair[1][:, None], identity),
            np.kron(identity, values_pair[0][:, None]),
            np.kron(identity, values_pair[1][:, None]),
        ],
        axis=1,
    )


def kernel_tables():
    derivative, second, side_signs, weights = mode_tables()
    derivative = derivative.astype(np.float32).astype(np.float64)
    second = second.astype(np.float32).astype(np.float64)
    identity = np.eye(P_SIZE)
    traces = side_table(side_signs)
    swapped = traces[:, [16 * g + j for g in (1, 0, 3, 2) for j in range(P_SIZE)]]
    pad = np.zeros((PLANE, 64))
    spread = np.concatenate(
        [
            np.kron(identity, second.T),
            np.kron(second.T, identity),
            np.kron(identity, derivative.T),
            np.kron(derivative.T, identity),
            traces, pad, swapped, pad,
        ],
        axis=1,
    ).astype(np.float32)
    spread_hi = spread.astype(jnp.bfloat16)
    spread_lo = (spread[:, : 2 * PLANE] - spread_hi[:, : 2 * PLANE].astype(np.float32)).astype(jnp.bfloat16)
    lift_signs = side_signs * weights[None, :]
    lift = np.concatenate([side_table(lift_signs).T, np.zeros((64, PLANE))], axis=0)
    lanes = np.arange(PLANE)
    flip = np.zeros((PLANE, PLANE))
    flip[lanes, (lanes % P_SIZE) * P_SIZE + lanes // P_SIZE] = 1.0
    return (
        jnp.asarray(spread_hi),
        jnp.asarray(spread_lo),
        jnp.asarray(lift, jnp.bfloat16),
        jnp.asarray(flip, jnp.bfloat16),
    )


def top_modes():
    ladder = np.arange(P_SIZE)
    first_idx, second_idx, third_idx = np.meshgrid(ladder, ladder, ladder, indexing="ij")
    return np.maximum(np.maximum(first_idx, second_idx), third_idx).reshape(1, -1).astype(np.int32)


def split_two(x):
    hi = x.astype(jnp.bfloat16)
    lo = (x - hi.astype(jnp.float32)).astype(jnp.bfloat16)
    return hi, lo


def mxu(a, b):
    return jnp.dot(a, b, preferred_element_type=jnp.float32)


def exact_pick(onehot, x):
    hi = x.astype(jnp.bfloat16)
    rest = x - hi.astype(jnp.float32)
    mid = rest.astype(jnp.bfloat16)
    lo = (rest - mid.astype(jnp.float32)).astype(jnp.bfloat16)
    return mxu(onehot, hi) + mxu(onehot, mid) + mxu(onehot, lo)


def end_traces(slabs):
    total = slabs[0] + slabs[1]
    even = slabs[0] - slabs[1]
    for a in range(2, P_SIZE):
        total = total + slabs[a]
        even = even + slabs[a] if a % 2 == 0 else even - slabs[a]
    return even, total


def turn(rows, codes, flip):
    lane = lax.broadcasted_iota(jnp.int32, (1, PLANE), 1)
    swapped = exact_pick_right(rows, flip)
    rows = jnp.where(codes % 2 == 1, swapped, rows)
    row_odd = (lane // P_SIZE) % 2 == 1
    col_odd = lane % 2 == 1
    negate = ((codes // 2) % 2 == 1) & row_odd
    negate = negate != (((codes // 4) % 2 == 1) & col_odd)
    return jnp.where(negate, -rows, rows)


def exact_pick_right(x, onehot):
    hi = x.astype(jnp.bfloat16)
    rest = x - hi.astype(jnp.float32)
    mid = rest.astype(jnp.bfloat16)
    lo = (rest - mid.astype(jnp.float32)).astype(jnp.bfloat16)
    return mxu(hi, onehot) + mxu(mid, onehot) + mxu(lo, onehot)


def section_body(
    v_ref, base_ref, top_ref, order_ref, weight_ref, lower_ref, upper_ref, pick_ref, turn_ref,
    spread_hi_ref, spread_lo_ref, lift_ref, flip_ref, out_ref, ends_ref, *, scale
):
    count = v_ref.shape[0]
    derivative, second, side_signs, weights = mode_tables()
    second = second.astype(np.float32)
    derivative = derivative.astype(np.float32)
    lift_signs = (side_signs * weights[None, :]).astype(np.float32)
    slabs = [v_ref[:, a * PLANE : (a + 1) * PLANE] for a in range(P_SIZE)]
    weight = weight_ref[...]
    diff0 = jnp.broadcast_to(weight[:, 0:1], (count, PLANE))
    vel0 = jnp.broadcast_to(weight[:, 3:4], (count, PLANE))
    first = []
    for k in range(P_SIZE):
        acc_s = None
        acc_d = None
        for n in range(k + 1, P_SIZE):
            if second[k, n] != 0.0:
                term = float(second[k, n]) * slabs[n]
                acc_s = term if acc_s is None else acc_s + term
            if derivative[k, n] != 0.0:
                term = float(derivative[k, n]) * slabs[n]
                acc_d = term if acc_d is None else acc_d + term
        part = jnp.zeros((count, PLANE), jnp.float32)
        if acc_s is not None:
            part = part + diff0 * acc_s
        if acc_d is not None:
            part = part - vel0 * acc_d
        first.append(part)
    stacked = jnp.concatenate(slabs, axis=0)
    hi, lo = split_two(stacked)
    spread_hi = spread_hi_ref[...]
    wide = mxu(hi, spread_hi) + mxu(lo, spread_hi)
    fine = mxu(hi, spread_lo_ref[...])
    weight_rows = jnp.concatenate([weight] * P_SIZE, axis=0)
    inner = (
        weight_rows[:, 2:3] * (wide[:, 0:PLANE] + fine[:, 0:PLANE])
        + weight_rows[:, 1:2] * (wide[:, PLANE : 2 * PLANE] + fine[:, PLANE : 2 * PLANE])
        - weight_rows[:, 5:6] * wide[:, 2 * PLANE : 3 * PLANE]
        - weight_rows[:, 4:5] * wide[:, 3 * PLANE : 4 * PLANE]
    )
    own = jnp.concatenate(
        [wide[a * count : (a + 1) * count, 4 * PLANE : 4 * PLANE + 128] for a in range(P_SIZE)], axis=1
    )
    other = jnp.concatenate(
        [wide[a * count : (a + 1) * count, 4 * PLANE + 128 : 4 * PLANE + 256] for a in range(P_SIZE)], axis=1
    )
    lane = lax.broadcasted_iota(jnp.int32, (1, P_SIZE * 128), 1) % 128
    across = jnp.zeros_like(own)
    for face in range(4):
        gathered = exact_pick(pick_ref[face], other)
        across = jnp.where(lane // P_SIZE == face, gathered, across)
    jump = own - across
    jump_rows = jnp.concatenate([jump[:, a * 128 : (a + 1) * 128] for a in range(P_SIZE)], axis=0)
    jhi, jlo = split_two(jump_rows)
    lift_mat = lift_ref[...]
    lifted = mxu(jhi, lift_mat) + mxu(jlo, lift_mat)
    even, total = end_traces(slabs)
    codes = turn_ref[...]
    flip = flip_ref[...]
    below = turn(exact_pick(pick_ref[4], lower_ref[...]), codes[:, 0:1], flip)
    above = turn(exact_pick(pick_ref[5], upper_ref[...]), codes[:, 1:2], flip)
    jump0 = even - below
    jump1 = total - above
    top = top_ref[...]
    order = order_ref[...]
    news = []
    for a in range(P_SIZE):
        rows = slice(a * count, (a + 1) * count)
        volume = first[a] + inner[rows]
        lift = lifted[rows] + float(lift_signs[0, a]) * jump0 + float(lift_signs[1, a]) * jump1
        live = top[:, a * PLANE : (a + 1) * PLANE] <= order
        update = jnp.where(live, volume - lift, 0.0)
        new = base_ref[:, a * PLANE : (a + 1) * PLANE] + scale * update
        out_ref[:, a * PLANE : (a + 1) * PLANE] = new
        news.append(new)
    even, total = end_traces(news)
    ends_ref[0] = even
    ends_ref[1] = total


def section(v, base, top, order, weight, lower, upper, picks, codes, tables, scale):
    count = v.shape[0]
    spec = pl.BlockSpec(memory_space=pltpu.VMEM)
    return pl.pallas_call(
        functools.partial(section_body, scale=scale),
        out_shape=(
            jax.ShapeDtypeStruct(v.shape, jnp.float32),
            jax.ShapeDtypeStruct((2, count, PLANE), jnp.float32),
        ),
        in_specs=[spec] * 13,
        out_specs=(spec, spec),
        compiler_params=pltpu.CompilerParams(vmem_limit_bytes=60 * 1024 * 1024),
    )(v, base, top, order, weight, lower, upper, picks, codes, *tables)


def prep_body(placed_ref, top_ref, order_ref, field_ref, ends_ref):
    news = []
    for a in range(P_SIZE):
        lanes = slice(a * PLANE, (a + 1) * PLANE)
        live = top_ref[:, lanes] <= order_ref[...]
        new = jnp.where(live, placed_ref[:, lanes], 0.0)
        field_ref[:, lanes] = new
        news.append(new)
    even, total = end_traces(news)
    ends_ref[0] = even
    ends_ref[1] = total


def prep(placed, top, order):
    count = placed.shape[0]
    spec = pl.BlockSpec(memory_space=pltpu.VMEM)
    return pl.pallas_call(
        prep_body,
        out_shape=(
            jax.ShapeDtypeStruct(placed.shape, jnp.float32),
            jax.ShapeDtypeStruct((2, count, PLANE), jnp.float32),
        ),
        in_specs=[spec] * 3,
        out_specs=(spec, spec),
    )(placed, top, order)


def exchange(ends):
    size = lax.axis_size("dom")
    up = [(i, i + 1) for i in range(size - 1)]
    down = [(i + 1, i) for i in range(size - 1)]
    return lax.ppermute(ends[1], "dom", up), lax.ppermute(ends[0], "dom", down)


def shards(
    coefficients, diffusion, velocity, orders, target, local_faces, partner_faces, partner_turns
):
    element_count = coefficients.shape[0]
    blocks_all = lax.axis_size(("dom", "face"))
    moving = element_count // 16
    destination = target // element_count
    new_slot = target % element_count
    here = lax.axis_index(("dom", "face"))
    side_info = jnp.concatenate(
        [
            diffusion,
            velocity,
            new_slot[:, None].astype(jnp.float32),
            orders[:, None].astype(jnp.float32),
        ],
        axis=1,
    )
    side_width = side_info.shape[1]
    shifts = (1, blocks_all - 1, blocks_all // 2)
    goal = (here + jnp.asarray(shifts, jnp.int32)) % blocks_all
    chosen = destination[None, :] == goal[:, None]
    rank = jnp.cumsum(chosen.astype(jnp.int32), axis=1) - 1
    hit = chosen[:, None, :] & (
        rank[:, None, :] == jnp.arange(moving, dtype=jnp.int32)[None, :, None]
    )
    rows = jnp.arange(element_count, dtype=jnp.int32)
    picked = jnp.sum(jnp.where(hit, rows[None, None, :], 0), axis=2).reshape(-1)
    side_rows = side_info[picked].reshape(len(shifts), 1, moving * side_width)
    side_rows = jnp.pad(side_rows, ((0, 0), (0, 0), (0, P_SIZE**3 - moving * side_width)))
    parcels = jnp.concatenate(
        [coefficients[picked].reshape(len(shifts), moving, P_SIZE**3), side_rows], axis=1
    )
    got_coef = [coefficients]
    got_side = [side_info]
    got_slot = [jnp.where(destination == here, new_slot, element_count)]
    for index, shift in enumerate(shifts):
        pairs = [(i, (i + shift) % blocks_all) for i in range(blocks_all)]
        arrived = lax.ppermute(parcels[index], ("dom", "face"), pairs)
        arrived_side = arrived[moving, : moving * side_width].reshape(moving, side_width)
        got_coef.append(arrived[:moving])
        got_side.append(arrived_side)
        got_slot.append(arrived_side[:, 6].astype(jnp.int32))
    got_coef = jnp.concatenate(got_coef, axis=0)
    got_side = jnp.concatenate(got_side, axis=0)
    got_slot = jnp.concatenate(got_slot, axis=0)
    hit = got_slot[None, :] == jnp.arange(element_count, dtype=jnp.int32)[:, None]
    got_rows = jnp.arange(got_slot.shape[0], dtype=jnp.int32)
    source = jnp.sum(jnp.where(hit, got_rows[None, :], 0), axis=1)
    placed_side = got_side[source]
    weight = jnp.concatenate(
        [placed_side[:, 0:6], jnp.zeros((element_count, 2), jnp.float32)], axis=1
    )
    order = placed_side[:, 7:8].astype(jnp.int32)
    top = jnp.asarray(top_modes())
    tables = kernel_tables()
    neighbours = jnp.concatenate([local_faces[0], partner_faces[0]], axis=0)
    picks = (
        neighbours[:, :, None] == jnp.arange(element_count, dtype=jnp.int32)[None, None, :]
    ).astype(jnp.bfloat16)
    codes = partner_turns[0].T
    field, ends = prep(got_coef[source], top, order)
    lower, upper = exchange(ends)
    half, ends = section(
        field, field, top, order, weight, lower, upper, picks, codes, tables, 0.5 * TIME_STEP
    )
    lower, upper = exchange(ends)
    advanced, _ = section(
        half, field, top, order, weight, lower, upper, picks, codes, tables, TIME_STEP
    )
    return advanced


def solution(mesh):
    in_specs = (
        P(("dom", "face"), None),
        P(("dom", "face"), None),
        P(("dom", "face"), None),
        P(("dom", "face")),
        P(("dom", "face")),
        P(("dom", "face"), None, None),
        P(("dom", "face"), None, None),
        P(("dom", "face"), None, None),
    )
    out_specs = P(("dom", "face"), None)
    return jax.shard_map(shards, mesh=mesh, in_specs=in_specs, out_specs=out_specs, check_vma=False)
```

```python
import functools
import jax
import jax.numpy as jnp
import numpy as np
from jax import lax
from jax.experimental import pallas as pl
from jax.experimental.pallas import tpu as pltpu
from jax.sharding import PartitionSpec as P

P_SIZE = 16
PLANE = P_SIZE * P_SIZE
TIME_STEP = 0.25


def mode_tables():
    ladder = np.arange(P_SIZE)
    spacing = ladder[None, :] - ladder[:, None]
    derivative = np.where(
        (spacing > 0) & (spacing % 2 == 1), (2.0 * ladder[:, None] + 1.0) / P_SIZE, 0.0
    )
    second = derivative @ derivative / P_SIZE
    side_signs = np.stack([(-1.0) ** ladder, np.ones(P_SIZE)])
    weights = (2.0 * ladder + 1.0) / (2.0 * P_SIZE)
    return (derivative, second, side_signs, weights)


def side_table(values_pair):
    identity = np.eye(P_SIZE)
    return np.concatenate(
        [
            np.kron(values_pair[0][:, None], identity),
            np.kron(values_pair[1][:, None], identity),
            np.kron(identity, values_pair[0][:, None]),
            np.kron(identity, values_pair[1][:, None]),
        ],
        axis=1,
    )


def kernel_tables():
    derivative, second, side_signs, weights = mode_tables()
    derivative = derivative.astype(np.float32).astype(np.float64)
    second = second.astype(np.float32).astype(np.float64)
    identity = np.eye(P_SIZE)
    traces = side_table(side_signs)
    swapped = traces[:, [16 * g + j for g in (1, 0, 3, 2) for j in range(P_SIZE)]]
    pad = np.zeros((PLANE, 64))
    spread = np.concatenate(
        [
            np.kron(identity, second.T),
            np.kron(second.T, identity),
            np.kron(identity, derivative.T),
            np.kron(derivative.T, identity),
            traces, pad, swapped, pad,
        ],
        axis=1,
    ).astype(np.float32)
    spread_hi = spread.astype(jnp.bfloat16)
    spread_lo = (spread[:, : 2 * PLANE] - spread_hi[:, : 2 * PLANE].astype(np.float32)).astype(jnp.bfloat16)
    lift_signs = side_signs * weights[None, :]
    lift = np.concatenate([side_table(lift_signs).T, np.zeros((64, PLANE))], axis=0)
    lanes = np.arange(PLANE)
    flip = np.zeros((PLANE, PLANE))
    flip[lanes, (lanes % P_SIZE) * P_SIZE + lanes // P_SIZE] = 1.0
    return (
        jnp.asarray(spread_hi),
        jnp.asarray(spread_lo),
        jnp.asarray(lift, jnp.bfloat16),
        jnp.asarray(flip, jnp.bfloat16),
    )


def top_modes():
    ladder = np.arange(P_SIZE)
    first_idx, second_idx, third_idx = np.meshgrid(ladder, ladder, ladder, indexing="ij")
    return np.maximum(np.maximum(first_idx, second_idx), third_idx).reshape(1, -1).astype(np.int32)


def split_two(x):
    hi = x.astype(jnp.bfloat16)
    lo = (x - hi.astype(jnp.float32)).astype(jnp.bfloat16)
    return hi, lo


def mxu(a, b):
    return jnp.dot(a, b, preferred_element_type=jnp.float32)


def exact_pick(onehot, x):
    hi = x.astype(jnp.bfloat16)
    rest = x - hi.astype(jnp.float32)
    mid = rest.astype(jnp.bfloat16)
    lo = (rest - mid.astype(jnp.float32)).astype(jnp.bfloat16)
    return mxu(onehot, hi) + mxu(onehot, mid) + mxu(onehot, lo)


def end_traces(slabs):
    total = slabs[0] + slabs[1]
    even = slabs[0] - slabs[1]
    for a in range(2, P_SIZE):
        total = total + slabs[a]
        even = even + slabs[a] if a % 2 == 0 else even - slabs[a]
    return even, total


def turn(rows, codes, flip):
    lane = lax.broadcasted_iota(jnp.int32, (1, PLANE), 1)
    swapped = exact_pick_right(rows, flip)
    rows = jnp.where(codes % 2 == 1, swapped, rows)
    row_odd = (lane // P_SIZE) % 2 == 1
    col_odd = lane % 2 == 1
    negate = ((codes // 2) % 2 == 1) & row_odd
    negate = negate != (((codes // 4) % 2 == 1) & col_odd)
    return jnp.where(negate, -rows, rows)


def exact_pick_right(x, onehot):
    hi = x.astype(jnp.bfloat16)
    rest = x - hi.astype(jnp.float32)
    mid = rest.astype(jnp.bfloat16)
    lo = (rest - mid.astype(jnp.float32)).astype(jnp.bfloat16)
    return mxu(hi, onehot) + mxu(mid, onehot) + mxu(lo, onehot)


def section_body(
    v_ref, base_ref, top_ref, order_ref, weight_ref, lower_ref, upper_ref, pick_ref, turn_ref,
    spread_hi_ref, spread_lo_ref, lift_ref, flip_ref, out_ref, even_ref, total_ref, *, scale
):
    count = v_ref.shape[0]
    derivative, second, side_signs, weights = mode_tables()
    second = second.astype(np.float32)
    derivative = derivative.astype(np.float32)
    lift_signs = (side_signs * weights[None, :]).astype(np.float32)
    slabs = [v_ref[:, a * PLANE : (a + 1) * PLANE] for a in range(P_SIZE)]
    weight = weight_ref[...]
    diff0 = jnp.broadcast_to(weight[:, 0:1], (count, PLANE))
    vel0 = jnp.broadcast_to(weight[:, 3:4], (count, PLANE))
    first = []
    for k in range(P_SIZE):
        acc_s = None
        acc_d = None
        for n in range(k + 1, P_SIZE):
            if second[k, n] != 0.0:
                term = float(second[k, n]) * slabs[n]
                acc_s = term if acc_s is None else acc_s + term
            if derivative[k, n] != 0.0:
                term = float(derivative[k, n]) * slabs[n]
                acc_d = term if acc_d is None else acc_d + term
        part = jnp.zeros((count, PLANE), jnp.float32)
        if acc_s is not None:
            part = part + diff0 * acc_s
        if acc_d is not None:
            part = part - vel0 * acc_d
        first.append(part)
    stacked = jnp.concatenate(slabs, axis=0)
    hi, lo = split_two(stacked)
    spread_hi = spread_hi_ref[...]
    wide = mxu(hi, spread_hi) + mxu(lo, spread_hi)
    fine = mxu(hi, spread_lo_ref[...])
    weight_rows = jnp.concatenate([weight] * P_SIZE, axis=0)
    inner = (
        weight_rows[:, 2:3] * (wide[:, 0:PLANE] + fine[:, 0:PLANE])
        + weight_rows[:, 1:2] * (wide[:, PLANE : 2 * PLANE] + fine[:, PLANE : 2 * PLANE])
        - weight_rows[:, 5:6] * wide[:, 2 * PLANE : 3 * PLANE]
        - weight_rows[:, 4:5] * wide[:, 3 * PLANE : 4 * PLANE]
    )
    own = jnp.concatenate(
        [wide[a * count : (a + 1) * count, 4 * PLANE : 4 * PLANE + 128] for a in range(P_SIZE)], axis=1
    )
    other = jnp.concatenate(
        [wide[a * count : (a + 1) * count, 4 * PLANE + 128 : 4 * PLANE + 256] for a in range(P_SIZE)], axis=1
    )
    lane = lax.broadcasted_iota(jnp.int32, (1, P_SIZE * 128), 1) % 128
    across = jnp.zeros_like(own)
    for face in range(4):
        gathered = exact_pick(pick_ref[face], other)
        across = jnp.where(lane // P_SIZE == face, gathered, across)
    jump = own - across
    jump_rows = jnp.concatenate([jump[:, a * 128 : (a + 1) * 128] for a in range(P_SIZE)], axis=0)
    jhi, jlo = split_two(jump_rows)
    lift_mat = lift_ref[...]
    lifted = mxu(jhi, lift_mat) + mxu(jlo, lift_mat)
    even, total = end_traces(slabs)
    codes = turn_ref[...]
    flip = flip_ref[...]
    below = turn(exact_pick(pick_ref[4], lower_ref[...]), codes[:, 0:1], flip)
    above = turn(exact_pick(pick_ref[5], upper_ref[...]), codes[:, 1:2], flip)
    jump0 = even - below
    jump1 = total - above
    top = top_ref[...]
    order = order_ref[...]
    news = []
    for a in range(P_SIZE):
        rows = slice(a * count, (a + 1) * count)
        volume = first[a] + inner[rows]
        lift = lifted[rows] + float(lift_signs[0, a]) * jump0 + float(lift_signs[1, a]) * jump1
        live = top[:, a * PLANE : (a + 1) * PLANE] <= order
        update = jnp.where(live, volume - lift, 0.0)
        new = base_ref[:, a * PLANE : (a + 1) * PLANE] + scale * update
        out_ref[:, a * PLANE : (a + 1) * PLANE] = new
        news.append(new)
    even, total = end_traces(news)
    even_ref[...] = even
    total_ref[...] = total


def section(v, base, top, order, weight, lower, upper, picks, codes, tables, scale):
    count = v.shape[0]
    spec = pl.BlockSpec(memory_space=pltpu.VMEM)
    return pl.pallas_call(
        functools.partial(section_body, scale=scale),
        out_shape=(
            jax.ShapeDtypeStruct(v.shape, jnp.float32),
            jax.ShapeDtypeStruct((count, PLANE), jnp.float32),
            jax.ShapeDtypeStruct((count, PLANE), jnp.float32),
        ),
        in_specs=[spec] * 13,
        out_specs=(spec, spec, spec),
        compiler_params=pltpu.CompilerParams(vmem_limit_bytes=60 * 1024 * 1024),
    )(v, base, top, order, weight, lower, upper, picks, codes, *tables)


def prep_body(placed_ref, top_ref, order_ref, field_ref, even_ref, total_ref):
    news = []
    for a in range(P_SIZE):
        lanes = slice(a * PLANE, (a + 1) * PLANE)
        live = top_ref[:, lanes] <= order_ref[...]
        new = jnp.where(live, placed_ref[:, lanes], 0.0)
        field_ref[:, lanes] = new
        news.append(new)
    even, total = end_traces(news)
    even_ref[...] = even
    total_ref[...] = total


def prep(placed, top, order):
    count = placed.shape[0]
    spec = pl.BlockSpec(memory_space=pltpu.VMEM)
    return pl.pallas_call(
        prep_body,
        out_shape=(
            jax.ShapeDtypeStruct(placed.shape, jnp.float32),
            jax.ShapeDtypeStruct((count, PLANE), jnp.float32),
            jax.ShapeDtypeStruct((count, PLANE), jnp.float32),
        ),
        in_specs=[spec] * 3,
        out_specs=(spec, spec, spec),
    )(placed, top, order)


def exchange(even, total):
    size = lax.axis_size("dom")
    up = [(i, (i + 1) % size) for i in range(size)]
    down = [((i + 1) % size, i) for i in range(size)]
    return lax.ppermute(total, "dom", up), lax.ppermute(even, "dom", down)


def shards(
    coefficients, diffusion, velocity, orders, target, local_faces, partner_faces, partner_turns
):
    element_count = coefficients.shape[0]
    blocks_all = lax.axis_size(("dom", "face"))
    moving = element_count // 16
    destination = target // element_count
    new_slot = target % element_count
    here = lax.axis_index(("dom", "face"))
    side_info = jnp.concatenate(
        [
            diffusion,
            velocity,
            new_slot[:, None].astype(jnp.float32),
            orders[:, None].astype(jnp.float32),
        ],
        axis=1,
    )
    side_width = side_info.shape[1]
    shifts = (1, blocks_all - 1, blocks_all // 2)
    goal = (here + jnp.asarray(shifts, jnp.int32)) % blocks_all
    chosen = destination[None, :] == goal[:, None]
    rank = jnp.cumsum(chosen.astype(jnp.int32), axis=1) - 1
    hit = chosen[:, None, :] & (
        rank[:, None, :] == jnp.arange(moving, dtype=jnp.int32)[None, :, None]
    )
    rows = jnp.arange(element_count, dtype=jnp.int32)
    picked = jnp.sum(jnp.where(hit, rows[None, None, :], 0), axis=2).reshape(-1)
    side_rows = side_info[picked].reshape(len(shifts), 1, moving * side_width)
    side_rows = jnp.pad(side_rows, ((0, 0), (0, 0), (0, P_SIZE**3 - moving * side_width)))
    parcels = jnp.concatenate(
        [coefficients[picked].reshape(len(shifts), moving, P_SIZE**3), side_rows], axis=1
    )
    got_coef = [coefficients]
    got_side = [side_info]
    got_slot = [jnp.where(destination == here, new_slot, element_count)]
    for index, shift in enumerate(shifts):
        pairs = [(i, (i + shift) % blocks_all) for i in range(blocks_all)]
        arrived = lax.ppermute(parcels[index], ("dom", "face"), pairs)
        arrived_side = arrived[moving, : moving * side_width].reshape(moving, side_width)
        got_coef.append(arrived[:moving])
        got_side.append(arrived_side)
        got_slot.append(arrived_side[:, 6].astype(jnp.int32))
    got_coef = jnp.concatenate(got_coef, axis=0)
    got_side = jnp.concatenate(got_side, axis=0)
    got_slot = jnp.concatenate(got_slot, axis=0)
    hit = got_slot[None, :] == jnp.arange(element_count, dtype=jnp.int32)[:, None]
    got_rows = jnp.arange(got_slot.shape[0], dtype=jnp.int32)
    source = jnp.sum(jnp.where(hit, got_rows[None, :], 0), axis=1)
    placed_side = got_side[source]
    weight = jnp.concatenate(
        [placed_side[:, 0:6], jnp.zeros((element_count, 2), jnp.float32)], axis=1
    )
    order = placed_side[:, 7:8].astype(jnp.int32)
    top = jnp.asarray(top_modes())
    tables = kernel_tables()
    neighbours = jnp.concatenate([local_faces[0], partner_faces[0]], axis=0)
    picks = (
        neighbours[:, :, None] == jnp.arange(element_count, dtype=jnp.int32)[None, None, :]
    ).astype(jnp.bfloat16)
    codes = partner_turns[0].T
    field, even, total = prep(got_coef[source], top, order)
    lower, upper = exchange(even, total)
    half, even, total = section(
        field, field, top, order, weight, lower, upper, picks, codes, tables, 0.5 * TIME_STEP
    )
    lower, upper = exchange(even, total)
    advanced, _, _ = section(
        half, field, top, order, weight, lower, upper, picks, codes, tables, TIME_STEP
    )
    return advanced


def solution(mesh):
    in_specs = (
        P(("dom", "face"), None),
        P(("dom", "face"), None),
        P(("dom", "face"), None),
        P(("dom", "face")),
        P(("dom", "face")),
        P(("dom", "face"), None, None),
        P(("dom", "face"), None, None),
        P(("dom", "face"), None, None),
    )
    out_specs = P(("dom", "face"), None)
    return jax.shard_map(shards, mesh=mesh, in_specs=in_specs, out_specs=out_specs, check_vma=False)
```

```python
import functools
import jax
import jax.numpy as jnp
import numpy as np
from jax import lax
from jax.experimental import pallas as pl
from jax.experimental.pallas import tpu as pltpu
from jax.sharding import PartitionSpec as P

P_SIZE = 16
PLANE = P_SIZE * P_SIZE
TIME_STEP = 0.25


def mode_tables():
    ladder = np.arange(P_SIZE)
    spacing = ladder[None, :] - ladder[:, None]
    derivative = np.where(
        (spacing > 0) & (spacing % 2 == 1), (2.0 * ladder[:, None] + 1.0) / P_SIZE, 0.0
    )
    second = derivative @ derivative / P_SIZE
    side_signs = np.stack([(-1.0) ** ladder, np.ones(P_SIZE)])
    weights = (2.0 * ladder + 1.0) / (2.0 * P_SIZE)
    return (derivative, second, side_signs, weights)


def side_table(values_pair):
    identity = np.eye(P_SIZE)
    return np.concatenate(
        [
            np.kron(values_pair[0][:, None], identity),
            np.kron(values_pair[1][:, None], identity),
            np.kron(identity, values_pair[0][:, None]),
            np.kron(identity, values_pair[1][:, None]),
        ],
        axis=1,
    )


def kernel_tables():
    derivative, second, side_signs, weights = mode_tables()
    derivative = derivative.astype(np.float32).astype(np.float64)
    second = second.astype(np.float32).astype(np.float64)
    identity = np.eye(P_SIZE)
    traces = side_table(side_signs)
    swapped = traces[:, [16 * g + j for g in (1, 0, 3, 2) for j in range(P_SIZE)]]
    pad = np.zeros((PLANE, 64))
    spread = np.concatenate(
        [
            np.kron(identity, second.T),
            np.kron(second.T, identity),
            np.kron(identity, derivative.T),
            np.kron(derivative.T, identity),
            traces, pad, swapped, pad,
        ],
        axis=1,
    ).astype(np.float32)
    spread_hi = spread.astype(jnp.bfloat16)
    spread_lo = (spread[:, : 2 * PLANE] - spread_hi[:, : 2 * PLANE].astype(np.float32)).astype(jnp.bfloat16)
    lift_signs = side_signs * weights[None, :]
    lift = np.concatenate([side_table(lift_signs).T, np.zeros((64, PLANE))], axis=0)
    lanes = np.arange(PLANE)
    flip = np.zeros((PLANE, PLANE))
    flip[lanes, (lanes % P_SIZE) * P_SIZE + lanes // P_SIZE] = 1.0
    return (
        jnp.asarray(spread_hi),
        jnp.asarray(spread_lo),
        jnp.asarray(lift, jnp.bfloat16),
        jnp.asarray(flip, jnp.bfloat16),
    )


def top_modes():
    ladder = np.arange(P_SIZE)
    first_idx, second_idx, third_idx = np.meshgrid(ladder, ladder, ladder, indexing="ij")
    return np.maximum(np.maximum(first_idx, second_idx), third_idx).reshape(1, -1).astype(np.int32)


def split_two(x):
    hi = x.astype(jnp.bfloat16)
    lo = (x - hi.astype(jnp.float32)).astype(jnp.bfloat16)
    return hi, lo


def mxu(a, b):
    return jnp.dot(a, b, preferred_element_type=jnp.float32)


def exact_pick(onehot, x):
    hi = x.astype(jnp.bfloat16)
    rest = x - hi.astype(jnp.float32)
    mid = rest.astype(jnp.bfloat16)
    lo = (rest - mid.astype(jnp.float32)).astype(jnp.bfloat16)
    return mxu(onehot, hi) + mxu(onehot, mid) + mxu(onehot, lo)


def end_traces(slabs):
    total = slabs[0] + slabs[1]
    even = slabs[0] - slabs[1]
    for a in range(2, P_SIZE):
        total = total + slabs[a]
        even = even + slabs[a] if a % 2 == 0 else even - slabs[a]
    return even, total


def turn(rows, codes, flip):
    lane = lax.broadcasted_iota(jnp.int32, (1, PLANE), 1)
    swapped = exact_pick_right(rows, flip)
    rows = jnp.where(codes % 2 == 1, swapped, rows)
    row_odd = (lane // P_SIZE) % 2 == 1
    col_odd = lane % 2 == 1
    negate = ((codes // 2) % 2 == 1) & row_odd
    negate = negate != (((codes // 4) % 2 == 1) & col_odd)
    return jnp.where(negate, -rows, rows)


def exact_pick_right(x, onehot):
    hi = x.astype(jnp.bfloat16)
    rest = x - hi.astype(jnp.float32)
    mid = rest.astype(jnp.bfloat16)
    lo = (rest - mid.astype(jnp.float32)).astype(jnp.bfloat16)
    return mxu(hi, onehot) + mxu(mid, onehot) + mxu(lo, onehot)


def inner_body(
    v_ref, weight_ref, pick_ref, spread_hi_ref, spread_lo_ref, lift_ref, partial_ref
):
    count = v_ref.shape[0]
    derivative, second, side_signs, weights = mode_tables()
    second = second.astype(np.float32)
    derivative = derivative.astype(np.float32)
    lift_signs = (side_signs * weights[None, :]).astype(np.float32)
    slabs = [v_ref[:, a * PLANE : (a + 1) * PLANE] for a in range(P_SIZE)]
    weight = weight_ref[...]
    diff0 = jnp.broadcast_to(weight[:, 0:1], (count, PLANE))
    vel0 = jnp.broadcast_to(weight[:, 3:4], (count, PLANE))
    first = []
    for k in range(P_SIZE):
        acc_s = None
        acc_d = None
        for n in range(k + 1, P_SIZE):
            if second[k, n] != 0.0:
                term = float(second[k, n]) * slabs[n]
                acc_s = term if acc_s is None else acc_s + term
            if derivative[k, n] != 0.0:
                term = float(derivative[k, n]) * slabs[n]
                acc_d = term if acc_d is None else acc_d + term
        part = jnp.zeros((count, PLANE), jnp.float32)
        if acc_s is not None:
            part = part + diff0 * acc_s
        if acc_d is not None:
            part = part - vel0 * acc_d
        first.append(part)
    stacked = jnp.concatenate(slabs, axis=0)
    hi, lo = split_two(stacked)
    spread_hi = spread_hi_ref[...]
    wide = mxu(hi, spread_hi) + mxu(lo, spread_hi)
    fine = mxu(hi, spread_lo_ref[...])
    weight_rows = jnp.concatenate([weight] * P_SIZE, axis=0)
    inner = (
        weight_rows[:, 2:3] * (wide[:, 0:PLANE] + fine[:, 0:PLANE])
        + weight_rows[:, 1:2] * (wide[:, PLANE : 2 * PLANE] + fine[:, PLANE : 2 * PLANE])
        - weight_rows[:, 5:6] * wide[:, 2 * PLANE : 3 * PLANE]
        - weight_rows[:, 4:5] * wide[:, 3 * PLANE : 4 * PLANE]
    )
    own = jnp.concatenate(
        [wide[a * count : (a + 1) * count, 4 * PLANE : 4 * PLANE + 128] for a in range(P_SIZE)], axis=1
    )
    other = jnp.concatenate(
        [wide[a * count : (a + 1) * count, 4 * PLANE + 128 : 4 * PLANE + 256] for a in range(P_SIZE)], axis=1
    )
    lane = lax.broadcasted_iota(jnp.int32, (1, P_SIZE * 128), 1) % 128
    across = jnp.zeros_like(own)
    for face in range(4):
        gathered = exact_pick(pick_ref[face], other)
        across = jnp.where(lane // P_SIZE == face, gathered, across)
    jump = own - across
    jump_rows = jnp.concatenate([jump[:, a * 128 : (a + 1) * 128] for a in range(P_SIZE)], axis=0)
    jhi, jlo = split_two(jump_rows)
    lift_mat = lift_ref[...]
    lifted = mxu(jhi, lift_mat) + mxu(jlo, lift_mat)
    even, total = end_traces(slabs)
    for a in range(P_SIZE):
        rows = slice(a * count, (a + 1) * count)
        own_lift = lifted[rows] + float(lift_signs[0, a]) * even + float(lift_signs[1, a]) * total
        partial_ref[:, a * PLANE : (a + 1) * PLANE] = first[a] + inner[rows] - own_lift


def outer_body(
    partial_ref, base_ref, top_ref, order_ref, lower_ref, upper_ref, pick_ref, turn_ref, flip_ref,
    out_ref, even_ref, total_ref, *, scale
):
    derivative, second, side_signs, weights = mode_tables()
    lift_signs = (side_signs * weights[None, :]).astype(np.float32)
    codes = turn_ref[...]
    flip = flip_ref[...]
    below = turn(exact_pick(pick_ref[4], lower_ref[...]), codes[:, 0:1], flip)
    above = turn(exact_pick(pick_ref[5], upper_ref[...]), codes[:, 1:2], flip)
    top = top_ref[...]
    order = order_ref[...]
    news = []
    for a in range(P_SIZE):
        lanes = slice(a * PLANE, (a + 1) * PLANE)
        update = (
            partial_ref[:, lanes]
            + float(lift_signs[0, a]) * below
            + float(lift_signs[1, a]) * above
        )
        live = top[:, lanes] <= order
        new = base_ref[:, lanes] + scale * jnp.where(live, update, 0.0)
        out_ref[:, lanes] = new
        news.append(new)
    even, total = end_traces(news)
    even_ref[...] = even
    total_ref[...] = total


def section(v, base, top, order, weight, lower, upper, picks, codes, tables, scale):
    count = v.shape[0]
    spread_hi, spread_lo, lift, flip = tables
    spec = pl.BlockSpec(memory_space=pltpu.VMEM)
    partial = pl.pallas_call(
        inner_body,
        out_shape=jax.ShapeDtypeStruct(v.shape, jnp.float32),
        in_specs=[spec] * 6,
        out_specs=spec,
        compiler_params=pltpu.CompilerParams(vmem_limit_bytes=60 * 1024 * 1024),
        cost_estimate=pl.CostEstimate(
            flops=2_500_000_000, transcendentals=0, bytes_accessed=4_000_000
        ),
    )(v, weight, picks, spread_hi, spread_lo, lift)
    lower, upper = exchange(*lower) if isinstance(lower, tuple) else (lower, upper)
    return pl.pallas_call(
        functools.partial(outer_body, scale=scale),
        out_shape=(
            jax.ShapeDtypeStruct(v.shape, jnp.float32),
            jax.ShapeDtypeStruct((count, PLANE), jnp.float32),
            jax.ShapeDtypeStruct((count, PLANE), jnp.float32),
        ),
        in_specs=[spec] * 9,
        out_specs=(spec, spec, spec),
    )(partial, base, top, order, lower, upper, picks, codes, flip)


def prep_body(placed_ref, top_ref, order_ref, field_ref, even_ref, total_ref):
    news = []
    for a in range(P_SIZE):
        lanes = slice(a * PLANE, (a + 1) * PLANE)
        live = top_ref[:, lanes] <= order_ref[...]
        new = jnp.where(live, placed_ref[:, lanes], 0.0)
        field_ref[:, lanes] = new
        news.append(new)
    even, total = end_traces(news)
    even_ref[...] = even
    total_ref[...] = total


def prep(placed, top, order):
    count = placed.shape[0]
    spec = pl.BlockSpec(memory_space=pltpu.VMEM)
    return pl.pallas_call(
        prep_body,
        out_shape=(
            jax.ShapeDtypeStruct(placed.shape, jnp.float32),
            jax.ShapeDtypeStruct((count, PLANE), jnp.float32),
            jax.ShapeDtypeStruct((count, PLANE), jnp.float32),
        ),
        in_specs=[spec] * 3,
        out_specs=(spec, spec, spec),
    )(placed, top, order)


def exchange(even, total):
    size = lax.axis_size("dom")
    up = [(i, (i + 1) % size) for i in range(size)]
    down = [((i + 1) % size, i) for i in range(size)]
    return lax.ppermute(total, "dom", up), lax.ppermute(even, "dom", down)


def shards(
    coefficients, diffusion, velocity, orders, target, local_faces, partner_faces, partner_turns
):
    element_count = coefficients.shape[0]
    blocks_all = lax.axis_size(("dom", "face"))
    moving = element_count // 16
    destination = target // element_count
    new_slot = target % element_count
    here = lax.axis_index(("dom", "face"))
    side_info = jnp.concatenate(
        [
            diffusion,
            velocity,
            new_slot[:, None].astype(jnp.float32),
            orders[:, None].astype(jnp.float32),
        ],
        axis=1,
    )
    side_width = side_info.shape[1]
    shifts = (1, blocks_all - 1, blocks_all // 2)
    goal = (here + jnp.asarray(shifts, jnp.int32)) % blocks_all
    chosen = destination[None, :] == goal[:, None]
    rank = jnp.cumsum(chosen.astype(jnp.int32), axis=1) - 1
    hit = chosen[:, None, :] & (
        rank[:, None, :] == jnp.arange(moving, dtype=jnp.int32)[None, :, None]
    )
    rows = jnp.arange(element_count, dtype=jnp.int32)
    picked = jnp.sum(jnp.where(hit, rows[None, None, :], 0), axis=2).reshape(-1)
    side_rows = side_info[picked].reshape(len(shifts), 1, moving * side_width)
    side_rows = jnp.pad(side_rows, ((0, 0), (0, 0), (0, P_SIZE**3 - moving * side_width)))
    parcels = jnp.concatenate(
        [coefficients[picked].reshape(len(shifts), moving, P_SIZE**3), side_rows], axis=1
    )
    got_coef = [coefficients]
    got_side = [side_info]
    got_slot = [jnp.where(destination == here, new_slot, element_count)]
    for index, shift in enumerate(shifts):
        pairs = [(i, (i + shift) % blocks_all) for i in range(blocks_all)]
        arrived = lax.ppermute(parcels[index], ("dom", "face"), pairs)
        arrived_side = arrived[moving, : moving * side_width].reshape(moving, side_width)
        got_coef.append(arrived[:moving])
        got_side.append(arrived_side)
        got_slot.append(arrived_side[:, 6].astype(jnp.int32))
    got_coef = jnp.concatenate(got_coef, axis=0)
    got_side = jnp.concatenate(got_side, axis=0)
    got_slot = jnp.concatenate(got_slot, axis=0)
    hit = got_slot[None, :] == jnp.arange(element_count, dtype=jnp.int32)[:, None]
    got_rows = jnp.arange(got_slot.shape[0], dtype=jnp.int32)
    source = jnp.sum(jnp.where(hit, got_rows[None, :], 0), axis=1)
    placed_side = got_side[source]
    weight = jnp.concatenate(
        [placed_side[:, 0:6], jnp.zeros((element_count, 2), jnp.float32)], axis=1
    )
    order = placed_side[:, 7:8].astype(jnp.int32)
    top = jnp.asarray(top_modes())
    tables = kernel_tables()
    neighbours = jnp.concatenate([local_faces[0], partner_faces[0]], axis=0)
    picks = (
        neighbours[:, :, None] == jnp.arange(element_count, dtype=jnp.int32)[None, None, :]
    ).astype(jnp.bfloat16)
    codes = partner_turns[0].T
    field, even, total = prep(got_coef[source], top, order)
    half, even, total = section(
        field, field, top, order, weight, (even, total), None, picks, codes, tables, 0.5 * TIME_STEP
    )
    advanced, _, _ = section(
        half, field, top, order, weight, (even, total), None, picks, codes, tables, TIME_STEP
    )
    return advanced


def solution(mesh):
    in_specs = (
        P(("dom", "face"), None),
        P(("dom", "face"), None),
        P(("dom", "face"), None),
        P(("dom", "face")),
        P(("dom", "face")),
        P(("dom", "face"), None, None),
        P(("dom", "face"), None, None),
        P(("dom", "face"), None, None),
    )
    out_specs = P(("dom", "face"), None)
    return jax.shard_map(shards, mesh=mesh, in_specs=in_specs, out_specs=out_specs, check_vma=False)
```

```python
import functools
import jax
import jax.numpy as jnp
import numpy as np
from jax import lax
from jax.experimental import pallas as pl
from jax.experimental.pallas import tpu as pltpu
from jax.sharding import PartitionSpec as P

P_SIZE = 16
PLANE = P_SIZE * P_SIZE
TIME_STEP = 0.25


def mode_tables():
    ladder = np.arange(P_SIZE)
    spacing = ladder[None, :] - ladder[:, None]
    derivative = np.where(
        (spacing > 0) & (spacing % 2 == 1), (2.0 * ladder[:, None] + 1.0) / P_SIZE, 0.0
    )
    second = derivative @ derivative / P_SIZE
    side_signs = np.stack([(-1.0) ** ladder, np.ones(P_SIZE)])
    weights = (2.0 * ladder + 1.0) / (2.0 * P_SIZE)
    return (derivative, second, side_signs, weights)


def side_table(values_pair):
    identity = np.eye(P_SIZE)
    return np.concatenate(
        [
            np.kron(values_pair[0][:, None], identity),
            np.kron(values_pair[1][:, None], identity),
            np.kron(identity, values_pair[0][:, None]),
            np.kron(identity, values_pair[1][:, None]),
        ],
        axis=1,
    )


def kernel_tables():
    derivative, second, side_signs, weights = mode_tables()
    derivative = derivative.astype(np.float32).astype(np.float64)
    second = second.astype(np.float32).astype(np.float64)
    identity = np.eye(P_SIZE)
    traces = side_table(side_signs)
    swapped = traces[:, [16 * g + j for g in (1, 0, 3, 2) for j in range(P_SIZE)]]
    pad = np.zeros((PLANE, 64))
    spread = np.concatenate(
        [
            np.kron(identity, second.T),
            np.kron(second.T, identity),
            np.kron(identity, derivative.T),
            np.kron(derivative.T, identity),
            traces, pad, swapped, pad,
        ],
        axis=1,
    ).astype(np.float32)
    spread_hi = spread.astype(jnp.bfloat16)
    spread_lo = (spread[:, : 2 * PLANE] - spread_hi[:, : 2 * PLANE].astype(np.float32)).astype(jnp.bfloat16)
    lift_signs = side_signs * weights[None, :]
    lift = np.concatenate([side_table(lift_signs).T, np.zeros((64, PLANE))], axis=0)
    lanes = np.arange(PLANE)
    flip = np.zeros((PLANE, PLANE))
    flip[lanes, (lanes % P_SIZE) * P_SIZE + lanes // P_SIZE] = 1.0
    return (
        jnp.asarray(spread_hi),
        jnp.asarray(spread_lo),
        jnp.asarray(lift, jnp.bfloat16),
        jnp.asarray(flip, jnp.bfloat16),
    )


def top_modes():
    ladder = np.arange(P_SIZE)
    first_idx, second_idx, third_idx = np.meshgrid(ladder, ladder, ladder, indexing="ij")
    return np.maximum(np.maximum(first_idx, second_idx), third_idx).reshape(1, -1).astype(np.int32)


def split_two(x):
    hi = x.astype(jnp.bfloat16)
    lo = (x - hi.astype(jnp.float32)).astype(jnp.bfloat16)
    return hi, lo


def mxu(a, b):
    return jnp.dot(a, b, preferred_element_type=jnp.float32)


def exact_pick(onehot, x):
    hi = x.astype(jnp.bfloat16)
    rest = x - hi.astype(jnp.float32)
    mid = rest.astype(jnp.bfloat16)
    lo = (rest - mid.astype(jnp.float32)).astype(jnp.bfloat16)
    return mxu(onehot, hi) + mxu(onehot, mid) + mxu(onehot, lo)


def end_traces(slabs):
    total = slabs[0] + slabs[1]
    even = slabs[0] - slabs[1]
    for a in range(2, P_SIZE):
        total = total + slabs[a]
        even = even + slabs[a] if a % 2 == 0 else even - slabs[a]
    return even, total


def turn(rows, codes, flip):
    lane = lax.broadcasted_iota(jnp.int32, (1, PLANE), 1)
    swapped = exact_pick_right(rows, flip)
    rows = jnp.where(codes % 2 == 1, swapped, rows)
    row_odd = (lane // P_SIZE) % 2 == 1
    col_odd = lane % 2 == 1
    negate = ((codes // 2) % 2 == 1) & row_odd
    negate = negate != (((codes // 4) % 2 == 1) & col_odd)
    return jnp.where(negate, -rows, rows)


def exact_pick_right(x, onehot):
    hi = x.astype(jnp.bfloat16)
    rest = x - hi.astype(jnp.float32)
    mid = rest.astype(jnp.bfloat16)
    lo = (rest - mid.astype(jnp.float32)).astype(jnp.bfloat16)
    return mxu(hi, onehot) + mxu(mid, onehot) + mxu(lo, onehot)


def inner_body(
    v_ref, weight_ref, pick_ref, spread_hi_ref, spread_lo_ref, lift_ref, partial_ref
):
    count = v_ref.shape[0]
    derivative, second, side_signs, weights = mode_tables()
    second = second.astype(np.float32)
    derivative = derivative.astype(np.float32)
    lift_signs = (side_signs * weights[None, :]).astype(np.float32)
    slabs = [v_ref[:, a * PLANE : (a + 1) * PLANE] for a in range(P_SIZE)]
    weight = weight_ref[...]
    diff0 = jnp.broadcast_to(weight[:, 0:1], (count, PLANE))
    vel0 = jnp.broadcast_to(weight[:, 3:4], (count, PLANE))
    first = []
    for k in range(P_SIZE):
        acc_s = None
        acc_d = None
        for n in range(k + 1, P_SIZE):
            if second[k, n] != 0.0:
                term = float(second[k, n]) * slabs[n]
                acc_s = term if acc_s is None else acc_s + term
            if derivative[k, n] != 0.0:
                term = float(derivative[k, n]) * slabs[n]
                acc_d = term if acc_d is None else acc_d + term
        part = jnp.zeros((count, PLANE), jnp.float32)
        if acc_s is not None:
            part = part + diff0 * acc_s
        if acc_d is not None:
            part = part - vel0 * acc_d
        first.append(part)
    stacked = jnp.concatenate(slabs, axis=0)
    hi, lo = split_two(stacked)
    spread_hi = spread_hi_ref[...]
    wide = mxu(hi, spread_hi) + mxu(lo, spread_hi)
    fine = mxu(hi, spread_lo_ref[...])
    weight_rows = jnp.concatenate([weight] * P_SIZE, axis=0)
    inner = (
        weight_rows[:, 2:3] * (wide[:, 0:PLANE] + fine[:, 0:PLANE])
        + weight_rows[:, 1:2] * (wide[:, PLANE : 2 * PLANE] + fine[:, PLANE : 2 * PLANE])
        - weight_rows[:, 5:6] * wide[:, 2 * PLANE : 3 * PLANE]
        - weight_rows[:, 4:5] * wide[:, 3 * PLANE : 4 * PLANE]
    )
    own = jnp.concatenate(
        [wide[a * count : (a + 1) * count, 4 * PLANE : 4 * PLANE + 128] for a in range(P_SIZE)], axis=1
    )
    other = jnp.concatenate(
        [wide[a * count : (a + 1) * count, 4 * PLANE + 128 : 4 * PLANE + 256] for a in range(P_SIZE)], axis=1
    )
    lane = lax.broadcasted_iota(jnp.int32, (1, P_SIZE * 128), 1) % 128
    across = jnp.zeros_like(own)
    for face in range(4):
        gathered = exact_pick(pick_ref[face], other)
        across = jnp.where(lane // P_SIZE == face, gathered, across)
    jump = own - across
    jump_rows = jnp.concatenate([jump[:, a * 128 : (a + 1) * 128] for a in range(P_SIZE)], axis=0)
    jhi, jlo = split_two(jump_rows)
    lift_mat = lift_ref[...]
    lifted = mxu(jhi, lift_mat) + mxu(jlo, lift_mat)
    even, total = end_traces(slabs)
    for a in range(P_SIZE):
        rows = slice(a * count, (a + 1) * count)
        own_lift = lifted[rows] + float(lift_signs[0, a]) * even + float(lift_signs[1, a]) * total
        partial_ref[:, a * PLANE : (a + 1) * PLANE] = first[a] + inner[rows] - own_lift


def outer_body(
    partial_ref, base_ref, top_ref, order_ref, lower_ref, upper_ref, pick_ref, turn_ref, flip_ref,
    out_ref, even_ref, total_ref, sides_ref, *, scale
):
    step = pl.program_id(0)

    @pl.when(step == 0)
    def _():
        codes = turn_ref[...]
        flip = flip_ref[...]
        sides_ref[0] = turn(exact_pick(pick_ref[4], lower_ref[...]), codes[:, 0:1], flip)
        sides_ref[1] = turn(exact_pick(pick_ref[5], upper_ref[...]), codes[:, 1:2], flip)
        even_ref[...] = jnp.zeros_like(even_ref)
        total_ref[...] = jnp.zeros_like(total_ref)

    weight = (2 * step + 1).astype(jnp.float32) / (2.0 * P_SIZE)
    sign = (1 - 2 * (step % 2)).astype(jnp.float32)
    update = partial_ref[...] + (sign * weight) * sides_ref[0] + weight * sides_ref[1]
    live = top_ref[...] <= order_ref[...]
    new = base_ref[...] + scale * jnp.where(live, update, 0.0)
    out_ref[...] = new
    even_ref[...] = even_ref[...] + sign * new
    total_ref[...] = total_ref[...] + new


def slab_spec(rows):
    return pl.BlockSpec((rows, PLANE), lambda a: (0, a))


def whole_spec(shape):
    return pl.BlockSpec(shape, lambda a: (0,) * len(shape))


def section(v, base, top, order, weight, lower, upper, picks, codes, tables, scale):
    count = v.shape[0]
    spread_hi, spread_lo, lift, flip = tables
    spec = pl.BlockSpec(memory_space=pltpu.VMEM)
    partial = pl.pallas_call(
        inner_body,
        out_shape=jax.ShapeDtypeStruct(v.shape, jnp.float32),
        in_specs=[spec] * 6,
        out_specs=spec,
        compiler_params=pltpu.CompilerParams(vmem_limit_bytes=60 * 1024 * 1024),
        cost_estimate=pl.CostEstimate(
            flops=2_500_000_000, transcendentals=0, bytes_accessed=4_000_000
        ),
    )(v, weight, picks, spread_hi, spread_lo, lift)
    lower, upper = exchange(*lower) if isinstance(lower, tuple) else (lower, upper)
    return pl.pallas_call(
        functools.partial(outer_body, scale=scale),
        out_shape=(
            jax.ShapeDtypeStruct(v.shape, jnp.float32),
            jax.ShapeDtypeStruct((count, PLANE), jnp.float32),
            jax.ShapeDtypeStruct((count, PLANE), jnp.float32),
        ),
        grid=(P_SIZE,),
        in_specs=[
            slab_spec(count),
            slab_spec(count),
            slab_spec(1),
            whole_spec(order.shape),
            whole_spec(lower.shape),
            whole_spec(upper.shape),
            whole_spec(picks.shape),
            whole_spec(codes.shape),
            whole_spec(flip.shape),
        ],
        out_specs=(slab_spec(count), whole_spec((count, PLANE)), whole_spec((count, PLANE))),
        scratch_shapes=[pltpu.VMEM((2, count, PLANE), jnp.float32)],
    )(partial, base, top, order, lower, upper, picks, codes, flip)


def prep_body(placed_ref, top_ref, order_ref, field_ref, even_ref, total_ref):
    step = pl.program_id(0)

    @pl.when(step == 0)
    def _():
        even_ref[...] = jnp.zeros_like(even_ref)
        total_ref[...] = jnp.zeros_like(total_ref)

    sign = (1 - 2 * (step % 2)).astype(jnp.float32)
    live = top_ref[...] <= order_ref[...]
    new = jnp.where(live, placed_ref[...], 0.0)
    field_ref[...] = new
    even_ref[...] = even_ref[...] + sign * new
    total_ref[...] = total_ref[...] + new


def prep(placed, top, order):
    count = placed.shape[0]
    return pl.pallas_call(
        prep_body,
        out_shape=(
            jax.ShapeDtypeStruct(placed.shape, jnp.float32),
            jax.ShapeDtypeStruct((count, PLANE), jnp.float32),
            jax.ShapeDtypeStruct((count, PLANE), jnp.float32),
        ),
        grid=(P_SIZE,),
        in_specs=[slab_spec(count), slab_spec(1), whole_spec(order.shape)],
        out_specs=(slab_spec(count), whole_spec((count, PLANE)), whole_spec((count, PLANE))),
    )(placed, top, order)


def exchange(even, total):
    size = lax.axis_size("dom")
    up = [(i, (i + 1) % size) for i in range(size)]
    down = [((i + 1) % size, i) for i in range(size)]
    return lax.ppermute(total, "dom", up), lax.ppermute(even, "dom", down)


def shards(
    coefficients, diffusion, velocity, orders, target, local_faces, partner_faces, partner_turns
):
    element_count = coefficients.shape[0]
    blocks_all = lax.axis_size(("dom", "face"))
    moving = element_count // 16
    destination = target // element_count
    new_slot = target % element_count
    here = lax.axis_index(("dom", "face"))
    side_info = jnp.concatenate(
        [
            diffusion,
            velocity,
            new_slot[:, None].astype(jnp.float32),
            orders[:, None].astype(jnp.float32),
        ],
        axis=1,
    )
    side_width = side_info.shape[1]
    shifts = (1, blocks_all - 1, blocks_all // 2)
    goal = (here + jnp.asarray(shifts, jnp.int32)) % blocks_all
    chosen = destination[None, :] == goal[:, None]
    rank = jnp.cumsum(chosen.astype(jnp.int32), axis=1) - 1
    hit = chosen[:, None, :] & (
        rank[:, None, :] == jnp.arange(moving, dtype=jnp.int32)[None, :, None]
    )
    rows = jnp.arange(element_count, dtype=jnp.int32)
    picked = jnp.sum(jnp.where(hit, rows[None, None, :], 0), axis=2).reshape(-1)
    side_rows = side_info[picked].reshape(len(shifts), 1, moving * side_width)
    side_rows = jnp.pad(side_rows, ((0, 0), (0, 0), (0, P_SIZE**3 - moving * side_width)))
    parcels = jnp.concatenate(
        [coefficients[picked].reshape(len(shifts), moving, P_SIZE**3), side_rows], axis=1
    )
    got_coef = [coefficients]
    got_side = [side_info]
    got_slot = [jnp.where(destination == here, new_slot, element_count)]
    for index, shift in enumerate(shifts):
        pairs = [(i, (i + shift) % blocks_all) for i in range(blocks_all)]
        arrived = lax.ppermute(parcels[index], ("dom", "face"), pairs)
        arrived_side = arrived[moving, : moving * side_width].reshape(moving, side_width)
        got_coef.append(arrived[:moving])
        got_side.append(arrived_side)
        got_slot.append(arrived_side[:, 6].astype(jnp.int32))
    got_coef = jnp.concatenate(got_coef, axis=0)
    got_side = jnp.concatenate(got_side, axis=0)
    got_slot = jnp.concatenate(got_slot, axis=0)
    hit = got_slot[None, :] == jnp.arange(element_count, dtype=jnp.int32)[:, None]
    got_rows = jnp.arange(got_slot.shape[0], dtype=jnp.int32)
    source = jnp.sum(jnp.where(hit, got_rows[None, :], 0), axis=1)
    placed_side = got_side[source]
    weight = jnp.concatenate(
        [placed_side[:, 0:6], jnp.zeros((element_count, 2), jnp.float32)], axis=1
    )
    order = placed_side[:, 7:8].astype(jnp.int32)
    top = jnp.asarray(top_modes())
    tables = kernel_tables()
    neighbours = jnp.concatenate([local_faces[0], partner_faces[0]], axis=0)
    picks = (
        neighbours[:, :, None] == jnp.arange(element_count, dtype=jnp.int32)[None, None, :]
    ).astype(jnp.bfloat16)
    codes = partner_turns[0].T
    field, even, total = prep(got_coef[source], top, order)
    half, even, total = section(
        field, field, top, order, weight, (even, total), None, picks, codes, tables, 0.5 * TIME_STEP
    )
    advanced, _, _ = section(
        half, field, top, order, weight, (even, total), None, picks, codes, tables, TIME_STEP
    )
    return advanced


def solution(mesh):
    in_specs = (
        P(("dom", "face"), None),
        P(("dom", "face"), None),
        P(("dom", "face"), None),
        P(("dom", "face")),
        P(("dom", "face")),
        P(("dom", "face"), None, None),
        P(("dom", "face"), None, None),
        P(("dom", "face"), None, None),
    )
    out_specs = P(("dom", "face"), None)
    return jax.shard_map(shards, mesh=mesh, in_specs=in_specs, out_specs=out_specs, check_vma=False)
```

```python
import functools
import jax
import jax.numpy as jnp
import numpy as np
from jax import lax
from jax.experimental import pallas as pl
from jax.experimental.pallas import tpu as pltpu
from jax.sharding import PartitionSpec as P

P_SIZE = 16
PLANE = P_SIZE * P_SIZE
TIME_STEP = 0.25


def mode_tables():
    ladder = np.arange(P_SIZE)
    spacing = ladder[None, :] - ladder[:, None]
    derivative = np.where(
        (spacing > 0) & (spacing % 2 == 1), (2.0 * ladder[:, None] + 1.0) / P_SIZE, 0.0
    )
    second = derivative @ derivative / P_SIZE
    side_signs = np.stack([(-1.0) ** ladder, np.ones(P_SIZE)])
    weights = (2.0 * ladder + 1.0) / (2.0 * P_SIZE)
    return (derivative, second, side_signs, weights)


def side_table(values_pair):
    identity = np.eye(P_SIZE)
    return np.concatenate(
        [
            np.kron(values_pair[0][:, None], identity),
            np.kron(values_pair[1][:, None], identity),
            np.kron(identity, values_pair[0][:, None]),
            np.kron(identity, values_pair[1][:, None]),
        ],
        axis=1,
    )


def kernel_tables():
    derivative, second, side_signs, weights = mode_tables()
    derivative = derivative.astype(np.float32).astype(np.float64)
    second = second.astype(np.float32).astype(np.float64)
    identity = np.eye(P_SIZE)
    traces = side_table(side_signs)
    swapped = traces[:, [16 * g + j for g in (1, 0, 3, 2) for j in range(P_SIZE)]]
    pad = np.zeros((PLANE, 64))
    spread = np.concatenate(
        [
            np.kron(identity, second.T),
            np.kron(second.T, identity),
            np.kron(identity, derivative.T),
            np.kron(derivative.T, identity),
            traces, pad, swapped, pad,
        ],
        axis=1,
    ).astype(np.float32)
    spread_hi = spread.astype(jnp.bfloat16)
    spread_lo = (spread[:, : 2 * PLANE] - spread_hi[:, : 2 * PLANE].astype(np.float32)).astype(jnp.bfloat16)
    lift_signs = side_signs * weights[None, :]
    lift = np.concatenate([side_table(lift_signs).T, np.zeros((64, PLANE))], axis=0)
    lanes = np.arange(PLANE)
    flip = np.zeros((PLANE, PLANE))
    flip[lanes, (lanes % P_SIZE) * P_SIZE + lanes // P_SIZE] = 1.0
    return (
        jnp.asarray(spread_hi),
        jnp.asarray(spread_lo),
        jnp.asarray(lift, jnp.bfloat16),
        jnp.asarray(flip, jnp.bfloat16),
    )


def top_modes():
    ladder = np.arange(P_SIZE)
    first_idx, second_idx, third_idx = np.meshgrid(ladder, ladder, ladder, indexing="ij")
    return np.maximum(np.maximum(first_idx, second_idx), third_idx).reshape(1, -1).astype(np.int32)


def split_two(x):
    hi = x.astype(jnp.bfloat16)
    lo = (x - hi.astype(jnp.float32)).astype(jnp.bfloat16)
    return hi, lo


def mxu(a, b):
    return jnp.dot(a, b, preferred_element_type=jnp.float32)


def exact_pick(onehot, x):
    hi = x.astype(jnp.bfloat16)
    rest = x - hi.astype(jnp.float32)
    mid = rest.astype(jnp.bfloat16)
    lo = (rest - mid.astype(jnp.float32)).astype(jnp.bfloat16)
    return mxu(onehot, hi) + mxu(onehot, mid) + mxu(onehot, lo)


def end_traces(slabs):
    total = slabs[0] + slabs[1]
    even = slabs[0] - slabs[1]
    for a in range(2, P_SIZE):
        total = total + slabs[a]
        even = even + slabs[a] if a % 2 == 0 else even - slabs[a]
    return even, total


def turn(rows, codes, flip):
    lane = lax.broadcasted_iota(jnp.int32, (1, PLANE), 1)
    swapped = exact_pick_right(rows, flip)
    rows = jnp.where(codes % 2 == 1, swapped, rows)
    row_odd = (lane // P_SIZE) % 2 == 1
    col_odd = lane % 2 == 1
    negate = ((codes // 2) % 2 == 1) & row_odd
    negate = negate != (((codes // 4) % 2 == 1) & col_odd)
    return jnp.where(negate, -rows, rows)


def exact_pick_right(x, onehot):
    hi = x.astype(jnp.bfloat16)
    rest = x - hi.astype(jnp.float32)
    mid = rest.astype(jnp.bfloat16)
    lo = (rest - mid.astype(jnp.float32)).astype(jnp.bfloat16)
    return mxu(hi, onehot) + mxu(mid, onehot) + mxu(lo, onehot)


def inner_body(v_ref, *refs, scale, shared):
    if shared:
        base_ref = v_ref
        weight_ref, top_ref, pick_ref, spread_hi_ref, spread_lo_ref, lift_ref, partial_ref = refs
    else:
        base_ref, weight_ref, top_ref, pick_ref, spread_hi_ref, spread_lo_ref, lift_ref, partial_ref = refs
    count = v_ref.shape[0]
    derivative, second, side_signs, weights = mode_tables()
    second = second.astype(np.float32)
    derivative = derivative.astype(np.float32)
    lift_signs = (side_signs * weights[None, :]).astype(np.float32)
    slabs = [v_ref[:, a * PLANE : (a + 1) * PLANE] for a in range(P_SIZE)]
    weight = weight_ref[...]
    diff0 = jnp.broadcast_to(weight[:, 0:1], (count, PLANE))
    vel0 = jnp.broadcast_to(weight[:, 3:4], (count, PLANE))
    first = []
    for k in range(P_SIZE):
        acc_s = None
        acc_d = None
        for n in range(k + 1, P_SIZE):
            if second[k, n] != 0.0:
                term = float(second[k, n]) * slabs[n]
                acc_s = term if acc_s is None else acc_s + term
            if derivative[k, n] != 0.0:
                term = float(derivative[k, n]) * slabs[n]
                acc_d = term if acc_d is None else acc_d + term
        part = jnp.zeros((count, PLANE), jnp.float32)
        if acc_s is not None:
            part = part + diff0 * acc_s
        if acc_d is not None:
            part = part - vel0 * acc_d
        first.append(part)
    stacked = jnp.concatenate(slabs, axis=0)
    hi, lo = split_two(stacked)
    spread_hi = spread_hi_ref[...]
    wide = mxu(hi, spread_hi) + mxu(lo, spread_hi)
    fine = mxu(hi, spread_lo_ref[...])
    weight_rows = jnp.concatenate([weight] * P_SIZE, axis=0)
    inner = (
        weight_rows[:, 2:3] * (wide[:, 0:PLANE] + fine[:, 0:PLANE])
        + weight_rows[:, 1:2] * (wide[:, PLANE : 2 * PLANE] + fine[:, PLANE : 2 * PLANE])
        - weight_rows[:, 5:6] * wide[:, 2 * PLANE : 3 * PLANE]
        - weight_rows[:, 4:5] * wide[:, 3 * PLANE : 4 * PLANE]
    )
    own = jnp.concatenate(
        [wide[a * count : (a + 1) * count, 4 * PLANE : 4 * PLANE + 128] for a in range(P_SIZE)], axis=1
    )
    other = jnp.concatenate(
        [wide[a * count : (a + 1) * count, 4 * PLANE + 128 : 4 * PLANE + 256] for a in range(P_SIZE)], axis=1
    )
    lane = lax.broadcasted_iota(jnp.int32, (1, P_SIZE * 128), 1) % 128
    across = jnp.zeros_like(own)
    for face in range(4):
        gathered = exact_pick(pick_ref[face], other)
        across = jnp.where(lane // P_SIZE == face, gathered, across)
    jump = own - across
    jump_rows = jnp.concatenate([jump[:, a * 128 : (a + 1) * 128] for a in range(P_SIZE)], axis=0)
    jhi, jlo = split_two(jump_rows)
    lift_mat = lift_ref[...]
    lifted = mxu(jhi, lift_mat) + mxu(jlo, lift_mat)
    even, total = end_traces(slabs)
    top = top_ref[...]
    order = weight[:, 7:8]
    for a in range(P_SIZE):
        rows = slice(a * count, (a + 1) * count)
        lanes = slice(a * PLANE, (a + 1) * PLANE)
        own_lift = lifted[rows] + float(lift_signs[0, a]) * even + float(lift_signs[1, a]) * total
        live = top[:, lanes] <= order
        update = jnp.where(live, first[a] + inner[rows] - own_lift, 0.0)
        partial_ref[:, lanes] = base_ref[:, lanes] + scale * update


def outer_body(
    pre_ref, top_ref, weight_ref, lower_ref, upper_ref, pick_ref, turn_ref, flip_ref,
    out_ref, even_ref, total_ref, *, scale
):
    derivative, second, side_signs, weights = mode_tables()
    lift_signs = (side_signs * weights[None, :]).astype(np.float32)
    codes = turn_ref[...]
    flip = flip_ref[...]
    below = turn(exact_pick(pick_ref[4], lower_ref[...]), codes[:, 0:1], flip)
    above = turn(exact_pick(pick_ref[5], upper_ref[...]), codes[:, 1:2], flip)
    top = top_ref[...]
    order = weight_ref[:, 7:8]
    news = []
    for a in range(P_SIZE):
        lanes = slice(a * PLANE, (a + 1) * PLANE)
        update = float(lift_signs[0, a]) * below + float(lift_signs[1, a]) * above
        live = top[:, lanes] <= order
        new = pre_ref[:, lanes] + scale * jnp.where(live, update, 0.0)
        out_ref[:, lanes] = new
        news.append(new)
    even, total = end_traces(news)
    even_ref[...] = even
    total_ref[...] = total


def section(v, base, top, weight, ends, picks, codes, tables, scale):
    count = v.shape[0]
    spread_hi, spread_lo, lift, flip = tables
    spec = pl.BlockSpec(memory_space=pltpu.VMEM)
    shared = base is None
    operands = (v,) + (() if shared else (base,)) + (weight, top, picks, spread_hi, spread_lo, lift)
    pre = pl.pallas_call(
        functools.partial(inner_body, scale=scale, shared=shared),
        out_shape=jax.ShapeDtypeStruct(v.shape, jnp.float32),
        in_specs=[spec] * len(operands),
        out_specs=spec,
        compiler_params=pltpu.CompilerParams(vmem_limit_bytes=60 * 1024 * 1024),
        cost_estimate=pl.CostEstimate(
            flops=2_500_000_000, transcendentals=0, bytes_accessed=4_000_000
        ),
    )(*operands)
    lower, upper = exchange(*ends)
    return pl.pallas_call(
        functools.partial(outer_body, scale=scale),
        out_shape=(
            jax.ShapeDtypeStruct(v.shape, jnp.float32),
            jax.ShapeDtypeStruct((count, PLANE), jnp.float32),
            jax.ShapeDtypeStruct((count, PLANE), jnp.float32),
        ),
        in_specs=[spec] * 8,
        out_specs=(spec, spec, spec),
    )(pre, top, weight, lower, upper, picks, codes, flip)


def prep_body(placed_ref, top_ref, weight_ref, field_ref, even_ref, total_ref):
    news = []
    for a in range(P_SIZE):
        lanes = slice(a * PLANE, (a + 1) * PLANE)
        live = top_ref[:, lanes] <= weight_ref[:, 7:8]
        new = jnp.where(live, placed_ref[:, lanes], 0.0)
        field_ref[:, lanes] = new
        news.append(new)
    even, total = end_traces(news)
    even_ref[...] = even
    total_ref[...] = total


def prep(placed, top, weight):
    count = placed.shape[0]
    spec = pl.BlockSpec(memory_space=pltpu.VMEM)
    return pl.pallas_call(
        prep_body,
        out_shape=(
            jax.ShapeDtypeStruct(placed.shape, jnp.float32),
            jax.ShapeDtypeStruct((count, PLANE), jnp.float32),
            jax.ShapeDtypeStruct((count, PLANE), jnp.float32),
        ),
        in_specs=[spec] * 3,
        out_specs=(spec, spec, spec),
    )(placed, top, weight)


def exchange(even, total):
    size = lax.axis_size("dom")
    up = [(i, (i + 1) % size) for i in range(size)]
    down = [((i + 1) % size, i) for i in range(size)]
    return lax.ppermute(total, "dom", up), lax.ppermute(even, "dom", down)


def shards(
    coefficients, diffusion, velocity, orders, target, local_faces, partner_faces, partner_turns
):
    element_count = coefficients.shape[0]
    blocks_all = lax.axis_size(("dom", "face"))
    moving = element_count // 16
    destination = target // element_count
    new_slot = target % element_count
    here = lax.axis_index(("dom", "face"))
    side_info = jnp.concatenate(
        [
            diffusion,
            velocity,
            new_slot[:, None].astype(jnp.float32),
            orders[:, None].astype(jnp.float32),
        ],
        axis=1,
    )
    side_width = side_info.shape[1]
    shifts = (1, blocks_all - 1, blocks_all // 2)
    goal = (here + jnp.asarray(shifts, jnp.int32)) % blocks_all
    chosen = destination[None, :] == goal[:, None]
    rank = jnp.cumsum(chosen.astype(jnp.int32), axis=1) - 1
    hit = chosen[:, None, :] & (
        rank[:, None, :] == jnp.arange(moving, dtype=jnp.int32)[None, :, None]
    )
    rows = jnp.arange(element_count, dtype=jnp.int32)
    picked = jnp.sum(jnp.where(hit, rows[None, None, :], 0), axis=2).reshape(-1)
    side_rows = side_info[picked].reshape(len(shifts), 1, moving * side_width)
    side_rows = jnp.pad(side_rows, ((0, 0), (0, 0), (0, P_SIZE**3 - moving * side_width)))
    parcels = jnp.concatenate(
        [coefficients[picked].reshape(len(shifts), moving, P_SIZE**3), side_rows], axis=1
    )
    got_coef = [coefficients]
    got_side = [side_info]
    got_slot = [jnp.where(destination == here, new_slot, element_count)]
    for index, shift in enumerate(shifts):
        pairs = [(i, (i + shift) % blocks_all) for i in range(blocks_all)]
        arrived = lax.ppermute(parcels[index], ("dom", "face"), pairs)
        arrived_side = arrived[moving, : moving * side_width].reshape(moving, side_width)
        got_coef.append(arrived[:moving])
        got_side.append(arrived_side)
        got_slot.append(arrived_side[:, 6].astype(jnp.int32))
    got_coef = jnp.concatenate(got_coef, axis=0)
    got_side = jnp.concatenate(got_side, axis=0)
    got_slot = jnp.concatenate(got_slot, axis=0)
    hit = got_slot[None, :] == jnp.arange(element_count, dtype=jnp.int32)[:, None]
    got_rows = jnp.arange(got_slot.shape[0], dtype=jnp.int32)
    source = jnp.sum(jnp.where(hit, got_rows[None, :], 0), axis=1)
    placed_side = got_side[source]
    weight = placed_side
    top = jnp.asarray(top_modes().astype(np.float32))
    tables = kernel_tables()
    neighbours = jnp.concatenate([local_faces[0], partner_faces[0]], axis=0)
    picks = (
        neighbours[:, :, None] == jnp.arange(element_count, dtype=jnp.int32)[None, None, :]
    ).astype(jnp.bfloat16)
    codes = partner_turns[0].T
    field, even, total = prep(got_coef[source], top, weight)
    half, even, total = section(
        field, None, top, weight, (even, total), picks, codes, tables, 0.5 * TIME_STEP
    )
    advanced, _, _ = section(
        half, field, top, weight, (even, total), picks, codes, tables, TIME_STEP
    )
    return advanced


def solution(mesh):
    in_specs = (
        P(("dom", "face"), None),
        P(("dom", "face"), None),
        P(("dom", "face"), None),
        P(("dom", "face")),
        P(("dom", "face")),
        P(("dom", "face"), None, None),
        P(("dom", "face"), None, None),
        P(("dom", "face"), None, None),
    )
    out_specs = P(("dom", "face"), None)
    return jax.shard_map(shards, mesh=mesh, in_specs=in_specs, out_specs=out_specs, check_vma=False)
```

```python
import functools
import jax
import jax.numpy as jnp
import numpy as np
from jax import lax
from jax.experimental import pallas as pl
from jax.experimental.pallas import tpu as pltpu
from jax.sharding import PartitionSpec as P

P_SIZE = 16
PLANE = P_SIZE * P_SIZE
TIME_STEP = 0.25


def mode_tables():
    ladder = np.arange(P_SIZE)
    spacing = ladder[None, :] - ladder[:, None]
    derivative = np.where(
        (spacing > 0) & (spacing % 2 == 1), (2.0 * ladder[:, None] + 1.0) / P_SIZE, 0.0
    )
    second = derivative @ derivative / P_SIZE
    side_signs = np.stack([(-1.0) ** ladder, np.ones(P_SIZE)])
    weights = (2.0 * ladder + 1.0) / (2.0 * P_SIZE)
    return (derivative, second, side_signs, weights)


def side_table(values_pair):
    identity = np.eye(P_SIZE)
    return np.concatenate(
        [
            np.kron(values_pair[0][:, None], identity),
            np.kron(values_pair[1][:, None], identity),
            np.kron(identity, values_pair[0][:, None]),
            np.kron(identity, values_pair[1][:, None]),
        ],
        axis=1,
    )


def kernel_tables():
    derivative, second, side_signs, weights = mode_tables()
    derivative = derivative.astype(np.float32).astype(np.float64)
    second = second.astype(np.float32).astype(np.float64)
    identity = np.eye(P_SIZE)
    traces = side_table(side_signs)
    swapped = traces[:, [16 * g + j for g in (1, 0, 3, 2) for j in range(P_SIZE)]]
    pad = np.zeros((PLANE, 64))
    spread = np.concatenate(
        [
            np.kron(identity, second.T),
            np.kron(second.T, identity),
            np.kron(identity, derivative.T),
            np.kron(derivative.T, identity),
            traces, pad, swapped, pad,
        ],
        axis=1,
    ).astype(np.float32)
    spread_hi = spread.astype(jnp.bfloat16)
    spread_lo = (spread[:, : 2 * PLANE] - spread_hi[:, : 2 * PLANE].astype(np.float32)).astype(jnp.bfloat16)
    lift_signs = side_signs * weights[None, :]
    lift = np.concatenate([side_table(lift_signs).T, np.zeros((64, PLANE))], axis=0)
    lanes = np.arange(PLANE)
    flip = np.zeros((PLANE, PLANE))
    flip[lanes, (lanes % P_SIZE) * P_SIZE + lanes // P_SIZE] = 1.0
    return (
        jnp.asarray(spread_hi),
        jnp.asarray(spread_lo),
        jnp.asarray(lift, jnp.bfloat16),
        jnp.asarray(flip, jnp.bfloat16),
    )


def top_modes():
    ladder = np.arange(P_SIZE)
    first_idx, second_idx, third_idx = np.meshgrid(ladder, ladder, ladder, indexing="ij")
    return np.maximum(np.maximum(first_idx, second_idx), third_idx).reshape(1, -1).astype(np.int32)


def split_two(x):
    hi = x.astype(jnp.bfloat16)
    lo = (x - hi.astype(jnp.float32)).astype(jnp.bfloat16)
    return hi, lo


def mxu(a, b):
    return jnp.dot(a, b, preferred_element_type=jnp.float32)


def exact_pick(onehot, x):
    hi = x.astype(jnp.bfloat16)
    rest = x - hi.astype(jnp.float32)
    mid = rest.astype(jnp.bfloat16)
    lo = (rest - mid.astype(jnp.float32)).astype(jnp.bfloat16)
    return mxu(onehot, hi) + mxu(onehot, mid) + mxu(onehot, lo)


def end_traces(slabs):
    total = slabs[0] + slabs[1]
    even = slabs[0] - slabs[1]
    for a in range(2, P_SIZE):
        total = total + slabs[a]
        even = even + slabs[a] if a % 2 == 0 else even - slabs[a]
    return even, total


def turn(rows, codes, flip):
    lane = lax.broadcasted_iota(jnp.int32, (1, PLANE), 1)
    swapped = exact_pick_right(rows, flip)
    rows = jnp.where(codes % 2 == 1, swapped, rows)
    row_odd = (lane // P_SIZE) % 2 == 1
    col_odd = lane % 2 == 1
    negate = ((codes // 2) % 2 == 1) & row_odd
    negate = negate != (((codes // 4) % 2 == 1) & col_odd)
    return jnp.where(negate, -rows, rows)


def exact_pick_right(x, onehot):
    hi = x.astype(jnp.bfloat16)
    rest = x - hi.astype(jnp.float32)
    mid = rest.astype(jnp.bfloat16)
    lo = (rest - mid.astype(jnp.float32)).astype(jnp.bfloat16)
    return mxu(hi, onehot) + mxu(mid, onehot) + mxu(lo, onehot)


def face_lift(below, above, live, a, scale):
    derivative, second, side_signs, weights = mode_tables()
    lift_signs = (side_signs * weights[None, :]).astype(np.float32)
    update = float(lift_signs[0, a]) * below + float(lift_signs[1, a]) * above
    return scale * jnp.where(live, update, 0.0)


def inner_body(*refs, scale, carried):
    if carried is None:
        v_ref, weight_ref, top_ref, pick_ref, spread_hi_ref, spread_lo_ref, lift_ref = refs[:7]
        base_ref = v_ref
    else:
        v_ref, below_ref, above_ref, base_ref, weight_ref, top_ref, pick_ref = refs[:7]
        spread_hi_ref, spread_lo_ref, lift_ref = refs[7:10]
    partial_ref, even_ref, total_ref = refs[-3:]
    count = v_ref.shape[0]
    derivative, second, side_signs, weights = mode_tables()
    second = second.astype(np.float32)
    derivative = derivative.astype(np.float32)
    lift_signs = (side_signs * weights[None, :]).astype(np.float32)
    weight = weight_ref[...]
    top = top_ref[...]
    order = weight[:, 7:8]
    slabs = [v_ref[:, a * PLANE : (a + 1) * PLANE] for a in range(P_SIZE)]
    if carried is not None:
        below = below_ref[...]
        above = above_ref[...]
        slabs = [
            slabs[a] + face_lift(below, above, top[:, a * PLANE : (a + 1) * PLANE] <= order, a, carried)
            for a in range(P_SIZE)
        ]
    diff0 = jnp.broadcast_to(weight[:, 0:1], (count, PLANE))
    vel0 = jnp.broadcast_to(weight[:, 3:4], (count, PLANE))
    first = []
    for k in range(P_SIZE):
        acc_s = None
        acc_d = None
        for n in range(k + 1, P_SIZE):
            if second[k, n] != 0.0:
                term = float(second[k, n]) * slabs[n]
                acc_s = term if acc_s is None else acc_s + term
            if derivative[k, n] != 0.0:
                term = float(derivative[k, n]) * slabs[n]
                acc_d = term if acc_d is None else acc_d + term
        part = jnp.zeros((count, PLANE), jnp.float32)
        if acc_s is not None:
            part = part + diff0 * acc_s
        if acc_d is not None:
            part = part - vel0 * acc_d
        first.append(part)
    stacked = jnp.concatenate(slabs, axis=0)
    hi, lo = split_two(stacked)
    spread_hi = spread_hi_ref[...]
    wide = mxu(hi, spread_hi) + mxu(lo, spread_hi)
    fine = mxu(hi, spread_lo_ref[...])
    weight_rows = jnp.concatenate([weight] * P_SIZE, axis=0)
    inner = (
        weight_rows[:, 2:3] * (wide[:, 0:PLANE] + fine[:, 0:PLANE])
        + weight_rows[:, 1:2] * (wide[:, PLANE : 2 * PLANE] + fine[:, PLANE : 2 * PLANE])
        - weight_rows[:, 5:6] * wide[:, 2 * PLANE : 3 * PLANE]
        - weight_rows[:, 4:5] * wide[:, 3 * PLANE : 4 * PLANE]
    )
    own = jnp.concatenate(
        [wide[a * count : (a + 1) * count, 4 * PLANE : 4 * PLANE + 128] for a in range(P_SIZE)], axis=1
    )
    other = jnp.concatenate(
        [wide[a * count : (a + 1) * count, 4 * PLANE + 128 : 4 * PLANE + 256] for a in range(P_SIZE)], axis=1
    )
    lane = lax.broadcasted_iota(jnp.int32, (1, P_SIZE * 128), 1) % 128
    across = jnp.zeros_like(own)
    for face in range(4):
        gathered = exact_pick(pick_ref[face], other)
        across = jnp.where(lane // P_SIZE == face, gathered, across)
    jump = own - across
    jump_rows = jnp.concatenate([jump[:, a * 128 : (a + 1) * 128] for a in range(P_SIZE)], axis=0)
    jhi, jlo = split_two(jump_rows)
    lift_mat = lift_ref[...]
    lifted = mxu(jhi, lift_mat) + mxu(jlo, lift_mat)
    even, total = end_traces(slabs)
    news = []
    for a in range(P_SIZE):
        rows = slice(a * count, (a + 1) * count)
        lanes = slice(a * PLANE, (a + 1) * PLANE)
        own_lift = lifted[rows] + float(lift_signs[0, a]) * even + float(lift_signs[1, a]) * total
        live = top[:, lanes] <= order
        update = jnp.where(live, first[a] + inner[rows] - own_lift, 0.0)
        new = base_ref[:, lanes] + scale * update
        partial_ref[:, lanes] = new
        news.append(new)
    even, total = end_traces(news)
    even_ref[...] = even
    total_ref[...] = total


def faces_body(
    lower_ref, upper_ref, pick_ref, turn_ref, flip_ref, top_ref, weight_ref, even_ref, total_ref,
    below_ref, above_ref, new_even_ref, new_total_ref, *, scale
):
    codes = turn_ref[...]
    flip = flip_ref[...]
    below = turn(exact_pick(pick_ref[4], lower_ref[...]), codes[:, 0:1], flip)
    above = turn(exact_pick(pick_ref[5], upper_ref[...]), codes[:, 1:2], flip)
    below_ref[...] = below
    above_ref[...] = above
    top = top_ref[...]
    order = weight_ref[:, 7:8]
    parts = [
        face_lift(below, above, top[:, a * PLANE : (a + 1) * PLANE] <= order, a, scale)
        for a in range(P_SIZE)
    ]
    even, total = end_traces(parts)
    new_even_ref[...] = even_ref[...] + even
    new_total_ref[...] = total_ref[...] + total


def outer_body(
    pre_ref, top_ref, weight_ref, lower_ref, upper_ref, pick_ref, turn_ref, flip_ref,
    out_ref, even_ref, total_ref, *, scale
):
    derivative, second, side_signs, weights = mode_tables()
    lift_signs = (side_signs * weights[None, :]).astype(np.float32)
    codes = turn_ref[...]
    flip = flip_ref[...]
    below = turn(exact_pick(pick_ref[4], lower_ref[...]), codes[:, 0:1], flip)
    above = turn(exact_pick(pick_ref[5], upper_ref[...]), codes[:, 1:2], flip)
    top = top_ref[...]
    order = weight_ref[:, 7:8]
    news = []
    for a in range(P_SIZE):
        lanes = slice(a * PLANE, (a + 1) * PLANE)
        update = float(lift_signs[0, a]) * below + float(lift_signs[1, a]) * above
        live = top[:, lanes] <= order
        new = pre_ref[:, lanes] + scale * jnp.where(live, update, 0.0)
        out_ref[:, lanes] = new
        news.append(new)
    even, total = end_traces(news)
    even_ref[...] = even
    total_ref[...] = total


def inner(operands, scale, carried):
    count = operands[0].shape[0]
    spec = pl.BlockSpec(memory_space=pltpu.VMEM)
    return pl.pallas_call(
        functools.partial(inner_body, scale=scale, carried=carried),
        out_shape=(
            jax.ShapeDtypeStruct(operands[0].shape, jnp.float32),
            jax.ShapeDtypeStruct((count, PLANE), jnp.float32),
            jax.ShapeDtypeStruct((count, PLANE), jnp.float32),
        ),
        in_specs=[spec] * len(operands),
        out_specs=(spec, spec, spec),
        compiler_params=pltpu.CompilerParams(vmem_limit_bytes=60 * 1024 * 1024),
        cost_estimate=pl.CostEstimate(
            flops=2_500_000_000, transcendentals=0, bytes_accessed=4_000_000
        ),
    )(*operands)


def faces(lower, upper, picks, codes, flip, top, weight, even, total, scale):
    count = lower.shape[0]
    spec = pl.BlockSpec(memory_space=pltpu.VMEM)
    square = jax.ShapeDtypeStruct((count, PLANE), jnp.float32)
    return pl.pallas_call(
        functools.partial(faces_body, scale=scale),
        out_shape=(square,) * 4,
        in_specs=[spec] * 9,
        out_specs=(spec,) * 4,
    )(lower, upper, picks, codes, flip, top, weight, even, total)


def outer(pre, top, weight, lower, upper, picks, codes, flip, scale):
    count = pre.shape[0]
    spec = pl.BlockSpec(memory_space=pltpu.VMEM)
    return pl.pallas_call(
        functools.partial(outer_body, scale=scale),
        out_shape=(
            jax.ShapeDtypeStruct(pre.shape, jnp.float32),
            jax.ShapeDtypeStruct((count, PLANE), jnp.float32),
            jax.ShapeDtypeStruct((count, PLANE), jnp.float32),
        ),
        in_specs=[spec] * 8,
        out_specs=(spec, spec, spec),
    )(pre, top, weight, lower, upper, picks, codes, flip)


def prep_body(placed_ref, top_ref, weight_ref, field_ref, even_ref, total_ref):
    news = []
    for a in range(P_SIZE):
        lanes = slice(a * PLANE, (a + 1) * PLANE)
        live = top_ref[:, lanes] <= weight_ref[:, 7:8]
        new = jnp.where(live, placed_ref[:, lanes], 0.0)
        field_ref[:, lanes] = new
        news.append(new)
    even, total = end_traces(news)
    even_ref[...] = even
    total_ref[...] = total


def prep(placed, top, weight):
    count = placed.shape[0]
    spec = pl.BlockSpec(memory_space=pltpu.VMEM)
    return pl.pallas_call(
        prep_body,
        out_shape=(
            jax.ShapeDtypeStruct(placed.shape, jnp.float32),
            jax.ShapeDtypeStruct((count, PLANE), jnp.float32),
            jax.ShapeDtypeStruct((count, PLANE), jnp.float32),
        ),
        in_specs=[spec] * 3,
        out_specs=(spec, spec, spec),
    )(placed, top, weight)


def exchange(even, total):
    size = lax.axis_size("dom")
    up = [(i, (i + 1) % size) for i in range(size)]
    down = [((i + 1) % size, i) for i in range(size)]
    return lax.ppermute(total, "dom", up), lax.ppermute(even, "dom", down)


def shards(
    coefficients, diffusion, velocity, orders, target, local_faces, partner_faces, partner_turns
):
    element_count = coefficients.shape[0]
    blocks_all = lax.axis_size(("dom", "face"))
    moving = element_count // 16
    destination = target // element_count
    new_slot = target % element_count
    here = lax.axis_index(("dom", "face"))
    side_info = jnp.concatenate(
        [
            diffusion,
            velocity,
            new_slot[:, None].astype(jnp.float32),
            orders[:, None].astype(jnp.float32),
        ],
        axis=1,
    )
    side_width = side_info.shape[1]
    shifts = (1, blocks_all - 1, blocks_all // 2)
    goal = (here + jnp.asarray(shifts, jnp.int32)) % blocks_all
    chosen = destination[None, :] == goal[:, None]
    rank = jnp.cumsum(chosen.astype(jnp.int32), axis=1) - 1
    hit = chosen[:, None, :] & (
        rank[:, None, :] == jnp.arange(moving, dtype=jnp.int32)[None, :, None]
    )
    rows = jnp.arange(element_count, dtype=jnp.int32)
    picked = jnp.sum(jnp.where(hit, rows[None, None, :], 0), axis=2).reshape(-1)
    side_rows = side_info[picked].reshape(len(shifts), 1, moving * side_width)
    side_rows = jnp.pad(side_rows, ((0, 0), (0, 0), (0, P_SIZE**3 - moving * side_width)))
    parcels = jnp.concatenate(
        [coefficients[picked].reshape(len(shifts), moving, P_SIZE**3), side_rows], axis=1
    )
    got_coef = [coefficients]
    got_side = [side_info]
    got_slot = [jnp.where(destination == here, new_slot, element_count)]
    for index, shift in enumerate(shifts):
        pairs = [(i, (i + shift) % blocks_all) for i in range(blocks_all)]
        arrived = lax.ppermute(parcels[index], ("dom", "face"), pairs)
        arrived_side = arrived[moving, : moving * side_width].reshape(moving, side_width)
        got_coef.append(arrived[:moving])
        got_side.append(arrived_side)
        got_slot.append(arrived_side[:, 6].astype(jnp.int32))
    got_coef = jnp.concatenate(got_coef, axis=0)
    got_side = jnp.concatenate(got_side, axis=0)
    got_slot = jnp.concatenate(got_slot, axis=0)
    hit = got_slot[None, :] == jnp.arange(element_count, dtype=jnp.int32)[:, None]
    got_rows = jnp.arange(got_slot.shape[0], dtype=jnp.int32)
    source = jnp.sum(jnp.where(hit, got_rows[None, :], 0), axis=1)
    placed_side = got_side[source]
    weight = placed_side
    top = jnp.asarray(top_modes().astype(np.float32))
    tables = kernel_tables()
    neighbours = jnp.concatenate([local_faces[0], partner_faces[0]], axis=0)
    picks = (
        neighbours[:, :, None] == jnp.arange(element_count, dtype=jnp.int32)[None, None, :]
    ).astype(jnp.bfloat16)
    codes = partner_turns[0].T
    spread_hi, spread_lo, lift, flip = tables
    field, even, total = prep(got_coef[source], top, weight)
    first_step = 0.5 * TIME_STEP
    lower, upper = exchange(even, total)
    pre, even, total = inner(
        (field, weight, top, picks, spread_hi, spread_lo, lift), first_step, None
    )
    below, above, even, total = faces(
        lower, upper, picks, codes, flip, top, weight, even, total, first_step
    )
    lower, upper = exchange(even, total)
    pre, _, _ = inner(
        (pre, below, above, field, weight, top, picks, spread_hi, spread_lo, lift),
        TIME_STEP,
        first_step,
    )
    advanced, _, _ = outer(pre, top, weight, lower, upper, picks, codes, flip, TIME_STEP)
    return advanced


def solution(mesh):
    in_specs = (
        P(("dom", "face"), None),
        P(("dom", "face"), None),
        P(("dom", "face"), None),
        P(("dom", "face")),
        P(("dom", "face")),
        P(("dom", "face"), None, None),
        P(("dom", "face"), None, None),
        P(("dom", "face"), None, None),
    )
    out_specs = P(("dom", "face"), None)
    return jax.shard_map(shards, mesh=mesh, in_specs=in_specs, out_specs=out_specs, check_vma=False)
```

```python
import functools
import jax
import jax.numpy as jnp
import numpy as np
from jax import lax
from jax.experimental import pallas as pl
from jax.experimental.pallas import tpu as pltpu
from jax.sharding import PartitionSpec as P

P_SIZE = 16
PLANE = P_SIZE * P_SIZE
TIME_STEP = 0.25


def mode_tables():
    ladder = np.arange(P_SIZE)
    spacing = ladder[None, :] - ladder[:, None]
    derivative = np.where(
        (spacing > 0) & (spacing % 2 == 1), (2.0 * ladder[:, None] + 1.0) / P_SIZE, 0.0
    )
    second = derivative @ derivative / P_SIZE
    side_signs = np.stack([(-1.0) ** ladder, np.ones(P_SIZE)])
    weights = (2.0 * ladder + 1.0) / (2.0 * P_SIZE)
    return (derivative, second, side_signs, weights)


def side_table(values_pair):
    identity = np.eye(P_SIZE)
    return np.concatenate(
        [
            np.kron(values_pair[0][:, None], identity),
            np.kron(values_pair[1][:, None], identity),
            np.kron(identity, values_pair[0][:, None]),
            np.kron(identity, values_pair[1][:, None]),
        ],
        axis=1,
    )


def kernel_tables():
    derivative, second, side_signs, weights = mode_tables()
    derivative = derivative.astype(np.float32).astype(np.float64)
    second = second.astype(np.float32).astype(np.float64)
    identity = np.eye(P_SIZE)
    traces = side_table(side_signs)
    swapped = traces[:, [16 * g + j for g in (1, 0, 3, 2) for j in range(P_SIZE)]]
    pad = np.zeros((PLANE, 64))
    spread = np.concatenate(
        [
            np.kron(identity, second.T),
            np.kron(second.T, identity),
            np.kron(identity, derivative.T),
            np.kron(derivative.T, identity),
            traces, pad, swapped, pad,
        ],
        axis=1,
    ).astype(np.float32)
    spread_hi = spread.astype(jnp.bfloat16)
    spread_lo = (spread[:, : 2 * PLANE] - spread_hi[:, : 2 * PLANE].astype(np.float32)).astype(jnp.bfloat16)
    lift_signs = side_signs * weights[None, :]
    lift = np.concatenate([side_table(lift_signs).T, np.zeros((64, PLANE))], axis=0)
    lanes = np.arange(PLANE)
    flip = np.zeros((PLANE, PLANE))
    flip[lanes, (lanes % P_SIZE) * P_SIZE + lanes // P_SIZE] = 1.0
    return (
        jnp.asarray(spread_hi),
        jnp.asarray(spread_lo),
        jnp.asarray(lift, jnp.bfloat16),
        jnp.asarray(flip, jnp.bfloat16),
    )


def top_modes():
    ladder = np.arange(P_SIZE)
    first_idx, second_idx, third_idx = np.meshgrid(ladder, ladder, ladder, indexing="ij")
    return np.maximum(np.maximum(first_idx, second_idx), third_idx).reshape(1, -1).astype(np.int32)


def split_two(x):
    hi = x.astype(jnp.bfloat16)
    lo = (x - hi.astype(jnp.float32)).astype(jnp.bfloat16)
    return hi, lo


def mxu(a, b):
    return jnp.dot(a, b, preferred_element_type=jnp.float32)


def split_three(x):
    hi = x.astype(jnp.bfloat16)
    rest = x - hi.astype(jnp.float32)
    mid = rest.astype(jnp.bfloat16)
    lo = (rest - mid.astype(jnp.float32)).astype(jnp.bfloat16)
    return hi, mid, lo


def exact_pick(onehot, x):
    width = x.shape[1]
    joined = mxu(onehot, jnp.concatenate(split_three(x), axis=1))
    return joined[:, :width] + joined[:, width : 2 * width] + joined[:, 2 * width :]


def exact_rows(x, onehot):
    count = x.shape[0]
    joined = mxu(jnp.concatenate(split_three(x), axis=0), onehot)
    return joined[:count] + joined[count : 2 * count] + joined[2 * count :]


def end_traces(slabs):
    total = slabs[0] + slabs[1]
    even = slabs[0] - slabs[1]
    for a in range(2, P_SIZE):
        total = total + slabs[a]
        even = even + slabs[a] if a % 2 == 0 else even - slabs[a]
    return even, total


def turn_pair(lower, upper, picks, codes, flip):
    count = lower.shape[0]
    picked = jnp.concatenate([exact_pick(picks[4], lower), exact_pick(picks[5], upper)], axis=0)
    swapped = exact_rows(picked, flip)
    lane = lax.broadcasted_iota(jnp.int32, (1, PLANE), 1)
    row_odd = (lane // P_SIZE) % 2 == 1
    col_odd = lane % 2 == 1
    sides = []
    for side in range(2):
        rows = slice(side * count, (side + 1) * count)
        code = codes[:, side : side + 1]
        chosen = jnp.where(code % 2 == 1, swapped[rows], picked[rows])
        negate = ((code // 2) % 2 == 1) & row_odd
        negate = negate != (((code // 4) % 2 == 1) & col_odd)
        sides.append(jnp.where(negate, -chosen, chosen))
    return sides


def face_lift(below, above, live, a, scale):
    derivative, second, side_signs, weights = mode_tables()
    lift_signs = (side_signs * weights[None, :]).astype(np.float32)
    update = float(lift_signs[0, a]) * below + float(lift_signs[1, a]) * above
    return scale * jnp.where(live, update, 0.0)


def inner_body(*refs, scale, carried):
    if carried is None:
        v_ref, weight_ref, top_ref, pick_ref, spread_hi_ref, spread_lo_ref, lift_ref = refs[:7]
        base_ref = v_ref
    else:
        v_ref, below_ref, above_ref, base_ref, weight_ref, top_ref, pick_ref = refs[:7]
        spread_hi_ref, spread_lo_ref, lift_ref = refs[7:10]
    partial_ref, even_ref, total_ref = refs[-3:]
    count = v_ref.shape[0]
    derivative, second, side_signs, weights = mode_tables()
    second = second.astype(np.float32)
    derivative = derivative.astype(np.float32)
    lift_signs = (side_signs * weights[None, :]).astype(np.float32)
    weight = weight_ref[...]
    top = top_ref[...]
    order = weight[:, 7:8]
    slabs = [v_ref[:, a * PLANE : (a + 1) * PLANE] for a in range(P_SIZE)]
    if carried is not None:
        below = below_ref[...]
        above = above_ref[...]
        slabs = [
            slabs[a] + face_lift(below, above, top[:, a * PLANE : (a + 1) * PLANE] <= order, a, carried)
            for a in range(P_SIZE)
        ]
    diff0 = jnp.broadcast_to(weight[:, 0:1], (count, PLANE))
    vel0 = jnp.broadcast_to(weight[:, 3:4], (count, PLANE))
    first = []
    for k in range(P_SIZE):
        acc_s = None
        acc_d = None
        for n in range(k + 1, P_SIZE):
            if second[k, n] != 0.0:
                term = float(second[k, n]) * slabs[n]
                acc_s = term if acc_s is None else acc_s + term
            if derivative[k, n] != 0.0:
                term = float(derivative[k, n]) * slabs[n]
                acc_d = term if acc_d is None else acc_d + term
        part = jnp.zeros((count, PLANE), jnp.float32)
        if acc_s is not None:
            part = part + diff0 * acc_s
        if acc_d is not None:
            part = part - vel0 * acc_d
        first.append(part)
    stacked = jnp.concatenate(slabs, axis=0)
    hi, lo = split_two(stacked)
    spread_hi = spread_hi_ref[...]
    wide = mxu(hi, spread_hi) + mxu(lo, spread_hi)
    fine = mxu(hi, spread_lo_ref[...])
    weight_rows = jnp.concatenate([weight] * P_SIZE, axis=0)
    inner = (
        weight_rows[:, 2:3] * (wide[:, 0:PLANE] + fine[:, 0:PLANE])
        + weight_rows[:, 1:2] * (wide[:, PLANE : 2 * PLANE] + fine[:, PLANE : 2 * PLANE])
        - weight_rows[:, 5:6] * wide[:, 2 * PLANE : 3 * PLANE]
        - weight_rows[:, 4:5] * wide[:, 3 * PLANE : 4 * PLANE]
    )
    own = jnp.concatenate(
        [wide[a * count : (a + 1) * count, 4 * PLANE : 4 * PLANE + 128] for a in range(P_SIZE)], axis=1
    )
    other = jnp.concatenate(
        [wide[a * count : (a + 1) * count, 4 * PLANE + 128 : 4 * PLANE + 256] for a in range(P_SIZE)], axis=1
    )
    lane = lax.broadcasted_iota(jnp.int32, (1, P_SIZE * 128), 1) % 128
    across = jnp.zeros_like(own)
    for face in range(4):
        gathered = exact_pick(pick_ref[face], other)
        across = jnp.where(lane // P_SIZE == face, gathered, across)
    jump = own - across
    jump_rows = jnp.concatenate([jump[:, a * 128 : (a + 1) * 128] for a in range(P_SIZE)], axis=0)
    jhi, jlo = split_two(jump_rows)
    lift_mat = lift_ref[...]
    lifted = mxu(jhi, lift_mat) + mxu(jlo, lift_mat)
    even, total = end_traces(slabs)
    news = []
    for a in range(P_SIZE):
        rows = slice(a * count, (a + 1) * count)
        lanes = slice(a * PLANE, (a + 1) * PLANE)
        own_lift = lifted[rows] + float(lift_signs[0, a]) * even + float(lift_signs[1, a]) * total
        live = top[:, lanes] <= order
        update = jnp.where(live, first[a] + inner[rows] - own_lift, 0.0)
        new = base_ref[:, lanes] + scale * update
        partial_ref[:, lanes] = new
        news.append(new)
    even, total = end_traces(news)
    even_ref[...] = even
    total_ref[...] = total


def faces_body(
    lower_ref, upper_ref, pick_ref, turn_ref, flip_ref, top_ref, weight_ref, even_ref, total_ref,
    below_ref, above_ref, new_even_ref, new_total_ref, *, scale
):
    below, above = turn_pair(lower_ref[...], upper_ref[...], pick_ref, turn_ref[...], flip_ref[...])
    below_ref[...] = below
    above_ref[...] = above
    top = top_ref[...]
    order = weight_ref[:, 7:8]
    parts = [
        face_lift(below, above, top[:, a * PLANE : (a + 1) * PLANE] <= order, a, scale)
        for a in range(P_SIZE)
    ]
    even, total = end_traces(parts)
    new_even_ref[...] = even_ref[...] + even
    new_total_ref[...] = total_ref[...] + total


def outer_body(
    pre_ref, top_ref, weight_ref, lower_ref, upper_ref, pick_ref, turn_ref, flip_ref,
    out_ref, even_ref, total_ref, *, scale
):
    derivative, second, side_signs, weights = mode_tables()
    lift_signs = (side_signs * weights[None, :]).astype(np.float32)
    below, above = turn_pair(lower_ref[...], upper_ref[...], pick_ref, turn_ref[...], flip_ref[...])
    top = top_ref[...]
    order = weight_ref[:, 7:8]
    news = []
    for a in range(P_SIZE):
        lanes = slice(a * PLANE, (a + 1) * PLANE)
        update = float(lift_signs[0, a]) * below + float(lift_signs[1, a]) * above
        live = top[:, lanes] <= order
        new = pre_ref[:, lanes] + scale * jnp.where(live, update, 0.0)
        out_ref[:, lanes] = new
        news.append(new)
    even, total = end_traces(news)
    even_ref[...] = even
    total_ref[...] = total


def inner(operands, scale, carried):
    count = operands[0].shape[0]
    spec = pl.BlockSpec(memory_space=pltpu.VMEM)
    return pl.pallas_call(
        functools.partial(inner_body, scale=scale, carried=carried),
        out_shape=(
            jax.ShapeDtypeStruct(operands[0].shape, jnp.float32),
            jax.ShapeDtypeStruct((count, PLANE), jnp.float32),
            jax.ShapeDtypeStruct((count, PLANE), jnp.float32),
        ),
        in_specs=[spec] * len(operands),
        out_specs=(spec, spec, spec),
        compiler_params=pltpu.CompilerParams(vmem_limit_bytes=60 * 1024 * 1024),
        cost_estimate=pl.CostEstimate(
            flops=2_500_000_000, transcendentals=0, bytes_accessed=4_000_000
        ),
    )(*operands)


def faces(lower, upper, picks, codes, flip, top, weight, even, total, scale):
    count = lower.shape[0]
    spec = pl.BlockSpec(memory_space=pltpu.VMEM)
    square = jax.ShapeDtypeStruct((count, PLANE), jnp.float32)
    return pl.pallas_call(
        functools.partial(faces_body, scale=scale),
        out_shape=(square,) * 4,
        in_specs=[spec] * 9,
        out_specs=(spec,) * 4,
    )(lower, upper, picks, codes, flip, top, weight, even, total)


def outer(pre, top, weight, lower, upper, picks, codes, flip, scale):
    count = pre.shape[0]
    spec = pl.BlockSpec(memory_space=pltpu.VMEM)
    return pl.pallas_call(
        functools.partial(outer_body, scale=scale),
        out_shape=(
            jax.ShapeDtypeStruct(pre.shape, jnp.float32),
            jax.ShapeDtypeStruct((count, PLANE), jnp.float32),
            jax.ShapeDtypeStruct((count, PLANE), jnp.float32),
        ),
        in_specs=[spec] * 8,
        out_specs=(spec, spec, spec),
    )(pre, top, weight, lower, upper, picks, codes, flip)


def prep_body(placed_ref, top_ref, weight_ref, field_ref, even_ref, total_ref):
    news = []
    for a in range(P_SIZE):
        lanes = slice(a * PLANE, (a + 1) * PLANE)
        live = top_ref[:, lanes] <= weight_ref[:, 7:8]
        new = jnp.where(live, placed_ref[:, lanes], 0.0)
        field_ref[:, lanes] = new
        news.append(new)
    even, total = end_traces(news)
    even_ref[...] = even
    total_ref[...] = total


def prep(placed, top, weight):
    count = placed.shape[0]
    spec = pl.BlockSpec(memory_space=pltpu.VMEM)
    return pl.pallas_call(
        prep_body,
        out_shape=(
            jax.ShapeDtypeStruct(placed.shape, jnp.float32),
            jax.ShapeDtypeStruct((count, PLANE), jnp.float32),
            jax.ShapeDtypeStruct((count, PLANE), jnp.float32),
        ),
        in_specs=[spec] * 3,
        out_specs=(spec, spec, spec),
    )(placed, top, weight)


def exchange(even, total):
    size = lax.axis_size("dom")
    up = [(i, (i + 1) % size) for i in range(size)]
    down = [((i + 1) % size, i) for i in range(size)]
    return lax.ppermute(total, "dom", up), lax.ppermute(even, "dom", down)


def shards(
    coefficients, diffusion, velocity, orders, target, local_faces, partner_faces, partner_turns
):
    element_count = coefficients.shape[0]
    blocks_all = lax.axis_size(("dom", "face"))
    moving = element_count // 16
    destination = target // element_count
    new_slot = target % element_count
    here = lax.axis_index(("dom", "face"))
    side_info = jnp.concatenate(
        [
            diffusion,
            velocity,
            new_slot[:, None].astype(jnp.float32),
            orders[:, None].astype(jnp.float32),
        ],
        axis=1,
    )
    side_width = side_info.shape[1]
    shifts = (1, blocks_all - 1, blocks_all // 2)
    goal = (here + jnp.asarray(shifts, jnp.int32)) % blocks_all
    chosen = destination[None, :] == goal[:, None]
    rank = jnp.cumsum(chosen.astype(jnp.int32), axis=1) - 1
    hit = chosen[:, None, :] & (
        rank[:, None, :] == jnp.arange(moving, dtype=jnp.int32)[None, :, None]
    )
    rows = jnp.arange(element_count, dtype=jnp.int32)
    picked = jnp.sum(jnp.where(hit, rows[None, None, :], 0), axis=2).reshape(-1)
    side_rows = side_info[picked].reshape(len(shifts), 1, moving * side_width)
    side_rows = jnp.pad(side_rows, ((0, 0), (0, 0), (0, P_SIZE**3 - moving * side_width)))
    parcels = jnp.concatenate(
        [coefficients[picked].reshape(len(shifts), moving, P_SIZE**3), side_rows], axis=1
    )
    got_coef = [coefficients]
    got_side = [side_info]
    got_slot = [jnp.where(destination == here, new_slot, element_count)]
    for index, shift in enumerate(shifts):
        pairs = [(i, (i + shift) % blocks_all) for i in range(blocks_all)]
        arrived = lax.ppermute(parcels[index], ("dom", "face"), pairs)
        arrived_side = arrived[moving, : moving * side_width].reshape(moving, side_width)
        got_coef.append(arrived[:moving])
        got_side.append(arrived_side)
        got_slot.append(arrived_side[:, 6].astype(jnp.int32))
    got_coef = jnp.concatenate(got_coef, axis=0)
    got_side = jnp.concatenate(got_side, axis=0)
    got_slot = jnp.concatenate(got_slot, axis=0)
    hit = got_slot[None, :] == jnp.arange(element_count, dtype=jnp.int32)[:, None]
    got_rows = jnp.arange(got_slot.shape[0], dtype=jnp.int32)
    source = jnp.sum(jnp.where(hit, got_rows[None, :], 0), axis=1)
    placed_side = got_side[source]
    weight = placed_side
    top = jnp.asarray(top_modes().astype(np.float32))
    tables = kernel_tables()
    neighbours = jnp.concatenate([local_faces[0], partner_faces[0]], axis=0)
    picks = (
        neighbours[:, :, None] == jnp.arange(element_count, dtype=jnp.int32)[None, None, :]
    ).astype(jnp.bfloat16)
    codes = partner_turns[0].T
    spread_hi, spread_lo, lift, flip = tables
    field, even, total = prep(got_coef[source], top, weight)
    first_step = 0.5 * TIME_STEP
    lower, upper = exchange(even, total)
    pre, even, total = inner(
        (field, weight, top, picks, spread_hi, spread_lo, lift), first_step, None
    )
    below, above, even, total = faces(
        lower, upper, picks, codes, flip, top, weight, even, total, first_step
    )
    lower, upper = exchange(even, total)
    pre, _, _ = inner(
        (pre, below, above, field, weight, top, picks, spread_hi, spread_lo, lift),
        TIME_STEP,
        first_step,
    )
    advanced, _, _ = outer(pre, top, weight, lower, upper, picks, codes, flip, TIME_STEP)
    return advanced


def solution(mesh):
    in_specs = (
        P(("dom", "face"), None),
        P(("dom", "face"), None),
        P(("dom", "face"), None),
        P(("dom", "face")),
        P(("dom", "face")),
        P(("dom", "face"), None, None),
        P(("dom", "face"), None, None),
        P(("dom", "face"), None, None),
    )
    out_specs = P(("dom", "face"), None)
    return jax.shard_map(shards, mesh=mesh, in_specs=in_specs, out_specs=out_specs, check_vma=False)
```

```python
import functools
import jax
import jax.numpy as jnp
import numpy as np
from jax import lax
from jax.experimental import pallas as pl
from jax.experimental.pallas import tpu as pltpu
from jax.sharding import PartitionSpec as P

P_SIZE = 16
PLANE = P_SIZE * P_SIZE
TIME_STEP = 0.25


def mode_tables():
    ladder = np.arange(P_SIZE)
    spacing = ladder[None, :] - ladder[:, None]
    derivative = np.where(
        (spacing > 0) & (spacing % 2 == 1), (2.0 * ladder[:, None] + 1.0) / P_SIZE, 0.0
    )
    second = derivative @ derivative / P_SIZE
    side_signs = np.stack([(-1.0) ** ladder, np.ones(P_SIZE)])
    weights = (2.0 * ladder + 1.0) / (2.0 * P_SIZE)
    return (derivative, second, side_signs, weights)


def side_table(values_pair):
    identity = np.eye(P_SIZE)
    return np.concatenate(
        [
            np.kron(values_pair[0][:, None], identity),
            np.kron(values_pair[1][:, None], identity),
            np.kron(identity, values_pair[0][:, None]),
            np.kron(identity, values_pair[1][:, None]),
        ],
        axis=1,
    )


def kernel_tables():
    derivative, second, side_signs, weights = mode_tables()
    derivative = derivative.astype(np.float32).astype(np.float64)
    second = second.astype(np.float32).astype(np.float64)
    identity = np.eye(P_SIZE)
    traces = side_table(side_signs)
    swapped = traces[:, [16 * g + j for g in (1, 0, 3, 2) for j in range(P_SIZE)]]
    pad = np.zeros((PLANE, 64))
    spread = np.concatenate(
        [
            np.kron(identity, second.T),
            np.kron(second.T, identity),
            np.kron(identity, derivative.T),
            np.kron(derivative.T, identity),
            traces, pad, swapped, pad,
        ],
        axis=1,
    ).astype(np.float32)
    spread_hi = spread.astype(jnp.bfloat16)
    spread_lo = (spread[:, : 2 * PLANE] - spread_hi[:, : 2 * PLANE].astype(np.float32)).astype(jnp.bfloat16)
    lift_signs = side_signs * weights[None, :]
    lift = np.concatenate([side_table(lift_signs).T, np.zeros((64, PLANE))], axis=0)
    lanes = np.arange(PLANE)
    flip = np.zeros((PLANE, PLANE))
    flip[lanes, (lanes % P_SIZE) * P_SIZE + lanes // P_SIZE] = 1.0
    return (
        jnp.asarray(spread_hi),
        jnp.asarray(spread_lo),
        jnp.asarray(lift, jnp.bfloat16),
        jnp.asarray(flip, jnp.bfloat16),
    )


def top_modes():
    ladder = np.arange(P_SIZE)
    first_idx, second_idx, third_idx = np.meshgrid(ladder, ladder, ladder, indexing="ij")
    return np.maximum(np.maximum(first_idx, second_idx), third_idx).reshape(1, -1).astype(np.int32)


def split_two(x):
    hi = x.astype(jnp.bfloat16)
    lo = (x - hi.astype(jnp.float32)).astype(jnp.bfloat16)
    return hi, lo


def mxu(a, b):
    return jnp.dot(a, b, preferred_element_type=jnp.float32)


def split_three(x):
    hi = x.astype(jnp.bfloat16)
    rest = x - hi.astype(jnp.float32)
    mid = rest.astype(jnp.bfloat16)
    lo = (rest - mid.astype(jnp.float32)).astype(jnp.bfloat16)
    return hi, mid, lo


def exact_pick(onehot, x):
    width = x.shape[1]
    joined = mxu(onehot, jnp.concatenate(split_three(x), axis=1))
    return joined[:, :width] + joined[:, width : 2 * width] + joined[:, 2 * width :]


def exact_rows(x, onehot):
    count = x.shape[0]
    joined = mxu(jnp.concatenate(split_three(x), axis=0), onehot)
    return joined[:count] + joined[count : 2 * count] + joined[2 * count :]


def end_traces(slabs):
    total = slabs[0] + slabs[1]
    even = slabs[0] - slabs[1]
    for a in range(2, P_SIZE):
        total = total + slabs[a]
        even = even + slabs[a] if a % 2 == 0 else even - slabs[a]
    return even, total


def turn_pair(lower, upper, picks, codes, flip):
    count = lower.shape[0]
    picked = jnp.concatenate([exact_pick(picks[4], lower), exact_pick(picks[5], upper)], axis=0)
    swapped = exact_rows(picked, flip)
    lane = lax.broadcasted_iota(jnp.int32, (1, PLANE), 1)
    row_odd = (lane // P_SIZE) % 2 == 1
    col_odd = lane % 2 == 1
    sides = []
    for side in range(2):
        rows = slice(side * count, (side + 1) * count)
        code = codes[:, side : side + 1]
        chosen = jnp.where(code % 2 == 1, swapped[rows], picked[rows])
        negate = ((code // 2) % 2 == 1) & row_odd
        negate = negate != (((code // 4) % 2 == 1) & col_odd)
        sides.append(jnp.where(negate, -chosen, chosen))
    return sides


def face_lift(below, above, live, a, scale):
    derivative, second, side_signs, weights = mode_tables()
    lift_signs = (side_signs * weights[None, :]).astype(np.float32)
    update = float(lift_signs[0, a]) * below + float(lift_signs[1, a]) * above
    return scale * jnp.where(live, update, 0.0)


def inner_body(*refs, scale, carried):
    if carried is None:
        v_ref, weight_ref, top_ref, pick_ref, spread_hi_ref, spread_lo_ref, lift_ref = refs[:7]
        base_ref = v_ref
    else:
        v_ref, below_ref, above_ref, base_ref, weight_ref, top_ref, pick_ref = refs[:7]
        spread_hi_ref, spread_lo_ref, lift_ref = refs[7:10]
    partial_ref, even_ref, total_ref = refs[-3:]
    count = v_ref.shape[0]
    derivative, second, side_signs, weights = mode_tables()
    second = second.astype(np.float32)
    derivative = derivative.astype(np.float32)
    lift_signs = (side_signs * weights[None, :]).astype(np.float32)
    weight = weight_ref[...]
    top = top_ref[...]
    order = weight[:, 7:8]
    slabs = [v_ref[:, a * PLANE : (a + 1) * PLANE] for a in range(P_SIZE)]
    if carried is not None:
        below = below_ref[...]
        above = above_ref[...]
        slabs = [
            slabs[a] + face_lift(below, above, top[:, a * PLANE : (a + 1) * PLANE] <= order, a, carried)
            for a in range(P_SIZE)
        ]
    diff0 = jnp.broadcast_to(weight[:, 0:1], (count, PLANE))
    vel0 = jnp.broadcast_to(weight[:, 3:4], (count, PLANE))
    first = []
    for k in range(P_SIZE):
        acc_s = None
        acc_d = None
        for n in range(k + 1, P_SIZE):
            if second[k, n] != 0.0:
                term = float(second[k, n]) * slabs[n]
                acc_s = term if acc_s is None else acc_s + term
            if derivative[k, n] != 0.0:
                term = float(derivative[k, n]) * slabs[n]
                acc_d = term if acc_d is None else acc_d + term
        part = jnp.zeros((count, PLANE), jnp.float32)
        if acc_s is not None:
            part = part + diff0 * acc_s
        if acc_d is not None:
            part = part - vel0 * acc_d
        first.append(part)
    stacked = jnp.concatenate(slabs, axis=0)
    hi, lo = split_two(stacked)
    spread_hi = spread_hi_ref[...]
    wide = mxu(hi, spread_hi) + mxu(lo, spread_hi)
    fine = mxu(hi, spread_lo_ref[...])
    weight_rows = jnp.concatenate([weight] * P_SIZE, axis=0)
    inner = (
        weight_rows[:, 2:3] * (wide[:, 0:PLANE] + fine[:, 0:PLANE])
        + weight_rows[:, 1:2] * (wide[:, PLANE : 2 * PLANE] + fine[:, PLANE : 2 * PLANE])
        - weight_rows[:, 5:6] * wide[:, 2 * PLANE : 3 * PLANE]
        - weight_rows[:, 4:5] * wide[:, 3 * PLANE : 4 * PLANE]
    )
    own = jnp.concatenate(
        [wide[a * count : (a + 1) * count, 4 * PLANE : 4 * PLANE + 128] for a in range(P_SIZE)], axis=1
    )
    other = jnp.concatenate(
        [wide[a * count : (a + 1) * count, 4 * PLANE + 128 : 4 * PLANE + 256] for a in range(P_SIZE)], axis=1
    )
    lane = lax.broadcasted_iota(jnp.int32, (1, P_SIZE * 128), 1) % 128
    across = jnp.zeros_like(own)
    for face in range(4):
        gathered = exact_pick(pick_ref[face], other)
        across = jnp.where(lane // P_SIZE == face, gathered, across)
    jump = own - across
    jump_rows = jnp.concatenate([jump[:, a * 128 : (a + 1) * 128] for a in range(P_SIZE)], axis=0)
    jhi, jlo = split_two(jump_rows)
    lift_mat = lift_ref[...]
    lifted = mxu(jhi, lift_mat) + mxu(jlo, lift_mat)
    even, total = end_traces(slabs)
    news = []
    for a in range(P_SIZE):
        rows = slice(a * count, (a + 1) * count)
        lanes = slice(a * PLANE, (a + 1) * PLANE)
        own_lift = lifted[rows] + float(lift_signs[0, a]) * even + float(lift_signs[1, a]) * total
        live = top[:, lanes] <= order
        update = jnp.where(live, first[a] + inner[rows] - own_lift, 0.0)
        new = base_ref[:, lanes] + scale * update
        partial_ref[:, lanes] = new
        news.append(new)
    even, total = end_traces(news)
    even_ref[...] = even
    total_ref[...] = total


def faces_body(
    lower_ref, upper_ref, pick_ref, turn_ref, flip_ref, top_ref, weight_ref, even_ref, total_ref,
    below_ref, above_ref, new_even_ref, new_total_ref, *, scale
):
    below, above = turn_pair(lower_ref[...], upper_ref[...], pick_ref, turn_ref[...], flip_ref[...])
    below_ref[...] = below
    above_ref[...] = above
    top = top_ref[...]
    order = weight_ref[:, 7:8]
    parts = [
        face_lift(below, above, top[:, a * PLANE : (a + 1) * PLANE] <= order, a, scale)
        for a in range(P_SIZE)
    ]
    even, total = end_traces(parts)
    new_even_ref[...] = even_ref[...] + even
    new_total_ref[...] = total_ref[...] + total


def outer_body(
    pre_ref, top_ref, weight_ref, lower_ref, upper_ref, pick_ref, turn_ref, flip_ref,
    out_ref, even_ref, total_ref, *, scale
):
    derivative, second, side_signs, weights = mode_tables()
    lift_signs = (side_signs * weights[None, :]).astype(np.float32)
    below, above = turn_pair(lower_ref[...], upper_ref[...], pick_ref, turn_ref[...], flip_ref[...])
    top = top_ref[...]
    order = weight_ref[:, 7:8]
    news = []
    for a in range(P_SIZE):
        lanes = slice(a * PLANE, (a + 1) * PLANE)
        update = float(lift_signs[0, a]) * below + float(lift_signs[1, a]) * above
        live = top[:, lanes] <= order
        new = pre_ref[:, lanes] + scale * jnp.where(live, update, 0.0)
        out_ref[:, lanes] = new
        news.append(new)
    even, total = end_traces(news)
    even_ref[...] = even
    total_ref[...] = total


def inner(operands, scale, carried):
    count = operands[0].shape[0]
    spec = pl.BlockSpec(memory_space=pltpu.VMEM)
    return pl.pallas_call(
        functools.partial(inner_body, scale=scale, carried=carried),
        out_shape=(
            jax.ShapeDtypeStruct(operands[0].shape, jnp.float32),
            jax.ShapeDtypeStruct((count, PLANE), jnp.float32),
            jax.ShapeDtypeStruct((count, PLANE), jnp.float32),
        ),
        in_specs=[spec] * len(operands),
        out_specs=(spec, spec, spec),
        compiler_params=pltpu.CompilerParams(vmem_limit_bytes=60 * 1024 * 1024),
        cost_estimate=pl.CostEstimate(
            flops=2_500_000_000, transcendentals=0, bytes_accessed=4_000_000
        ),
    )(*operands)


def faces(lower, upper, picks, codes, flip, top, weight, even, total, scale):
    count = lower.shape[0]
    spec = pl.BlockSpec(memory_space=pltpu.VMEM)
    square = jax.ShapeDtypeStruct((count, PLANE), jnp.float32)
    return pl.pallas_call(
        functools.partial(faces_body, scale=scale),
        out_shape=(square,) * 4,
        in_specs=[spec] * 9,
        out_specs=(spec,) * 4,
    )(lower, upper, picks, codes, flip, top, weight, even, total)


def outer(pre, top, weight, lower, upper, picks, codes, flip, scale):
    count = pre.shape[0]
    spec = pl.BlockSpec(memory_space=pltpu.VMEM)
    return pl.pallas_call(
        functools.partial(outer_body, scale=scale),
        out_shape=(
            jax.ShapeDtypeStruct(pre.shape, jnp.float32),
            jax.ShapeDtypeStruct((count, PLANE), jnp.float32),
            jax.ShapeDtypeStruct((count, PLANE), jnp.float32),
        ),
        in_specs=[spec] * 8,
        out_specs=(spec, spec, spec),
    )(pre, top, weight, lower, upper, picks, codes, flip)


def prep_body(
    coef_ref, first_ref, second_ref, third_ref, source_ref, top_ref, weight_ref,
    field_ref, even_ref, total_ref
):
    count = coef_ref.shape[0]
    source = source_ref[...]
    lane = lax.broadcasted_iota(jnp.int32, (1, count), 1)
    local = (source == lane).astype(jnp.bfloat16)
    pieces = split_three(coef_ref[...])
    order = weight_ref[:, 7:8]
    news = []
    for a in range(P_SIZE):
        lanes = slice(a * PLANE, (a + 1) * PLANE)
        joined = mxu(local, jnp.concatenate([piece[:, lanes] for piece in pieces], axis=1))
        placed = joined[:, :PLANE] + joined[:, PLANE : 2 * PLANE] + joined[:, 2 * PLANE :]
        moving = first_ref.shape[0] - 1
        for index, parcel_ref in enumerate((first_ref, second_ref, third_ref)):
            for row in range(moving):
                hit = source == count + moving * index + row
                placed = jnp.where(hit, parcel_ref[row : row + 1, lanes], placed)
        live = top_ref[:, lanes] <= order
        new = jnp.where(live, placed, 0.0)
        field_ref[:, lanes] = new
        news.append(new)
    even, total = end_traces(news)
    even_ref[...] = even
    total_ref[...] = total


def prep(coefficients, parcels, source, top, weight):
    count = coefficients.shape[0]
    spec = pl.BlockSpec(memory_space=pltpu.VMEM)
    return pl.pallas_call(
        prep_body,
        out_shape=(
            jax.ShapeDtypeStruct(coefficients.shape, jnp.float32),
            jax.ShapeDtypeStruct((count, PLANE), jnp.float32),
            jax.ShapeDtypeStruct((count, PLANE), jnp.float32),
        ),
        in_specs=[spec] * 7,
        out_specs=(spec, spec, spec),
    )(coefficients, *parcels, source, top, weight)


def exchange(even, total):
    size = lax.axis_size("dom")
    up = [(i, (i + 1) % size) for i in range(size)]
    down = [((i + 1) % size, i) for i in range(size)]
    return lax.ppermute(total, "dom", up), lax.ppermute(even, "dom", down)


def shards(
    coefficients, diffusion, velocity, orders, target, local_faces, partner_faces, partner_turns
):
    element_count = coefficients.shape[0]
    blocks_all = lax.axis_size(("dom", "face"))
    moving = element_count // 16
    destination = target // element_count
    new_slot = target % element_count
    here = lax.axis_index(("dom", "face"))
    side_info = jnp.concatenate(
        [
            diffusion,
            velocity,
            new_slot[:, None].astype(jnp.float32),
            orders[:, None].astype(jnp.float32),
        ],
        axis=1,
    )
    side_width = side_info.shape[1]
    shifts = (1, blocks_all - 1, blocks_all // 2)
    goal = (here + jnp.asarray(shifts, jnp.int32)) % blocks_all
    chosen = destination[None, :] == goal[:, None]
    rank = jnp.cumsum(chosen.astype(jnp.int32), axis=1) - 1
    hit = chosen[:, None, :] & (
        rank[:, None, :] == jnp.arange(moving, dtype=jnp.int32)[None, :, None]
    )
    rows = jnp.arange(element_count, dtype=jnp.int32)
    picked = jnp.sum(jnp.where(hit, rows[None, None, :], 0), axis=2).reshape(-1)
    side_rows = side_info[picked].reshape(len(shifts), 1, moving * side_width)
    side_rows = jnp.pad(side_rows, ((0, 0), (0, 0), (0, P_SIZE**3 - moving * side_width)))
    parcels = jnp.concatenate(
        [coefficients[picked].reshape(len(shifts), moving, P_SIZE**3), side_rows], axis=1
    )
    arrivals = []
    got_side = [side_info]
    got_slot = [jnp.where(destination == here, new_slot, element_count)]
    for index, shift in enumerate(shifts):
        pairs = [(i, (i + shift) % blocks_all) for i in range(blocks_all)]
        arrived = lax.ppermute(parcels[index], ("dom", "face"), pairs)
        arrived_side = arrived[moving, : moving * side_width].reshape(moving, side_width)
        arrivals.append(arrived)
        got_side.append(arrived_side)
        got_slot.append(arrived_side[:, 6].astype(jnp.int32))
    got_side = jnp.concatenate(got_side, axis=0)
    got_slot = jnp.concatenate(got_slot, axis=0)
    hit = got_slot[None, :] == jnp.arange(element_count, dtype=jnp.int32)[:, None]
    got_rows = jnp.arange(got_slot.shape[0], dtype=jnp.int32)
    source = jnp.sum(jnp.where(hit, got_rows[None, :], 0), axis=1)
    placed_side = got_side[source]
    weight = placed_side
    top = jnp.asarray(top_modes().astype(np.float32))
    tables = kernel_tables()
    neighbours = jnp.concatenate([local_faces[0], partner_faces[0]], axis=0)
    picks = (
        neighbours[:, :, None] == jnp.arange(element_count, dtype=jnp.int32)[None, None, :]
    ).astype(jnp.bfloat16)
    codes = partner_turns[0].T
    spread_hi, spread_lo, lift, flip = tables
    field, even, total = prep(coefficients, arrivals, source[:, None], top, weight)
    first_step = 0.5 * TIME_STEP
    lower, upper = exchange(even, total)
    pre, even, total = inner(
        (field, weight, top, picks, spread_hi, spread_lo, lift), first_step, None
    )
    below, above, even, total = faces(
        lower, upper, picks, codes, flip, top, weight, even, total, first_step
    )
    lower, upper = exchange(even, total)
    pre, _, _ = inner(
        (pre, below, above, field, weight, top, picks, spread_hi, spread_lo, lift),
        TIME_STEP,
        first_step,
    )
    advanced, _, _ = outer(pre, top, weight, lower, upper, picks, codes, flip, TIME_STEP)
    return advanced


def solution(mesh):
    in_specs = (
        P(("dom", "face"), None),
        P(("dom", "face"), None),
        P(("dom", "face"), None),
        P(("dom", "face")),
        P(("dom", "face")),
        P(("dom", "face"), None, None),
        P(("dom", "face"), None, None),
        P(("dom", "face"), None, None),
    )
    out_specs = P(("dom", "face"), None)
    return jax.shard_map(shards, mesh=mesh, in_specs=in_specs, out_specs=out_specs, check_vma=False)
```

```python
import functools
import jax
import jax.numpy as jnp
import numpy as np
from jax import lax
from jax.experimental import pallas as pl
from jax.experimental.pallas import tpu as pltpu
from jax.sharding import PartitionSpec as P

P_SIZE = 16
PLANE = P_SIZE * P_SIZE
TIME_STEP = 0.25


def mode_tables():
    ladder = np.arange(P_SIZE)
    spacing = ladder[None, :] - ladder[:, None]
    derivative = np.where(
        (spacing > 0) & (spacing % 2 == 1), (2.0 * ladder[:, None] + 1.0) / P_SIZE, 0.0
    )
    second = derivative @ derivative / P_SIZE
    side_signs = np.stack([(-1.0) ** ladder, np.ones(P_SIZE)])
    weights = (2.0 * ladder + 1.0) / (2.0 * P_SIZE)
    return (derivative, second, side_signs, weights)


def side_table(values_pair):
    identity = np.eye(P_SIZE)
    return np.concatenate(
        [
            np.kron(values_pair[0][:, None], identity),
            np.kron(values_pair[1][:, None], identity),
            np.kron(identity, values_pair[0][:, None]),
            np.kron(identity, values_pair[1][:, None]),
        ],
        axis=1,
    )


def kernel_tables():
    derivative, second, side_signs, weights = mode_tables()
    derivative = derivative.astype(np.float32).astype(np.float64)
    second = second.astype(np.float32).astype(np.float64)
    identity = np.eye(P_SIZE)
    traces = side_table(side_signs)
    swapped = traces[:, [16 * g + j for g in (1, 0, 3, 2) for j in range(P_SIZE)]]
    pad = np.zeros((PLANE, 64))
    spread = np.concatenate(
        [
            np.kron(identity, second.T),
            np.kron(second.T, identity),
            np.kron(identity, derivative.T),
            np.kron(derivative.T, identity),
            traces, pad, swapped, pad,
        ],
        axis=1,
    ).astype(np.float32)
    spread_hi = spread.astype(jnp.bfloat16)
    spread_lo = (spread[:, : 2 * PLANE] - spread_hi[:, : 2 * PLANE].astype(np.float32)).astype(jnp.bfloat16)
    lift_signs = side_signs * weights[None, :]
    lift = np.concatenate([side_table(lift_signs).T, np.zeros((64, PLANE))], axis=0)
    lanes = np.arange(PLANE)
    flip = np.zeros((PLANE, PLANE))
    flip[lanes, (lanes % P_SIZE) * P_SIZE + lanes // P_SIZE] = 1.0
    return (
        jnp.asarray(spread_hi),
        jnp.asarray(spread_lo),
        jnp.asarray(lift, jnp.bfloat16),
        jnp.asarray(flip, jnp.bfloat16),
    )


def top_modes():
    ladder = np.arange(P_SIZE)
    first_idx, second_idx, third_idx = np.meshgrid(ladder, ladder, ladder, indexing="ij")
    return np.maximum(np.maximum(first_idx, second_idx), third_idx).reshape(1, -1).astype(np.int32)


def split_two(x):
    hi = x.astype(jnp.bfloat16)
    lo = (x - hi.astype(jnp.float32)).astype(jnp.bfloat16)
    return hi, lo


def mxu(a, b):
    return jnp.dot(a, b, preferred_element_type=jnp.float32)


def split_three(x):
    hi = x.astype(jnp.bfloat16)
    rest = x - hi.astype(jnp.float32)
    mid = rest.astype(jnp.bfloat16)
    lo = (rest - mid.astype(jnp.float32)).astype(jnp.bfloat16)
    return hi, mid, lo


def exact_pick(onehot, x):
    width = x.shape[1]
    joined = mxu(onehot, jnp.concatenate(split_three(x), axis=1))
    return joined[:, :width] + joined[:, width : 2 * width] + joined[:, 2 * width :]


def exact_rows(x, onehot):
    count = x.shape[0]
    joined = mxu(jnp.concatenate(split_three(x), axis=0), onehot)
    return joined[:count] + joined[count : 2 * count] + joined[2 * count :]


def end_traces(slabs):
    total = slabs[0] + slabs[1]
    even = slabs[0] - slabs[1]
    for a in range(2, P_SIZE):
        total = total + slabs[a]
        even = even + slabs[a] if a % 2 == 0 else even - slabs[a]
    return even, total


def turn_pair(lower, upper, picks, codes, flip):
    count = lower.shape[0]
    picked = jnp.concatenate([exact_pick(picks[4], lower), exact_pick(picks[5], upper)], axis=0)
    swapped = exact_rows(picked, flip)
    lane = lax.broadcasted_iota(jnp.int32, (1, PLANE), 1)
    row_odd = (lane // P_SIZE) % 2 == 1
    col_odd = lane % 2 == 1
    sides = []
    for side in range(2):
        rows = slice(side * count, (side + 1) * count)
        code = codes[:, side : side + 1]
        chosen = jnp.where(code % 2 == 1, swapped[rows], picked[rows])
        negate = ((code // 2) % 2 == 1) & row_odd
        negate = negate != (((code // 4) % 2 == 1) & col_odd)
        sides.append(jnp.where(negate, -chosen, chosen))
    return sides


def face_lift(below, above, live, a, scale):
    derivative, second, side_signs, weights = mode_tables()
    lift_signs = (side_signs * weights[None, :]).astype(np.float32)
    update = float(lift_signs[0, a]) * below + float(lift_signs[1, a]) * above
    return scale * jnp.where(live, update, 0.0)


def inner_body(*refs, scale, carried, final):
    if carried is None:
        v_ref, weight_ref, top_ref, pick_ref, spread_hi_ref, spread_lo_ref, lift_ref = refs[:7]
        base_ref = v_ref
    else:
        v_ref, below_ref, above_ref, base_ref, weight_ref, top_ref, pick_ref = refs[:7]
        spread_hi_ref, spread_lo_ref, lift_ref = refs[7:10]
    if final:
        lower_ref, upper_ref, turn_ref, flip_ref = refs[10:14]
        partial_ref = refs[-1]
    else:
        partial_ref, even_ref, total_ref = refs[-3:]
    count = v_ref.shape[0]
    derivative, second, side_signs, weights = mode_tables()
    second = second.astype(np.float32)
    derivative = derivative.astype(np.float32)
    lift_signs = (side_signs * weights[None, :]).astype(np.float32)
    weight = weight_ref[...]
    top = top_ref[...]
    order = weight[:, 7:8]
    slabs = [v_ref[:, a * PLANE : (a + 1) * PLANE] for a in range(P_SIZE)]
    if carried is not None:
        below = below_ref[...]
        above = above_ref[...]
        slabs = [
            slabs[a] + face_lift(below, above, top[:, a * PLANE : (a + 1) * PLANE] <= order, a, carried)
            for a in range(P_SIZE)
        ]
    diff0 = jnp.broadcast_to(weight[:, 0:1], (count, PLANE))
    vel0 = jnp.broadcast_to(weight[:, 3:4], (count, PLANE))
    first = []
    for k in range(P_SIZE):
        acc_s = None
        acc_d = None
        for n in range(k + 1, P_SIZE):
            if second[k, n] != 0.0:
                term = float(second[k, n]) * slabs[n]
                acc_s = term if acc_s is None else acc_s + term
            if derivative[k, n] != 0.0:
                term = float(derivative[k, n]) * slabs[n]
                acc_d = term if acc_d is None else acc_d + term
        part = jnp.zeros((count, PLANE), jnp.float32)
        if acc_s is not None:
            part = part + diff0 * acc_s
        if acc_d is not None:
            part = part - vel0 * acc_d
        first.append(part)
    stacked = jnp.concatenate(slabs, axis=0)
    hi, lo = split_two(stacked)
    spread_hi = spread_hi_ref[...]
    wide = mxu(hi, spread_hi) + mxu(lo, spread_hi)
    fine = mxu(hi, spread_lo_ref[...])
    weight_rows = jnp.concatenate([weight] * P_SIZE, axis=0)
    inner = (
        weight_rows[:, 2:3] * (wide[:, 0:PLANE] + fine[:, 0:PLANE])
        + weight_rows[:, 1:2] * (wide[:, PLANE : 2 * PLANE] + fine[:, PLANE : 2 * PLANE])
        - weight_rows[:, 5:6] * wide[:, 2 * PLANE : 3 * PLANE]
        - weight_rows[:, 4:5] * wide[:, 3 * PLANE : 4 * PLANE]
    )
    own = jnp.concatenate(
        [wide[a * count : (a + 1) * count, 4 * PLANE : 4 * PLANE + 128] for a in range(P_SIZE)], axis=1
    )
    other = jnp.concatenate(
        [wide[a * count : (a + 1) * count, 4 * PLANE + 128 : 4 * PLANE + 256] for a in range(P_SIZE)], axis=1
    )
    lane = lax.broadcasted_iota(jnp.int32, (1, P_SIZE * 128), 1) % 128
    across = jnp.zeros_like(own)
    for face in range(4):
        gathered = exact_pick(pick_ref[face], other)
        across = jnp.where(lane // P_SIZE == face, gathered, across)
    jump = own - across
    jump_rows = jnp.concatenate([jump[:, a * 128 : (a + 1) * 128] for a in range(P_SIZE)], axis=0)
    jhi, jlo = split_two(jump_rows)
    lift_mat = lift_ref[...]
    lifted = mxu(jhi, lift_mat) + mxu(jlo, lift_mat)
    even, total = end_traces(slabs)
    if final:
        below, above = turn_pair(
            lower_ref[...], upper_ref[...], pick_ref, turn_ref[...], flip_ref[...]
        )
    news = []
    for a in range(P_SIZE):
        rows = slice(a * count, (a + 1) * count)
        lanes = slice(a * PLANE, (a + 1) * PLANE)
        own_lift = lifted[rows] + float(lift_signs[0, a]) * even + float(lift_signs[1, a]) * total
        if final:
            own_lift = own_lift - float(lift_signs[0, a]) * below - float(lift_signs[1, a]) * above
        live = top[:, lanes] <= order
        update = jnp.where(live, first[a] + inner[rows] - own_lift, 0.0)
        new = base_ref[:, lanes] + scale * update
        partial_ref[:, lanes] = new
        news.append(new)
    if not final:
        even, total = end_traces(news)
        even_ref[...] = even
        total_ref[...] = total


def faces_body(
    lower_ref, upper_ref, pick_ref, turn_ref, flip_ref, top_ref, weight_ref, even_ref, total_ref,
    below_ref, above_ref, new_even_ref, new_total_ref, *, scale
):
    below, above = turn_pair(lower_ref[...], upper_ref[...], pick_ref, turn_ref[...], flip_ref[...])
    below_ref[...] = below
    above_ref[...] = above
    top = top_ref[...]
    order = weight_ref[:, 7:8]
    parts = [
        face_lift(below, above, top[:, a * PLANE : (a + 1) * PLANE] <= order, a, scale)
        for a in range(P_SIZE)
    ]
    even, total = end_traces(parts)
    new_even_ref[...] = even_ref[...] + even
    new_total_ref[...] = total_ref[...] + total


def outer_body(
    pre_ref, top_ref, weight_ref, lower_ref, upper_ref, pick_ref, turn_ref, flip_ref,
    out_ref, even_ref, total_ref, *, scale
):
    derivative, second, side_signs, weights = mode_tables()
    lift_signs = (side_signs * weights[None, :]).astype(np.float32)
    below, above = turn_pair(lower_ref[...], upper_ref[...], pick_ref, turn_ref[...], flip_ref[...])
    top = top_ref[...]
    order = weight_ref[:, 7:8]
    news = []
    for a in range(P_SIZE):
        lanes = slice(a * PLANE, (a + 1) * PLANE)
        update = float(lift_signs[0, a]) * below + float(lift_signs[1, a]) * above
        live = top[:, lanes] <= order
        new = pre_ref[:, lanes] + scale * jnp.where(live, update, 0.0)
        out_ref[:, lanes] = new
        news.append(new)
    even, total = end_traces(news)
    even_ref[...] = even
    total_ref[...] = total


def inner(operands, scale, carried, final=False):
    count = operands[0].shape[0]
    spec = pl.BlockSpec(memory_space=pltpu.VMEM)
    square = jax.ShapeDtypeStruct((count, PLANE), jnp.float32)
    field = jax.ShapeDtypeStruct(operands[0].shape, jnp.float32)
    return pl.pallas_call(
        functools.partial(inner_body, scale=scale, carried=carried, final=final),
        out_shape=field if final else (field, square, square),
        in_specs=[spec] * len(operands),
        out_specs=spec if final else (spec, spec, spec),
        compiler_params=pltpu.CompilerParams(vmem_limit_bytes=60 * 1024 * 1024),
        cost_estimate=pl.CostEstimate(
            flops=2_500_000_000, transcendentals=0, bytes_accessed=4_000_000
        ),
    )(*operands)


def faces(lower, upper, picks, codes, flip, top, weight, even, total, scale):
    count = lower.shape[0]
    spec = pl.BlockSpec(memory_space=pltpu.VMEM)
    square = jax.ShapeDtypeStruct((count, PLANE), jnp.float32)
    return pl.pallas_call(
        functools.partial(faces_body, scale=scale),
        out_shape=(square,) * 4,
        in_specs=[spec] * 9,
        out_specs=(spec,) * 4,
    )(lower, upper, picks, codes, flip, top, weight, even, total)


def outer(pre, top, weight, lower, upper, picks, codes, flip, scale):
    count = pre.shape[0]
    spec = pl.BlockSpec(memory_space=pltpu.VMEM)
    return pl.pallas_call(
        functools.partial(outer_body, scale=scale),
        out_shape=(
            jax.ShapeDtypeStruct(pre.shape, jnp.float32),
            jax.ShapeDtypeStruct((count, PLANE), jnp.float32),
            jax.ShapeDtypeStruct((count, PLANE), jnp.float32),
        ),
        in_specs=[spec] * 8,
        out_specs=(spec, spec, spec),
    )(pre, top, weight, lower, upper, picks, codes, flip)


def prep_body(placed_ref, top_ref, weight_ref, field_ref, even_ref, total_ref):
    news = []
    for a in range(P_SIZE):
        lanes = slice(a * PLANE, (a + 1) * PLANE)
        live = top_ref[:, lanes] <= weight_ref[:, 7:8]
        new = jnp.where(live, placed_ref[:, lanes], 0.0)
        field_ref[:, lanes] = new
        news.append(new)
    even, total = end_traces(news)
    even_ref[...] = even
    total_ref[...] = total


def prep(placed, top, weight):
    count = placed.shape[0]
    spec = pl.BlockSpec(memory_space=pltpu.VMEM)
    return pl.pallas_call(
        prep_body,
        out_shape=(
            jax.ShapeDtypeStruct(placed.shape, jnp.float32),
            jax.ShapeDtypeStruct((count, PLANE), jnp.float32),
            jax.ShapeDtypeStruct((count, PLANE), jnp.float32),
        ),
        in_specs=[spec] * 3,
        out_specs=(spec, spec, spec),
    )(placed, top, weight)


def exchange(even, total):
    size = lax.axis_size("dom")
    up = [(i, (i + 1) % size) for i in range(size)]
    down = [((i + 1) % size, i) for i in range(size)]
    return lax.ppermute(total, "dom", up), lax.ppermute(even, "dom", down)


def shards(
    coefficients, diffusion, velocity, orders, target, local_faces, partner_faces, partner_turns
):
    element_count = coefficients.shape[0]
    blocks_all = lax.axis_size(("dom", "face"))
    moving = element_count // 16
    destination = target // element_count
    new_slot = target % element_count
    here = lax.axis_index(("dom", "face"))
    side_info = jnp.concatenate(
        [
            diffusion,
            velocity,
            new_slot[:, None].astype(jnp.float32),
            orders[:, None].astype(jnp.float32),
        ],
        axis=1,
    )
    side_width = side_info.shape[1]
    shifts = (1, blocks_all - 1, blocks_all // 2)
    goal = (here + jnp.asarray(shifts, jnp.int32)) % blocks_all
    chosen = destination[None, :] == goal[:, None]
    rank = jnp.cumsum(chosen.astype(jnp.int32), axis=1) - 1
    hit = chosen[:, None, :] & (
        rank[:, None, :] == jnp.arange(moving, dtype=jnp.int32)[None, :, None]
    )
    rows = jnp.arange(element_count, dtype=jnp.int32)
    picked = jnp.sum(jnp.where(hit, rows[None, None, :], 0), axis=2).reshape(-1)
    side_rows = side_info[picked].reshape(len(shifts), 1, moving * side_width)
    side_rows = jnp.pad(side_rows, ((0, 0), (0, 0), (0, P_SIZE**3 - moving * side_width)))
    parcels = jnp.concatenate(
        [coefficients[picked].reshape(len(shifts), moving, P_SIZE**3), side_rows], axis=1
    )
    got_coef = [coefficients]
    got_side = [side_info]
    got_slot = [jnp.where(destination == here, new_slot, element_count)]
    for index, shift in enumerate(shifts):
        pairs = [(i, (i + shift) % blocks_all) for i in range(blocks_all)]
        arrived = lax.ppermute(parcels[index], ("dom", "face"), pairs)
        arrived_side = arrived[moving, : moving * side_width].reshape(moving, side_width)
        got_coef.append(arrived[:moving])
        got_side.append(arrived_side)
        got_slot.append(arrived_side[:, 6].astype(jnp.int32))
    got_coef = jnp.concatenate(got_coef, axis=0)
    got_side = jnp.concatenate(got_side, axis=0)
    got_slot = jnp.concatenate(got_slot, axis=0)
    hit = got_slot[None, :] == jnp.arange(element_count, dtype=jnp.int32)[:, None]
    got_rows = jnp.arange(got_slot.shape[0], dtype=jnp.int32)
    source = jnp.sum(jnp.where(hit, got_rows[None, :], 0), axis=1)
    placed_side = got_side[source]
    weight = placed_side
    top = jnp.asarray(top_modes().astype(np.float32))
    tables = kernel_tables()
    neighbours = jnp.concatenate([local_faces[0], partner_faces[0]], axis=0)
    picks = (
        neighbours[:, :, None] == jnp.arange(element_count, dtype=jnp.int32)[None, None, :]
    ).astype(jnp.bfloat16)
    codes = partner_turns[0].T
    spread_hi, spread_lo, lift, flip = tables
    field, even, total = prep(got_coef[source], top, weight)
    first_step = 0.5 * TIME_STEP
    lower, upper = exchange(even, total)
    pre, even, total = inner(
        (field, weight, top, picks, spread_hi, spread_lo, lift), first_step, None
    )
    below, above, even, total = faces(
        lower, upper, picks, codes, flip, top, weight, even, total, first_step
    )
    lower, upper = exchange(even, total)
    advanced = inner(
        (pre, below, above, field, weight, top, picks, spread_hi, spread_lo, lift)
        + (lower, upper, codes, flip),
        TIME_STEP,
        first_step,
        final=True,
    )
    return advanced


def solution(mesh):
    in_specs = (
        P(("dom", "face"), None),
        P(("dom", "face"), None),
        P(("dom", "face"), None),
        P(("dom", "face")),
        P(("dom", "face")),
        P(("dom", "face"), None, None),
        P(("dom", "face"), None, None),
        P(("dom", "face"), None, None),
    )
    out_specs = P(("dom", "face"), None)
    return jax.shard_map(shards, mesh=mesh, in_specs=in_specs, out_specs=out_specs, check_vma=False)
```

```python
import functools
import jax
import jax.numpy as jnp
import numpy as np
from jax import lax
from jax.experimental import pallas as pl
from jax.experimental.pallas import tpu as pltpu
from jax.sharding import PartitionSpec as P

P_SIZE = 16
PLANE = P_SIZE * P_SIZE
TIME_STEP = 0.25


def mode_tables():
    ladder = np.arange(P_SIZE)
    spacing = ladder[None, :] - ladder[:, None]
    derivative = np.where(
        (spacing > 0) & (spacing % 2 == 1), (2.0 * ladder[:, None] + 1.0) / P_SIZE, 0.0
    )
    second = derivative @ derivative / P_SIZE
    side_signs = np.stack([(-1.0) ** ladder, np.ones(P_SIZE)])
    weights = (2.0 * ladder + 1.0) / (2.0 * P_SIZE)
    return (derivative, second, side_signs, weights)


def side_table(values_pair):
    identity = np.eye(P_SIZE)
    return np.concatenate(
        [
            np.kron(values_pair[0][:, None], identity),
            np.kron(values_pair[1][:, None], identity),
            np.kron(identity, values_pair[0][:, None]),
            np.kron(identity, values_pair[1][:, None]),
        ],
        axis=1,
    )


def kernel_tables():
    derivative, second, side_signs, weights = mode_tables()
    derivative = derivative.astype(np.float32).astype(np.float64)
    second = second.astype(np.float32).astype(np.float64)
    identity = np.eye(P_SIZE)
    traces = side_table(side_signs)
    swapped = traces[:, [16 * g + j for g in (1, 0, 3, 2) for j in range(P_SIZE)]]
    pad = np.zeros((PLANE, 64))
    spread = np.concatenate(
        [
            np.kron(identity, second.T),
            np.kron(second.T, identity),
            np.kron(identity, derivative.T),
            np.kron(derivative.T, identity),
            traces, pad, swapped, pad,
        ],
        axis=1,
    ).astype(np.float32)
    spread_hi = spread.astype(jnp.bfloat16)
    spread_lo = (spread[:, : 2 * PLANE] - spread_hi[:, : 2 * PLANE].astype(np.float32)).astype(jnp.bfloat16)
    lift_signs = side_signs * weights[None, :]
    lift = np.concatenate([side_table(lift_signs).T, np.zeros((64, PLANE))], axis=0)
    lanes = np.arange(PLANE)
    flip = np.zeros((PLANE, PLANE))
    flip[lanes, (lanes % P_SIZE) * P_SIZE + lanes // P_SIZE] = 1.0
    return (
        jnp.asarray(spread_hi),
        jnp.asarray(spread_lo),
        jnp.asarray(lift, jnp.bfloat16),
        jnp.asarray(flip, jnp.bfloat16),
    )


def top_modes():
    ladder = np.arange(P_SIZE)
    first_idx, second_idx, third_idx = np.meshgrid(ladder, ladder, ladder, indexing="ij")
    return np.maximum(np.maximum(first_idx, second_idx), third_idx).reshape(1, -1).astype(np.int32)


def split_two(x):
    hi = x.astype(jnp.bfloat16)
    lo = (x - hi.astype(jnp.float32)).astype(jnp.bfloat16)
    return hi, lo


def mxu(a, b):
    return jnp.dot(a, b, preferred_element_type=jnp.float32)


def split_three(x):
    hi = x.astype(jnp.bfloat16)
    rest = x - hi.astype(jnp.float32)
    mid = rest.astype(jnp.bfloat16)
    lo = (rest - mid.astype(jnp.float32)).astype(jnp.bfloat16)
    return hi, mid, lo


def exact_pick(onehot, x):
    width = x.shape[1]
    joined = mxu(onehot, jnp.concatenate(split_three(x), axis=1))
    return joined[:, :width] + joined[:, width : 2 * width] + joined[:, 2 * width :]


def exact_rows(x, onehot):
    count = x.shape[0]
    joined = mxu(jnp.concatenate(split_three(x), axis=0), onehot)
    return joined[:count] + joined[count : 2 * count] + joined[2 * count :]


def end_traces(slabs):
    total = slabs[0] + slabs[1]
    even = slabs[0] - slabs[1]
    for a in range(2, P_SIZE):
        total = total + slabs[a]
        even = even + slabs[a] if a % 2 == 0 else even - slabs[a]
    return even, total


def turn_pair(lower, upper, picks, codes, flip):
    count = lower.shape[0]
    picked = jnp.concatenate([exact_pick(picks[4], lower), exact_pick(picks[5], upper)], axis=0)
    swapped = exact_rows(picked, flip)
    lane = lax.broadcasted_iota(jnp.int32, (1, PLANE), 1)
    row_odd = (lane // P_SIZE) % 2 == 1
    col_odd = lane % 2 == 1
    sides = []
    for side in range(2):
        rows = slice(side * count, (side + 1) * count)
        code = codes[:, side : side + 1]
        chosen = jnp.where(code % 2 == 1, swapped[rows], picked[rows])
        negate = ((code // 2) % 2 == 1) & row_odd
        negate = negate != (((code // 4) % 2 == 1) & col_odd)
        sides.append(jnp.where(negate, -chosen, chosen))
    return sides


def face_lift(below, above, live, a, scale):
    derivative, second, side_signs, weights = mode_tables()
    lift_signs = (side_signs * weights[None, :]).astype(np.float32)
    update = float(lift_signs[0, a]) * below + float(lift_signs[1, a]) * above
    return scale * jnp.where(live, update, 0.0)


def inner_body(*refs, scale, carried, final):
    if carried is None:
        v_ref, weight_ref, top_ref, pick_ref, spread_hi_ref, spread_lo_ref, lift_ref = refs[:7]
        base_ref = v_ref
    else:
        v_ref, below_ref, above_ref, base_ref, weight_ref, top_ref, pick_ref = refs[:7]
        spread_hi_ref, spread_lo_ref, lift_ref = refs[7:10]
    if final:
        lower_ref, upper_ref, turn_ref, flip_ref = refs[10:14]
        partial_ref = refs[-1]
    else:
        partial_ref, even_ref, total_ref = refs[-3:]
    count = v_ref.shape[0]
    derivative, second, side_signs, weights = mode_tables()
    second = second.astype(np.float32)
    derivative = derivative.astype(np.float32)
    lift_signs = (side_signs * weights[None, :]).astype(np.float32)
    weight = weight_ref[...]
    top = top_ref[...]
    order = weight[:, 7:8]
    slabs = [v_ref[:, a * PLANE : (a + 1) * PLANE] for a in range(P_SIZE)]
    if carried is not None:
        below = below_ref[...]
        above = above_ref[...]
        slabs = [
            slabs[a] + face_lift(below, above, top[:, a * PLANE : (a + 1) * PLANE] <= order, a, carried)
            for a in range(P_SIZE)
        ]
    diff0 = jnp.broadcast_to(weight[:, 0:1], (count, PLANE))
    vel0 = jnp.broadcast_to(weight[:, 3:4], (count, PLANE))
    half = count // 2
    low = P_SIZE // 2

    def kept(a, x):
        return x if a < low else x[half:]

    def start(a):
        return a * count if a < low else low * count + (a - low) * half

    upper_slabs = [s[half:] for s in slabs]
    first = []
    for k in range(P_SIZE):
        parts = []
        for rows, source in ((slice(0, half), slabs), (slice(half, count), upper_slabs)):
            if rows.start == 0 and k >= low:
                continue
            acc_s = None
            acc_d = None
            top_n = low if rows.start == 0 else P_SIZE
            for n in range(k + 1, top_n):
                piece = source[n] if rows.start else source[n][:half]
                if second[k, n] != 0.0:
                    term = float(second[k, n]) * piece
                    acc_s = term if acc_s is None else acc_s + term
                if derivative[k, n] != 0.0:
                    term = float(derivative[k, n]) * piece
                    acc_d = term if acc_d is None else acc_d + term
            part = jnp.zeros((half, PLANE), jnp.float32)
            if acc_s is not None:
                part = part + diff0[rows] * acc_s
            if acc_d is not None:
                part = part - vel0[rows] * acc_d
            parts.append(part)
        first.append(parts[0] if len(parts) == 1 else jnp.concatenate(parts, axis=0))
    stacked = jnp.concatenate([kept(a, slabs[a]) for a in range(P_SIZE)], axis=0)
    hi, lo = split_two(stacked)
    spread_hi = spread_hi_ref[...]
    wide = mxu(hi, spread_hi) + mxu(lo, spread_hi)
    fine = mxu(hi, spread_lo_ref[...])
    weight_rows = jnp.concatenate([kept(a, weight) for a in range(P_SIZE)], axis=0)
    inner = (
        weight_rows[:, 2:3] * (wide[:, 0:PLANE] + fine[:, 0:PLANE])
        + weight_rows[:, 1:2] * (wide[:, PLANE : 2 * PLANE] + fine[:, PLANE : 2 * PLANE])
        - weight_rows[:, 5:6] * wide[:, 2 * PLANE : 3 * PLANE]
        - weight_rows[:, 4:5] * wide[:, 3 * PLANE : 4 * PLANE]
    )
    blank = jnp.zeros((half, 128), jnp.float32)

    def trace_block(a, offset):
        rows = wide[start(a) : start(a) + (count if a < low else half), offset : offset + 128]
        return rows if a < low else jnp.concatenate([blank, rows], axis=0)

    own = jnp.concatenate([trace_block(a, 4 * PLANE) for a in range(P_SIZE)], axis=1)
    other = jnp.concatenate([trace_block(a, 4 * PLANE + 128) for a in range(P_SIZE)], axis=1)
    lane = lax.broadcasted_iota(jnp.int32, (1, P_SIZE * 128), 1) % 128
    across = jnp.zeros_like(own)
    for face in range(4):
        gathered = exact_pick(pick_ref[face], other)
        across = jnp.where(lane // P_SIZE == face, gathered, across)
    jump = own - across
    jump_rows = jnp.concatenate(
        [kept(a, jump[:, a * 128 : (a + 1) * 128]) for a in range(P_SIZE)], axis=0
    )
    jhi, jlo = split_two(jump_rows)
    lift_mat = lift_ref[...]
    lifted = mxu(jhi, lift_mat) + mxu(jlo, lift_mat)
    even, total = end_traces(slabs)
    if final:
        below, above = turn_pair(
            lower_ref[...], upper_ref[...], pick_ref, turn_ref[...], flip_ref[...]
        )
    news = []
    for a in range(P_SIZE):
        rows = slice(start(a), start(a) + (count if a < low else half))
        lanes = slice(a * PLANE, (a + 1) * PLANE)
        own_lift = lifted[rows] + float(lift_signs[0, a]) * kept(a, even)
        own_lift = own_lift + float(lift_signs[1, a]) * kept(a, total)
        if final:
            own_lift = own_lift - float(lift_signs[0, a]) * kept(a, below)
            own_lift = own_lift - float(lift_signs[1, a]) * kept(a, above)
        live = kept(a, top[:, lanes] <= order)
        update = jnp.where(live, first[a] + inner[rows] - own_lift, 0.0)
        if a < low:
            new = base_ref[:, lanes] + scale * update
        else:
            new = jnp.concatenate(
                [base_ref[:half, lanes] + 0.0, base_ref[half:, lanes] + scale * update], axis=0
            )
        partial_ref[:, lanes] = new
        news.append(new)
    if not final:
        even, total = end_traces(news)
        even_ref[...] = even
        total_ref[...] = total


def faces_body(
    lower_ref, upper_ref, pick_ref, turn_ref, flip_ref, top_ref, weight_ref, even_ref, total_ref,
    below_ref, above_ref, new_even_ref, new_total_ref, *, scale
):
    below, above = turn_pair(lower_ref[...], upper_ref[...], pick_ref, turn_ref[...], flip_ref[...])
    below_ref[...] = below
    above_ref[...] = above
    top = top_ref[...]
    order = weight_ref[:, 7:8]
    parts = [
        face_lift(below, above, top[:, a * PLANE : (a + 1) * PLANE] <= order, a, scale)
        for a in range(P_SIZE)
    ]
    even, total = end_traces(parts)
    new_even_ref[...] = even_ref[...] + even
    new_total_ref[...] = total_ref[...] + total


def outer_body(
    pre_ref, top_ref, weight_ref, lower_ref, upper_ref, pick_ref, turn_ref, flip_ref,
    out_ref, even_ref, total_ref, *, scale
):
    derivative, second, side_signs, weights = mode_tables()
    lift_signs = (side_signs * weights[None, :]).astype(np.float32)
    below, above = turn_pair(lower_ref[...], upper_ref[...], pick_ref, turn_ref[...], flip_ref[...])
    top = top_ref[...]
    order = weight_ref[:, 7:8]
    news = []
    for a in range(P_SIZE):
        lanes = slice(a * PLANE, (a + 1) * PLANE)
        update = float(lift_signs[0, a]) * below + float(lift_signs[1, a]) * above
        live = top[:, lanes] <= order
        new = pre_ref[:, lanes] + scale * jnp.where(live, update, 0.0)
        out_ref[:, lanes] = new
        news.append(new)
    even, total = end_traces(news)
    even_ref[...] = even
    total_ref[...] = total


def inner(operands, scale, carried, final=False):
    count = operands[0].shape[0]
    spec = pl.BlockSpec(memory_space=pltpu.VMEM)
    square = jax.ShapeDtypeStruct((count, PLANE), jnp.float32)
    field = jax.ShapeDtypeStruct(operands[0].shape, jnp.float32)
    return pl.pallas_call(
        functools.partial(inner_body, scale=scale, carried=carried, final=final),
        out_shape=field if final else (field, square, square),
        in_specs=[spec] * len(operands),
        out_specs=spec if final else (spec, spec, spec),
        compiler_params=pltpu.CompilerParams(vmem_limit_bytes=60 * 1024 * 1024),
        cost_estimate=pl.CostEstimate(
            flops=2_500_000_000, transcendentals=0, bytes_accessed=4_000_000
        ),
    )(*operands)


def faces(lower, upper, picks, codes, flip, top, weight, even, total, scale):
    count = lower.shape[0]
    spec = pl.BlockSpec(memory_space=pltpu.VMEM)
    square = jax.ShapeDtypeStruct((count, PLANE), jnp.float32)
    return pl.pallas_call(
        functools.partial(faces_body, scale=scale),
        out_shape=(square,) * 4,
        in_specs=[spec] * 9,
        out_specs=(spec,) * 4,
    )(lower, upper, picks, codes, flip, top, weight, even, total)


def outer(pre, top, weight, lower, upper, picks, codes, flip, scale):
    count = pre.shape[0]
    spec = pl.BlockSpec(memory_space=pltpu.VMEM)
    return pl.pallas_call(
        functools.partial(outer_body, scale=scale),
        out_shape=(
            jax.ShapeDtypeStruct(pre.shape, jnp.float32),
            jax.ShapeDtypeStruct((count, PLANE), jnp.float32),
            jax.ShapeDtypeStruct((count, PLANE), jnp.float32),
        ),
        in_specs=[spec] * 8,
        out_specs=(spec, spec, spec),
    )(pre, top, weight, lower, upper, picks, codes, flip)


def prep_body(placed_ref, top_ref, weight_ref, field_ref, even_ref, total_ref):
    news = []
    for a in range(P_SIZE):
        lanes = slice(a * PLANE, (a + 1) * PLANE)
        live = top_ref[:, lanes] <= weight_ref[:, 7:8]
        new = jnp.where(live, placed_ref[:, lanes], 0.0)
        field_ref[:, lanes] = new
        news.append(new)
    even, total = end_traces(news)
    even_ref[...] = even
    total_ref[...] = total


def prep(placed, top, weight):
    count = placed.shape[0]
    spec = pl.BlockSpec(memory_space=pltpu.VMEM)
    return pl.pallas_call(
        prep_body,
        out_shape=(
            jax.ShapeDtypeStruct(placed.shape, jnp.float32),
            jax.ShapeDtypeStruct((count, PLANE), jnp.float32),
            jax.ShapeDtypeStruct((count, PLANE), jnp.float32),
        ),
        in_specs=[spec] * 3,
        out_specs=(spec, spec, spec),
    )(placed, top, weight)


def exchange(even, total):
    size = lax.axis_size("dom")
    up = [(i, (i + 1) % size) for i in range(size)]
    down = [((i + 1) % size, i) for i in range(size)]
    return lax.ppermute(total, "dom", up), lax.ppermute(even, "dom", down)


def shards(
    coefficients, diffusion, velocity, orders, target, local_faces, partner_faces, partner_turns
):
    element_count = coefficients.shape[0]
    blocks_all = lax.axis_size(("dom", "face"))
    moving = element_count // 16
    destination = target // element_count
    new_slot = target % element_count
    here = lax.axis_index(("dom", "face"))
    side_info = jnp.concatenate(
        [
            diffusion,
            velocity,
            new_slot[:, None].astype(jnp.float32),
            orders[:, None].astype(jnp.float32),
        ],
        axis=1,
    )
    side_width = side_info.shape[1]
    shifts = (1, blocks_all - 1, blocks_all // 2)
    goal = (here + jnp.asarray(shifts, jnp.int32)) % blocks_all
    chosen = destination[None, :] == goal[:, None]
    rank = jnp.cumsum(chosen.astype(jnp.int32), axis=1) - 1
    hit = chosen[:, None, :] & (
        rank[:, None, :] == jnp.arange(moving, dtype=jnp.int32)[None, :, None]
    )
    rows = jnp.arange(element_count, dtype=jnp.int32)
    picked = jnp.sum(jnp.where(hit, rows[None, None, :], 0), axis=2).reshape(-1)
    side_rows = side_info[picked].reshape(len(shifts), 1, moving * side_width)
    side_rows = jnp.pad(side_rows, ((0, 0), (0, 0), (0, P_SIZE**3 - moving * side_width)))
    parcels = jnp.concatenate(
        [coefficients[picked].reshape(len(shifts), moving, P_SIZE**3), side_rows], axis=1
    )
    got_coef = [coefficients]
    got_side = [side_info]
    got_slot = [jnp.where(destination == here, new_slot, element_count)]
    for index, shift in enumerate(shifts):
        pairs = [(i, (i + shift) % blocks_all) for i in range(blocks_all)]
        arrived = lax.ppermute(parcels[index], ("dom", "face"), pairs)
        arrived_side = arrived[moving, : moving * side_width].reshape(moving, side_width)
        got_coef.append(arrived[:moving])
        got_side.append(arrived_side)
        got_slot.append(arrived_side[:, 6].astype(jnp.int32))
    got_coef = jnp.concatenate(got_coef, axis=0)
    got_side = jnp.concatenate(got_side, axis=0)
    got_slot = jnp.concatenate(got_slot, axis=0)
    hit = got_slot[None, :] == jnp.arange(element_count, dtype=jnp.int32)[:, None]
    got_rows = jnp.arange(got_slot.shape[0], dtype=jnp.int32)
    source = jnp.sum(jnp.where(hit, got_rows[None, :], 0), axis=1)
    placed_side = got_side[source]
    weight = placed_side
    top = jnp.asarray(top_modes().astype(np.float32))
    tables = kernel_tables()
    neighbours = jnp.concatenate([local_faces[0], partner_faces[0]], axis=0)
    picks = (
        neighbours[:, :, None] == jnp.arange(element_count, dtype=jnp.int32)[None, None, :]
    ).astype(jnp.bfloat16)
    codes = partner_turns[0].T
    spread_hi, spread_lo, lift, flip = tables
    field, even, total = prep(got_coef[source], top, weight)
    first_step = 0.5 * TIME_STEP
    lower, upper = exchange(even, total)
    pre, even, total = inner(
        (field, weight, top, picks, spread_hi, spread_lo, lift), first_step, None
    )
    below, above, even, total = faces(
        lower, upper, picks, codes, flip, top, weight, even, total, first_step
    )
    lower, upper = exchange(even, total)
    advanced = inner(
        (pre, below, above, field, weight, top, picks, spread_hi, spread_lo, lift)
        + (lower, upper, codes, flip),
        TIME_STEP,
        first_step,
        final=True,
    )
    return advanced


def solution(mesh):
    in_specs = (
        P(("dom", "face"), None),
        P(("dom", "face"), None),
        P(("dom", "face"), None),
        P(("dom", "face")),
        P(("dom", "face")),
        P(("dom", "face"), None, None),
        P(("dom", "face"), None, None),
        P(("dom", "face"), None, None),
    )
    out_specs = P(("dom", "face"), None)
    return jax.shard_map(shards, mesh=mesh, in_specs=in_specs, out_specs=out_specs, check_vma=False)
```

```python
import functools
import jax
import jax.numpy as jnp
import numpy as np
from jax import lax
from jax.experimental import pallas as pl
from jax.experimental.pallas import tpu as pltpu
from jax.sharding import PartitionSpec as P

P_SIZE = 16
PLANE = P_SIZE * P_SIZE
TIME_STEP = 0.25


def mode_tables():
    ladder = np.arange(P_SIZE)
    spacing = ladder[None, :] - ladder[:, None]
    derivative = np.where(
        (spacing > 0) & (spacing % 2 == 1), (2.0 * ladder[:, None] + 1.0) / P_SIZE, 0.0
    )
    second = derivative @ derivative / P_SIZE
    side_signs = np.stack([(-1.0) ** ladder, np.ones(P_SIZE)])
    weights = (2.0 * ladder + 1.0) / (2.0 * P_SIZE)
    return (derivative, second, side_signs, weights)


def side_table(values_pair):
    identity = np.eye(P_SIZE)
    return np.concatenate(
        [
            np.kron(values_pair[0][:, None], identity),
            np.kron(values_pair[1][:, None], identity),
            np.kron(identity, values_pair[0][:, None]),
            np.kron(identity, values_pair[1][:, None]),
        ],
        axis=1,
    )


def kernel_tables():
    derivative, second, side_signs, weights = mode_tables()
    derivative = derivative.astype(np.float32).astype(np.float64)
    second = second.astype(np.float32).astype(np.float64)
    identity = np.eye(P_SIZE)
    traces = side_table(side_signs)
    swapped = traces[:, [16 * g + j for g in (1, 0, 3, 2) for j in range(P_SIZE)]]
    pad = np.zeros((PLANE, 64))
    spread = np.concatenate(
        [
            np.kron(identity, second.T),
            np.kron(second.T, identity),
            np.kron(identity, derivative.T),
            np.kron(derivative.T, identity),
            traces, pad, swapped, pad,
        ],
        axis=1,
    ).astype(np.float32)
    spread_hi = spread.astype(jnp.bfloat16)
    spread_lo = (spread[:, : 2 * PLANE] - spread_hi[:, : 2 * PLANE].astype(np.float32)).astype(jnp.bfloat16)
    lift_signs = side_signs * weights[None, :]
    lift = np.concatenate([side_table(lift_signs).T, np.zeros((64, PLANE))], axis=0)
    lanes = np.arange(PLANE)
    flip = np.zeros((PLANE, PLANE))
    flip[lanes, (lanes % P_SIZE) * P_SIZE + lanes // P_SIZE] = 1.0
    return (
        jnp.asarray(spread_hi),
        jnp.asarray(spread_lo),
        jnp.asarray(lift, jnp.bfloat16),
        jnp.asarray(flip, jnp.bfloat16),
    )


def top_modes():
    ladder = np.arange(P_SIZE)
    first_idx, second_idx, third_idx = np.meshgrid(ladder, ladder, ladder, indexing="ij")
    return np.maximum(np.maximum(first_idx, second_idx), third_idx).reshape(1, -1).astype(np.int32)


def split_two(x):
    hi = x.astype(jnp.bfloat16)
    lo = (x - hi.astype(jnp.float32)).astype(jnp.bfloat16)
    return hi, lo


def mxu(a, b):
    return jnp.dot(a, b, preferred_element_type=jnp.float32)


def split_three(x):
    hi = x.astype(jnp.bfloat16)
    rest = x - hi.astype(jnp.float32)
    mid = rest.astype(jnp.bfloat16)
    lo = (rest - mid.astype(jnp.float32)).astype(jnp.bfloat16)
    return hi, mid, lo


def exact_pick(onehot, x):
    width = x.shape[1]
    joined = mxu(onehot, jnp.concatenate(split_three(x), axis=1))
    return joined[:, :width] + joined[:, width : 2 * width] + joined[:, 2 * width :]


def exact_rows(x, onehot):
    count = x.shape[0]
    joined = mxu(jnp.concatenate(split_three(x), axis=0), onehot)
    return joined[:count] + joined[count : 2 * count] + joined[2 * count :]


def end_traces(slabs):
    total = slabs[0] + slabs[1]
    even = slabs[0] - slabs[1]
    for a in range(2, P_SIZE):
        total = total + slabs[a]
        even = even + slabs[a] if a % 2 == 0 else even - slabs[a]
    return even, total


def turn_pair(lower, upper, picks, codes, flip):
    count = lower.shape[0]
    picked = jnp.concatenate([exact_pick(picks[4], lower), exact_pick(picks[5], upper)], axis=0)
    swapped = exact_rows(picked, flip)
    lane = lax.broadcasted_iota(jnp.int32, (1, PLANE), 1)
    row_odd = (lane // P_SIZE) % 2 == 1
    col_odd = lane % 2 == 1
    sides = []
    for side in range(2):
        rows = slice(side * count, (side + 1) * count)
        code = codes[:, side : side + 1]
        chosen = jnp.where(code % 2 == 1, swapped[rows], picked[rows])
        negate = ((code // 2) % 2 == 1) & row_odd
        negate = negate != (((code // 4) % 2 == 1) & col_odd)
        sides.append(jnp.where(negate, -chosen, chosen))
    return sides


def face_lift(below, above, live, a, scale):
    derivative, second, side_signs, weights = mode_tables()
    lift_signs = (side_signs * weights[None, :]).astype(np.float32)
    update = float(lift_signs[0, a]) * below + float(lift_signs[1, a]) * above
    return scale * jnp.where(live, update, 0.0)


def inner_body(*refs, scale, carried, final):
    if carried is None:
        v_ref, weight_ref, top_ref, pick_ref, spread_hi_ref, spread_lo_ref, lift_ref = refs[:7]
        base_ref = v_ref
    else:
        v_ref, below_ref, above_ref, base_ref, weight_ref, top_ref, pick_ref = refs[:7]
        spread_hi_ref, spread_lo_ref, lift_ref = refs[7:10]
    if final:
        lower_ref, upper_ref, turn_ref, flip_ref = refs[10:14]
        partial_ref = refs[-1]
    else:
        partial_ref, even_ref, total_ref = refs[-3:]
    count = v_ref.shape[0]
    derivative, second, side_signs, weights = mode_tables()
    second = second.astype(np.float32)
    derivative = derivative.astype(np.float32)
    lift_signs = (side_signs * weights[None, :]).astype(np.float32)
    weight = weight_ref[...]
    top = top_ref[...]
    order = weight[:, 7:8]
    slabs = [v_ref[:, a * PLANE : (a + 1) * PLANE] for a in range(P_SIZE)]
    if carried is not None:
        below = below_ref[...]
        above = above_ref[...]
        slabs = [
            slabs[a] + face_lift(below, above, top[:, a * PLANE : (a + 1) * PLANE] <= order, a, carried)
            for a in range(P_SIZE)
        ]
    diff0 = jnp.broadcast_to(weight[:, 0:1], (count, PLANE))
    vel0 = jnp.broadcast_to(weight[:, 3:4], (count, PLANE))
    half = count // 2
    low = P_SIZE // 2

    def kept(a, x):
        return x if a < low else x[half:]

    def start(a):
        return a * count if a < low else low * count + (a - low) * half

    upper_slabs = [s[half:] for s in slabs]
    first = []
    for k in range(P_SIZE):
        parts = []
        for rows, source in ((slice(0, half), slabs), (slice(half, count), upper_slabs)):
            if rows.start == 0 and k >= low:
                continue
            acc_s = None
            acc_d = None
            top_n = low if rows.start == 0 else P_SIZE
            for n in range(k + 1, top_n):
                piece = source[n] if rows.start else source[n][:half]
                if second[k, n] != 0.0:
                    term = float(second[k, n]) * piece
                    acc_s = term if acc_s is None else acc_s + term
                if derivative[k, n] != 0.0:
                    term = float(derivative[k, n]) * piece
                    acc_d = term if acc_d is None else acc_d + term
            part = jnp.zeros((half, PLANE), jnp.float32)
            if acc_s is not None:
                part = part + diff0[rows] * acc_s
            if acc_d is not None:
                part = part - vel0[rows] * acc_d
            parts.append(part)
        first.append(parts[0] if len(parts) == 1 else jnp.concatenate(parts, axis=0))
    stacked = jnp.concatenate([kept(a, slabs[a]) for a in range(P_SIZE)], axis=0)
    hi, lo = split_two(stacked)
    spread_hi = spread_hi_ref[...]
    wide = mxu(hi, spread_hi) + mxu(lo, spread_hi)
    fine = mxu(hi, spread_lo_ref[...])
    weight_rows = jnp.concatenate([kept(a, weight) for a in range(P_SIZE)], axis=0)
    inner = (
        weight_rows[:, 2:3] * (wide[:, 0:PLANE] + fine[:, 0:PLANE])
        + weight_rows[:, 1:2] * (wide[:, PLANE : 2 * PLANE] + fine[:, PLANE : 2 * PLANE])
        - weight_rows[:, 5:6] * wide[:, 2 * PLANE : 3 * PLANE]
        - weight_rows[:, 4:5] * wide[:, 3 * PLANE : 4 * PLANE]
    )
    blank = jnp.zeros((half, 128), jnp.float32)

    def trace_block(a, offset):
        rows = wide[start(a) : start(a) + (count if a < low else half), offset : offset + 128]
        return rows if a < low else jnp.concatenate([blank, rows], axis=0)

    own = jnp.concatenate([trace_block(a, 4 * PLANE) for a in range(P_SIZE)], axis=1)
    other = jnp.concatenate([trace_block(a, 4 * PLANE + 128) for a in range(P_SIZE)], axis=1)
    lane = lax.broadcasted_iota(jnp.int32, (1, P_SIZE * 128), 1) % 128
    across = jnp.zeros_like(own)
    for face in range(4):
        gathered = exact_pick(pick_ref[face], other)
        across = jnp.where(lane // P_SIZE == face, gathered, across)
    jump = own - across
    jump_rows = jnp.concatenate(
        [kept(a, jump[:, a * 128 : (a + 1) * 128]) for a in range(P_SIZE)], axis=0
    )
    jhi, jlo = split_two(jump_rows)
    lift_mat = lift_ref[...]
    lifted = mxu(jhi, lift_mat) + mxu(jlo, lift_mat)
    even, total = end_traces(slabs)
    if final:
        below, above = turn_pair(
            lower_ref[...], upper_ref[...], pick_ref, turn_ref[...], flip_ref[...]
        )
    news = []
    for a in range(P_SIZE):
        rows = slice(start(a), start(a) + (count if a < low else half))
        lanes = slice(a * PLANE, (a + 1) * PLANE)
        own_lift = lifted[rows] + float(lift_signs[0, a]) * kept(a, even)
        own_lift = own_lift + float(lift_signs[1, a]) * kept(a, total)
        if final:
            own_lift = own_lift - float(lift_signs[0, a]) * kept(a, below)
            own_lift = own_lift - float(lift_signs[1, a]) * kept(a, above)
        live = kept(a, top[:, lanes] <= order)
        update = jnp.where(live, first[a] + inner[rows] - own_lift, 0.0)
        if a < low:
            new = base_ref[:, lanes] + scale * update
        else:
            new = jnp.concatenate(
                [base_ref[:half, lanes] + 0.0, base_ref[half:, lanes] + scale * update], axis=0
            )
        partial_ref[:, lanes] = new
        news.append(new)
    if not final:
        even, total = end_traces(news)
        even_ref[...] = even
        total_ref[...] = total


def faces_body(
    lower_ref, upper_ref, pick_ref, turn_ref, flip_ref, top_ref, weight_ref, even_ref, total_ref,
    below_ref, above_ref, new_even_ref, new_total_ref, *, scale
):
    below, above = turn_pair(lower_ref[...], upper_ref[...], pick_ref, turn_ref[...], flip_ref[...])
    below_ref[...] = below
    above_ref[...] = above
    top = top_ref[...]
    order = weight_ref[:, 7:8]
    parts = [
        face_lift(below, above, top[:, a * PLANE : (a + 1) * PLANE] <= order, a, scale)
        for a in range(P_SIZE)
    ]
    even, total = end_traces(parts)
    new_even_ref[...] = even_ref[...] + even
    new_total_ref[...] = total_ref[...] + total


def outer_body(
    pre_ref, top_ref, weight_ref, lower_ref, upper_ref, pick_ref, turn_ref, flip_ref,
    out_ref, even_ref, total_ref, *, scale
):
    derivative, second, side_signs, weights = mode_tables()
    lift_signs = (side_signs * weights[None, :]).astype(np.float32)
    below, above = turn_pair(lower_ref[...], upper_ref[...], pick_ref, turn_ref[...], flip_ref[...])
    top = top_ref[...]
    order = weight_ref[:, 7:8]
    news = []
    for a in range(P_SIZE):
        lanes = slice(a * PLANE, (a + 1) * PLANE)
        update = float(lift_signs[0, a]) * below + float(lift_signs[1, a]) * above
        live = top[:, lanes] <= order
        new = pre_ref[:, lanes] + scale * jnp.where(live, update, 0.0)
        out_ref[:, lanes] = new
        news.append(new)
    even, total = end_traces(news)
    even_ref[...] = even
    total_ref[...] = total


def inner(operands, scale, carried, final=False):
    count = operands[0].shape[0]
    spec = pl.BlockSpec(memory_space=pltpu.VMEM)
    square = jax.ShapeDtypeStruct((count, PLANE), jnp.float32)
    field = jax.ShapeDtypeStruct(operands[0].shape, jnp.float32)
    return pl.pallas_call(
        functools.partial(inner_body, scale=scale, carried=carried, final=final),
        out_shape=field if final else (field, square, square),
        in_specs=[spec] * len(operands),
        out_specs=spec if final else (spec, spec, spec),
        compiler_params=pltpu.CompilerParams(vmem_limit_bytes=60 * 1024 * 1024),
        cost_estimate=pl.CostEstimate(
            flops=2_500_000_000, transcendentals=0, bytes_accessed=4_000_000
        ),
    )(*operands)


def faces(lower, upper, picks, codes, flip, top, weight, even, total, scale):
    count = lower.shape[0]
    spec = pl.BlockSpec(memory_space=pltpu.VMEM)
    square = jax.ShapeDtypeStruct((count, PLANE), jnp.float32)
    return pl.pallas_call(
        functools.partial(faces_body, scale=scale),
        out_shape=(square,) * 4,
        in_specs=[spec] * 9,
        out_specs=(spec,) * 4,
    )(lower, upper, picks, codes, flip, top, weight, even, total)


def outer(pre, top, weight, lower, upper, picks, codes, flip, scale):
    count = pre.shape[0]
    spec = pl.BlockSpec(memory_space=pltpu.VMEM)
    return pl.pallas_call(
        functools.partial(outer_body, scale=scale),
        out_shape=(
            jax.ShapeDtypeStruct(pre.shape, jnp.float32),
            jax.ShapeDtypeStruct((count, PLANE), jnp.float32),
            jax.ShapeDtypeStruct((count, PLANE), jnp.float32),
        ),
        in_specs=[spec] * 8,
        out_specs=(spec, spec, spec),
    )(pre, top, weight, lower, upper, picks, codes, flip)


def prep_body(placed_ref, top_ref, weight_ref, field_ref, even_ref, total_ref):
    news = []
    for a in range(P_SIZE):
        lanes = slice(a * PLANE, (a + 1) * PLANE)
        live = top_ref[:, lanes] <= weight_ref[:, 7:8]
        new = jnp.where(live, placed_ref[:, lanes], 0.0)
        field_ref[:, lanes] = new
        news.append(new)
    even, total = end_traces(news)
    even_ref[...] = even
    total_ref[...] = total


def prep(placed, top, weight):
    count = placed.shape[0]
    spec = pl.BlockSpec(memory_space=pltpu.VMEM)
    return pl.pallas_call(
        prep_body,
        out_shape=(
            jax.ShapeDtypeStruct(placed.shape, jnp.float32),
            jax.ShapeDtypeStruct((count, PLANE), jnp.float32),
            jax.ShapeDtypeStruct((count, PLANE), jnp.float32),
        ),
        in_specs=[spec] * 3,
        out_specs=(spec, spec, spec),
    )(placed, top, weight)


def exchange(even, total):
    size = lax.axis_size("dom")
    up = [(i, (i + 1) % size) for i in range(size)]
    down = [((i + 1) % size, i) for i in range(size)]
    return lax.ppermute(total, "dom", up), lax.ppermute(even, "dom", down)


def shards(
    coefficients, diffusion, velocity, orders, target, local_faces, partner_faces, partner_turns
):
    element_count = coefficients.shape[0]
    blocks_all = lax.axis_size(("dom", "face"))
    moving = element_count // 16
    destination = target // element_count
    new_slot = target % element_count
    here = lax.axis_index(("dom", "face"))
    side_info = jnp.concatenate(
        [
            diffusion,
            velocity,
            new_slot[:, None].astype(jnp.float32),
            orders[:, None].astype(jnp.float32),
        ],
        axis=1,
    )
    side_width = side_info.shape[1]
    shifts = (1, blocks_all - 1, blocks_all // 2)
    goal = (here + jnp.asarray(shifts, jnp.int32)) % blocks_all
    chosen = destination[None, :] == goal[:, None]
    rank = jnp.cumsum(chosen.astype(jnp.int32), axis=1) - 1
    hit = chosen[:, None, :] & (
        rank[:, None, :] == jnp.arange(moving, dtype=jnp.int32)[None, :, None]
    )
    rows = jnp.arange(element_count, dtype=jnp.int32)
    picked = jnp.sum(jnp.where(hit, rows[None, None, :], 0), axis=2).reshape(-1)
    side_rows = side_info[picked].reshape(len(shifts), 1, moving * side_width)
    side_rows = jnp.pad(side_rows, ((0, 0), (0, 0), (0, P_SIZE**3 - moving * side_width)))
    parcels = jnp.concatenate(
        [
            jnp.einsum(
                "qjr,rc->qjc", hit.astype(jnp.float32), coefficients, precision=lax.Precision.HIGHEST
            ),
            side_rows,
        ],
        axis=1,
    )
    got_coef = [coefficients]
    got_side = [side_info]
    got_slot = [jnp.where(destination == here, new_slot, element_count)]
    for index, shift in enumerate(shifts):
        pairs = [(i, (i + shift) % blocks_all) for i in range(blocks_all)]
        arrived = lax.ppermute(parcels[index], ("dom", "face"), pairs)
        arrived_side = arrived[moving, : moving * side_width].reshape(moving, side_width)
        got_coef.append(arrived[:moving])
        got_side.append(arrived_side)
        got_slot.append(arrived_side[:, 6].astype(jnp.int32))
    got_coef = jnp.concatenate(got_coef, axis=0)
    got_side = jnp.concatenate(got_side, axis=0)
    got_slot = jnp.concatenate(got_slot, axis=0)
    hit = got_slot[None, :] == jnp.arange(element_count, dtype=jnp.int32)[:, None]
    got_rows = jnp.arange(got_slot.shape[0], dtype=jnp.int32)
    source = jnp.sum(jnp.where(hit, got_rows[None, :], 0), axis=1)
    placing = (got_slot[None, :] == jnp.arange(element_count, dtype=jnp.int32)[:, None]).astype(
        jnp.float32
    )
    placed_side = got_side[source]
    weight = placed_side
    top = jnp.asarray(top_modes().astype(np.float32))
    tables = kernel_tables()
    neighbours = jnp.concatenate([local_faces[0], partner_faces[0]], axis=0)
    picks = (
        neighbours[:, :, None] == jnp.arange(element_count, dtype=jnp.int32)[None, None, :]
    ).astype(jnp.bfloat16)
    codes = partner_turns[0].T
    spread_hi, spread_lo, lift, flip = tables
    placed = jnp.dot(placing, got_coef, precision=lax.Precision.HIGHEST)
    field, even, total = prep(placed, top, weight)
    first_step = 0.5 * TIME_STEP
    lower, upper = exchange(even, total)
    pre, even, total = inner(
        (field, weight, top, picks, spread_hi, spread_lo, lift), first_step, None
    )
    below, above, even, total = faces(
        lower, upper, picks, codes, flip, top, weight, even, total, first_step
    )
    lower, upper = exchange(even, total)
    advanced = inner(
        (pre, below, above, field, weight, top, picks, spread_hi, spread_lo, lift)
        + (lower, upper, codes, flip),
        TIME_STEP,
        first_step,
        final=True,
    )
    return advanced


def solution(mesh):
    in_specs = (
        P(("dom", "face"), None),
        P(("dom", "face"), None),
        P(("dom", "face"), None),
        P(("dom", "face")),
        P(("dom", "face")),
        P(("dom", "face"), None, None),
        P(("dom", "face"), None, None),
        P(("dom", "face"), None, None),
    )
    out_specs = P(("dom", "face"), None)
    return jax.shard_map(shards, mesh=mesh, in_specs=in_specs, out_specs=out_specs, check_vma=False)
```

```python
import functools
import jax
import jax.numpy as jnp
import numpy as np
from jax import lax
from jax.experimental import pallas as pl
from jax.experimental.pallas import tpu as pltpu
from jax.sharding import PartitionSpec as P

P_SIZE = 16
PLANE = P_SIZE * P_SIZE
TIME_STEP = 0.25


def mode_tables():
    ladder = np.arange(P_SIZE)
    spacing = ladder[None, :] - ladder[:, None]
    derivative = np.where(
        (spacing > 0) & (spacing % 2 == 1), (2.0 * ladder[:, None] + 1.0) / P_SIZE, 0.0
    )
    second = derivative @ derivative / P_SIZE
    side_signs = np.stack([(-1.0) ** ladder, np.ones(P_SIZE)])
    weights = (2.0 * ladder + 1.0) / (2.0 * P_SIZE)
    return (derivative, second, side_signs, weights)


def side_table(values_pair):
    identity = np.eye(P_SIZE)
    return np.concatenate(
        [
            np.kron(values_pair[0][:, None], identity),
            np.kron(values_pair[1][:, None], identity),
            np.kron(identity, values_pair[0][:, None]),
            np.kron(identity, values_pair[1][:, None]),
        ],
        axis=1,
    )


def kernel_tables():
    derivative, second, side_signs, weights = mode_tables()
    derivative = derivative.astype(np.float32).astype(np.float64)
    second = second.astype(np.float32).astype(np.float64)
    identity = np.eye(P_SIZE)
    traces = side_table(side_signs)
    swapped = traces[:, [16 * g + j for g in (1, 0, 3, 2) for j in range(P_SIZE)]]
    pad = np.zeros((PLANE, 64))
    spread = np.concatenate(
        [
            np.kron(identity, second.T),
            np.kron(second.T, identity),
            np.kron(identity, derivative.T),
            np.kron(derivative.T, identity),
            traces, pad, swapped, pad,
        ],
        axis=1,
    ).astype(np.float32)
    spread_hi = spread.astype(jnp.bfloat16)
    spread_lo = (spread[:, : 2 * PLANE] - spread_hi[:, : 2 * PLANE].astype(np.float32)).astype(jnp.bfloat16)
    lift_signs = side_signs * weights[None, :]
    lift = np.concatenate([side_table(lift_signs).T, np.zeros((64, PLANE))], axis=0)
    lanes = np.arange(PLANE)
    flip = np.zeros((PLANE, PLANE))
    flip[lanes, (lanes % P_SIZE) * P_SIZE + lanes // P_SIZE] = 1.0
    return (
        jnp.asarray(spread_hi),
        jnp.asarray(spread_lo),
        jnp.asarray(lift, jnp.bfloat16),
        jnp.asarray(flip, jnp.bfloat16),
    )


def top_modes():
    ladder = np.arange(P_SIZE)
    first_idx, second_idx, third_idx = np.meshgrid(ladder, ladder, ladder, indexing="ij")
    return np.maximum(np.maximum(first_idx, second_idx), third_idx).reshape(1, -1).astype(np.int32)


def split_two(x):
    hi = x.astype(jnp.bfloat16)
    lo = (x - hi.astype(jnp.float32)).astype(jnp.bfloat16)
    return hi, lo


def mxu(a, b):
    return jnp.dot(a, b, preferred_element_type=jnp.float32)


def split_three(x):
    hi = x.astype(jnp.bfloat16)
    rest = x - hi.astype(jnp.float32)
    mid = rest.astype(jnp.bfloat16)
    lo = (rest - mid.astype(jnp.float32)).astype(jnp.bfloat16)
    return hi, mid, lo


def exact_pick(onehot, x):
    width = x.shape[1]
    joined = mxu(onehot, jnp.concatenate(split_three(x), axis=1))
    return joined[:, :width] + joined[:, width : 2 * width] + joined[:, 2 * width :]


def exact_rows(x, onehot):
    count = x.shape[0]
    joined = mxu(jnp.concatenate(split_three(x), axis=0), onehot)
    return joined[:count] + joined[count : 2 * count] + joined[2 * count :]


def end_traces(slabs):
    total = slabs[0] + slabs[1]
    even = slabs[0] - slabs[1]
    for a in range(2, P_SIZE):
        total = total + slabs[a]
        even = even + slabs[a] if a % 2 == 0 else even - slabs[a]
    return even, total


def turn_pair(lower, upper, picks, codes, flip):
    count = lower.shape[0]
    picked = jnp.concatenate([exact_pick(picks[4], lower), exact_pick(picks[5], upper)], axis=0)
    swapped = exact_rows(picked, flip)
    lane = lax.broadcasted_iota(jnp.int32, (1, PLANE), 1)
    row_odd = (lane // P_SIZE) % 2 == 1
    col_odd = lane % 2 == 1
    sides = []
    for side in range(2):
        rows = slice(side * count, (side + 1) * count)
        code = codes[:, side : side + 1]
        chosen = jnp.where(code % 2 == 1, swapped[rows], picked[rows])
        negate = ((code // 2) % 2 == 1) & row_odd
        negate = negate != (((code // 4) % 2 == 1) & col_odd)
        sides.append(jnp.where(negate, -chosen, chosen))
    return sides


def face_lift(below, above, live, a, scale):
    derivative, second, side_signs, weights = mode_tables()
    lift_signs = (side_signs * weights[None, :]).astype(np.float32)
    update = float(lift_signs[0, a]) * below + float(lift_signs[1, a]) * above
    return scale * jnp.where(live, update, 0.0)


def inner_body(*refs, scale, carried, final):
    refs, (hi_buf, lo_buf, lift_buf, table_sems) = refs[:-4], refs[-4:]
    if carried is None:
        v_ref, weight_ref, top_ref, pick_ref, spread_hi_ref, spread_lo_ref, lift_ref = refs[:7]
        base_ref = v_ref
    else:
        v_ref, below_ref, above_ref, base_ref, weight_ref, top_ref, pick_ref = refs[:7]
        spread_hi_ref, spread_lo_ref, lift_ref = refs[7:10]
    if final:
        lower_ref, upper_ref, turn_ref, flip_ref = refs[10:14]
        partial_ref = refs[-1]
    else:
        partial_ref, even_ref, total_ref = refs[-3:]
    table_copies = [
        pltpu.make_async_copy(source, target, table_sems.at[index])
        for index, (source, target) in enumerate(
            ((spread_hi_ref, hi_buf), (spread_lo_ref, lo_buf), (lift_ref, lift_buf))
        )
    ]
    for copy in table_copies:
        copy.start()
    count = v_ref.shape[0]
    derivative, second, side_signs, weights = mode_tables()
    second = second.astype(np.float32)
    derivative = derivative.astype(np.float32)
    lift_signs = (side_signs * weights[None, :]).astype(np.float32)
    weight = weight_ref[...]
    top = top_ref[...]
    order = weight[:, 7:8]
    slabs = [v_ref[:, a * PLANE : (a + 1) * PLANE] for a in range(P_SIZE)]
    if carried is not None:
        below = below_ref[...]
        above = above_ref[...]
        slabs = [
            slabs[a] + face_lift(below, above, top[:, a * PLANE : (a + 1) * PLANE] <= order, a, carried)
            for a in range(P_SIZE)
        ]
    diff0 = jnp.broadcast_to(weight[:, 0:1], (count, PLANE))
    vel0 = jnp.broadcast_to(weight[:, 3:4], (count, PLANE))
    half = count // 2
    low = P_SIZE // 2

    def kept(a, x):
        return x if a < low else x[half:]

    def start(a):
        return a * count if a < low else low * count + (a - low) * half

    upper_slabs = [s[half:] for s in slabs]
    first = []
    for k in range(P_SIZE):
        parts = []
        for rows, source in ((slice(0, half), slabs), (slice(half, count), upper_slabs)):
            if rows.start == 0 and k >= low:
                continue
            acc_s = None
            acc_d = None
            top_n = low if rows.start == 0 else P_SIZE
            for n in range(k + 1, top_n):
                piece = source[n] if rows.start else source[n][:half]
                if second[k, n] != 0.0:
                    term = float(second[k, n]) * piece
                    acc_s = term if acc_s is None else acc_s + term
                if derivative[k, n] != 0.0:
                    term = float(derivative[k, n]) * piece
                    acc_d = term if acc_d is None else acc_d + term
            part = jnp.zeros((half, PLANE), jnp.float32)
            if acc_s is not None:
                part = part + diff0[rows] * acc_s
            if acc_d is not None:
                part = part - vel0[rows] * acc_d
            parts.append(part)
        first.append(parts[0] if len(parts) == 1 else jnp.concatenate(parts, axis=0))
    stacked = jnp.concatenate([kept(a, slabs[a]) for a in range(P_SIZE)], axis=0)
    hi, lo = split_two(stacked)
    table_copies[0].wait()
    table_copies[1].wait()
    spread_hi = hi_buf[...]
    wide = mxu(hi, spread_hi) + mxu(lo, spread_hi)
    fine = mxu(hi, lo_buf[...])
    weight_rows = jnp.concatenate([kept(a, weight) for a in range(P_SIZE)], axis=0)
    inner = (
        weight_rows[:, 2:3] * (wide[:, 0:PLANE] + fine[:, 0:PLANE])
        + weight_rows[:, 1:2] * (wide[:, PLANE : 2 * PLANE] + fine[:, PLANE : 2 * PLANE])
        - weight_rows[:, 5:6] * wide[:, 2 * PLANE : 3 * PLANE]
        - weight_rows[:, 4:5] * wide[:, 3 * PLANE : 4 * PLANE]
    )
    blank = jnp.zeros((half, 128), jnp.float32)

    def trace_block(a, offset):
        rows = wide[start(a) : start(a) + (count if a < low else half), offset : offset + 128]
        return rows if a < low else jnp.concatenate([blank, rows], axis=0)

    own = jnp.concatenate([trace_block(a, 4 * PLANE) for a in range(P_SIZE)], axis=1)
    other = jnp.concatenate([trace_block(a, 4 * PLANE + 128) for a in range(P_SIZE)], axis=1)
    lane = lax.broadcasted_iota(jnp.int32, (1, P_SIZE * 128), 1) % 128
    across = jnp.zeros_like(own)
    for face in range(4):
        gathered = exact_pick(pick_ref[face], other)
        across = jnp.where(lane // P_SIZE == face, gathered, across)
    jump = own - across
    jump_rows = jnp.concatenate(
        [kept(a, jump[:, a * 128 : (a + 1) * 128]) for a in range(P_SIZE)], axis=0
    )
    jhi, jlo = split_two(jump_rows)
    table_copies[2].wait()
    lift_mat = lift_buf[...]
    lifted = mxu(jhi, lift_mat) + mxu(jlo, lift_mat)
    even, total = end_traces(slabs)
    if final:
        below, above = turn_pair(
            lower_ref[...], upper_ref[...], pick_ref, turn_ref[...], flip_ref[...]
        )
    news = []
    for a in range(P_SIZE):
        rows = slice(start(a), start(a) + (count if a < low else half))
        lanes = slice(a * PLANE, (a + 1) * PLANE)
        own_lift = lifted[rows] + float(lift_signs[0, a]) * kept(a, even)
        own_lift = own_lift + float(lift_signs[1, a]) * kept(a, total)
        if final:
            own_lift = own_lift - float(lift_signs[0, a]) * kept(a, below)
            own_lift = own_lift - float(lift_signs[1, a]) * kept(a, above)
        live = kept(a, top[:, lanes] <= order)
        update = jnp.where(live, first[a] + inner[rows] - own_lift, 0.0)
        if a < low:
            new = base_ref[:, lanes] + scale * update
        else:
            new = jnp.concatenate(
                [base_ref[:half, lanes] + 0.0, base_ref[half:, lanes] + scale * update], axis=0
            )
        partial_ref[:, lanes] = new
        news.append(new)
    if not final:
        even, total = end_traces(news)
        even_ref[...] = even
        total_ref[...] = total


def faces_body(
    lower_ref, upper_ref, pick_ref, turn_ref, flip_ref, top_ref, weight_ref, even_ref, total_ref,
    below_ref, above_ref, new_even_ref, new_total_ref, *, scale
):
    below, above = turn_pair(lower_ref[...], upper_ref[...], pick_ref, turn_ref[...], flip_ref[...])
    below_ref[...] = below
    above_ref[...] = above
    top = top_ref[...]
    order = weight_ref[:, 7:8]
    parts = [
        face_lift(below, above, top[:, a * PLANE : (a + 1) * PLANE] <= order, a, scale)
        for a in range(P_SIZE)
    ]
    even, total = end_traces(parts)
    new_even_ref[...] = even_ref[...] + even
    new_total_ref[...] = total_ref[...] + total


def outer_body(
    pre_ref, top_ref, weight_ref, lower_ref, upper_ref, pick_ref, turn_ref, flip_ref,
    out_ref, even_ref, total_ref, *, scale
):
    derivative, second, side_signs, weights = mode_tables()
    lift_signs = (side_signs * weights[None, :]).astype(np.float32)
    below, above = turn_pair(lower_ref[...], upper_ref[...], pick_ref, turn_ref[...], flip_ref[...])
    top = top_ref[...]
    order = weight_ref[:, 7:8]
    news = []
    for a in range(P_SIZE):
        lanes = slice(a * PLANE, (a + 1) * PLANE)
        update = float(lift_signs[0, a]) * below + float(lift_signs[1, a]) * above
        live = top[:, lanes] <= order
        new = pre_ref[:, lanes] + scale * jnp.where(live, update, 0.0)
        out_ref[:, lanes] = new
        news.append(new)
    even, total = end_traces(news)
    even_ref[...] = even
    total_ref[...] = total


def inner(operands, scale, carried, final=False):
    count = operands[0].shape[0]
    spec = pl.BlockSpec(memory_space=pltpu.VMEM)
    square = jax.ShapeDtypeStruct((count, PLANE), jnp.float32)
    field = jax.ShapeDtypeStruct(operands[0].shape, jnp.float32)
    first_table = 4 if carried is None else 7
    in_specs = [spec] * len(operands)
    for index in range(first_table, first_table + 3):
        in_specs[index] = pl.BlockSpec(memory_space=pl.ANY)
    tables = operands[first_table : first_table + 3]
    return pl.pallas_call(
        functools.partial(inner_body, scale=scale, carried=carried, final=final),
        out_shape=field if final else (field, square, square),
        in_specs=in_specs,
        out_specs=spec if final else (spec, spec, spec),
        scratch_shapes=[pltpu.VMEM(table.shape, table.dtype) for table in tables]
        + [pltpu.SemaphoreType.DMA((3,))],
        compiler_params=pltpu.CompilerParams(vmem_limit_bytes=60 * 1024 * 1024),
        cost_estimate=pl.CostEstimate(
            flops=2_500_000_000, transcendentals=0, bytes_accessed=4_000_000
        ),
    )(*operands)


def faces(lower, upper, picks, codes, flip, top, weight, even, total, scale):
    count = lower.shape[0]
    spec = pl.BlockSpec(memory_space=pltpu.VMEM)
    square = jax.ShapeDtypeStruct((count, PLANE), jnp.float32)
    return pl.pallas_call(
        functools.partial(faces_body, scale=scale),
        out_shape=(square,) * 4,
        in_specs=[spec] * 9,
        out_specs=(spec,) * 4,
    )(lower, upper, picks, codes, flip, top, weight, even, total)


def outer(pre, top, weight, lower, upper, picks, codes, flip, scale):
    count = pre.shape[0]
    spec = pl.BlockSpec(memory_space=pltpu.VMEM)
    return pl.pallas_call(
        functools.partial(outer_body, scale=scale),
        out_shape=(
            jax.ShapeDtypeStruct(pre.shape, jnp.float32),
            jax.ShapeDtypeStruct((count, PLANE), jnp.float32),
            jax.ShapeDtypeStruct((count, PLANE), jnp.float32),
        ),
        in_specs=[spec] * 8,
        out_specs=(spec, spec, spec),
    )(pre, top, weight, lower, upper, picks, codes, flip)


def prep_body(placed_ref, top_ref, weight_ref, field_ref, even_ref, total_ref):
    news = []
    for a in range(P_SIZE):
        lanes = slice(a * PLANE, (a + 1) * PLANE)
        live = top_ref[:, lanes] <= weight_ref[:, 7:8]
        new = jnp.where(live, placed_ref[:, lanes], 0.0)
        field_ref[:, lanes] = new
        news.append(new)
    even, total = end_traces(news)
    even_ref[...] = even
    total_ref[...] = total


def prep(placed, top, weight):
    count = placed.shape[0]
    spec = pl.BlockSpec(memory_space=pltpu.VMEM)
    return pl.pallas_call(
        prep_body,
        out_shape=(
            jax.ShapeDtypeStruct(placed.shape, jnp.float32),
            jax.ShapeDtypeStruct((count, PLANE), jnp.float32),
            jax.ShapeDtypeStruct((count, PLANE), jnp.float32),
        ),
        in_specs=[spec] * 3,
        out_specs=(spec, spec, spec),
    )(placed, top, weight)


def exchange(even, total):
    size = lax.axis_size("dom")
    up = [(i, (i + 1) % size) for i in range(size)]
    down = [((i + 1) % size, i) for i in range(size)]
    return lax.ppermute(total, "dom", up), lax.ppermute(even, "dom", down)


def shards(
    coefficients, diffusion, velocity, orders, target, local_faces, partner_faces, partner_turns
):
    element_count = coefficients.shape[0]
    blocks_all = lax.axis_size(("dom", "face"))
    moving = element_count // 16
    destination = target // element_count
    new_slot = target % element_count
    here = lax.axis_index(("dom", "face"))
    side_info = jnp.concatenate(
        [
            diffusion,
            velocity,
            new_slot[:, None].astype(jnp.float32),
            orders[:, None].astype(jnp.float32),
        ],
        axis=1,
    )
    side_width = side_info.shape[1]
    shifts = (1, blocks_all - 1, blocks_all // 2)
    goal = (here + jnp.asarray(shifts, jnp.int32)) % blocks_all
    chosen = destination[None, :] == goal[:, None]
    rank = jnp.cumsum(chosen.astype(jnp.int32), axis=1) - 1
    hit = chosen[:, None, :] & (
        rank[:, None, :] == jnp.arange(moving, dtype=jnp.int32)[None, :, None]
    )
    rows = jnp.arange(element_count, dtype=jnp.int32)
    picked = jnp.sum(jnp.where(hit, rows[None, None, :], 0), axis=2).reshape(-1)
    side_rows = side_info[picked].reshape(len(shifts), 1, moving * side_width)
    side_rows = jnp.pad(side_rows, ((0, 0), (0, 0), (0, P_SIZE**3 - moving * side_width)))
    parcels = jnp.concatenate(
        [
            jnp.einsum(
                "qjr,rc->qjc", hit.astype(jnp.float32), coefficients, precision=lax.Precision.HIGHEST
            ),
            side_rows,
        ],
        axis=1,
    )
    got_coef = [coefficients]
    got_side = [side_info]
    got_slot = [jnp.where(destination == here, new_slot, element_count)]
    for index, shift in enumerate(shifts):
        pairs = [(i, (i + shift) % blocks_all) for i in range(blocks_all)]
        arrived = lax.ppermute(parcels[index], ("dom", "face"), pairs)
        arrived_side = arrived[moving, : moving * side_width].reshape(moving, side_width)
        got_coef.append(arrived[:moving])
        got_side.append(arrived_side)
        got_slot.append(arrived_side[:, 6].astype(jnp.int32))
    got_coef = jnp.concatenate(got_coef, axis=0)
    got_side = jnp.concatenate(got_side, axis=0)
    got_slot = jnp.concatenate(got_slot, axis=0)
    hit = got_slot[None, :] == jnp.arange(element_count, dtype=jnp.int32)[:, None]
    got_rows = jnp.arange(got_slot.shape[0], dtype=jnp.int32)
    source = jnp.sum(jnp.where(hit, got_rows[None, :], 0), axis=1)
    placing = (got_slot[None, :] == jnp.arange(element_count, dtype=jnp.int32)[:, None]).astype(
        jnp.float32
    )
    placed_side = got_side[source]
    weight = placed_side
    top = jnp.asarray(top_modes().astype(np.float32))
    tables = kernel_tables()
    neighbours = jnp.concatenate([local_faces[0], partner_faces[0]], axis=0)
    picks = (
        neighbours[:, :, None] == jnp.arange(element_count, dtype=jnp.int32)[None, None, :]
    ).astype(jnp.bfloat16)
    codes = partner_turns[0].T
    spread_hi, spread_lo, lift, flip = tables
    placed = jnp.dot(placing, got_coef, precision=lax.Precision.HIGHEST)
    field, even, total = prep(placed, top, weight)
    first_step = 0.5 * TIME_STEP
    lower, upper = exchange(even, total)
    pre, even, total = inner(
        (field, weight, top, picks, spread_hi, spread_lo, lift), first_step, None
    )
    below, above, even, total = faces(
        lower, upper, picks, codes, flip, top, weight, even, total, first_step
    )
    lower, upper = exchange(even, total)
    advanced = inner(
        (pre, below, above, field, weight, top, picks, spread_hi, spread_lo, lift)
        + (lower, upper, codes, flip),
        TIME_STEP,
        first_step,
        final=True,
    )
    return advanced


def solution(mesh):
    in_specs = (
        P(("dom", "face"), None),
        P(("dom", "face"), None),
        P(("dom", "face"), None),
        P(("dom", "face")),
        P(("dom", "face")),
        P(("dom", "face"), None, None),
        P(("dom", "face"), None, None),
        P(("dom", "face"), None, None),
    )
    out_specs = P(("dom", "face"), None)
    return jax.shard_map(shards, mesh=mesh, in_specs=in_specs, out_specs=out_specs, check_vma=False)
```

```python
import functools
import jax
import jax.numpy as jnp
import numpy as np
from jax import lax
from jax.experimental import pallas as pl
from jax.experimental.pallas import tpu as pltpu
from jax.sharding import PartitionSpec as P

P_SIZE = 16
PLANE = P_SIZE * P_SIZE
TIME_STEP = 0.25


def mode_tables():
    ladder = np.arange(P_SIZE)
    spacing = ladder[None, :] - ladder[:, None]
    derivative = np.where(
        (spacing > 0) & (spacing % 2 == 1), (2.0 * ladder[:, None] + 1.0) / P_SIZE, 0.0
    )
    second = derivative @ derivative / P_SIZE
    side_signs = np.stack([(-1.0) ** ladder, np.ones(P_SIZE)])
    weights = (2.0 * ladder + 1.0) / (2.0 * P_SIZE)
    return (derivative, second, side_signs, weights)


def side_table(values_pair):
    identity = np.eye(P_SIZE)
    return np.concatenate(
        [
            np.kron(values_pair[0][:, None], identity),
            np.kron(values_pair[1][:, None], identity),
            np.kron(identity, values_pair[0][:, None]),
            np.kron(identity, values_pair[1][:, None]),
        ],
        axis=1,
    )


def kernel_tables():
    derivative, second, side_signs, weights = mode_tables()
    derivative = derivative.astype(np.float32).astype(np.float64)
    second = second.astype(np.float32).astype(np.float64)
    identity = np.eye(P_SIZE)
    traces = side_table(side_signs)
    swapped = traces[:, [16 * g + j for g in (1, 0, 3, 2) for j in range(P_SIZE)]]
    pad = np.zeros((PLANE, 64))
    spread = np.concatenate(
        [
            np.kron(identity, second.T),
            np.kron(second.T, identity),
            np.kron(identity, derivative.T),
            np.kron(derivative.T, identity),
            traces, pad, swapped, pad,
        ],
        axis=1,
    ).astype(np.float32)
    spread_hi = spread.astype(jnp.bfloat16)
    spread_lo = (spread[:, : 2 * PLANE] - spread_hi[:, : 2 * PLANE].astype(np.float32)).astype(jnp.bfloat16)
    lift_signs = side_signs * weights[None, :]
    lift = np.concatenate([side_table(lift_signs).T, np.zeros((64, PLANE))], axis=0)
    lanes = np.arange(PLANE)
    flip = np.zeros((PLANE, PLANE))
    flip[lanes, (lanes % P_SIZE) * P_SIZE + lanes // P_SIZE] = 1.0
    return (
        jnp.asarray(spread_hi),
        jnp.asarray(spread_lo),
        jnp.asarray(lift, jnp.bfloat16),
        jnp.asarray(flip, jnp.bfloat16),
    )


def top_modes():
    ladder = np.arange(P_SIZE)
    first_idx, second_idx, third_idx = np.meshgrid(ladder, ladder, ladder, indexing="ij")
    return np.maximum(np.maximum(first_idx, second_idx), third_idx).reshape(1, -1).astype(np.int32)


def split_two(x):
    hi = x.astype(jnp.bfloat16)
    lo = (x - hi.astype(jnp.float32)).astype(jnp.bfloat16)
    return hi, lo


def mxu(a, b):
    return jnp.dot(a, b, preferred_element_type=jnp.float32)


def split_three(x):
    hi = x.astype(jnp.bfloat16)
    rest = x - hi.astype(jnp.float32)
    mid = rest.astype(jnp.bfloat16)
    lo = (rest - mid.astype(jnp.float32)).astype(jnp.bfloat16)
    return hi, mid, lo


def exact_pick(onehot, x):
    width = x.shape[1]
    joined = mxu(onehot, jnp.concatenate(split_three(x), axis=1))
    return joined[:, :width] + joined[:, width : 2 * width] + joined[:, 2 * width :]


def exact_rows(x, onehot):
    count = x.shape[0]
    joined = mxu(jnp.concatenate(split_three(x), axis=0), onehot)
    return joined[:count] + joined[count : 2 * count] + joined[2 * count :]


def end_traces(slabs):
    total = slabs[0] + slabs[1]
    even = slabs[0] - slabs[1]
    for a in range(2, P_SIZE):
        total = total + slabs[a]
        even = even + slabs[a] if a % 2 == 0 else even - slabs[a]
    return even, total


def turn_pair(lower, upper, picks, codes, flip):
    count = lower.shape[0]
    picked = jnp.concatenate([exact_pick(picks[4], lower), exact_pick(picks[5], upper)], axis=0)
    swapped = exact_rows(picked, flip)
    lane = lax.broadcasted_iota(jnp.int32, (1, PLANE), 1)
    row_odd = (lane // P_SIZE) % 2 == 1
    col_odd = lane % 2 == 1
    sides = []
    for side in range(2):
        rows = slice(side * count, (side + 1) * count)
        code = codes[:, side : side + 1]
        chosen = jnp.where(code % 2 == 1, swapped[rows], picked[rows])
        negate = ((code // 2) % 2 == 1) & row_odd
        negate = negate != (((code // 4) % 2 == 1) & col_odd)
        sides.append(jnp.where(negate, -chosen, chosen))
    return sides


def face_lift(below, above, live, a, scale):
    derivative, second, side_signs, weights = mode_tables()
    lift_signs = (side_signs * weights[None, :]).astype(np.float32)
    update = float(lift_signs[0, a]) * below + float(lift_signs[1, a]) * above
    return scale * jnp.where(live, update, 0.0)


def inner_body(*refs, scale, carried, final):
    if carried is None:
        v_ref, weight_ref, top_ref, pick_ref, spread_hi_ref, spread_lo_ref, lift_ref = refs[:7]
        base_ref = v_ref
    else:
        v_ref, below_ref, above_ref, base_ref, weight_ref, top_ref, pick_ref = refs[:7]
        spread_hi_ref, spread_lo_ref, lift_ref = refs[7:10]
    if final:
        lower_ref, upper_ref, turn_ref, flip_ref = refs[10:14]
        partial_ref = refs[-1]
    else:
        partial_ref, even_ref, total_ref = refs[-3:]
    count = v_ref.shape[0]
    derivative, second, side_signs, weights = mode_tables()
    second = second.astype(np.float32)
    derivative = derivative.astype(np.float32)
    lift_signs = (side_signs * weights[None, :]).astype(np.float32)
    weight = weight_ref[...]
    top = top_ref[...]
    order = weight[:, 7:8]
    slabs = [v_ref[:, a * PLANE : (a + 1) * PLANE] for a in range(P_SIZE)]
    if carried is not None:
        below = below_ref[...]
        above = above_ref[...]
        slabs = [
            slabs[a] + face_lift(below, above, top[:, a * PLANE : (a + 1) * PLANE] <= order, a, carried)
            for a in range(P_SIZE)
        ]
    diff0 = jnp.broadcast_to(weight[:, 0:1], (count, PLANE))
    vel0 = jnp.broadcast_to(weight[:, 3:4], (count, PLANE))
    half = count // 2
    low = P_SIZE // 2

    def kept(a, x):
        return x if a < low else x[half:]

    def start(a):
        return a * count if a < low else low * count + (a - low) * half

    upper_slabs = [s[half:] for s in slabs]
    first = []
    for k in range(P_SIZE):
        parts = []
        for rows, source in ((slice(0, half), slabs), (slice(half, count), upper_slabs)):
            if rows.start == 0 and k >= low:
                continue
            acc_s = None
            acc_d = None
            top_n = low if rows.start == 0 else P_SIZE
            for n in range(k + 1, top_n):
                piece = source[n] if rows.start else source[n][:half]
                if second[k, n] != 0.0:
                    term = float(second[k, n]) * piece
                    acc_s = term if acc_s is None else acc_s + term
                if derivative[k, n] != 0.0:
                    term = float(derivative[k, n]) * piece
                    acc_d = term if acc_d is None else acc_d + term
            part = jnp.zeros((half, PLANE), jnp.float32)
            if acc_s is not None:
                part = part + diff0[rows] * acc_s
            if acc_d is not None:
                part = part - vel0[rows] * acc_d
            parts.append(part)
        first.append(parts[0] if len(parts) == 1 else jnp.concatenate(parts, axis=0))
    stacked = jnp.concatenate([kept(a, slabs[a]) for a in range(P_SIZE)], axis=0)
    hi, lo = split_two(stacked)
    spread_hi = spread_hi_ref[...]
    wide = mxu(hi, spread_hi) + mxu(lo, spread_hi)
    fine = mxu(hi, spread_lo_ref[...])
    weight_rows = jnp.concatenate([kept(a, weight) for a in range(P_SIZE)], axis=0)
    inner = (
        weight_rows[:, 2:3] * (wide[:, 0:PLANE] + fine[:, 0:PLANE])
        + weight_rows[:, 1:2] * (wide[:, PLANE : 2 * PLANE] + fine[:, PLANE : 2 * PLANE])
        - weight_rows[:, 5:6] * wide[:, 2 * PLANE : 3 * PLANE]
        - weight_rows[:, 4:5] * wide[:, 3 * PLANE : 4 * PLANE]
    )
    blank = jnp.zeros((half, 128), jnp.float32)

    def trace_block(a, offset):
        rows = wide[start(a) : start(a) + (count if a < low else half), offset : offset + 128]
        return rows if a < low else jnp.concatenate([blank, rows], axis=0)

    own = jnp.concatenate([trace_block(a, 4 * PLANE) for a in range(P_SIZE)], axis=1)
    other = jnp.concatenate([trace_block(a, 4 * PLANE + 128) for a in range(P_SIZE)], axis=1)
    lane = lax.broadcasted_iota(jnp.int32, (1, P_SIZE * 128), 1) % 128
    across = jnp.zeros_like(own)
    for face in range(4):
        gathered = exact_pick(pick_ref[face], other)
        across = jnp.where(lane // P_SIZE == face, gathered, across)
    jump = own - across
    jump_rows = jnp.concatenate(
        [kept(a, jump[:, a * 128 : (a + 1) * 128]) for a in range(P_SIZE)], axis=0
    )
    jhi, jlo = split_two(jump_rows)
    lift_mat = lift_ref[...]
    lifted = mxu(jhi, lift_mat) + mxu(jlo, lift_mat)
    even, total = end_traces(slabs)
    if final:
        below, above = turn_pair(
            lower_ref[...], upper_ref[...], pick_ref, turn_ref[...], flip_ref[...]
        )
    news = []
    for a in range(P_SIZE):
        rows = slice(start(a), start(a) + (count if a < low else half))
        lanes = slice(a * PLANE, (a + 1) * PLANE)
        own_lift = lifted[rows] + float(lift_signs[0, a]) * kept(a, even)
        own_lift = own_lift + float(lift_signs[1, a]) * kept(a, total)
        if final:
            own_lift = own_lift - float(lift_signs[0, a]) * kept(a, below)
            own_lift = own_lift - float(lift_signs[1, a]) * kept(a, above)
        live = kept(a, top[:, lanes] <= order)
        update = jnp.where(live, first[a] + inner[rows] - own_lift, 0.0)
        if a < low:
            new = base_ref[:, lanes] + scale * update
        else:
            new = jnp.concatenate(
                [base_ref[:half, lanes] + 0.0, base_ref[half:, lanes] + scale * update], axis=0
            )
        partial_ref[:, lanes] = new
        news.append(new)
    if not final:
        even, total = end_traces(news)
        even_ref[...] = even
        total_ref[...] = total


def faces_body(
    lower_ref, upper_ref, pick_ref, turn_ref, flip_ref, top_ref, weight_ref, even_ref, total_ref,
    below_ref, above_ref, new_even_ref, new_total_ref, *, scale
):
    below, above = turn_pair(lower_ref[...], upper_ref[...], pick_ref, turn_ref[...], flip_ref[...])
    below_ref[...] = below
    above_ref[...] = above
    top = top_ref[...]
    order = weight_ref[:, 7:8]
    parts = [
        face_lift(below, above, top[:, a * PLANE : (a + 1) * PLANE] <= order, a, scale)
        for a in range(P_SIZE)
    ]
    even, total = end_traces(parts)
    new_even_ref[...] = even_ref[...] + even
    new_total_ref[...] = total_ref[...] + total


def outer_body(
    pre_ref, top_ref, weight_ref, lower_ref, upper_ref, pick_ref, turn_ref, flip_ref,
    out_ref, even_ref, total_ref, *, scale
):
    derivative, second, side_signs, weights = mode_tables()
    lift_signs = (side_signs * weights[None, :]).astype(np.float32)
    below, above = turn_pair(lower_ref[...], upper_ref[...], pick_ref, turn_ref[...], flip_ref[...])
    top = top_ref[...]
    order = weight_ref[:, 7:8]
    news = []
    for a in range(P_SIZE):
        lanes = slice(a * PLANE, (a + 1) * PLANE)
        update = float(lift_signs[0, a]) * below + float(lift_signs[1, a]) * above
        live = top[:, lanes] <= order
        new = pre_ref[:, lanes] + scale * jnp.where(live, update, 0.0)
        out_ref[:, lanes] = new
        news.append(new)
    even, total = end_traces(news)
    even_ref[...] = even
    total_ref[...] = total


def inner(operands, scale, carried, final=False):
    count = operands[0].shape[0]
    spec = pl.BlockSpec(memory_space=pltpu.VMEM)
    square = jax.ShapeDtypeStruct((count, PLANE), jnp.float32)
    field = jax.ShapeDtypeStruct(operands[0].shape, jnp.float32)
    return pl.pallas_call(
        functools.partial(inner_body, scale=scale, carried=carried, final=final),
        out_shape=field if final else (field, square, square),
        in_specs=[spec] * len(operands),
        out_specs=spec if final else (spec, spec, spec),
        compiler_params=pltpu.CompilerParams(vmem_limit_bytes=60 * 1024 * 1024),
        cost_estimate=pl.CostEstimate(
            flops=2_500_000_000, transcendentals=0, bytes_accessed=4_000_000
        ),
    )(*operands)


def faces(lower, upper, picks, codes, flip, top, weight, even, total, scale):
    count = lower.shape[0]
    spec = pl.BlockSpec(memory_space=pltpu.VMEM)
    square = jax.ShapeDtypeStruct((count, PLANE), jnp.float32)
    return pl.pallas_call(
        functools.partial(faces_body, scale=scale),
        out_shape=(square,) * 4,
        in_specs=[spec] * 9,
        out_specs=(spec,) * 4,
    )(lower, upper, picks, codes, flip, top, weight, even, total)


def outer(pre, top, weight, lower, upper, picks, codes, flip, scale):
    count = pre.shape[0]
    spec = pl.BlockSpec(memory_space=pltpu.VMEM)
    return pl.pallas_call(
        functools.partial(outer_body, scale=scale),
        out_shape=(
            jax.ShapeDtypeStruct(pre.shape, jnp.float32),
            jax.ShapeDtypeStruct((count, PLANE), jnp.float32),
            jax.ShapeDtypeStruct((count, PLANE), jnp.float32),
        ),
        in_specs=[spec] * 8,
        out_specs=(spec, spec, spec),
    )(pre, top, weight, lower, upper, picks, codes, flip)


def prep_body(placed_ref, top_ref, weight_ref, field_ref, even_ref, total_ref):
    news = []
    for a in range(P_SIZE):
        lanes = slice(a * PLANE, (a + 1) * PLANE)
        live = top_ref[:, lanes] <= weight_ref[:, 7:8]
        new = jnp.where(live, placed_ref[:, lanes], 0.0)
        field_ref[:, lanes] = new
        news.append(new)
    even, total = end_traces(news)
    even_ref[...] = even
    total_ref[...] = total


def prep(placed, top, weight):
    count = placed.shape[0]
    spec = pl.BlockSpec(memory_space=pltpu.VMEM)
    return pl.pallas_call(
        prep_body,
        out_shape=(
            jax.ShapeDtypeStruct(placed.shape, jnp.float32),
            jax.ShapeDtypeStruct((count, PLANE), jnp.float32),
            jax.ShapeDtypeStruct((count, PLANE), jnp.float32),
        ),
        in_specs=[spec] * 3,
        out_specs=(spec, spec, spec),
    )(placed, top, weight)


def exchange(even, total):
    size = lax.axis_size("dom")
    up = [(i, (i + 1) % size) for i in range(size)]
    down = [((i + 1) % size, i) for i in range(size)]
    return lax.ppermute(total, "dom", up), lax.ppermute(even, "dom", down)


def shards(
    coefficients, diffusion, velocity, orders, target, local_faces, partner_faces, partner_turns
):
    element_count = coefficients.shape[0]
    blocks_all = lax.axis_size(("dom", "face"))
    moving = element_count // 16
    destination = target // element_count
    new_slot = target % element_count
    here = lax.axis_index(("dom", "face"))
    side_info = jnp.concatenate(
        [
            diffusion,
            velocity,
            new_slot[:, None].astype(jnp.float32),
            orders[:, None].astype(jnp.float32),
        ],
        axis=1,
    )
    side_width = side_info.shape[1]
    shifts = (1, blocks_all - 1, blocks_all // 2)
    goal = (here + jnp.asarray(shifts, jnp.int32)) % blocks_all
    chosen = destination[None, :] == goal[:, None]
    rank = jnp.cumsum(chosen.astype(jnp.int32), axis=1) - 1
    hit = chosen[:, None, :] & (
        rank[:, None, :] == jnp.arange(moving, dtype=jnp.int32)[None, :, None]
    )
    rows = jnp.arange(element_count, dtype=jnp.int32)
    picked = jnp.sum(jnp.where(hit, rows[None, None, :], 0), axis=2).reshape(-1)
    side_rows = side_info[picked].reshape(len(shifts), 1, moving * side_width)
    side_rows = jnp.pad(side_rows, ((0, 0), (0, 0), (0, P_SIZE**3 - moving * side_width)))
    parcels = jnp.concatenate(
        [
            jnp.einsum(
                "qjr,rc->qjc", hit.astype(jnp.float32), coefficients, precision=lax.Precision.HIGHEST
            ),
            side_rows,
        ],
        axis=1,
    )
    got_coef = [coefficients]
    got_side = [side_info]
    got_slot = [jnp.where(destination == here, new_slot, element_count)]
    for index, shift in enumerate(shifts):
        pairs = [(i, (i + shift) % blocks_all) for i in range(blocks_all)]
        arrived = lax.ppermute(parcels[index], ("dom", "face"), pairs)
        arrived_side = arrived[moving, : moving * side_width].reshape(moving, side_width)
        got_coef.append(arrived[:moving])
        got_side.append(arrived_side)
        got_slot.append(arrived_side[:, 6].astype(jnp.int32))
    got_coef = jnp.concatenate(got_coef, axis=0)
    got_side = jnp.concatenate(got_side, axis=0)
    got_slot = jnp.concatenate(got_slot, axis=0)
    hit = got_slot[None, :] == jnp.arange(element_count, dtype=jnp.int32)[:, None]
    got_rows = jnp.arange(got_slot.shape[0], dtype=jnp.int32)
    source = jnp.sum(jnp.where(hit, got_rows[None, :], 0), axis=1)
    placing = (got_slot[None, :] == jnp.arange(element_count, dtype=jnp.int32)[:, None]).astype(
        jnp.float32
    )
    placed_side = got_side[source]
    weight = placed_side
    top = jnp.asarray(top_modes().astype(np.float32))
    tables = kernel_tables()
    neighbours = jnp.concatenate([local_faces[0], partner_faces[0]], axis=0)
    picks = (
        neighbours[:, :, None] == jnp.arange(element_count, dtype=jnp.int32)[None, None, :]
    ).astype(jnp.bfloat16)
    codes = partner_turns[0].T
    spread_hi, spread_lo, lift, flip = tables
    placed = jnp.dot(placing, got_coef, precision=lax.Precision.HIGHEST)
    field = jnp.where(top <= weight[:, 7:8], placed, 0.0)
    slabs = [field[:, a * PLANE : (a + 1) * PLANE] for a in range(P_SIZE)]
    even, total = end_traces(slabs)
    first_step = 0.5 * TIME_STEP
    lower, upper = exchange(even, total)
    pre, even, total = inner(
        (field, weight, top, picks, spread_hi, spread_lo, lift), first_step, None
    )
    below, above, even, total = faces(
        lower, upper, picks, codes, flip, top, weight, even, total, first_step
    )
    lower, upper = exchange(even, total)
    advanced = inner(
        (pre, below, above, field, weight, top, picks, spread_hi, spread_lo, lift)
        + (lower, upper, codes, flip),
        TIME_STEP,
        first_step,
        final=True,
    )
    return advanced


def solution(mesh):
    in_specs = (
        P(("dom", "face"), None),
        P(("dom", "face"), None),
        P(("dom", "face"), None),
        P(("dom", "face")),
        P(("dom", "face")),
        P(("dom", "face"), None, None),
        P(("dom", "face"), None, None),
        P(("dom", "face"), None, None),
    )
    out_specs = P(("dom", "face"), None)
    return jax.shard_map(shards, mesh=mesh, in_specs=in_specs, out_specs=out_specs, check_vma=False)
```

```python
import functools
import jax
import jax.numpy as jnp
import numpy as np
from jax import lax
from jax.experimental import pallas as pl
from jax.experimental.pallas import tpu as pltpu
from jax.sharding import PartitionSpec as P

P_SIZE = 16
PLANE = P_SIZE * P_SIZE
TIME_STEP = 0.25


def mode_tables():
    ladder = np.arange(P_SIZE)
    spacing = ladder[None, :] - ladder[:, None]
    derivative = np.where(
        (spacing > 0) & (spacing % 2 == 1), (2.0 * ladder[:, None] + 1.0) / P_SIZE, 0.0
    )
    second = derivative @ derivative / P_SIZE
    side_signs = np.stack([(-1.0) ** ladder, np.ones(P_SIZE)])
    weights = (2.0 * ladder + 1.0) / (2.0 * P_SIZE)
    return (derivative, second, side_signs, weights)


def side_table(values_pair):
    identity = np.eye(P_SIZE)
    return np.concatenate(
        [
            np.kron(values_pair[0][:, None], identity),
            np.kron(values_pair[1][:, None], identity),
            np.kron(identity, values_pair[0][:, None]),
            np.kron(identity, values_pair[1][:, None]),
        ],
        axis=1,
    )


def kernel_tables():
    derivative, second, side_signs, weights = mode_tables()
    derivative = derivative.astype(np.float32).astype(np.float64)
    second = second.astype(np.float32).astype(np.float64)
    identity = np.eye(P_SIZE)
    traces = side_table(side_signs)
    swapped = traces[:, [16 * g + j for g in (1, 0, 3, 2) for j in range(P_SIZE)]]
    pad = np.zeros((PLANE, 64))
    spread = np.concatenate(
        [
            np.kron(identity, second.T),
            np.kron(second.T, identity),
            np.kron(identity, derivative.T),
            np.kron(derivative.T, identity),
            traces, pad, swapped, pad,
        ],
        axis=1,
    ).astype(np.float32)
    spread_hi = spread.astype(jnp.bfloat16)
    spread_lo = (spread[:, : 2 * PLANE] - spread_hi[:, : 2 * PLANE].astype(np.float32)).astype(jnp.bfloat16)
    lift_signs = side_signs * weights[None, :]
    lift = np.concatenate([side_table(lift_signs).T, np.zeros((64, PLANE))], axis=0)
    lanes = np.arange(PLANE)
    flip = np.zeros((PLANE, PLANE))
    flip[lanes, (lanes % P_SIZE) * P_SIZE + lanes // P_SIZE] = 1.0
    return (
        jnp.asarray(spread_hi),
        jnp.asarray(spread_lo),
        jnp.asarray(lift, jnp.bfloat16),
        jnp.asarray(flip, jnp.bfloat16),
    )


def top_modes():
    ladder = np.arange(P_SIZE)
    first_idx, second_idx, third_idx = np.meshgrid(ladder, ladder, ladder, indexing="ij")
    return np.maximum(np.maximum(first_idx, second_idx), third_idx).reshape(1, -1).astype(np.int32)


def split_two(x):
    hi = x.astype(jnp.bfloat16)
    lo = (x - hi.astype(jnp.float32)).astype(jnp.bfloat16)
    return hi, lo


def mxu(a, b):
    return jnp.dot(a, b, preferred_element_type=jnp.float32)


def split_three(x):
    hi = x.astype(jnp.bfloat16)
    rest = x - hi.astype(jnp.float32)
    mid = rest.astype(jnp.bfloat16)
    lo = (rest - mid.astype(jnp.float32)).astype(jnp.bfloat16)
    return hi, mid, lo


def exact_pick(onehot, x):
    width = x.shape[1]
    joined = mxu(onehot, jnp.concatenate(split_three(x), axis=1))
    return joined[:, :width] + joined[:, width : 2 * width] + joined[:, 2 * width :]


def exact_rows(x, onehot):
    count = x.shape[0]
    joined = mxu(jnp.concatenate(split_three(x), axis=0), onehot)
    return joined[:count] + joined[count : 2 * count] + joined[2 * count :]


def end_traces(slabs):
    total = slabs[0] + slabs[1]
    even = slabs[0] - slabs[1]
    for a in range(2, P_SIZE):
        total = total + slabs[a]
        even = even + slabs[a] if a % 2 == 0 else even - slabs[a]
    return even, total


def turn_pair(lower, upper, picks, codes, flip):
    count = lower.shape[0]
    picked = jnp.concatenate([exact_pick(picks[4], lower), exact_pick(picks[5], upper)], axis=0)
    swapped = exact_rows(picked, flip)
    lane = lax.broadcasted_iota(jnp.int32, (1, PLANE), 1)
    row_odd = (lane // P_SIZE) % 2 == 1
    col_odd = lane % 2 == 1
    sides = []
    for side in range(2):
        rows = slice(side * count, (side + 1) * count)
        code = codes[:, side : side + 1]
        chosen = jnp.where(code % 2 == 1, swapped[rows], picked[rows])
        negate = ((code // 2) % 2 == 1) & row_odd
        negate = negate != (((code // 4) % 2 == 1) & col_odd)
        sides.append(jnp.where(negate, -chosen, chosen))
    return sides


def face_lift(below, above, live, a, scale):
    derivative, second, side_signs, weights = mode_tables()
    lift_signs = (side_signs * weights[None, :]).astype(np.float32)
    update = float(lift_signs[0, a]) * below + float(lift_signs[1, a]) * above
    return scale * jnp.where(live, update, 0.0)


def inner_body(*refs, scale, carried, final):
    if carried is None:
        v_ref, weight_ref, top_ref, pick_ref, spread_hi_ref, spread_lo_ref, lift_ref = refs[:7]
        base_ref = v_ref
    else:
        v_ref, below_ref, above_ref, base_ref, weight_ref, top_ref, pick_ref = refs[:7]
        spread_hi_ref, spread_lo_ref, lift_ref = refs[7:10]
    if final:
        lower_ref, upper_ref, turn_ref, flip_ref = refs[10:14]
        partial_ref = refs[-1]
    else:
        partial_ref, even_ref, total_ref = refs[-3:]
    count = v_ref.shape[0]
    derivative, second, side_signs, weights = mode_tables()
    second = second.astype(np.float32)
    derivative = derivative.astype(np.float32)
    lift_signs = (side_signs * weights[None, :]).astype(np.float32)
    weight = weight_ref[...]
    top = top_ref[...]
    order = weight[:, 7:8]
    slabs = [v_ref[:, a * PLANE : (a + 1) * PLANE] for a in range(P_SIZE)]
    if carried is not None:
        below = below_ref[...]
        above = above_ref[...]
        slabs = [
            slabs[a] + face_lift(below, above, top[:, a * PLANE : (a + 1) * PLANE] <= order, a, carried)
            for a in range(P_SIZE)
        ]
    diff0 = jnp.broadcast_to(weight[:, 0:1], (count, PLANE))
    vel0 = jnp.broadcast_to(weight[:, 3:4], (count, PLANE))
    half = count // 2
    low = P_SIZE // 2

    def kept(a, x):
        return x if a < low else x[half:]

    def start(a):
        return a * count if a < low else low * count + (a - low) * half

    upper_slabs = [s[half:] for s in slabs]
    first = []
    for k in range(P_SIZE):
        parts = []
        for rows, source in ((slice(0, half), slabs), (slice(half, count), upper_slabs)):
            if rows.start == 0 and k >= low:
                continue
            acc_s = None
            acc_d = None
            top_n = low if rows.start == 0 else P_SIZE
            for n in range(k + 1, top_n):
                piece = source[n] if rows.start else source[n][:half]
                if second[k, n] != 0.0:
                    term = float(second[k, n]) * piece
                    acc_s = term if acc_s is None else acc_s + term
                if derivative[k, n] != 0.0:
                    term = float(derivative[k, n]) * piece
                    acc_d = term if acc_d is None else acc_d + term
            part = jnp.zeros((half, PLANE), jnp.float32)
            if acc_s is not None:
                part = part + diff0[rows] * acc_s
            if acc_d is not None:
                part = part - vel0[rows] * acc_d
            parts.append(part)
        first.append(parts[0] if len(parts) == 1 else jnp.concatenate(parts, axis=0))
    stacked = jnp.concatenate([kept(a, slabs[a]) for a in range(P_SIZE)], axis=0)
    hi, lo = split_two(stacked)
    spread_hi = spread_hi_ref[...]
    wide = mxu(hi, spread_hi) + mxu(lo, spread_hi)
    fine = mxu(hi, spread_lo_ref[...])
    weight_rows = jnp.concatenate([kept(a, weight) for a in range(P_SIZE)], axis=0)
    inner = (
        weight_rows[:, 2:3] * (wide[:, 0:PLANE] + fine[:, 0:PLANE])
        + weight_rows[:, 1:2] * (wide[:, PLANE : 2 * PLANE] + fine[:, PLANE : 2 * PLANE])
        - weight_rows[:, 5:6] * wide[:, 2 * PLANE : 3 * PLANE]
        - weight_rows[:, 4:5] * wide[:, 3 * PLANE : 4 * PLANE]
    )
    blank = jnp.zeros((half, 128), jnp.float32)

    def trace_block(a, offset):
        rows = wide[start(a) : start(a) + (count if a < low else half), offset : offset + 128]
        return rows if a < low else jnp.concatenate([blank, rows], axis=0)

    own = jnp.concatenate([trace_block(a, 4 * PLANE) for a in range(P_SIZE)], axis=1)
    other = jnp.concatenate([trace_block(a, 4 * PLANE + 128) for a in range(P_SIZE)], axis=1)
    lane = lax.broadcasted_iota(jnp.int32, (1, P_SIZE * 128), 1) % 128
    across = jnp.zeros_like(own)
    for face in range(4):
        gathered = exact_pick(pick_ref[face], other)
        across = jnp.where(lane // P_SIZE == face, gathered, across)
    jump = own - across
    jump_rows = jnp.concatenate(
        [kept(a, jump[:, a * 128 : (a + 1) * 128]) for a in range(P_SIZE)], axis=0
    )
    jhi, jlo = split_two(jump_rows)
    lift_mat = lift_ref[...]
    lifted = mxu(jhi, lift_mat) + mxu(jlo, lift_mat)
    even, total = end_traces(slabs)
    if final:
        below, above = turn_pair(
            lower_ref[...], upper_ref[...], pick_ref, turn_ref[...], flip_ref[...]
        )
    news = []
    for a in range(P_SIZE):
        rows = slice(start(a), start(a) + (count if a < low else half))
        lanes = slice(a * PLANE, (a + 1) * PLANE)
        own_lift = lifted[rows] + float(lift_signs[0, a]) * kept(a, even)
        own_lift = own_lift + float(lift_signs[1, a]) * kept(a, total)
        if final:
            own_lift = own_lift - float(lift_signs[0, a]) * kept(a, below)
            own_lift = own_lift - float(lift_signs[1, a]) * kept(a, above)
        live = kept(a, top[:, lanes] <= order)
        update = jnp.where(live, first[a] + inner[rows] - own_lift, 0.0)
        if a < low:
            new = base_ref[:, lanes] + scale * update
        else:
            new = jnp.concatenate(
                [base_ref[:half, lanes] + 0.0, base_ref[half:, lanes] + scale * update], axis=0
            )
        partial_ref[:, lanes] = new
        news.append(new)
    if not final:
        even, total = end_traces(news)
        even_ref[...] = even
        total_ref[...] = total


def faces_body(
    lower_ref, upper_ref, pick_ref, turn_ref, flip_ref, top_ref, weight_ref, even_ref, total_ref,
    below_ref, above_ref, new_even_ref, new_total_ref, *, scale
):
    below, above = turn_pair(lower_ref[...], upper_ref[...], pick_ref, turn_ref[...], flip_ref[...])
    below_ref[...] = below
    above_ref[...] = above
    top = top_ref[...]
    order = weight_ref[:, 7:8]
    parts = [
        face_lift(below, above, top[:, a * PLANE : (a + 1) * PLANE] <= order, a, scale)
        for a in range(P_SIZE)
    ]
    even, total = end_traces(parts)
    new_even_ref[...] = even_ref[...] + even
    new_total_ref[...] = total_ref[...] + total


def outer_body(
    pre_ref, top_ref, weight_ref, lower_ref, upper_ref, pick_ref, turn_ref, flip_ref,
    out_ref, even_ref, total_ref, *, scale
):
    derivative, second, side_signs, weights = mode_tables()
    lift_signs = (side_signs * weights[None, :]).astype(np.float32)
    below, above = turn_pair(lower_ref[...], upper_ref[...], pick_ref, turn_ref[...], flip_ref[...])
    top = top_ref[...]
    order = weight_ref[:, 7:8]
    news = []
    for a in range(P_SIZE):
        lanes = slice(a * PLANE, (a + 1) * PLANE)
        update = float(lift_signs[0, a]) * below + float(lift_signs[1, a]) * above
        live = top[:, lanes] <= order
        new = pre_ref[:, lanes] + scale * jnp.where(live, update, 0.0)
        out_ref[:, lanes] = new
        news.append(new)
    even, total = end_traces(news)
    even_ref[...] = even
    total_ref[...] = total


def inner(operands, scale, carried, final=False):
    count = operands[0].shape[0]
    spec = pl.BlockSpec(memory_space=pltpu.VMEM)
    square = jax.ShapeDtypeStruct((count, PLANE), jnp.float32)
    field = jax.ShapeDtypeStruct(operands[0].shape, jnp.float32)
    return pl.pallas_call(
        functools.partial(inner_body, scale=scale, carried=carried, final=final),
        out_shape=field if final else (field, square, square),
        in_specs=[spec] * len(operands),
        out_specs=spec if final else (spec, spec, spec),
        compiler_params=pltpu.CompilerParams(vmem_limit_bytes=60 * 1024 * 1024),
        cost_estimate=pl.CostEstimate(
            flops=2_500_000_000, transcendentals=0, bytes_accessed=4_000_000
        ),
    )(*operands)


def faces(lower, upper, picks, codes, flip, top, weight, even, total, scale):
    count = lower.shape[0]
    spec = pl.BlockSpec(memory_space=pltpu.VMEM)
    square = jax.ShapeDtypeStruct((count, PLANE), jnp.float32)
    return pl.pallas_call(
        functools.partial(faces_body, scale=scale),
        out_shape=(square,) * 4,
        in_specs=[spec] * 9,
        out_specs=(spec,) * 4,
    )(lower, upper, picks, codes, flip, top, weight, even, total)


def outer(pre, top, weight, lower, upper, picks, codes, flip, scale):
    count = pre.shape[0]
    spec = pl.BlockSpec(memory_space=pltpu.VMEM)
    return pl.pallas_call(
        functools.partial(outer_body, scale=scale),
        out_shape=(
            jax.ShapeDtypeStruct(pre.shape, jnp.float32),
            jax.ShapeDtypeStruct((count, PLANE), jnp.float32),
            jax.ShapeDtypeStruct((count, PLANE), jnp.float32),
        ),
        in_specs=[spec] * 8,
        out_specs=(spec, spec, spec),
    )(pre, top, weight, lower, upper, picks, codes, flip)


def prep_body(placed_ref, top_ref, weight_ref, field_ref, even_ref, total_ref):
    news = []
    for a in range(P_SIZE):
        lanes = slice(a * PLANE, (a + 1) * PLANE)
        live = top_ref[:, lanes] <= weight_ref[:, 7:8]
        new = jnp.where(live, placed_ref[:, lanes], 0.0)
        field_ref[:, lanes] = new
        news.append(new)
    even, total = end_traces(news)
    even_ref[...] = even
    total_ref[...] = total


def prep(placed, top, weight):
    count = placed.shape[0]
    spec = pl.BlockSpec(memory_space=pltpu.VMEM)
    return pl.pallas_call(
        prep_body,
        out_shape=(
            jax.ShapeDtypeStruct(placed.shape, jnp.float32),
            jax.ShapeDtypeStruct((count, PLANE), jnp.float32),
            jax.ShapeDtypeStruct((count, PLANE), jnp.float32),
        ),
        in_specs=[spec] * 3,
        out_specs=(spec, spec, spec),
    )(placed, top, weight)


def exchange(even, total):
    size = lax.axis_size("dom")
    up = [(i, (i + 1) % size) for i in range(size)]
    down = [((i + 1) % size, i) for i in range(size)]
    return lax.ppermute(total, "dom", up), lax.ppermute(even, "dom", down)


def shards(
    coefficients, diffusion, velocity, orders, target, local_faces, partner_faces, partner_turns
):
    element_count = coefficients.shape[0]
    blocks_all = lax.axis_size(("dom", "face"))
    moving = element_count // 16
    destination = target // element_count
    new_slot = target % element_count
    here = lax.axis_index(("dom", "face"))
    side_info = jnp.concatenate(
        [
            diffusion,
            velocity,
            new_slot[:, None].astype(jnp.float32),
            orders[:, None].astype(jnp.float32),
        ],
        axis=1,
    )
    side_width = side_info.shape[1]
    shifts = (1, blocks_all - 1, blocks_all // 2)
    goal = (here + jnp.asarray(shifts, jnp.int32)) % blocks_all
    chosen = destination[None, :] == goal[:, None]
    rank = jnp.cumsum(chosen.astype(jnp.int32), axis=1) - 1
    hit = chosen[:, None, :] & (
        rank[:, None, :] == jnp.arange(moving, dtype=jnp.int32)[None, :, None]
    )
    width = P_SIZE**3
    carried_rows = jnp.concatenate(
        [coefficients, side_info, jnp.zeros((element_count, 128 - side_width), jnp.float32)],
        axis=1,
    )
    parcels = jnp.einsum(
        "qjr,rc->qjc", hit.astype(jnp.float32), carried_rows, precision=lax.Precision.HIGHEST
    )
    got_rows = [carried_rows]
    got_slot = [jnp.where(destination == here, new_slot, element_count)]
    for index, shift in enumerate(shifts):
        pairs = [(i, (i + shift) % blocks_all) for i in range(blocks_all)]
        arrived = lax.ppermute(parcels[index], ("dom", "face"), pairs)
        got_rows.append(arrived)
        got_slot.append(arrived[:, width + 6].astype(jnp.int32))
    got_rows = jnp.concatenate(got_rows, axis=0)
    got_slot = jnp.concatenate(got_slot, axis=0)
    placing = (got_slot[None, :] == jnp.arange(element_count, dtype=jnp.int32)[:, None]).astype(
        jnp.float32
    )
    placed_rows = jnp.dot(placing, got_rows, precision=lax.Precision.HIGHEST)
    placed_side = placed_rows[:, width : width + side_width]
    weight = placed_side
    top = jnp.asarray(top_modes().astype(np.float32))
    tables = kernel_tables()
    neighbours = jnp.concatenate([local_faces[0], partner_faces[0]], axis=0)
    picks = (
        neighbours[:, :, None] == jnp.arange(element_count, dtype=jnp.int32)[None, None, :]
    ).astype(jnp.bfloat16)
    codes = partner_turns[0].T
    spread_hi, spread_lo, lift, flip = tables
    placed = placed_rows[:, :width]
    field = jnp.where(top <= weight[:, 7:8], placed, 0.0)
    slabs = [field[:, a * PLANE : (a + 1) * PLANE] for a in range(P_SIZE)]
    even, total = end_traces(slabs)
    first_step = 0.5 * TIME_STEP
    lower, upper = exchange(even, total)
    pre, even, total = inner(
        (field, weight, top, picks, spread_hi, spread_lo, lift), first_step, None
    )
    below, above, even, total = faces(
        lower, upper, picks, codes, flip, top, weight, even, total, first_step
    )
    lower, upper = exchange(even, total)
    advanced = inner(
        (pre, below, above, field, weight, top, picks, spread_hi, spread_lo, lift)
        + (lower, upper, codes, flip),
        TIME_STEP,
        first_step,
        final=True,
    )
    return advanced


def solution(mesh):
    in_specs = (
        P(("dom", "face"), None),
        P(("dom", "face"), None),
        P(("dom", "face"), None),
        P(("dom", "face")),
        P(("dom", "face")),
        P(("dom", "face"), None, None),
        P(("dom", "face"), None, None),
        P(("dom", "face"), None, None),
    )
    out_specs = P(("dom", "face"), None)
    return jax.shard_map(shards, mesh=mesh, in_specs=in_specs, out_specs=out_specs, check_vma=False)
```

```python
import functools
import jax
import jax.numpy as jnp
import numpy as np
from jax import lax
from jax.experimental import pallas as pl
from jax.experimental.pallas import tpu as pltpu
from jax.sharding import PartitionSpec as P

P_SIZE = 16
PLANE = P_SIZE * P_SIZE
TIME_STEP = 0.25


def mode_tables():
    ladder = np.arange(P_SIZE)
    spacing = ladder[None, :] - ladder[:, None]
    derivative = np.where(
        (spacing > 0) & (spacing % 2 == 1), (2.0 * ladder[:, None] + 1.0) / P_SIZE, 0.0
    )
    second = derivative @ derivative / P_SIZE
    side_signs = np.stack([(-1.0) ** ladder, np.ones(P_SIZE)])
    weights = (2.0 * ladder + 1.0) / (2.0 * P_SIZE)
    return (derivative, second, side_signs, weights)


def side_table(values_pair):
    identity = np.eye(P_SIZE)
    return np.concatenate(
        [
            np.kron(values_pair[0][:, None], identity),
            np.kron(values_pair[1][:, None], identity),
            np.kron(identity, values_pair[0][:, None]),
            np.kron(identity, values_pair[1][:, None]),
        ],
        axis=1,
    )


def kernel_tables():
    derivative, second, side_signs, weights = mode_tables()
    derivative = derivative.astype(np.float32).astype(np.float64)
    second = second.astype(np.float32).astype(np.float64)
    identity = np.eye(P_SIZE)
    traces = side_table(side_signs)
    swapped = traces[:, [16 * g + j for g in (1, 0, 3, 2) for j in range(P_SIZE)]]
    pad = np.zeros((PLANE, 64))
    spread = np.concatenate(
        [
            np.kron(identity, second.T),
            np.kron(second.T, identity),
            np.kron(identity, derivative.T),
            np.kron(derivative.T, identity),
            traces, pad, swapped, pad,
        ],
        axis=1,
    ).astype(np.float32)
    spread_hi = spread.astype(jnp.bfloat16)
    spread_lo = (spread[:, : 2 * PLANE] - spread_hi[:, : 2 * PLANE].astype(np.float32)).astype(jnp.bfloat16)
    lift_signs = side_signs * weights[None, :]
    lift = np.concatenate([side_table(lift_signs).T, np.zeros((64, PLANE))], axis=0)
    lanes = np.arange(PLANE)
    flip = np.zeros((PLANE, PLANE))
    flip[lanes, (lanes % P_SIZE) * P_SIZE + lanes // P_SIZE] = 1.0
    return (
        jnp.asarray(spread_hi),
        jnp.asarray(spread_lo),
        jnp.asarray(lift, jnp.bfloat16),
        jnp.asarray(flip, jnp.bfloat16),
    )


def top_modes():
    ladder = np.arange(P_SIZE)
    first_idx, second_idx, third_idx = np.meshgrid(ladder, ladder, ladder, indexing="ij")
    return np.maximum(np.maximum(first_idx, second_idx), third_idx).reshape(1, -1).astype(np.int32)


def split_two(x):
    hi = x.astype(jnp.bfloat16)
    lo = (x - hi.astype(jnp.float32)).astype(jnp.bfloat16)
    return hi, lo


def mxu(a, b):
    return jnp.dot(a, b, preferred_element_type=jnp.float32)


def split_three(x):
    hi = x.astype(jnp.bfloat16)
    rest = x - hi.astype(jnp.float32)
    mid = rest.astype(jnp.bfloat16)
    lo = (rest - mid.astype(jnp.float32)).astype(jnp.bfloat16)
    return hi, mid, lo


def exact_pick(onehot, x):
    width = x.shape[1]
    joined = mxu(onehot, jnp.concatenate(split_three(x), axis=1))
    return joined[:, :width] + joined[:, width : 2 * width] + joined[:, 2 * width :]


def exact_rows(x, onehot):
    count = x.shape[0]
    joined = mxu(jnp.concatenate(split_three(x), axis=0), onehot)
    return joined[:count] + joined[count : 2 * count] + joined[2 * count :]


def end_traces(slabs):
    total = slabs[0] + slabs[1]
    even = slabs[0] - slabs[1]
    for a in range(2, P_SIZE):
        total = total + slabs[a]
        even = even + slabs[a] if a % 2 == 0 else even - slabs[a]
    return even, total


def turn_pair(lower, upper, picks, codes, flip):
    count = lower.shape[0]
    picked = jnp.concatenate([exact_pick(picks[4], lower), exact_pick(picks[5], upper)], axis=0)
    swapped = exact_rows(picked, flip)
    lane = lax.broadcasted_iota(jnp.int32, (1, PLANE), 1)
    row_odd = (lane // P_SIZE) % 2 == 1
    col_odd = lane % 2 == 1
    sides = []
    for side in range(2):
        rows = slice(side * count, (side + 1) * count)
        code = codes[:, side : side + 1]
        chosen = jnp.where(code % 2 == 1, swapped[rows], picked[rows])
        negate = ((code // 2) % 2 == 1) & row_odd
        negate = negate != (((code // 4) % 2 == 1) & col_odd)
        sides.append(jnp.where(negate, -chosen, chosen))
    return sides


def face_lift(below, above, live, a, scale):
    derivative, second, side_signs, weights = mode_tables()
    lift_signs = (side_signs * weights[None, :]).astype(np.float32)
    update = float(lift_signs[0, a]) * below + float(lift_signs[1, a]) * above
    return scale * jnp.where(live, update, 0.0)


def inner_body(*refs, scale, carried, final):
    if carried is None:
        v_ref, weight_ref, top_ref, pick_ref, spread_hi_ref, spread_lo_ref, lift_ref = refs[:7]
        base_ref = v_ref
    else:
        v_ref, below_ref, above_ref, base_ref, weight_ref, top_ref, pick_ref = refs[:7]
        spread_hi_ref, spread_lo_ref, lift_ref = refs[7:10]
    if final:
        lower_ref, upper_ref, turn_ref, flip_ref = refs[10:14]
        partial_ref = refs[-1]
    else:
        partial_ref, even_ref, total_ref = refs[-3:]
    count = v_ref.shape[0]
    derivative, second, side_signs, weights = mode_tables()
    second = second.astype(np.float32)
    derivative = derivative.astype(np.float32)
    lift_signs = (side_signs * weights[None, :]).astype(np.float32)
    weight = weight_ref[...]
    top = top_ref[...]
    order = weight[:, 7:8]
    slabs = [v_ref[:, a * PLANE : (a + 1) * PLANE] for a in range(P_SIZE)]
    if carried is not None:
        below = below_ref[...]
        above = above_ref[...]
        slabs = [
            slabs[a] + face_lift(below, above, top[:, a * PLANE : (a + 1) * PLANE] <= order, a, carried)
            for a in range(P_SIZE)
        ]
    diff0 = jnp.broadcast_to(weight[:, 0:1], (count, PLANE))
    vel0 = jnp.broadcast_to(weight[:, 3:4], (count, PLANE))
    half = count // 2
    low = P_SIZE // 2

    def kept(a, x):
        return x if a < low else x[half:]

    def start(a):
        return a * count if a < low else low * count + (a - low) * half

    upper_slabs = [s[half:] for s in slabs]
    first = []
    for k in range(P_SIZE):
        parts = []
        for rows, source in ((slice(0, half), slabs), (slice(half, count), upper_slabs)):
            if rows.start == 0 and k >= low:
                continue
            acc_s = None
            acc_d = None
            top_n = low if rows.start == 0 else P_SIZE
            for n in range(k + 1, top_n):
                piece = source[n] if rows.start else source[n][:half]
                if second[k, n] != 0.0:
                    term = float(second[k, n]) * piece
                    acc_s = term if acc_s is None else acc_s + term
                if derivative[k, n] != 0.0:
                    term = float(derivative[k, n]) * piece
                    acc_d = term if acc_d is None else acc_d + term
            part = jnp.zeros((half, PLANE), jnp.float32)
            if acc_s is not None:
                part = part + diff0[rows] * acc_s
            if acc_d is not None:
                part = part - vel0[rows] * acc_d
            parts.append(part)
        first.append(parts[0] if len(parts) == 1 else jnp.concatenate(parts, axis=0))
    stacked = jnp.concatenate([kept(a, slabs[a]) for a in range(P_SIZE)], axis=0)
    hi, lo = split_two(stacked)
    spread_hi = spread_hi_ref[...]
    wide = mxu(hi, spread_hi) + mxu(lo, spread_hi)
    fine = mxu(hi, spread_lo_ref[...])
    weight_rows = jnp.concatenate([kept(a, weight) for a in range(P_SIZE)], axis=0)
    inner = (
        weight_rows[:, 2:3] * (wide[:, 0:PLANE] + fine[:, 0:PLANE])
        + weight_rows[:, 1:2] * (wide[:, PLANE : 2 * PLANE] + fine[:, PLANE : 2 * PLANE])
        - weight_rows[:, 5:6] * wide[:, 2 * PLANE : 3 * PLANE]
        - weight_rows[:, 4:5] * wide[:, 3 * PLANE : 4 * PLANE]
    )
    blank = jnp.zeros((half, 128), jnp.float32)

    def trace_block(a, offset):
        rows = wide[start(a) : start(a) + (count if a < low else half), offset : offset + 128]
        return rows if a < low else jnp.concatenate([blank, rows], axis=0)

    own = jnp.concatenate([trace_block(a, 4 * PLANE) for a in range(P_SIZE)], axis=1)
    other = jnp.concatenate([trace_block(a, 4 * PLANE + 128) for a in range(P_SIZE)], axis=1)
    lane = lax.broadcasted_iota(jnp.int32, (1, P_SIZE * 128), 1) % 128
    across = jnp.zeros_like(own)
    for face in range(4):
        gathered = exact_pick(pick_ref[face], other)
        across = jnp.where(lane // P_SIZE == face, gathered, across)
    jump = own - across
    jump_rows = jnp.concatenate(
        [kept(a, jump[:, a * 128 : (a + 1) * 128]) for a in range(P_SIZE)], axis=0
    )
    jhi, jlo = split_two(jump_rows)
    lift_mat = lift_ref[...]
    lifted = mxu(jhi, lift_mat) + mxu(jlo, lift_mat)
    even, total = end_traces(slabs)
    if final:
        below, above = turn_pair(
            lower_ref[...], upper_ref[...], pick_ref, turn_ref[...], flip_ref[...]
        )
    news = []
    for a in range(P_SIZE):
        rows = slice(start(a), start(a) + (count if a < low else half))
        lanes = slice(a * PLANE, (a + 1) * PLANE)
        own_lift = lifted[rows] + float(lift_signs[0, a]) * kept(a, even)
        own_lift = own_lift + float(lift_signs[1, a]) * kept(a, total)
        if final:
            own_lift = own_lift - float(lift_signs[0, a]) * kept(a, below)
            own_lift = own_lift - float(lift_signs[1, a]) * kept(a, above)
        live = kept(a, top[:, lanes] <= order)
        update = jnp.where(live, first[a] + inner[rows] - own_lift, 0.0)
        if a < low:
            new = base_ref[:, lanes] + scale * update
        else:
            new = jnp.concatenate(
                [base_ref[:half, lanes] + 0.0, base_ref[half:, lanes] + scale * update], axis=0
            )
        partial_ref[:, lanes] = new
        news.append(new)
    if not final:
        even, total = end_traces(news)
        even_ref[...] = even
        total_ref[...] = total


def faces_body(
    lower_ref, upper_ref, pick_ref, turn_ref, flip_ref, top_ref, weight_ref, even_ref, total_ref,
    below_ref, above_ref, new_even_ref, new_total_ref, *, scale
):
    below, above = turn_pair(lower_ref[...], upper_ref[...], pick_ref, turn_ref[...], flip_ref[...])
    below_ref[...] = below
    above_ref[...] = above
    top = top_ref[...]
    order = weight_ref[:, 7:8]
    parts = [
        face_lift(below, above, top[:, a * PLANE : (a + 1) * PLANE] <= order, a, scale)
        for a in range(P_SIZE)
    ]
    even, total = end_traces(parts)
    new_even_ref[...] = even_ref[...] + even
    new_total_ref[...] = total_ref[...] + total


def outer_body(
    pre_ref, top_ref, weight_ref, lower_ref, upper_ref, pick_ref, turn_ref, flip_ref,
    out_ref, even_ref, total_ref, *, scale
):
    derivative, second, side_signs, weights = mode_tables()
    lift_signs = (side_signs * weights[None, :]).astype(np.float32)
    below, above = turn_pair(lower_ref[...], upper_ref[...], pick_ref, turn_ref[...], flip_ref[...])
    top = top_ref[...]
    order = weight_ref[:, 7:8]
    news = []
    for a in range(P_SIZE):
        lanes = slice(a * PLANE, (a + 1) * PLANE)
        update = float(lift_signs[0, a]) * below + float(lift_signs[1, a]) * above
        live = top[:, lanes] <= order
        new = pre_ref[:, lanes] + scale * jnp.where(live, update, 0.0)
        out_ref[:, lanes] = new
        news.append(new)
    even, total = end_traces(news)
    even_ref[...] = even
    total_ref[...] = total


def inner(operands, scale, carried, final=False):
    count = operands[0].shape[0]
    spec = pl.BlockSpec(memory_space=pltpu.VMEM)
    square = jax.ShapeDtypeStruct((count, PLANE), jnp.float32)
    field = jax.ShapeDtypeStruct(operands[0].shape, jnp.float32)
    return pl.pallas_call(
        functools.partial(inner_body, scale=scale, carried=carried, final=final),
        out_shape=field if final else (field, square, square),
        in_specs=[spec] * len(operands),
        out_specs=spec if final else (spec, spec, spec),
        compiler_params=pltpu.CompilerParams(vmem_limit_bytes=60 * 1024 * 1024),
        cost_estimate=pl.CostEstimate(
            flops=2_500_000_000, transcendentals=0, bytes_accessed=4_000_000
        ),
    )(*operands)


def faces(lower, upper, picks, codes, flip, top, weight, even, total, scale):
    count = lower.shape[0]
    spec = pl.BlockSpec(memory_space=pltpu.VMEM)
    square = jax.ShapeDtypeStruct((count, PLANE), jnp.float32)
    return pl.pallas_call(
        functools.partial(faces_body, scale=scale),
        out_shape=(square,) * 4,
        in_specs=[spec] * 9,
        out_specs=(spec,) * 4,
    )(lower, upper, picks, codes, flip, top, weight, even, total)


def outer(pre, top, weight, lower, upper, picks, codes, flip, scale):
    count = pre.shape[0]
    spec = pl.BlockSpec(memory_space=pltpu.VMEM)
    return pl.pallas_call(
        functools.partial(outer_body, scale=scale),
        out_shape=(
            jax.ShapeDtypeStruct(pre.shape, jnp.float32),
            jax.ShapeDtypeStruct((count, PLANE), jnp.float32),
            jax.ShapeDtypeStruct((count, PLANE), jnp.float32),
        ),
        in_specs=[spec] * 8,
        out_specs=(spec, spec, spec),
    )(pre, top, weight, lower, upper, picks, codes, flip)


def prep_body(placed_ref, top_ref, weight_ref, field_ref, even_ref, total_ref):
    news = []
    for a in range(P_SIZE):
        lanes = slice(a * PLANE, (a + 1) * PLANE)
        live = top_ref[:, lanes] <= weight_ref[:, 7:8]
        new = jnp.where(live, placed_ref[:, lanes], 0.0)
        field_ref[:, lanes] = new
        news.append(new)
    even, total = end_traces(news)
    even_ref[...] = even
    total_ref[...] = total


def prep(placed, top, weight):
    count = placed.shape[0]
    spec = pl.BlockSpec(memory_space=pltpu.VMEM)
    return pl.pallas_call(
        prep_body,
        out_shape=(
            jax.ShapeDtypeStruct(placed.shape, jnp.float32),
            jax.ShapeDtypeStruct((count, PLANE), jnp.float32),
            jax.ShapeDtypeStruct((count, PLANE), jnp.float32),
        ),
        in_specs=[spec] * 3,
        out_specs=(spec, spec, spec),
    )(placed, top, weight)


def exchange(even, total):
    size = lax.axis_size("dom")
    up = [(i, (i + 1) % size) for i in range(size)]
    down = [((i + 1) % size, i) for i in range(size)]
    return lax.ppermute(total, "dom", up), lax.ppermute(even, "dom", down)


def shards(
    coefficients, diffusion, velocity, orders, target, local_faces, partner_faces, partner_turns
):
    element_count = coefficients.shape[0]
    blocks_all = lax.axis_size(("dom", "face"))
    moving = element_count // 16
    destination = target // element_count
    new_slot = target % element_count
    here = lax.axis_index(("dom", "face"))
    side_info = jnp.concatenate(
        [
            diffusion,
            velocity,
            new_slot[:, None].astype(jnp.float32),
            orders[:, None].astype(jnp.float32),
        ],
        axis=1,
    )
    side_width = side_info.shape[1]
    shifts = (1, blocks_all - 1, blocks_all // 2)
    goal = (here + jnp.asarray(shifts, jnp.int32)) % blocks_all
    chosen = destination[None, :] == goal[:, None]
    rank = jnp.cumsum(chosen.astype(jnp.int32), axis=1) - 1
    hit = chosen[:, None, :] & (
        rank[:, None, :] == jnp.arange(moving, dtype=jnp.int32)[None, :, None]
    )
    width = P_SIZE**3
    exact = lax.Precision.HIGHEST
    side_lanes = jnp.concatenate(
        [
            diffusion.T,
            velocity.T,
            new_slot[None, :].astype(jnp.float32),
            orders[None, :].astype(jnp.float32),
            jnp.zeros((128 - side_width, element_count), jnp.float32),
        ],
        axis=0,
    )
    hit_values = hit.astype(jnp.float32)
    parcels = jnp.concatenate(
        [
            jnp.einsum("qjr,rc->qjc", hit_values, coefficients, precision=exact),
            jnp.einsum("qjr,cr->qjc", hit_values, side_lanes, precision=exact),
        ],
        axis=2,
    )
    arrivals = []
    got_slot = [jnp.where(destination == here, new_slot, element_count)]
    for index, shift in enumerate(shifts):
        pairs = [(i, (i + shift) % blocks_all) for i in range(blocks_all)]
        arrived = lax.ppermute(parcels[index], ("dom", "face"), pairs)
        arrivals.append(arrived)
        got_slot.append(arrived[:, width + 6].astype(jnp.int32))
    arrivals = jnp.concatenate(arrivals, axis=0)
    got_slot = jnp.concatenate(got_slot, axis=0)
    placing = (got_slot[None, :] == jnp.arange(element_count, dtype=jnp.int32)[:, None]).astype(
        jnp.float32
    )
    staying, coming = placing[:, :element_count], placing[:, element_count:]
    placed = jnp.dot(
        placing, jnp.concatenate([coefficients, arrivals[:, :width]], axis=0), precision=exact
    )
    placed_side = jnp.einsum("sr,cr->sc", staying, side_lanes, precision=exact) + jnp.dot(
        coming, arrivals[:, width:], precision=exact
    )
    placed_side = placed_side[:, :side_width]
    weight = placed_side
    top = jnp.asarray(top_modes().astype(np.float32))
    tables = kernel_tables()
    neighbours = jnp.concatenate([local_faces[0], partner_faces[0]], axis=0)
    picks = (
        neighbours[:, :, None] == jnp.arange(element_count, dtype=jnp.int32)[None, None, :]
    ).astype(jnp.bfloat16)
    codes = partner_turns[0].T
    spread_hi, spread_lo, lift, flip = tables
    field = jnp.where(top <= weight[:, 7:8], placed, 0.0)
    slabs = [field[:, a * PLANE : (a + 1) * PLANE] for a in range(P_SIZE)]
    even, total = end_traces(slabs)
    first_step = 0.5 * TIME_STEP
    lower, upper = exchange(even, total)
    pre, even, total = inner(
        (field, weight, top, picks, spread_hi, spread_lo, lift), first_step, None
    )
    below, above, even, total = faces(
        lower, upper, picks, codes, flip, top, weight, even, total, first_step
    )
    lower, upper = exchange(even, total)
    advanced = inner(
        (pre, below, above, field, weight, top, picks, spread_hi, spread_lo, lift)
        + (lower, upper, codes, flip),
        TIME_STEP,
        first_step,
        final=True,
    )
    return advanced


def solution(mesh):
    in_specs = (
        P(("dom", "face"), None),
        P(("dom", "face"), None),
        P(("dom", "face"), None),
        P(("dom", "face")),
        P(("dom", "face")),
        P(("dom", "face"), None, None),
        P(("dom", "face"), None, None),
        P(("dom", "face"), None, None),
    )
    out_specs = P(("dom", "face"), None)
    return jax.shard_map(shards, mesh=mesh, in_specs=in_specs, out_specs=out_specs, check_vma=False)
```

```python
import functools
import jax
import jax.numpy as jnp
import numpy as np
from jax import lax
from jax.experimental import pallas as pl
from jax.experimental.pallas import tpu as pltpu
from jax.sharding import PartitionSpec as P

P_SIZE = 16
PLANE = P_SIZE * P_SIZE
TIME_STEP = 0.25


def mode_tables():
    ladder = np.arange(P_SIZE)
    spacing = ladder[None, :] - ladder[:, None]
    derivative = np.where(
        (spacing > 0) & (spacing % 2 == 1), (2.0 * ladder[:, None] + 1.0) / P_SIZE, 0.0
    )
    second = derivative @ derivative / P_SIZE
    side_signs = np.stack([(-1.0) ** ladder, np.ones(P_SIZE)])
    weights = (2.0 * ladder + 1.0) / (2.0 * P_SIZE)
    return (derivative, second, side_signs, weights)


def side_table(values_pair):
    identity = np.eye(P_SIZE)
    return np.concatenate(
        [
            np.kron(values_pair[0][:, None], identity),
            np.kron(values_pair[1][:, None], identity),
            np.kron(identity, values_pair[0][:, None]),
            np.kron(identity, values_pair[1][:, None]),
        ],
        axis=1,
    )


def kernel_tables():
    derivative, second, side_signs, weights = mode_tables()
    derivative = derivative.astype(np.float32).astype(np.float64)
    second = second.astype(np.float32).astype(np.float64)
    identity = np.eye(P_SIZE)
    traces = side_table(side_signs)
    swapped = traces[:, [16 * g + j for g in (1, 0, 3, 2) for j in range(P_SIZE)]]
    pad = np.zeros((PLANE, 64))
    spread = np.concatenate(
        [
            np.kron(identity, second.T),
            np.kron(second.T, identity),
            np.kron(identity, derivative.T),
            np.kron(derivative.T, identity),
            traces, pad, swapped, pad,
        ],
        axis=1,
    ).astype(np.float32)
    spread_hi = spread.astype(jnp.bfloat16)
    spread_lo = (spread[:, : 2 * PLANE] - spread_hi[:, : 2 * PLANE].astype(np.float32)).astype(jnp.bfloat16)
    lift_signs = side_signs * weights[None, :]
    lift = np.concatenate([side_table(lift_signs).T, np.zeros((64, PLANE))], axis=0)
    lanes = np.arange(PLANE)
    flip = np.zeros((PLANE, PLANE))
    flip[lanes, (lanes % P_SIZE) * P_SIZE + lanes // P_SIZE] = 1.0
    return (
        jnp.asarray(spread_hi),
        jnp.asarray(spread_lo),
        jnp.asarray(lift, jnp.bfloat16),
        jnp.asarray(flip, jnp.bfloat16),
    )


def top_modes():
    ladder = np.arange(P_SIZE)
    first_idx, second_idx, third_idx = np.meshgrid(ladder, ladder, ladder, indexing="ij")
    return np.maximum(np.maximum(first_idx, second_idx), third_idx).reshape(1, -1).astype(np.int32)


def split_two(x):
    hi = x.astype(jnp.bfloat16)
    lo = (x - hi.astype(jnp.float32)).astype(jnp.bfloat16)
    return hi, lo


def mxu(a, b):
    return jnp.dot(a, b, preferred_element_type=jnp.float32)


def split_three(x):
    hi = x.astype(jnp.bfloat16)
    rest = x - hi.astype(jnp.float32)
    mid = rest.astype(jnp.bfloat16)
    lo = (rest - mid.astype(jnp.float32)).astype(jnp.bfloat16)
    return hi, mid, lo


def exact_pick(onehot, x):
    width = x.shape[1]
    joined = mxu(onehot, jnp.concatenate(split_three(x), axis=1))
    return joined[:, :width] + joined[:, width : 2 * width] + joined[:, 2 * width :]


def exact_rows(x, onehot):
    count = x.shape[0]
    joined = mxu(jnp.concatenate(split_three(x), axis=0), onehot)
    return joined[:count] + joined[count : 2 * count] + joined[2 * count :]


def end_traces(slabs):
    total = slabs[0] + slabs[1]
    even = slabs[0] - slabs[1]
    for a in range(2, P_SIZE):
        total = total + slabs[a]
        even = even + slabs[a] if a % 2 == 0 else even - slabs[a]
    return even, total


def turn_pair(lower, upper, picks, codes, flip):
    count = lower.shape[0]
    picked = jnp.concatenate([exact_pick(picks[4], lower), exact_pick(picks[5], upper)], axis=0)
    swapped = exact_rows(picked, flip)
    lane = lax.broadcasted_iota(jnp.int32, (1, PLANE), 1)
    row_odd = (lane // P_SIZE) % 2 == 1
    col_odd = lane % 2 == 1
    sides = []
    for side in range(2):
        rows = slice(side * count, (side + 1) * count)
        code = codes[:, side : side + 1]
        chosen = jnp.where(code % 2 == 1, swapped[rows], picked[rows])
        negate = ((code // 2) % 2 == 1) & row_odd
        negate = negate != (((code // 4) % 2 == 1) & col_odd)
        sides.append(jnp.where(negate, -chosen, chosen))
    return sides


def face_lift(below, above, live, a, scale):
    derivative, second, side_signs, weights = mode_tables()
    lift_signs = (side_signs * weights[None, :]).astype(np.float32)
    update = float(lift_signs[0, a]) * below + float(lift_signs[1, a]) * above
    return scale * jnp.where(live, update, 0.0)


def inner_body(*refs, scale, carried, final):
    if carried is None:
        v_ref, weight_ref, top_ref, pick_ref, spread_hi_ref, spread_lo_ref, lift_ref = refs[:7]
        base_ref = v_ref
    else:
        v_ref, below_ref, above_ref, base_ref, weight_ref, top_ref, pick_ref = refs[:7]
        spread_hi_ref, spread_lo_ref, lift_ref = refs[7:10]
    if final:
        lower_ref, upper_ref, turn_ref, flip_ref = refs[10:14]
        partial_ref = refs[-1]
    else:
        partial_ref, even_ref, total_ref = refs[-3:]
    count = v_ref.shape[0]
    derivative, second, side_signs, weights = mode_tables()
    second = second.astype(np.float32)
    derivative = derivative.astype(np.float32)
    lift_signs = (side_signs * weights[None, :]).astype(np.float32)
    weight = weight_ref[...]
    top = top_ref[...]
    order = weight[:, 7:8]
    slabs = [v_ref[:, a * PLANE : (a + 1) * PLANE] for a in range(P_SIZE)]
    if carried is not None:
        below = below_ref[...]
        above = above_ref[...]
        slabs = [
            slabs[a] + face_lift(below, above, top[:, a * PLANE : (a + 1) * PLANE] <= order, a, carried)
            for a in range(P_SIZE)
        ]
    diff0 = jnp.broadcast_to(weight[:, 0:1], (count, PLANE))
    vel0 = jnp.broadcast_to(weight[:, 3:4], (count, PLANE))
    half = count // 2
    low = P_SIZE // 2

    def kept(a, x):
        return x if a < low else x[half:]

    def start(a):
        return a * count if a < low else low * count + (a - low) * half

    upper_slabs = [s[half:] for s in slabs]
    first = []
    for k in range(P_SIZE):
        parts = []
        for rows, source in ((slice(0, half), slabs), (slice(half, count), upper_slabs)):
            if rows.start == 0 and k >= low:
                continue
            acc_s = None
            acc_d = None
            top_n = low if rows.start == 0 else P_SIZE
            for n in range(k + 1, top_n):
                piece = source[n] if rows.start else source[n][:half]
                if second[k, n] != 0.0:
                    term = float(second[k, n]) * piece
                    acc_s = term if acc_s is None else acc_s + term
                if derivative[k, n] != 0.0:
                    term = float(derivative[k, n]) * piece
                    acc_d = term if acc_d is None else acc_d + term
            part = jnp.zeros((half, PLANE), jnp.float32)
            if acc_s is not None:
                part = part + diff0[rows] * acc_s
            if acc_d is not None:
                part = part - vel0[rows] * acc_d
            parts.append(part)
        first.append(parts[0] if len(parts) == 1 else jnp.concatenate(parts, axis=0))
    stacked = jnp.concatenate([kept(a, slabs[a]) for a in range(P_SIZE)], axis=0)
    hi, lo = split_two(stacked)
    spread_hi = spread_hi_ref[...]
    wide = mxu(hi, spread_hi) + mxu(lo, spread_hi)
    fine = mxu(hi, spread_lo_ref[...])
    weight_rows = jnp.concatenate([kept(a, weight) for a in range(P_SIZE)], axis=0)
    inner = (
        weight_rows[:, 2:3] * (wide[:, 0:PLANE] + fine[:, 0:PLANE])
        + weight_rows[:, 1:2] * (wide[:, PLANE : 2 * PLANE] + fine[:, PLANE : 2 * PLANE])
        - weight_rows[:, 5:6] * wide[:, 2 * PLANE : 3 * PLANE]
        - weight_rows[:, 4:5] * wide[:, 3 * PLANE : 4 * PLANE]
    )
    blank = jnp.zeros((half, 128), jnp.float32)

    def trace_block(a, offset):
        rows = wide[start(a) : start(a) + (count if a < low else half), offset : offset + 128]
        return rows if a < low else jnp.concatenate([blank, rows], axis=0)

    own = jnp.concatenate([trace_block(a, 4 * PLANE) for a in range(P_SIZE)], axis=1)
    other = jnp.concatenate([trace_block(a, 4 * PLANE + 128) for a in range(P_SIZE)], axis=1)
    lane = lax.broadcasted_iota(jnp.int32, (1, P_SIZE * 128), 1) % 128
    across = jnp.zeros_like(own)
    for face in range(4):
        gathered = exact_pick(pick_ref[face], other)
        across = jnp.where(lane // P_SIZE == face, gathered, across)
    jump = own - across
    jump_rows = jnp.concatenate(
        [kept(a, jump[:, a * 128 : (a + 1) * 128]) for a in range(P_SIZE)], axis=0
    )
    jhi, jlo = split_two(jump_rows)
    lift_mat = lift_ref[...]
    lifted = mxu(jhi, lift_mat) + mxu(jlo, lift_mat)
    even, total = end_traces(slabs)
    if final:
        below, above = turn_pair(
            lower_ref[...], upper_ref[...], pick_ref, turn_ref[...], flip_ref[...]
        )
    news = []
    for a in range(P_SIZE):
        rows = slice(start(a), start(a) + (count if a < low else half))
        lanes = slice(a * PLANE, (a + 1) * PLANE)
        own_lift = lifted[rows] + float(lift_signs[0, a]) * kept(a, even)
        own_lift = own_lift + float(lift_signs[1, a]) * kept(a, total)
        if final:
            own_lift = own_lift - float(lift_signs[0, a]) * kept(a, below)
            own_lift = own_lift - float(lift_signs[1, a]) * kept(a, above)
        live = kept(a, top[:, lanes] <= order)
        update = jnp.where(live, first[a] + inner[rows] - own_lift, 0.0)
        if a < low:
            new = base_ref[:, lanes] + scale * update
        else:
            new = jnp.concatenate(
                [base_ref[:half, lanes] + 0.0, base_ref[half:, lanes] + scale * update], axis=0
            )
        partial_ref[:, lanes] = new
        news.append(new)
    if not final:
        even, total = end_traces(news)
        even_ref[...] = even
        total_ref[...] = total


def faces_body(
    lower_ref, upper_ref, pick_ref, turn_ref, flip_ref, top_ref, weight_ref, even_ref, total_ref,
    below_ref, above_ref, new_even_ref, new_total_ref, *, scale
):
    below, above = turn_pair(lower_ref[...], upper_ref[...], pick_ref, turn_ref[...], flip_ref[...])
    below_ref[...] = below
    above_ref[...] = above
    top = top_ref[...]
    order = weight_ref[:, 7:8]
    parts = [
        face_lift(below, above, top[:, a * PLANE : (a + 1) * PLANE] <= order, a, scale)
        for a in range(P_SIZE)
    ]
    even, total = end_traces(parts)
    new_even_ref[...] = even_ref[...] + even
    new_total_ref[...] = total_ref[...] + total


def outer_body(
    pre_ref, top_ref, weight_ref, lower_ref, upper_ref, pick_ref, turn_ref, flip_ref,
    out_ref, even_ref, total_ref, *, scale
):
    derivative, second, side_signs, weights = mode_tables()
    lift_signs = (side_signs * weights[None, :]).astype(np.float32)
    below, above = turn_pair(lower_ref[...], upper_ref[...], pick_ref, turn_ref[...], flip_ref[...])
    top = top_ref[...]
    order = weight_ref[:, 7:8]
    news = []
    for a in range(P_SIZE):
        lanes = slice(a * PLANE, (a + 1) * PLANE)
        update = float(lift_signs[0, a]) * below + float(lift_signs[1, a]) * above
        live = top[:, lanes] <= order
        new = pre_ref[:, lanes] + scale * jnp.where(live, update, 0.0)
        out_ref[:, lanes] = new
        news.append(new)
    even, total = end_traces(news)
    even_ref[...] = even
    total_ref[...] = total


def inner(operands, scale, carried, final=False):
    count = operands[0].shape[0]
    spec = pl.BlockSpec(memory_space=pltpu.VMEM)
    square = jax.ShapeDtypeStruct((count, PLANE), jnp.float32)
    field = jax.ShapeDtypeStruct(operands[0].shape, jnp.float32)
    return pl.pallas_call(
        functools.partial(inner_body, scale=scale, carried=carried, final=final),
        out_shape=field if final else (field, square, square),
        in_specs=[spec] * len(operands),
        out_specs=spec if final else (spec, spec, spec),
        compiler_params=pltpu.CompilerParams(vmem_limit_bytes=60 * 1024 * 1024),
        cost_estimate=pl.CostEstimate(
            flops=2_500_000_000, transcendentals=0, bytes_accessed=4_000_000
        ),
    )(*operands)


def faces(lower, upper, picks, codes, flip, top, weight, even, total, scale):
    count = lower.shape[0]
    spec = pl.BlockSpec(memory_space=pltpu.VMEM)
    square = jax.ShapeDtypeStruct((count, PLANE), jnp.float32)
    return pl.pallas_call(
        functools.partial(faces_body, scale=scale),
        out_shape=(square,) * 4,
        in_specs=[spec] * 9,
        out_specs=(spec,) * 4,
    )(lower, upper, picks, codes, flip, top, weight, even, total)


def outer(pre, top, weight, lower, upper, picks, codes, flip, scale):
    count = pre.shape[0]
    spec = pl.BlockSpec(memory_space=pltpu.VMEM)
    return pl.pallas_call(
        functools.partial(outer_body, scale=scale),
        out_shape=(
            jax.ShapeDtypeStruct(pre.shape, jnp.float32),
            jax.ShapeDtypeStruct((count, PLANE), jnp.float32),
            jax.ShapeDtypeStruct((count, PLANE), jnp.float32),
        ),
        in_specs=[spec] * 8,
        out_specs=(spec, spec, spec),
    )(pre, top, weight, lower, upper, picks, codes, flip)


def prep_body(placed_ref, top_ref, weight_ref, field_ref, even_ref, total_ref):
    news = []
    for a in range(P_SIZE):
        lanes = slice(a * PLANE, (a + 1) * PLANE)
        live = top_ref[:, lanes] <= weight_ref[:, 7:8]
        new = jnp.where(live, placed_ref[:, lanes], 0.0)
        field_ref[:, lanes] = new
        news.append(new)
    even, total = end_traces(news)
    even_ref[...] = even
    total_ref[...] = total


def prep(placed, top, weight):
    count = placed.shape[0]
    spec = pl.BlockSpec(memory_space=pltpu.VMEM)
    return pl.pallas_call(
        prep_body,
        out_shape=(
            jax.ShapeDtypeStruct(placed.shape, jnp.float32),
            jax.ShapeDtypeStruct((count, PLANE), jnp.float32),
            jax.ShapeDtypeStruct((count, PLANE), jnp.float32),
        ),
        in_specs=[spec] * 3,
        out_specs=(spec, spec, spec),
    )(placed, top, weight)


def exchange(even, total):
    size = lax.axis_size("dom")
    up = [(i, (i + 1) % size) for i in range(size)]
    down = [((i + 1) % size, i) for i in range(size)]
    return lax.ppermute(total, "dom", up), lax.ppermute(even, "dom", down)


def shards(
    coefficients, diffusion, velocity, orders, target, local_faces, partner_faces, partner_turns
):
    element_count = coefficients.shape[0]
    blocks_all = lax.axis_size(("dom", "face"))
    moving = element_count // 16
    destination = target // element_count
    new_slot = target % element_count
    here = lax.axis_index(("dom", "face"))
    side_info = jnp.concatenate(
        [
            diffusion,
            velocity,
            new_slot[:, None].astype(jnp.float32),
            orders[:, None].astype(jnp.float32),
        ],
        axis=1,
    )
    side_width = side_info.shape[1]
    shifts = (1, blocks_all - 1, blocks_all // 2)
    goal = (here + jnp.asarray(shifts, jnp.int32)) % blocks_all
    chosen = destination[None, :] == goal[:, None]
    rank = jnp.cumsum(chosen.astype(jnp.int32), axis=1) - 1
    hit = chosen[:, None, :] & (
        rank[:, None, :] == jnp.arange(moving, dtype=jnp.int32)[None, :, None]
    )
    width = P_SIZE**3
    exact = lax.Precision.HIGHEST
    counts = jnp.concatenate(
        [new_slot[None, :].astype(jnp.float32), orders[None, :].astype(jnp.float32)], axis=0
    )
    hit_values = hit.astype(jnp.float32)
    parcels = jnp.concatenate(
        [
            jnp.einsum("qjr,rc->qjc", hit_values, coefficients, precision=exact),
            jnp.einsum("qjr,rc->qjc", hit_values, diffusion, precision=exact),
            jnp.einsum("qjr,rc->qjc", hit_values, velocity, precision=exact),
            jnp.einsum("qjr,cr->qjc", hit_values, counts, precision=exact),
            jnp.zeros(hit.shape[:2] + (128 - side_width,), jnp.float32),
        ],
        axis=2,
    )
    arrivals = []
    got_slot = [jnp.where(destination == here, new_slot, element_count)]
    for index, shift in enumerate(shifts):
        pairs = [(i, (i + shift) % blocks_all) for i in range(blocks_all)]
        arrived = lax.ppermute(parcels[index], ("dom", "face"), pairs)
        arrivals.append(arrived)
        got_slot.append(arrived[:, width + 6].astype(jnp.int32))
    arrivals = jnp.concatenate(arrivals, axis=0)
    got_slot = jnp.concatenate(got_slot, axis=0)
    placing = (got_slot[None, :] == jnp.arange(element_count, dtype=jnp.int32)[:, None]).astype(
        jnp.float32
    )
    staying, coming = placing[:, :element_count], placing[:, element_count:]
    placed = jnp.dot(
        placing, jnp.concatenate([coefficients, arrivals[:, :width]], axis=0), precision=exact
    )
    placed_side = jnp.concatenate(
        [
            jnp.dot(staying, diffusion, precision=exact),
            jnp.dot(staying, velocity, precision=exact),
            jnp.einsum("sr,cr->sc", staying, counts, precision=exact),
        ],
        axis=1,
    ) + jnp.dot(coming, arrivals[:, width : width + side_width], precision=exact)
    weight = placed_side
    top = jnp.asarray(top_modes().astype(np.float32))
    tables = kernel_tables()
    neighbours = jnp.concatenate([local_faces[0], partner_faces[0]], axis=0)
    picks = (
        neighbours[:, :, None] == jnp.arange(element_count, dtype=jnp.int32)[None, None, :]
    ).astype(jnp.bfloat16)
    codes = partner_turns[0].T
    spread_hi, spread_lo, lift, flip = tables
    field = jnp.where(top <= weight[:, 7:8], placed, 0.0)
    slabs = [field[:, a * PLANE : (a + 1) * PLANE] for a in range(P_SIZE)]
    even, total = end_traces(slabs)
    first_step = 0.5 * TIME_STEP
    lower, upper = exchange(even, total)
    pre, even, total = inner(
        (field, weight, top, picks, spread_hi, spread_lo, lift), first_step, None
    )
    below, above, even, total = faces(
        lower, upper, picks, codes, flip, top, weight, even, total, first_step
    )
    lower, upper = exchange(even, total)
    advanced = inner(
        (pre, below, above, field, weight, top, picks, spread_hi, spread_lo, lift)
        + (lower, upper, codes, flip),
        TIME_STEP,
        first_step,
        final=True,
    )
    return advanced


def solution(mesh):
    in_specs = (
        P(("dom", "face"), None),
        P(("dom", "face"), None),
        P(("dom", "face"), None),
        P(("dom", "face")),
        P(("dom", "face")),
        P(("dom", "face"), None, None),
        P(("dom", "face"), None, None),
        P(("dom", "face"), None, None),
    )
    out_specs = P(("dom", "face"), None)
    return jax.shard_map(shards, mesh=mesh, in_specs=in_specs, out_specs=out_specs, check_vma=False)
```

```python
import functools
import jax
import jax.numpy as jnp
import numpy as np
from jax import lax
from jax.experimental import pallas as pl
from jax.experimental.pallas import tpu as pltpu
from jax.sharding import PartitionSpec as P

P_SIZE = 16
PLANE = P_SIZE * P_SIZE
TIME_STEP = 0.25


def mode_tables():
    ladder = np.arange(P_SIZE)
    spacing = ladder[None, :] - ladder[:, None]
    derivative = np.where(
        (spacing > 0) & (spacing % 2 == 1), (2.0 * ladder[:, None] + 1.0) / P_SIZE, 0.0
    )
    second = derivative @ derivative / P_SIZE
    side_signs = np.stack([(-1.0) ** ladder, np.ones(P_SIZE)])
    weights = (2.0 * ladder + 1.0) / (2.0 * P_SIZE)
    return (derivative, second, side_signs, weights)


def side_table(values_pair):
    identity = np.eye(P_SIZE)
    return np.concatenate(
        [
            np.kron(values_pair[0][:, None], identity),
            np.kron(values_pair[1][:, None], identity),
            np.kron(identity, values_pair[0][:, None]),
            np.kron(identity, values_pair[1][:, None]),
        ],
        axis=1,
    )


def kernel_tables():
    derivative, second, side_signs, weights = mode_tables()
    derivative = derivative.astype(np.float32).astype(np.float64)
    second = second.astype(np.float32).astype(np.float64)
    identity = np.eye(P_SIZE)
    traces = side_table(side_signs)
    swapped = traces[:, [16 * g + j for g in (1, 0, 3, 2) for j in range(P_SIZE)]]
    pad = np.zeros((PLANE, 64))
    spread = np.concatenate(
        [
            np.kron(identity, second.T),
            np.kron(second.T, identity),
            np.kron(identity, derivative.T),
            np.kron(derivative.T, identity),
            traces, pad, swapped, pad,
        ],
        axis=1,
    ).astype(np.float32)
    spread_hi = spread.astype(jnp.bfloat16)
    spread_lo = (spread[:, : 2 * PLANE] - spread_hi[:, : 2 * PLANE].astype(np.float32)).astype(jnp.bfloat16)
    lift_signs = side_signs * weights[None, :]
    lift = np.concatenate([side_table(lift_signs).T, np.zeros((64, PLANE))], axis=0)
    lanes = np.arange(PLANE)
    flip = np.zeros((PLANE, PLANE))
    flip[lanes, (lanes % P_SIZE) * P_SIZE + lanes // P_SIZE] = 1.0
    return (
        jnp.asarray(spread_hi),
        jnp.asarray(spread_lo),
        jnp.asarray(lift, jnp.bfloat16),
        jnp.asarray(flip, jnp.bfloat16),
    )


def top_modes():
    ladder = np.arange(P_SIZE)
    first_idx, second_idx, third_idx = np.meshgrid(ladder, ladder, ladder, indexing="ij")
    return np.maximum(np.maximum(first_idx, second_idx), third_idx).reshape(1, -1).astype(np.int32)


def split_two(x):
    hi = x.astype(jnp.bfloat16)
    lo = (x - hi.astype(jnp.float32)).astype(jnp.bfloat16)
    return hi, lo


def mxu(a, b):
    return jnp.dot(a, b, preferred_element_type=jnp.float32)


def split_three(x):
    hi = x.astype(jnp.bfloat16)
    rest = x - hi.astype(jnp.float32)
    mid = rest.astype(jnp.bfloat16)
    lo = (rest - mid.astype(jnp.float32)).astype(jnp.bfloat16)
    return hi, mid, lo


def exact_pick(onehot, x):
    width = x.shape[1]
    joined = mxu(onehot, jnp.concatenate(split_three(x), axis=1))
    return joined[:, :width] + joined[:, width : 2 * width] + joined[:, 2 * width :]


def exact_rows(x, onehot):
    count = x.shape[0]
    joined = mxu(jnp.concatenate(split_three(x), axis=0), onehot)
    return joined[:count] + joined[count : 2 * count] + joined[2 * count :]


def end_traces(slabs):
    total = slabs[0] + slabs[1]
    even = slabs[0] - slabs[1]
    for a in range(2, P_SIZE):
        total = total + slabs[a]
        even = even + slabs[a] if a % 2 == 0 else even - slabs[a]
    return even, total


def turn_pair(lower, upper, picks, codes, flip):
    count = lower.shape[0]
    picked = jnp.concatenate([exact_pick(picks[4], lower), exact_pick(picks[5], upper)], axis=0)
    swapped = exact_rows(picked, flip)
    lane = lax.broadcasted_iota(jnp.int32, (1, PLANE), 1)
    row_odd = (lane // P_SIZE) % 2 == 1
    col_odd = lane % 2 == 1
    sides = []
    for side in range(2):
        rows = slice(side * count, (side + 1) * count)
        code = codes[:, side : side + 1]
        chosen = jnp.where(code % 2 == 1, swapped[rows], picked[rows])
        negate = ((code // 2) % 2 == 1) & row_odd
        negate = negate != (((code // 4) % 2 == 1) & col_odd)
        sides.append(jnp.where(negate, -chosen, chosen))
    return sides


def face_lift(below, above, live, a, scale):
    derivative, second, side_signs, weights = mode_tables()
    lift_signs = (side_signs * weights[None, :]).astype(np.float32)
    update = float(lift_signs[0, a]) * below + float(lift_signs[1, a]) * above
    return scale * jnp.where(live, update, 0.0)


def inner_body(*refs, scale, carried, final):
    if carried is None:
        v_ref, weight_ref, top_ref, pick_ref, spread_hi_ref, spread_lo_ref, lift_ref = refs[:7]
        base_ref = v_ref
    else:
        v_ref, below_ref, above_ref, base_ref, weight_ref, top_ref, pick_ref = refs[:7]
        spread_hi_ref, spread_lo_ref, lift_ref = refs[7:10]
    if final:
        lower_ref, upper_ref, turn_ref, flip_ref = refs[10:14]
        partial_ref = refs[-1]
    else:
        partial_ref, even_ref, total_ref = refs[-3:]
    count = v_ref.shape[0]
    derivative, second, side_signs, weights = mode_tables()
    second = second.astype(np.float32)
    derivative = derivative.astype(np.float32)
    lift_signs = (side_signs * weights[None, :]).astype(np.float32)
    weight = weight_ref[...]
    top = top_ref[...]
    order = weight[:, 7:8]
    slabs = [v_ref[:, a * PLANE : (a + 1) * PLANE] for a in range(P_SIZE)]
    if carried is not None:
        below = below_ref[...]
        above = above_ref[...]
        slabs = [
            slabs[a] + face_lift(below, above, top[:, a * PLANE : (a + 1) * PLANE] <= order, a, carried)
            for a in range(P_SIZE)
        ]
    diff0 = jnp.broadcast_to(weight[:, 0:1], (count, PLANE))
    vel0 = jnp.broadcast_to(weight[:, 3:4], (count, PLANE))
    half = count // 2
    low = P_SIZE // 2

    def kept(a, x):
        return x if a < low else x[half:]

    def start(a):
        return a * count if a < low else low * count + (a - low) * half

    upper_slabs = [s[half:] for s in slabs]
    first = []
    for k in range(P_SIZE):
        parts = []
        for rows, source in ((slice(0, half), slabs), (slice(half, count), upper_slabs)):
            if rows.start == 0 and k >= low:
                continue
            acc_s = None
            acc_d = None
            top_n = low if rows.start == 0 else P_SIZE
            for n in range(k + 1, top_n):
                piece = source[n] if rows.start else source[n][:half]
                if second[k, n] != 0.0:
                    term = float(second[k, n]) * piece
                    acc_s = term if acc_s is None else acc_s + term
                if derivative[k, n] != 0.0:
                    term = float(derivative[k, n]) * piece
                    acc_d = term if acc_d is None else acc_d + term
            part = jnp.zeros((half, PLANE), jnp.float32)
            if acc_s is not None:
                part = part + diff0[rows] * acc_s
            if acc_d is not None:
                part = part - vel0[rows] * acc_d
            parts.append(part)
        first.append(parts[0] if len(parts) == 1 else jnp.concatenate(parts, axis=0))
    stacked = jnp.concatenate([kept(a, slabs[a]) for a in range(P_SIZE)], axis=0)
    hi, lo = split_two(stacked)
    spread_hi = spread_hi_ref[...]
    wide = mxu(hi, spread_hi) + mxu(lo, spread_hi)
    fine = mxu(hi, spread_lo_ref[...])
    weight_rows = jnp.concatenate([kept(a, weight) for a in range(P_SIZE)], axis=0)
    inner = (
        weight_rows[:, 2:3] * (wide[:, 0:PLANE] + fine[:, 0:PLANE])
        + weight_rows[:, 1:2] * (wide[:, PLANE : 2 * PLANE] + fine[:, PLANE : 2 * PLANE])
        - weight_rows[:, 5:6] * wide[:, 2 * PLANE : 3 * PLANE]
        - weight_rows[:, 4:5] * wide[:, 3 * PLANE : 4 * PLANE]
    )
    blank = jnp.zeros((half, 128), jnp.float32)

    def trace_block(a, offset):
        rows = wide[start(a) : start(a) + (count if a < low else half), offset : offset + 128]
        return rows if a < low else jnp.concatenate([blank, rows], axis=0)

    own = jnp.concatenate([trace_block(a, 4 * PLANE) for a in range(P_SIZE)], axis=1)
    other = jnp.concatenate([trace_block(a, 4 * PLANE + 128) for a in range(P_SIZE)], axis=1)
    lane = lax.broadcasted_iota(jnp.int32, (1, P_SIZE * 128), 1) % 128
    across = jnp.zeros_like(own)
    for face in range(4):
        gathered = exact_pick(pick_ref[face], other)
        across = jnp.where(lane // P_SIZE == face, gathered, across)
    jump = own - across
    jump_rows = jnp.concatenate(
        [kept(a, jump[:, a * 128 : (a + 1) * 128]) for a in range(P_SIZE)], axis=0
    )
    jhi, jlo = split_two(jump_rows)
    lift_mat = lift_ref[...]
    lifted = mxu(jhi, lift_mat) + mxu(jlo, lift_mat)
    even, total = end_traces(slabs)
    if final:
        below, above = turn_pair(
            lower_ref[...], upper_ref[...], pick_ref, turn_ref[...], flip_ref[...]
        )
    news = []
    for a in range(P_SIZE):
        rows = slice(start(a), start(a) + (count if a < low else half))
        lanes = slice(a * PLANE, (a + 1) * PLANE)
        own_lift = lifted[rows] + float(lift_signs[0, a]) * kept(a, even)
        own_lift = own_lift + float(lift_signs[1, a]) * kept(a, total)
        if final:
            own_lift = own_lift - float(lift_signs[0, a]) * kept(a, below)
            own_lift = own_lift - float(lift_signs[1, a]) * kept(a, above)
        live = kept(a, top[:, lanes] <= order)
        update = jnp.where(live, first[a] + inner[rows] - own_lift, 0.0)
        if a < low:
            new = base_ref[:, lanes] + scale * update
        else:
            new = jnp.concatenate(
                [base_ref[:half, lanes] + 0.0, base_ref[half:, lanes] + scale * update], axis=0
            )
        partial_ref[:, lanes] = new
        news.append(new)
    if not final:
        even, total = end_traces(news)
        even_ref[...] = even
        total_ref[...] = total


def faces_body(
    lower_ref, upper_ref, pick_ref, turn_ref, flip_ref, top_ref, weight_ref, even_ref, total_ref,
    below_ref, above_ref, new_even_ref, new_total_ref, *, scale
):
    below, above = turn_pair(lower_ref[...], upper_ref[...], pick_ref, turn_ref[...], flip_ref[...])
    below_ref[...] = below
    above_ref[...] = above
    top = top_ref[...]
    order = weight_ref[:, 7:8]
    parts = [
        face_lift(below, above, top[:, a * PLANE : (a + 1) * PLANE] <= order, a, scale)
        for a in range(P_SIZE)
    ]
    even, total = end_traces(parts)
    new_even_ref[...] = even_ref[...] + even
    new_total_ref[...] = total_ref[...] + total


def outer_body(
    pre_ref, top_ref, weight_ref, lower_ref, upper_ref, pick_ref, turn_ref, flip_ref,
    out_ref, even_ref, total_ref, *, scale
):
    derivative, second, side_signs, weights = mode_tables()
    lift_signs = (side_signs * weights[None, :]).astype(np.float32)
    below, above = turn_pair(lower_ref[...], upper_ref[...], pick_ref, turn_ref[...], flip_ref[...])
    top = top_ref[...]
    order = weight_ref[:, 7:8]
    news = []
    for a in range(P_SIZE):
        lanes = slice(a * PLANE, (a + 1) * PLANE)
        update = float(lift_signs[0, a]) * below + float(lift_signs[1, a]) * above
        live = top[:, lanes] <= order
        new = pre_ref[:, lanes] + scale * jnp.where(live, update, 0.0)
        out_ref[:, lanes] = new
        news.append(new)
    even, total = end_traces(news)
    even_ref[...] = even
    total_ref[...] = total


def inner(operands, scale, carried, final=False):
    count = operands[0].shape[0]
    spec = pl.BlockSpec(memory_space=pltpu.VMEM)
    square = jax.ShapeDtypeStruct((count, PLANE), jnp.float32)
    field = jax.ShapeDtypeStruct(operands[0].shape, jnp.float32)
    return pl.pallas_call(
        functools.partial(inner_body, scale=scale, carried=carried, final=final),
        out_shape=field if final else (field, square, square),
        in_specs=[spec] * len(operands),
        out_specs=spec if final else (spec, spec, spec),
        compiler_params=pltpu.CompilerParams(vmem_limit_bytes=60 * 1024 * 1024),
        cost_estimate=pl.CostEstimate(
            flops=2_500_000_000, transcendentals=0, bytes_accessed=4_000_000
        ),
    )(*operands)


def faces(lower, upper, picks, codes, flip, top, weight, even, total, scale):
    count = lower.shape[0]
    spec = pl.BlockSpec(memory_space=pltpu.VMEM)
    square = jax.ShapeDtypeStruct((count, PLANE), jnp.float32)
    return pl.pallas_call(
        functools.partial(faces_body, scale=scale),
        out_shape=(square,) * 4,
        in_specs=[spec] * 9,
        out_specs=(spec,) * 4,
    )(lower, upper, picks, codes, flip, top, weight, even, total)


def outer(pre, top, weight, lower, upper, picks, codes, flip, scale):
    count = pre.shape[0]
    spec = pl.BlockSpec(memory_space=pltpu.VMEM)
    return pl.pallas_call(
        functools.partial(outer_body, scale=scale),
        out_shape=(
            jax.ShapeDtypeStruct(pre.shape, jnp.float32),
            jax.ShapeDtypeStruct((count, PLANE), jnp.float32),
            jax.ShapeDtypeStruct((count, PLANE), jnp.float32),
        ),
        in_specs=[spec] * 8,
        out_specs=(spec, spec, spec),
    )(pre, top, weight, lower, upper, picks, codes, flip)


def prep_body(placed_ref, top_ref, weight_ref, field_ref, even_ref, total_ref):
    news = []
    for a in range(P_SIZE):
        lanes = slice(a * PLANE, (a + 1) * PLANE)
        live = top_ref[:, lanes] <= weight_ref[:, 7:8]
        new = jnp.where(live, placed_ref[:, lanes], 0.0)
        field_ref[:, lanes] = new
        news.append(new)
    even, total = end_traces(news)
    even_ref[...] = even
    total_ref[...] = total


def prep(placed, top, weight):
    count = placed.shape[0]
    spec = pl.BlockSpec(memory_space=pltpu.VMEM)
    return pl.pallas_call(
        prep_body,
        out_shape=(
            jax.ShapeDtypeStruct(placed.shape, jnp.float32),
            jax.ShapeDtypeStruct((count, PLANE), jnp.float32),
            jax.ShapeDtypeStruct((count, PLANE), jnp.float32),
        ),
        in_specs=[spec] * 3,
        out_specs=(spec, spec, spec),
    )(placed, top, weight)


def exchange(even, total):
    size = lax.axis_size("dom")
    up = [(i, (i + 1) % size) for i in range(size)]
    down = [((i + 1) % size, i) for i in range(size)]
    return lax.ppermute(total, "dom", up), lax.ppermute(even, "dom", down)


def shards(
    coefficients, diffusion, velocity, orders, target, local_faces, partner_faces, partner_turns
):
    element_count = coefficients.shape[0]
    blocks_all = lax.axis_size(("dom", "face"))
    moving = element_count // 16
    destination = target // element_count
    new_slot = target % element_count
    here = lax.axis_index(("dom", "face"))
    side_info = jnp.concatenate(
        [
            diffusion,
            velocity,
            new_slot[:, None].astype(jnp.float32),
            orders[:, None].astype(jnp.float32),
        ],
        axis=1,
    )
    side_width = side_info.shape[1]
    shifts = (1, blocks_all - 1, blocks_all // 2)
    goal = (here + jnp.asarray(shifts, jnp.int32)) % blocks_all
    chosen = destination[None, :] == goal[:, None]
    ladder = np.arange(element_count)
    before = jnp.asarray((ladder[:, None] < ladder[None, :]).astype(np.float32))
    rank = jnp.dot(chosen.astype(jnp.float32), before, precision=lax.Precision.HIGHEST)
    hit = chosen[:, None, :] & (
        rank[:, None, :] == jnp.arange(moving, dtype=jnp.float32)[None, :, None]
    )
    width = P_SIZE**3
    exact = lax.Precision.HIGHEST
    counts = jnp.concatenate(
        [new_slot[None, :].astype(jnp.float32), orders[None, :].astype(jnp.float32)], axis=0
    )
    hit_values = hit.astype(jnp.float32)
    parcels = jnp.concatenate(
        [
            jnp.einsum("qjr,rc->qjc", hit_values, coefficients, precision=exact),
            jnp.einsum("qjr,rc->qjc", hit_values, diffusion, precision=exact),
            jnp.einsum("qjr,rc->qjc", hit_values, velocity, precision=exact),
            jnp.einsum("qjr,cr->qjc", hit_values, counts, precision=exact),
            jnp.zeros(hit.shape[:2] + (128 - side_width,), jnp.float32),
        ],
        axis=2,
    )
    arrivals = []
    got_slot = [jnp.where(destination == here, new_slot, element_count)]
    for index, shift in enumerate(shifts):
        pairs = [(i, (i + shift) % blocks_all) for i in range(blocks_all)]
        arrived = lax.ppermute(parcels[index], ("dom", "face"), pairs)
        arrivals.append(arrived)
        got_slot.append(arrived[:, width + 6].astype(jnp.int32))
    arrivals = jnp.concatenate(arrivals, axis=0)
    got_slot = jnp.concatenate(got_slot, axis=0)
    placing = (got_slot[None, :] == jnp.arange(element_count, dtype=jnp.int32)[:, None]).astype(
        jnp.float32
    )
    staying, coming = placing[:, :element_count], placing[:, element_count:]
    placed = jnp.dot(
        placing, jnp.concatenate([coefficients, arrivals[:, :width]], axis=0), precision=exact
    )
    placed_side = jnp.concatenate(
        [
            jnp.dot(staying, diffusion, precision=exact),
            jnp.dot(staying, velocity, precision=exact),
            jnp.einsum("sr,cr->sc", staying, counts, precision=exact),
        ],
        axis=1,
    ) + jnp.dot(coming, arrivals[:, width : width + side_width], precision=exact)
    weight = placed_side
    top = jnp.asarray(top_modes().astype(np.float32))
    tables = kernel_tables()
    neighbours = jnp.concatenate([local_faces[0], partner_faces[0]], axis=0)
    picks = (
        neighbours[:, :, None] == jnp.arange(element_count, dtype=jnp.int32)[None, None, :]
    ).astype(jnp.bfloat16)
    codes = partner_turns[0].T
    spread_hi, spread_lo, lift, flip = tables
    field = jnp.where(top <= weight[:, 7:8], placed, 0.0)
    slabs = [field[:, a * PLANE : (a + 1) * PLANE] for a in range(P_SIZE)]
    even, total = end_traces(slabs)
    first_step = 0.5 * TIME_STEP
    lower, upper = exchange(even, total)
    pre, even, total = inner(
        (field, weight, top, picks, spread_hi, spread_lo, lift), first_step, None
    )
    below, above, even, total = faces(
        lower, upper, picks, codes, flip, top, weight, even, total, first_step
    )
    lower, upper = exchange(even, total)
    advanced = inner(
        (pre, below, above, field, weight, top, picks, spread_hi, spread_lo, lift)
        + (lower, upper, codes, flip),
        TIME_STEP,
        first_step,
        final=True,
    )
    return advanced


def solution(mesh):
    in_specs = (
        P(("dom", "face"), None),
        P(("dom", "face"), None),
        P(("dom", "face"), None),
        P(("dom", "face")),
        P(("dom", "face")),
        P(("dom", "face"), None, None),
        P(("dom", "face"), None, None),
        P(("dom", "face"), None, None),
    )
    out_specs = P(("dom", "face"), None)
    return jax.shard_map(shards, mesh=mesh, in_specs=in_specs, out_specs=out_specs, check_vma=False)
```

```python
import functools
import jax
import jax.numpy as jnp
import numpy as np
from jax import lax
from jax.experimental import pallas as pl
from jax.experimental.pallas import tpu as pltpu
from jax.sharding import PartitionSpec as P

P_SIZE = 16
PLANE = P_SIZE * P_SIZE
TIME_STEP = 0.25


def mode_tables():
    ladder = np.arange(P_SIZE)
    spacing = ladder[None, :] - ladder[:, None]
    derivative = np.where(
        (spacing > 0) & (spacing % 2 == 1), (2.0 * ladder[:, None] + 1.0) / P_SIZE, 0.0
    )
    second = derivative @ derivative / P_SIZE
    side_signs = np.stack([(-1.0) ** ladder, np.ones(P_SIZE)])
    weights = (2.0 * ladder + 1.0) / (2.0 * P_SIZE)
    return (derivative, second, side_signs, weights)


def side_table(values_pair):
    identity = np.eye(P_SIZE)
    return np.concatenate(
        [
            np.kron(values_pair[0][:, None], identity),
            np.kron(values_pair[1][:, None], identity),
            np.kron(identity, values_pair[0][:, None]),
            np.kron(identity, values_pair[1][:, None]),
        ],
        axis=1,
    )


def kernel_tables():
    derivative, second, side_signs, weights = mode_tables()
    derivative = derivative.astype(np.float32).astype(np.float64)
    second = second.astype(np.float32).astype(np.float64)
    identity = np.eye(P_SIZE)
    traces = side_table(side_signs)
    swapped = traces[:, [16 * g + j for g in (1, 0, 3, 2) for j in range(P_SIZE)]]
    pad = np.zeros((PLANE, 64))
    spread = np.concatenate(
        [
            np.kron(identity, second.T),
            np.kron(second.T, identity),
            np.kron(identity, derivative.T),
            np.kron(derivative.T, identity),
            traces, pad, swapped, pad,
        ],
        axis=1,
    ).astype(np.float32)
    spread_hi = spread.astype(jnp.bfloat16)
    spread_lo = (spread[:, : 2 * PLANE] - spread_hi[:, : 2 * PLANE].astype(np.float32)).astype(jnp.bfloat16)
    lift_signs = side_signs * weights[None, :]
    lift = np.concatenate([side_table(lift_signs).T, np.zeros((64, PLANE))], axis=0)
    lanes = np.arange(PLANE)
    flip = np.zeros((PLANE, PLANE))
    flip[lanes, (lanes % P_SIZE) * P_SIZE + lanes // P_SIZE] = 1.0
    return (
        jnp.asarray(spread_hi),
        jnp.asarray(spread_lo),
        jnp.asarray(lift, jnp.bfloat16),
        jnp.asarray(flip, jnp.bfloat16),
    )


def top_modes():
    ladder = np.arange(P_SIZE)
    first_idx, second_idx, third_idx = np.meshgrid(ladder, ladder, ladder, indexing="ij")
    return np.maximum(np.maximum(first_idx, second_idx), third_idx).reshape(1, -1).astype(np.int32)


def split_two(x):
    hi = x.astype(jnp.bfloat16)
    lo = (x - hi.astype(jnp.float32)).astype(jnp.bfloat16)
    return hi, lo


def mxu(a, b):
    return jnp.dot(a, b, preferred_element_type=jnp.float32)


def split_three(x):
    hi = x.astype(jnp.bfloat16)
    rest = x - hi.astype(jnp.float32)
    mid = rest.astype(jnp.bfloat16)
    lo = (rest - mid.astype(jnp.float32)).astype(jnp.bfloat16)
    return hi, mid, lo


def exact_pick(onehot, x):
    width = x.shape[1]
    joined = mxu(onehot, jnp.concatenate(split_three(x), axis=1))
    return joined[:, :width] + joined[:, width : 2 * width] + joined[:, 2 * width :]


def exact_rows(x, onehot):
    count = x.shape[0]
    joined = mxu(jnp.concatenate(split_three(x), axis=0), onehot)
    return joined[:count] + joined[count : 2 * count] + joined[2 * count :]


def end_traces(slabs):
    total = slabs[0] + slabs[1]
    even = slabs[0] - slabs[1]
    for a in range(2, P_SIZE):
        total = total + slabs[a]
        even = even + slabs[a] if a % 2 == 0 else even - slabs[a]
    return even, total


def turn_pair(lower, upper, picks, codes, flip):
    count = lower.shape[0]
    picked = jnp.concatenate([exact_pick(picks[4], lower), exact_pick(picks[5], upper)], axis=0)
    swapped = exact_rows(picked, flip)
    lane = lax.broadcasted_iota(jnp.int32, (1, PLANE), 1)
    row_odd = (lane // P_SIZE) % 2 == 1
    col_odd = lane % 2 == 1
    sides = []
    for side in range(2):
        rows = slice(side * count, (side + 1) * count)
        code = codes[:, side : side + 1]
        chosen = jnp.where(code % 2 == 1, swapped[rows], picked[rows])
        negate = ((code // 2) % 2 == 1) & row_odd
        negate = negate != (((code // 4) % 2 == 1) & col_odd)
        sides.append(jnp.where(negate, -chosen, chosen))
    return sides


def face_lift(below, above, live, a, scale):
    derivative, second, side_signs, weights = mode_tables()
    lift_signs = (side_signs * weights[None, :]).astype(np.float32)
    update = float(lift_signs[0, a]) * below + float(lift_signs[1, a]) * above
    return scale * jnp.where(live, update, 0.0)


def inner_body(*refs, scale, carried, final):
    if carried is None:
        v_ref, weight_ref, top_ref, pick_ref, spread_hi_ref, spread_lo_ref, lift_ref = refs[:7]
        base_ref = v_ref
    else:
        v_ref, below_ref, above_ref, base_ref, weight_ref, top_ref, pick_ref = refs[:7]
        spread_hi_ref, spread_lo_ref, lift_ref = refs[7:10]
    if final:
        lower_ref, upper_ref, turn_ref, flip_ref = refs[10:14]
        partial_ref = refs[-1]
    else:
        partial_ref, even_ref, total_ref = refs[-3:]
    count = v_ref.shape[0]
    derivative, second, side_signs, weights = mode_tables()
    second = second.astype(np.float32)
    derivative = derivative.astype(np.float32)
    lift_signs = (side_signs * weights[None, :]).astype(np.float32)
    weight = weight_ref[...]
    top = top_ref[...]
    order = weight[:, 7:8]
    slabs = [v_ref[:, a * PLANE : (a + 1) * PLANE] for a in range(P_SIZE)]
    if carried is not None:
        below = below_ref[...]
        above = above_ref[...]
        slabs = [
            slabs[a] + face_lift(below, above, top[:, a * PLANE : (a + 1) * PLANE] <= order, a, carried)
            for a in range(P_SIZE)
        ]
    diff0 = jnp.broadcast_to(weight[:, 0:1], (count, PLANE))
    vel0 = jnp.broadcast_to(weight[:, 3:4], (count, PLANE))
    half = count // 2
    low = P_SIZE // 2

    def kept(a, x):
        return x if a < low else x[half:]

    def start(a):
        return a * count if a < low else low * count + (a - low) * half

    upper_slabs = [s[half:] for s in slabs]
    first = []
    for k in range(P_SIZE):
        parts = []
        for rows, source in ((slice(0, half), slabs), (slice(half, count), upper_slabs)):
            if rows.start == 0 and k >= low:
                continue
            acc_s = None
            acc_d = None
            top_n = low if rows.start == 0 else P_SIZE
            for n in range(k + 1, top_n):
                piece = source[n] if rows.start else source[n][:half]
                if second[k, n] != 0.0:
                    term = float(second[k, n]) * piece
                    acc_s = term if acc_s is None else acc_s + term
                if derivative[k, n] != 0.0:
                    term = float(derivative[k, n]) * piece
                    acc_d = term if acc_d is None else acc_d + term
            part = jnp.zeros((half, PLANE), jnp.float32)
            if acc_s is not None:
                part = part + diff0[rows] * acc_s
            if acc_d is not None:
                part = part - vel0[rows] * acc_d
            parts.append(part)
        first.append(parts[0] if len(parts) == 1 else jnp.concatenate(parts, axis=0))
    stacked = jnp.concatenate([kept(a, slabs[a]) for a in range(P_SIZE)], axis=0)
    hi, lo = split_two(stacked)
    spread_hi = spread_hi_ref[...]
    wide = mxu(hi, spread_hi) + mxu(lo, spread_hi)
    fine = mxu(hi, spread_lo_ref[...])
    weight_rows = jnp.concatenate([kept(a, weight) for a in range(P_SIZE)], axis=0)
    inner = (
        weight_rows[:, 2:3] * (wide[:, 0:PLANE] + fine[:, 0:PLANE])
        + weight_rows[:, 1:2] * (wide[:, PLANE : 2 * PLANE] + fine[:, PLANE : 2 * PLANE])
        - weight_rows[:, 5:6] * wide[:, 2 * PLANE : 3 * PLANE]
        - weight_rows[:, 4:5] * wide[:, 3 * PLANE : 4 * PLANE]
    )
    blank = jnp.zeros((half, 128), jnp.float32)

    def trace_block(a, offset):
        rows = wide[start(a) : start(a) + (count if a < low else half), offset : offset + 128]
        return rows if a < low else jnp.concatenate([blank, rows], axis=0)

    own = jnp.concatenate([trace_block(a, 4 * PLANE) for a in range(P_SIZE)], axis=1)
    other = jnp.concatenate([trace_block(a, 4 * PLANE + 128) for a in range(P_SIZE)], axis=1)
    lane = lax.broadcasted_iota(jnp.int32, (1, P_SIZE * 128), 1) % 128
    across = jnp.zeros_like(own)
    for face in range(4):
        gathered = exact_pick(pick_ref[face], other)
        across = jnp.where(lane // P_SIZE == face, gathered, across)
    jump = own - across
    jump_rows = jnp.concatenate(
        [kept(a, jump[:, a * 128 : (a + 1) * 128]) for a in range(P_SIZE)], axis=0
    )
    jhi, jlo = split_two(jump_rows)
    lift_mat = lift_ref[...]
    lifted = mxu(jhi, lift_mat) + mxu(jlo, lift_mat)
    even, total = end_traces(slabs)
    if final:
        below, above = turn_pair(
            lower_ref[...], upper_ref[...], pick_ref, turn_ref[...], flip_ref[...]
        )
    news = []
    for a in range(P_SIZE):
        rows = slice(start(a), start(a) + (count if a < low else half))
        lanes = slice(a * PLANE, (a + 1) * PLANE)
        own_lift = lifted[rows] + float(lift_signs[0, a]) * kept(a, even)
        own_lift = own_lift + float(lift_signs[1, a]) * kept(a, total)
        if final:
            own_lift = own_lift - float(lift_signs[0, a]) * kept(a, below)
            own_lift = own_lift - float(lift_signs[1, a]) * kept(a, above)
        live = kept(a, top[:, lanes] <= order)
        update = jnp.where(live, first[a] + inner[rows] - own_lift, 0.0)
        if a < low:
            new = base_ref[:, lanes] + scale * update
        else:
            new = jnp.concatenate(
                [base_ref[:half, lanes] + 0.0, base_ref[half:, lanes] + scale * update], axis=0
            )
        partial_ref[:, lanes] = new
        news.append(new)
    if not final:
        even, total = end_traces(news)
        even_ref[...] = even
        total_ref[...] = total


def faces_body(
    lower_ref, upper_ref, pick_ref, turn_ref, flip_ref, top_ref, weight_ref, even_ref, total_ref,
    below_ref, above_ref, new_even_ref, new_total_ref, *, scale
):
    below, above = turn_pair(lower_ref[...], upper_ref[...], pick_ref, turn_ref[...], flip_ref[...])
    below_ref[...] = below
    above_ref[...] = above
    top = top_ref[...]
    order = weight_ref[:, 7:8]
    parts = [
        face_lift(below, above, top[:, a * PLANE : (a + 1) * PLANE] <= order, a, scale)
        for a in range(P_SIZE)
    ]
    even, total = end_traces(parts)
    new_even_ref[...] = even_ref[...] + even
    new_total_ref[...] = total_ref[...] + total


def outer_body(
    pre_ref, top_ref, weight_ref, lower_ref, upper_ref, pick_ref, turn_ref, flip_ref,
    out_ref, even_ref, total_ref, *, scale
):
    derivative, second, side_signs, weights = mode_tables()
    lift_signs = (side_signs * weights[None, :]).astype(np.float32)
    below, above = turn_pair(lower_ref[...], upper_ref[...], pick_ref, turn_ref[...], flip_ref[...])
    top = top_ref[...]
    order = weight_ref[:, 7:8]
    news = []
    for a in range(P_SIZE):
        lanes = slice(a * PLANE, (a + 1) * PLANE)
        update = float(lift_signs[0, a]) * below + float(lift_signs[1, a]) * above
        live = top[:, lanes] <= order
        new = pre_ref[:, lanes] + scale * jnp.where(live, update, 0.0)
        out_ref[:, lanes] = new
        news.append(new)
    even, total = end_traces(news)
    even_ref[...] = even
    total_ref[...] = total


def inner(operands, scale, carried, final=False):
    count = operands[0].shape[0]
    spec = pl.BlockSpec(memory_space=pltpu.VMEM)
    square = jax.ShapeDtypeStruct((count, PLANE), jnp.float32)
    field = jax.ShapeDtypeStruct(operands[0].shape, jnp.float32)
    return pl.pallas_call(
        functools.partial(inner_body, scale=scale, carried=carried, final=final),
        out_shape=field if final else (field, square, square),
        in_specs=[spec] * len(operands),
        out_specs=spec if final else (spec, spec, spec),
        compiler_params=pltpu.CompilerParams(vmem_limit_bytes=60 * 1024 * 1024),
        cost_estimate=pl.CostEstimate(
            flops=2_500_000_000, transcendentals=0, bytes_accessed=4_000_000
        ),
    )(*operands)


def faces(lower, upper, picks, codes, flip, top, weight, even, total, scale):
    count = lower.shape[0]
    spec = pl.BlockSpec(memory_space=pltpu.VMEM)
    square = jax.ShapeDtypeStruct((count, PLANE), jnp.float32)
    return pl.pallas_call(
        functools.partial(faces_body, scale=scale),
        out_shape=(square,) * 4,
        in_specs=[spec] * 9,
        out_specs=(spec,) * 4,
    )(lower, upper, picks, codes, flip, top, weight, even, total)


def outer(pre, top, weight, lower, upper, picks, codes, flip, scale):
    count = pre.shape[0]
    spec = pl.BlockSpec(memory_space=pltpu.VMEM)
    return pl.pallas_call(
        functools.partial(outer_body, scale=scale),
        out_shape=(
            jax.ShapeDtypeStruct(pre.shape, jnp.float32),
            jax.ShapeDtypeStruct((count, PLANE), jnp.float32),
            jax.ShapeDtypeStruct((count, PLANE), jnp.float32),
        ),
        in_specs=[spec] * 8,
        out_specs=(spec, spec, spec),
    )(pre, top, weight, lower, upper, picks, codes, flip)


def prep_body(placed_ref, top_ref, weight_ref, field_ref, even_ref, total_ref):
    news = []
    for a in range(P_SIZE):
        lanes = slice(a * PLANE, (a + 1) * PLANE)
        live = top_ref[:, lanes] <= weight_ref[:, 7:8]
        new = jnp.where(live, placed_ref[:, lanes], 0.0)
        field_ref[:, lanes] = new
        news.append(new)
    even, total = end_traces(news)
    even_ref[...] = even
    total_ref[...] = total


def prep(placed, top, weight):
    count = placed.shape[0]
    spec = pl.BlockSpec(memory_space=pltpu.VMEM)
    return pl.pallas_call(
        prep_body,
        out_shape=(
            jax.ShapeDtypeStruct(placed.shape, jnp.float32),
            jax.ShapeDtypeStruct((count, PLANE), jnp.float32),
            jax.ShapeDtypeStruct((count, PLANE), jnp.float32),
        ),
        in_specs=[spec] * 3,
        out_specs=(spec, spec, spec),
    )(placed, top, weight)


def exchange(even, total):
    size = lax.axis_size("dom")
    up = [(i, (i + 1) % size) for i in range(size)]
    down = [((i + 1) % size, i) for i in range(size)]
    return lax.ppermute(total, "dom", up), lax.ppermute(even, "dom", down)


def shards(
    coefficients, diffusion, velocity, orders, target, local_faces, partner_faces, partner_turns
):
    element_count = coefficients.shape[0]
    blocks_all = lax.axis_size(("dom", "face"))
    moving = element_count // 16
    destination = target // element_count
    new_slot = target % element_count
    here = lax.axis_index(("dom", "face"))
    side_info = jnp.concatenate(
        [
            diffusion,
            velocity,
            new_slot[:, None].astype(jnp.float32),
            orders[:, None].astype(jnp.float32),
        ],
        axis=1,
    )
    side_width = side_info.shape[1]
    shifts = (1, blocks_all - 1, blocks_all // 2)
    offset = (destination - here + blocks_all) % blocks_all
    chosen = offset[None, :] == jnp.asarray(shifts, jnp.int32)[:, None]
    rank = jnp.cumsum(chosen.astype(jnp.int32), axis=1) - 1
    hit = chosen[:, None, :] & (
        rank[:, None, :] == jnp.arange(moving, dtype=jnp.int32)[None, :, None]
    )
    width = P_SIZE**3
    exact = lax.Precision.HIGHEST
    counts = jnp.concatenate(
        [new_slot[None, :].astype(jnp.float32), orders[None, :].astype(jnp.float32)], axis=0
    )
    hit_values = hit.astype(jnp.float32)
    parcels = jnp.concatenate(
        [
            jnp.einsum("qjr,rc->qjc", hit_values, coefficients, precision=exact),
            jnp.einsum("qjr,rc->qjc", hit_values, diffusion, precision=exact),
            jnp.einsum("qjr,rc->qjc", hit_values, velocity, precision=exact),
            jnp.einsum("qjr,cr->qjc", hit_values, counts, precision=exact),
            jnp.zeros(hit.shape[:2] + (128 - side_width,), jnp.float32),
        ],
        axis=2,
    )
    arrivals = []
    got_slot = [jnp.where(destination == here, new_slot, element_count)]
    for index, shift in enumerate(shifts):
        pairs = [(i, (i + shift) % blocks_all) for i in range(blocks_all)]
        arrived = lax.ppermute(parcels[index], ("dom", "face"), pairs)
        arrivals.append(arrived)
        got_slot.append(arrived[:, width + 6].astype(jnp.int32))
    arrivals = jnp.concatenate(arrivals, axis=0)
    got_slot = jnp.concatenate(got_slot, axis=0)
    placing = (got_slot[None, :] == jnp.arange(element_count, dtype=jnp.int32)[:, None]).astype(
        jnp.float32
    )
    staying, coming = placing[:, :element_count], placing[:, element_count:]
    placed = jnp.dot(
        placing, jnp.concatenate([coefficients, arrivals[:, :width]], axis=0), precision=exact
    )
    placed_side = jnp.concatenate(
        [
            jnp.dot(staying, diffusion, precision=exact),
            jnp.dot(staying, velocity, precision=exact),
            jnp.einsum("sr,cr->sc", staying, counts, precision=exact),
        ],
        axis=1,
    ) + jnp.dot(coming, arrivals[:, width : width + side_width], precision=exact)
    weight = placed_side
    top = jnp.asarray(top_modes().astype(np.float32))
    tables = kernel_tables()
    neighbours = jnp.concatenate([local_faces[0], partner_faces[0]], axis=0)
    picks = (
        neighbours[:, :, None] == jnp.arange(element_count, dtype=jnp.int32)[None, None, :]
    ).astype(jnp.bfloat16)
    codes = partner_turns[0].T
    spread_hi, spread_lo, lift, flip = tables
    field = jnp.where(top <= weight[:, 7:8], placed, 0.0)
    slabs = [field[:, a * PLANE : (a + 1) * PLANE] for a in range(P_SIZE)]
    even, total = end_traces(slabs)
    first_step = 0.5 * TIME_STEP
    lower, upper = exchange(even, total)
    pre, even, total = inner(
        (field, weight, top, picks, spread_hi, spread_lo, lift), first_step, None
    )
    below, above, even, total = faces(
        lower, upper, picks, codes, flip, top, weight, even, total, first_step
    )
    lower, upper = exchange(even, total)
    advanced = inner(
        (pre, below, above, field, weight, top, picks, spread_hi, spread_lo, lift)
        + (lower, upper, codes, flip),
        TIME_STEP,
        first_step,
        final=True,
    )
    return advanced


def solution(mesh):
    in_specs = (
        P(("dom", "face"), None),
        P(("dom", "face"), None),
        P(("dom", "face"), None),
        P(("dom", "face")),
        P(("dom", "face")),
        P(("dom", "face"), None, None),
        P(("dom", "face"), None, None),
        P(("dom", "face"), None, None),
    )
    out_specs = P(("dom", "face"), None)
    return jax.shard_map(shards, mesh=mesh, in_specs=in_specs, out_specs=out_specs, check_vma=False)
```

```python
import functools
import jax
import jax.numpy as jnp
import numpy as np
from jax import lax
from jax.experimental import pallas as pl
from jax.experimental.pallas import tpu as pltpu
from jax.sharding import PartitionSpec as P

P_SIZE = 16
PLANE = P_SIZE * P_SIZE
TIME_STEP = 0.25


def mode_tables():
    ladder = np.arange(P_SIZE)
    spacing = ladder[None, :] - ladder[:, None]
    derivative = np.where(
        (spacing > 0) & (spacing % 2 == 1), (2.0 * ladder[:, None] + 1.0) / P_SIZE, 0.0
    )
    second = derivative @ derivative / P_SIZE
    side_signs = np.stack([(-1.0) ** ladder, np.ones(P_SIZE)])
    weights = (2.0 * ladder + 1.0) / (2.0 * P_SIZE)
    return (derivative, second, side_signs, weights)


def side_table(values_pair):
    identity = np.eye(P_SIZE)
    return np.concatenate(
        [
            np.kron(values_pair[0][:, None], identity),
            np.kron(values_pair[1][:, None], identity),
            np.kron(identity, values_pair[0][:, None]),
            np.kron(identity, values_pair[1][:, None]),
        ],
        axis=1,
    )


def kernel_tables():
    derivative, second, side_signs, weights = mode_tables()
    derivative = derivative.astype(np.float32).astype(np.float64)
    second = second.astype(np.float32).astype(np.float64)
    identity = np.eye(P_SIZE)
    traces = side_table(side_signs)
    swapped = traces[:, [16 * g + j for g in (1, 0, 3, 2) for j in range(P_SIZE)]]
    pad = np.zeros((PLANE, 64))
    spread = np.concatenate(
        [
            np.kron(identity, second.T),
            np.kron(second.T, identity),
            np.kron(identity, derivative.T),
            np.kron(derivative.T, identity),
            traces, swapped,
        ],
        axis=1,
    ).astype(np.float32)
    spread_hi = spread.astype(jnp.bfloat16)
    spread_lo = (spread[:, : 2 * PLANE] - spread_hi[:, : 2 * PLANE].astype(np.float32)).astype(jnp.bfloat16)
    lift_signs = side_signs * weights[None, :]
    lift = np.concatenate([side_table(lift_signs).T, np.zeros((64, PLANE))], axis=0)
    lanes = np.arange(PLANE)
    flip = np.zeros((PLANE, PLANE))
    flip[lanes, (lanes % P_SIZE) * P_SIZE + lanes // P_SIZE] = 1.0
    return (
        jnp.asarray(spread_hi),
        jnp.asarray(spread_lo),
        jnp.asarray(lift, jnp.bfloat16),
        jnp.asarray(flip, jnp.bfloat16),
    )


def top_modes():
    ladder = np.arange(P_SIZE)
    first_idx, second_idx, third_idx = np.meshgrid(ladder, ladder, ladder, indexing="ij")
    return np.maximum(np.maximum(first_idx, second_idx), third_idx).reshape(1, -1).astype(np.int32)


def split_two(x):
    hi = x.astype(jnp.bfloat16)
    lo = (x - hi.astype(jnp.float32)).astype(jnp.bfloat16)
    return hi, lo


def mxu(a, b):
    return jnp.dot(a, b, preferred_element_type=jnp.float32)


def split_three(x):
    hi = x.astype(jnp.bfloat16)
    rest = x - hi.astype(jnp.float32)
    mid = rest.astype(jnp.bfloat16)
    lo = (rest - mid.astype(jnp.float32)).astype(jnp.bfloat16)
    return hi, mid, lo


def exact_pick(onehot, x):
    width = x.shape[1]
    joined = mxu(onehot, jnp.concatenate(split_three(x), axis=1))
    return joined[:, :width] + joined[:, width : 2 * width] + joined[:, 2 * width :]


def exact_rows(x, onehot):
    count = x.shape[0]
    joined = mxu(jnp.concatenate(split_three(x), axis=0), onehot)
    return joined[:count] + joined[count : 2 * count] + joined[2 * count :]


def end_traces(slabs):
    total = slabs[0] + slabs[1]
    even = slabs[0] - slabs[1]
    for a in range(2, P_SIZE):
        total = total + slabs[a]
        even = even + slabs[a] if a % 2 == 0 else even - slabs[a]
    return even, total


def turn_pair(lower, upper, picks, codes, flip):
    count = lower.shape[0]
    picked = jnp.concatenate([exact_pick(picks[4], lower), exact_pick(picks[5], upper)], axis=0)
    swapped = exact_rows(picked, flip)
    lane = lax.broadcasted_iota(jnp.int32, (1, PLANE), 1)
    row_odd = (lane // P_SIZE) % 2 == 1
    col_odd = lane % 2 == 1
    sides = []
    for side in range(2):
        rows = slice(side * count, (side + 1) * count)
        code = codes[:, side : side + 1]
        chosen = jnp.where(code % 2 == 1, swapped[rows], picked[rows])
        negate = ((code // 2) % 2 == 1) & row_odd
        negate = negate != (((code // 4) % 2 == 1) & col_odd)
        sides.append(jnp.where(negate, -chosen, chosen))
    return sides


def face_lift(below, above, live, a, scale):
    derivative, second, side_signs, weights = mode_tables()
    lift_signs = (side_signs * weights[None, :]).astype(np.float32)
    update = float(lift_signs[0, a]) * below + float(lift_signs[1, a]) * above
    return scale * jnp.where(live, update, 0.0)


def inner_body(*refs, scale, carried, final):
    if carried is None:
        v_ref, weight_ref, top_ref, pick_ref, spread_hi_ref, spread_lo_ref, lift_ref = refs[:7]
        base_ref = v_ref
    else:
        v_ref, below_ref, above_ref, base_ref, weight_ref, top_ref, pick_ref = refs[:7]
        spread_hi_ref, spread_lo_ref, lift_ref = refs[7:10]
    if final:
        lower_ref, upper_ref, turn_ref, flip_ref = refs[10:14]
        partial_ref = refs[-1]
    else:
        partial_ref, even_ref, total_ref = refs[-3:]
    count = v_ref.shape[0]
    derivative, second, side_signs, weights = mode_tables()
    second = second.astype(np.float32)
    derivative = derivative.astype(np.float32)
    lift_signs = (side_signs * weights[None, :]).astype(np.float32)
    weight = weight_ref[...]
    top = top_ref[...]
    order = weight[:, 7:8]
    slabs = [v_ref[:, a * PLANE : (a + 1) * PLANE] for a in range(P_SIZE)]
    if carried is not None:
        below = below_ref[...]
        above = above_ref[...]
        slabs = [
            slabs[a] + face_lift(below, above, top[:, a * PLANE : (a + 1) * PLANE] <= order, a, carried)
            for a in range(P_SIZE)
        ]
    diff0 = jnp.broadcast_to(weight[:, 0:1], (count, PLANE))
    vel0 = jnp.broadcast_to(weight[:, 3:4], (count, PLANE))
    half = count // 2
    low = P_SIZE // 2

    def kept(a, x):
        return x if a < low else x[half:]

    def start(a):
        return a * count if a < low else low * count + (a - low) * half

    upper_slabs = [s[half:] for s in slabs]
    first = []
    for k in range(P_SIZE):
        parts = []
        for rows, source in ((slice(0, half), slabs), (slice(half, count), upper_slabs)):
            if rows.start == 0 and k >= low:
                continue
            acc_s = None
            acc_d = None
            top_n = low if rows.start == 0 else P_SIZE
            for n in range(k + 1, top_n):
                piece = source[n] if rows.start else source[n][:half]
                if second[k, n] != 0.0:
                    term = float(second[k, n]) * piece
                    acc_s = term if acc_s is None else acc_s + term
                if derivative[k, n] != 0.0:
                    term = float(derivative[k, n]) * piece
                    acc_d = term if acc_d is None else acc_d + term
            part = jnp.zeros((half, PLANE), jnp.float32)
            if acc_s is not None:
                part = part + diff0[rows] * acc_s
            if acc_d is not None:
                part = part - vel0[rows] * acc_d
            parts.append(part)
        first.append(parts[0] if len(parts) == 1 else jnp.concatenate(parts, axis=0))
    stacked = jnp.concatenate([kept(a, slabs[a]) for a in range(P_SIZE)], axis=0)
    hi, lo = split_two(stacked)
    spread_hi = spread_hi_ref[...]
    wide = mxu(hi, spread_hi) + mxu(lo, spread_hi)
    fine = mxu(hi, spread_lo_ref[...])
    weight_rows = jnp.concatenate([kept(a, weight) for a in range(P_SIZE)], axis=0)
    inner = (
        weight_rows[:, 2:3] * (wide[:, 0:PLANE] + fine[:, 0:PLANE])
        + weight_rows[:, 1:2] * (wide[:, PLANE : 2 * PLANE] + fine[:, PLANE : 2 * PLANE])
        - weight_rows[:, 5:6] * wide[:, 2 * PLANE : 3 * PLANE]
        - weight_rows[:, 4:5] * wide[:, 3 * PLANE : 4 * PLANE]
    )
    blank = jnp.zeros((half, 128), jnp.float32)

    def trace_block(a, offset):
        rows = wide[start(a) : start(a) + (count if a < low else half), offset : offset + 128]
        return rows if a < low else jnp.concatenate([blank, rows], axis=0)

    own = jnp.concatenate([trace_block(a, 4 * PLANE) for a in range(P_SIZE)], axis=1)
    other = own
    lane = lax.broadcasted_iota(jnp.int32, (1, P_SIZE * 128), 1) % 128
    across = jnp.zeros_like(own)
    for face in range(4):
        gathered = pltpu.roll(exact_pick(pick_ref[face], other), P_SIZE * 128 - 64, 1)
        across = jnp.where(lane // P_SIZE == face, gathered, across)
    jump = own - across
    jump_rows = jnp.concatenate(
        [kept(a, jump[:, a * 128 : (a + 1) * 128]) for a in range(P_SIZE)], axis=0
    )
    jhi, jlo = split_two(jump_rows)
    lift_mat = lift_ref[...]
    lifted = mxu(jhi, lift_mat) + mxu(jlo, lift_mat)
    even, total = end_traces(slabs)
    if final:
        below, above = turn_pair(
            lower_ref[...], upper_ref[...], pick_ref, turn_ref[...], flip_ref[...]
        )
    news = []
    for a in range(P_SIZE):
        rows = slice(start(a), start(a) + (count if a < low else half))
        lanes = slice(a * PLANE, (a + 1) * PLANE)
        own_lift = lifted[rows] + float(lift_signs[0, a]) * kept(a, even)
        own_lift = own_lift + float(lift_signs[1, a]) * kept(a, total)
        if final:
            own_lift = own_lift - float(lift_signs[0, a]) * kept(a, below)
            own_lift = own_lift - float(lift_signs[1, a]) * kept(a, above)
        live = kept(a, top[:, lanes] <= order)
        update = jnp.where(live, first[a] + inner[rows] - own_lift, 0.0)
        if a < low:
            new = base_ref[:, lanes] + scale * update
        else:
            new = jnp.concatenate(
                [base_ref[:half, lanes] + 0.0, base_ref[half:, lanes] + scale * update], axis=0
            )
        partial_ref[:, lanes] = new
        news.append(new)
    if not final:
        even, total = end_traces(news)
        even_ref[...] = even
        total_ref[...] = total


def faces_body(
    lower_ref, upper_ref, pick_ref, turn_ref, flip_ref, top_ref, weight_ref, even_ref, total_ref,
    below_ref, above_ref, new_even_ref, new_total_ref, *, scale
):
    below, above = turn_pair(lower_ref[...], upper_ref[...], pick_ref, turn_ref[...], flip_ref[...])
    below_ref[...] = below
    above_ref[...] = above
    top = top_ref[...]
    order = weight_ref[:, 7:8]
    parts = [
        face_lift(below, above, top[:, a * PLANE : (a + 1) * PLANE] <= order, a, scale)
        for a in range(P_SIZE)
    ]
    even, total = end_traces(parts)
    new_even_ref[...] = even_ref[...] + even
    new_total_ref[...] = total_ref[...] + total


def outer_body(
    pre_ref, top_ref, weight_ref, lower_ref, upper_ref, pick_ref, turn_ref, flip_ref,
    out_ref, even_ref, total_ref, *, scale
):
    derivative, second, side_signs, weights = mode_tables()
    lift_signs = (side_signs * weights[None, :]).astype(np.float32)
    below, above = turn_pair(lower_ref[...], upper_ref[...], pick_ref, turn_ref[...], flip_ref[...])
    top = top_ref[...]
    order = weight_ref[:, 7:8]
    news = []
    for a in range(P_SIZE):
        lanes = slice(a * PLANE, (a + 1) * PLANE)
        update = float(lift_signs[0, a]) * below + float(lift_signs[1, a]) * above
        live = top[:, lanes] <= order
        new = pre_ref[:, lanes] + scale * jnp.where(live, update, 0.0)
        out_ref[:, lanes] = new
        news.append(new)
    even, total = end_traces(news)
    even_ref[...] = even
    total_ref[...] = total


def inner(operands, scale, carried, final=False):
    count = operands[0].shape[0]
    spec = pl.BlockSpec(memory_space=pltpu.VMEM)
    square = jax.ShapeDtypeStruct((count, PLANE), jnp.float32)
    field = jax.ShapeDtypeStruct(operands[0].shape, jnp.float32)
    return pl.pallas_call(
        functools.partial(inner_body, scale=scale, carried=carried, final=final),
        out_shape=field if final else (field, square, square),
        in_specs=[spec] * len(operands),
        out_specs=spec if final else (spec, spec, spec),
        compiler_params=pltpu.CompilerParams(vmem_limit_bytes=60 * 1024 * 1024),
        cost_estimate=pl.CostEstimate(
            flops=2_500_000_000, transcendentals=0, bytes_accessed=4_000_000
        ),
    )(*operands)


def faces(lower, upper, picks, codes, flip, top, weight, even, total, scale):
    count = lower.shape[0]
    spec = pl.BlockSpec(memory_space=pltpu.VMEM)
    square = jax.ShapeDtypeStruct((count, PLANE), jnp.float32)
    return pl.pallas_call(
        functools.partial(faces_body, scale=scale),
        out_shape=(square,) * 4,
        in_specs=[spec] * 9,
        out_specs=(spec,) * 4,
    )(lower, upper, picks, codes, flip, top, weight, even, total)


def outer(pre, top, weight, lower, upper, picks, codes, flip, scale):
    count = pre.shape[0]
    spec = pl.BlockSpec(memory_space=pltpu.VMEM)
    return pl.pallas_call(
        functools.partial(outer_body, scale=scale),
        out_shape=(
            jax.ShapeDtypeStruct(pre.shape, jnp.float32),
            jax.ShapeDtypeStruct((count, PLANE), jnp.float32),
            jax.ShapeDtypeStruct((count, PLANE), jnp.float32),
        ),
        in_specs=[spec] * 8,
        out_specs=(spec, spec, spec),
    )(pre, top, weight, lower, upper, picks, codes, flip)


def prep_body(placed_ref, top_ref, weight_ref, field_ref, even_ref, total_ref):
    news = []
    for a in range(P_SIZE):
        lanes = slice(a * PLANE, (a + 1) * PLANE)
        live = top_ref[:, lanes] <= weight_ref[:, 7:8]
        new = jnp.where(live, placed_ref[:, lanes], 0.0)
        field_ref[:, lanes] = new
        news.append(new)
    even, total = end_traces(news)
    even_ref[...] = even
    total_ref[...] = total


def prep(placed, top, weight):
    count = placed.shape[0]
    spec = pl.BlockSpec(memory_space=pltpu.VMEM)
    return pl.pallas_call(
        prep_body,
        out_shape=(
            jax.ShapeDtypeStruct(placed.shape, jnp.float32),
            jax.ShapeDtypeStruct((count, PLANE), jnp.float32),
            jax.ShapeDtypeStruct((count, PLANE), jnp.float32),
        ),
        in_specs=[spec] * 3,
        out_specs=(spec, spec, spec),
    )(placed, top, weight)


def exchange(even, total):
    size = lax.axis_size("dom")
    up = [(i, (i + 1) % size) for i in range(size)]
    down = [((i + 1) % size, i) for i in range(size)]
    return lax.ppermute(total, "dom", up), lax.ppermute(even, "dom", down)


def shards(
    coefficients, diffusion, velocity, orders, target, local_faces, partner_faces, partner_turns
):
    element_count = coefficients.shape[0]
    blocks_all = lax.axis_size(("dom", "face"))
    moving = element_count // 16
    destination = target // element_count
    new_slot = target % element_count
    here = lax.axis_index(("dom", "face"))
    side_info = jnp.concatenate(
        [
            diffusion,
            velocity,
            new_slot[:, None].astype(jnp.float32),
            orders[:, None].astype(jnp.float32),
        ],
        axis=1,
    )
    side_width = side_info.shape[1]
    shifts = (1, blocks_all - 1, blocks_all // 2)
    goal = (here + jnp.asarray(shifts, jnp.int32)) % blocks_all
    chosen = destination[None, :] == goal[:, None]
    rank = jnp.cumsum(chosen.astype(jnp.int32), axis=1) - 1
    hit = chosen[:, None, :] & (
        rank[:, None, :] == jnp.arange(moving, dtype=jnp.int32)[None, :, None]
    )
    width = P_SIZE**3
    exact = lax.Precision.HIGHEST
    counts = jnp.concatenate(
        [new_slot[None, :].astype(jnp.float32), orders[None, :].astype(jnp.float32)], axis=0
    )
    hit_values = hit.astype(jnp.float32)
    parcels = jnp.concatenate(
        [
            jnp.einsum("qjr,rc->qjc", hit_values, coefficients, precision=exact),
            jnp.einsum("qjr,rc->qjc", hit_values, diffusion, precision=exact),
            jnp.einsum("qjr,rc->qjc", hit_values, velocity, precision=exact),
            jnp.einsum("qjr,cr->qjc", hit_values, counts, precision=exact),
            jnp.zeros(hit.shape[:2] + (128 - side_width,), jnp.float32),
        ],
        axis=2,
    )
    arrivals = []
    got_slot = [jnp.where(destination == here, new_slot, element_count)]
    for index, shift in enumerate(shifts):
        pairs = [(i, (i + shift) % blocks_all) for i in range(blocks_all)]
        arrived = lax.ppermute(parcels[index], ("dom", "face"), pairs)
        arrivals.append(arrived)
        got_slot.append(arrived[:, width + 6].astype(jnp.int32))
    arrivals = jnp.concatenate(arrivals, axis=0)
    got_slot = jnp.concatenate(got_slot, axis=0)
    placing = (got_slot[None, :] == jnp.arange(element_count, dtype=jnp.int32)[:, None]).astype(
        jnp.float32
    )
    staying, coming = placing[:, :element_count], placing[:, element_count:]
    placed = jnp.dot(
        placing, jnp.concatenate([coefficients, arrivals[:, :width]], axis=0), precision=exact
    )
    placed_side = jnp.concatenate(
        [
            jnp.dot(staying, diffusion, precision=exact),
            jnp.dot(staying, velocity, precision=exact),
            jnp.einsum("sr,cr->sc", staying, counts, precision=exact),
        ],
        axis=1,
    ) + jnp.dot(coming, arrivals[:, width : width + side_width], precision=exact)
    weight = placed_side
    top = jnp.asarray(top_modes().astype(np.float32))
    tables = kernel_tables()
    neighbours = jnp.concatenate([local_faces[0], partner_faces[0]], axis=0)
    picks = (
        neighbours[:, :, None] == jnp.arange(element_count, dtype=jnp.int32)[None, None, :]
    ).astype(jnp.bfloat16)
    codes = partner_turns[0].T
    spread_hi, spread_lo, lift, flip = tables
    field = jnp.where(top <= weight[:, 7:8], placed, 0.0)
    slabs = [field[:, a * PLANE : (a + 1) * PLANE] for a in range(P_SIZE)]
    even, total = end_traces(slabs)
    first_step = 0.5 * TIME_STEP
    lower, upper = exchange(even, total)
    pre, even, total = inner(
        (field, weight, top, picks, spread_hi, spread_lo, lift), first_step, None
    )
    below, above, even, total = faces(
        lower, upper, picks, codes, flip, top, weight, even, total, first_step
    )
    lower, upper = exchange(even, total)
    advanced = inner(
        (pre, below, above, field, weight, top, picks, spread_hi, spread_lo, lift)
        + (lower, upper, codes, flip),
        TIME_STEP,
        first_step,
        final=True,
    )
    return advanced


def solution(mesh):
    in_specs = (
        P(("dom", "face"), None),
        P(("dom", "face"), None),
        P(("dom", "face"), None),
        P(("dom", "face")),
        P(("dom", "face")),
        P(("dom", "face"), None, None),
        P(("dom", "face"), None, None),
        P(("dom", "face"), None, None),
    )
    out_specs = P(("dom", "face"), None)
    return jax.shard_map(shards, mesh=mesh, in_specs=in_specs, out_specs=out_specs, check_vma=False)
```

```python
import functools
import jax
import jax.numpy as jnp
import numpy as np
from jax import lax
from jax.experimental import pallas as pl
from jax.experimental.pallas import tpu as pltpu
from jax.sharding import PartitionSpec as P

P_SIZE = 16
PLANE = P_SIZE * P_SIZE
TIME_STEP = 0.25


def mode_tables():
    ladder = np.arange(P_SIZE)
    spacing = ladder[None, :] - ladder[:, None]
    derivative = np.where(
        (spacing > 0) & (spacing % 2 == 1), (2.0 * ladder[:, None] + 1.0) / P_SIZE, 0.0
    )
    second = derivative @ derivative / P_SIZE
    side_signs = np.stack([(-1.0) ** ladder, np.ones(P_SIZE)])
    weights = (2.0 * ladder + 1.0) / (2.0 * P_SIZE)
    return (derivative, second, side_signs, weights)


def side_table(values_pair):
    identity = np.eye(P_SIZE)
    return np.concatenate(
        [
            np.kron(values_pair[0][:, None], identity),
            np.kron(values_pair[1][:, None], identity),
            np.kron(identity, values_pair[0][:, None]),
            np.kron(identity, values_pair[1][:, None]),
        ],
        axis=1,
    )


def kernel_tables():
    derivative, second, side_signs, weights = mode_tables()
    derivative = derivative.astype(np.float32).astype(np.float64)
    second = second.astype(np.float32).astype(np.float64)
    identity = np.eye(P_SIZE)
    traces = side_table(side_signs)
    swapped = traces[:, [16 * g + j for g in (1, 0, 3, 2) for j in range(P_SIZE)]]
    pad = np.zeros((PLANE, 64))
    spread = np.concatenate(
        [
            np.kron(identity, second.T),
            np.kron(second.T, identity),
            np.kron(identity, derivative.T),
            np.kron(derivative.T, identity),
            traces, pad, swapped, pad,
        ],
        axis=1,
    ).astype(np.float32)
    spread_hi = spread.astype(jnp.bfloat16)
    spread_lo = (spread[:, : 2 * PLANE] - spread_hi[:, : 2 * PLANE].astype(np.float32)).astype(jnp.bfloat16)
    lift_signs = side_signs * weights[None, :]
    lift = np.concatenate([side_table(lift_signs).T, np.zeros((64, PLANE))], axis=0)
    lanes = np.arange(PLANE)
    flip = np.zeros((PLANE, PLANE))
    flip[lanes, (lanes % P_SIZE) * P_SIZE + lanes // P_SIZE] = 1.0
    return (
        jnp.asarray(spread_hi),
        jnp.asarray(spread_lo),
        jnp.asarray(lift, jnp.bfloat16),
        jnp.asarray(flip, jnp.bfloat16),
    )


def top_modes():
    ladder = np.arange(P_SIZE)
    first_idx, second_idx, third_idx = np.meshgrid(ladder, ladder, ladder, indexing="ij")
    return np.maximum(np.maximum(first_idx, second_idx), third_idx).reshape(1, -1).astype(np.int32)


def split_two(x):
    hi = x.astype(jnp.bfloat16)
    lo = (x - hi.astype(jnp.float32)).astype(jnp.bfloat16)
    return hi, lo


def mxu(a, b):
    return jnp.dot(a, b, preferred_element_type=jnp.float32)


def split_three(x):
    hi = x.astype(jnp.bfloat16)
    rest = x - hi.astype(jnp.float32)
    mid = rest.astype(jnp.bfloat16)
    lo = (rest - mid.astype(jnp.float32)).astype(jnp.bfloat16)
    return hi, mid, lo


def exact_pick(onehot, x):
    width = x.shape[1]
    joined = mxu(onehot, jnp.concatenate(split_three(x), axis=1))
    return joined[:, :width] + joined[:, width : 2 * width] + joined[:, 2 * width :]


def exact_rows(x, onehot):
    count = x.shape[0]
    joined = mxu(jnp.concatenate(split_three(x), axis=0), onehot)
    return joined[:count] + joined[count : 2 * count] + joined[2 * count :]


def end_traces(slabs):
    total = slabs[0] + slabs[1]
    even = slabs[0] - slabs[1]
    for a in range(2, P_SIZE):
        total = total + slabs[a]
        even = even + slabs[a] if a % 2 == 0 else even - slabs[a]
    return even, total


def turn_pair(lower, upper, picks, codes, flip):
    count = lower.shape[0]
    picked = jnp.concatenate([exact_pick(picks[4], lower), exact_pick(picks[5], upper)], axis=0)
    swapped = exact_rows(picked, flip)
    lane = lax.broadcasted_iota(jnp.int32, (1, PLANE), 1)
    row_odd = (lane // P_SIZE) % 2 == 1
    col_odd = lane % 2 == 1
    sides = []
    for side in range(2):
        rows = slice(side * count, (side + 1) * count)
        code = codes[:, side : side + 1]
        chosen = jnp.where(code % 2 == 1, swapped[rows], picked[rows])
        negate = ((code // 2) % 2 == 1) & row_odd
        negate = negate != (((code // 4) % 2 == 1) & col_odd)
        sides.append(jnp.where(negate, -chosen, chosen))
    return sides


def face_lift(below, above, live, a, scale):
    derivative, second, side_signs, weights = mode_tables()
    lift_signs = (side_signs * weights[None, :]).astype(np.float32)
    update = float(lift_signs[0, a]) * below + float(lift_signs[1, a]) * above
    return scale * jnp.where(live, update, 0.0)


def inner_body(*refs, scale, carried, final):
    if carried is None:
        v_ref, weight_ref, top_ref, pick_ref, spread_hi_ref, spread_lo_ref, lift_ref = refs[:7]
        base_ref = v_ref
    else:
        v_ref, below_ref, above_ref, base_ref, weight_ref, top_ref, pick_ref = refs[:7]
        spread_hi_ref, spread_lo_ref, lift_ref = refs[7:10]
    if final:
        lower_ref, upper_ref, turn_ref, flip_ref = refs[10:14]
        partial_ref = refs[-1]
    else:
        partial_ref, even_ref, total_ref = refs[-3:]
    count = v_ref.shape[0]
    derivative, second, side_signs, weights = mode_tables()
    second = second.astype(np.float32)
    derivative = derivative.astype(np.float32)
    lift_signs = (side_signs * weights[None, :]).astype(np.float32)
    weight = weight_ref[...]
    top = top_ref[...]
    order = weight[:, 7:8]
    slabs = [v_ref[:, a * PLANE : (a + 1) * PLANE] for a in range(P_SIZE)]
    if carried is not None:
        below = below_ref[...]
        above = above_ref[...]
        slabs = [
            slabs[a] + face_lift(below, above, top[:, a * PLANE : (a + 1) * PLANE] <= order, a, carried)
            for a in range(P_SIZE)
        ]
    diff0 = jnp.broadcast_to(weight[:, 0:1], (count, PLANE))
    vel0 = jnp.broadcast_to(weight[:, 3:4], (count, PLANE))
    half = count // 2
    low = P_SIZE // 2

    def kept(a, x):
        return x if a < low else x[half:]

    def start(a):
        return a * count if a < low else low * count + (a - low) * half

    upper_slabs = [s[half:] for s in slabs]
    first = []
    for k in range(P_SIZE):
        parts = []
        for rows, source in ((slice(0, half), slabs), (slice(half, count), upper_slabs)):
            if rows.start == 0 and k >= low:
                continue
            acc_s = None
            acc_d = None
            top_n = low if rows.start == 0 else P_SIZE
            for n in range(k + 1, top_n):
                piece = source[n] if rows.start else source[n][:half]
                if second[k, n] != 0.0:
                    term = float(second[k, n]) * piece
                    acc_s = term if acc_s is None else acc_s + term
                if derivative[k, n] != 0.0:
                    term = float(derivative[k, n]) * piece
                    acc_d = term if acc_d is None else acc_d + term
            part = jnp.zeros((half, PLANE), jnp.float32)
            if acc_s is not None:
                part = part + diff0[rows] * acc_s
            if acc_d is not None:
                part = part - vel0[rows] * acc_d
            parts.append(part)
        first.append(parts[0] if len(parts) == 1 else jnp.concatenate(parts, axis=0))
    stacked = jnp.concatenate([kept(a, slabs[a]) for a in range(P_SIZE)], axis=0)
    hi, lo = split_two(stacked)
    spread_hi = spread_hi_ref[...]
    wide = mxu(hi, spread_hi) + mxu(lo, spread_hi)
    fine = mxu(hi, spread_lo_ref[...])
    weight_rows = jnp.concatenate([kept(a, weight) for a in range(P_SIZE)], axis=0)
    inner = (
        weight_rows[:, 2:3] * (wide[:, 0:PLANE] + fine[:, 0:PLANE])
        + weight_rows[:, 1:2] * (wide[:, PLANE : 2 * PLANE] + fine[:, PLANE : 2 * PLANE])
        - weight_rows[:, 5:6] * wide[:, 2 * PLANE : 3 * PLANE]
        - weight_rows[:, 4:5] * wide[:, 3 * PLANE : 4 * PLANE]
    )
    blank = jnp.zeros((half, 128), jnp.float32)

    def trace_block(a, offset):
        rows = wide[start(a) : start(a) + (count if a < low else half), offset : offset + 128]
        return rows if a < low else jnp.concatenate([blank, rows], axis=0)

    own = jnp.concatenate([trace_block(a, 4 * PLANE) for a in range(P_SIZE)], axis=1)
    other = jnp.concatenate([trace_block(a, 4 * PLANE + 128) for a in range(P_SIZE)], axis=1)
    lane = lax.broadcasted_iota(jnp.int32, (1, P_SIZE * 128), 1) % 128
    across = jnp.zeros_like(own)
    for face in range(4):
        gathered = exact_pick(pick_ref[face], other)
        across = jnp.where(lane // P_SIZE == face, gathered, across)
    jump = own - across
    jump_rows = jnp.concatenate(
        [kept(a, jump[:, a * 128 : (a + 1) * 128]) for a in range(P_SIZE)], axis=0
    )
    jhi, jlo = split_two(jump_rows)
    lift_mat = lift_ref[...]
    lifted = mxu(jhi, lift_mat) + mxu(jlo, lift_mat)
    even, total = end_traces(slabs)
    if final:
        below, above = turn_pair(
            lower_ref[...], upper_ref[...], pick_ref, turn_ref[...], flip_ref[...]
        )
    news = []
    for a in range(P_SIZE):
        rows = slice(start(a), start(a) + (count if a < low else half))
        lanes = slice(a * PLANE, (a + 1) * PLANE)
        own_lift = lifted[rows] + float(lift_signs[0, a]) * kept(a, even)
        own_lift = own_lift + float(lift_signs[1, a]) * kept(a, total)
        if final:
            own_lift = own_lift - float(lift_signs[0, a]) * kept(a, below)
            own_lift = own_lift - float(lift_signs[1, a]) * kept(a, above)
        live = kept(a, top[:, lanes] <= order)
        update = jnp.where(live, first[a] + inner[rows] - own_lift, 0.0)
        if a < low:
            new = base_ref[:, lanes] + scale * update
        else:
            new = jnp.concatenate(
                [base_ref[:half, lanes] + 0.0, base_ref[half:, lanes] + scale * update], axis=0
            )
        partial_ref[:, lanes] = new
        news.append(new)
    if not final:
        even, total = end_traces(news)
        even_ref[...] = even
        total_ref[...] = total


def faces_body(
    lower_ref, upper_ref, pick_ref, turn_ref, flip_ref, top_ref, weight_ref, even_ref, total_ref,
    below_ref, above_ref, new_even_ref, new_total_ref, held_ref, held_sems, *, scale
):
    arrivals = [
        pltpu.make_async_copy(source, held_ref.at[index], held_sems.at[index])
        for index, source in enumerate((lower_ref, upper_ref))
    ]
    for copy in arrivals:
        copy.start()
    for copy in arrivals:
        copy.wait()
    below, above = turn_pair(held_ref[0], held_ref[1], pick_ref, turn_ref[...], flip_ref[...])
    below_ref[...] = below
    above_ref[...] = above
    top = top_ref[...]
    order = weight_ref[:, 7:8]
    parts = [
        face_lift(below, above, top[:, a * PLANE : (a + 1) * PLANE] <= order, a, scale)
        for a in range(P_SIZE)
    ]
    even, total = end_traces(parts)
    new_even_ref[...] = even_ref[...] + even
    new_total_ref[...] = total_ref[...] + total


def outer_body(
    pre_ref, top_ref, weight_ref, lower_ref, upper_ref, pick_ref, turn_ref, flip_ref,
    out_ref, even_ref, total_ref, *, scale
):
    derivative, second, side_signs, weights = mode_tables()
    lift_signs = (side_signs * weights[None, :]).astype(np.float32)
    below, above = turn_pair(lower_ref[...], upper_ref[...], pick_ref, turn_ref[...], flip_ref[...])
    top = top_ref[...]
    order = weight_ref[:, 7:8]
    news = []
    for a in range(P_SIZE):
        lanes = slice(a * PLANE, (a + 1) * PLANE)
        update = float(lift_signs[0, a]) * below + float(lift_signs[1, a]) * above
        live = top[:, lanes] <= order
        new = pre_ref[:, lanes] + scale * jnp.where(live, update, 0.0)
        out_ref[:, lanes] = new
        news.append(new)
    even, total = end_traces(news)
    even_ref[...] = even
    total_ref[...] = total


def inner(operands, scale, carried, final=False):
    count = operands[0].shape[0]
    spec = pl.BlockSpec(memory_space=pltpu.VMEM)
    square = jax.ShapeDtypeStruct((count, PLANE), jnp.float32)
    field = jax.ShapeDtypeStruct(operands[0].shape, jnp.float32)
    return pl.pallas_call(
        functools.partial(inner_body, scale=scale, carried=carried, final=final),
        out_shape=field if final else (field, square, square),
        in_specs=[spec] * len(operands),
        out_specs=spec if final else (spec, spec, spec),
        compiler_params=pltpu.CompilerParams(vmem_limit_bytes=60 * 1024 * 1024),
        cost_estimate=pl.CostEstimate(
            flops=2_500_000_000, transcendentals=0, bytes_accessed=4_000_000
        ),
    )(*operands)


def faces(lower, upper, picks, codes, flip, top, weight, even, total, scale):
    count = lower.shape[0]
    spec = pl.BlockSpec(memory_space=pltpu.VMEM)
    square = jax.ShapeDtypeStruct((count, PLANE), jnp.float32)
    return pl.pallas_call(
        functools.partial(faces_body, scale=scale),
        out_shape=(square,) * 4,
        in_specs=[pl.BlockSpec(memory_space=pl.ANY)] * 2 + [spec] * 7,
        out_specs=(spec,) * 4,
        scratch_shapes=[pltpu.VMEM((2, count, PLANE), jnp.float32), pltpu.SemaphoreType.DMA((2,))],
    )(lower, upper, picks, codes, flip, top, weight, even, total)


def outer(pre, top, weight, lower, upper, picks, codes, flip, scale):
    count = pre.shape[0]
    spec = pl.BlockSpec(memory_space=pltpu.VMEM)
    return pl.pallas_call(
        functools.partial(outer_body, scale=scale),
        out_shape=(
            jax.ShapeDtypeStruct(pre.shape, jnp.float32),
            jax.ShapeDtypeStruct((count, PLANE), jnp.float32),
            jax.ShapeDtypeStruct((count, PLANE), jnp.float32),
        ),
        in_specs=[spec] * 8,
        out_specs=(spec, spec, spec),
    )(pre, top, weight, lower, upper, picks, codes, flip)


def prep_body(placed_ref, top_ref, weight_ref, field_ref, even_ref, total_ref):
    news = []
    for a in range(P_SIZE):
        lanes = slice(a * PLANE, (a + 1) * PLANE)
        live = top_ref[:, lanes] <= weight_ref[:, 7:8]
        new = jnp.where(live, placed_ref[:, lanes], 0.0)
        field_ref[:, lanes] = new
        news.append(new)
    even, total = end_traces(news)
    even_ref[...] = even
    total_ref[...] = total


def prep(placed, top, weight):
    count = placed.shape[0]
    spec = pl.BlockSpec(memory_space=pltpu.VMEM)
    return pl.pallas_call(
        prep_body,
        out_shape=(
            jax.ShapeDtypeStruct(placed.shape, jnp.float32),
            jax.ShapeDtypeStruct((count, PLANE), jnp.float32),
            jax.ShapeDtypeStruct((count, PLANE), jnp.float32),
        ),
        in_specs=[spec] * 3,
        out_specs=(spec, spec, spec),
    )(placed, top, weight)


def exchange(even, total):
    size = lax.axis_size("dom")
    up = [(i, (i + 1) % size) for i in range(size)]
    down = [((i + 1) % size, i) for i in range(size)]
    return lax.ppermute(total, "dom", up), lax.ppermute(even, "dom", down)


def shards(
    coefficients, diffusion, velocity, orders, target, local_faces, partner_faces, partner_turns
):
    element_count = coefficients.shape[0]
    blocks_all = lax.axis_size(("dom", "face"))
    moving = element_count // 16
    destination = target // element_count
    new_slot = target % element_count
    here = lax.axis_index(("dom", "face"))
    side_info = jnp.concatenate(
        [
            diffusion,
            velocity,
            new_slot[:, None].astype(jnp.float32),
            orders[:, None].astype(jnp.float32),
        ],
        axis=1,
    )
    side_width = side_info.shape[1]
    shifts = (1, blocks_all - 1, blocks_all // 2)
    goal = (here + jnp.asarray(shifts, jnp.int32)) % blocks_all
    chosen = destination[None, :] == goal[:, None]
    rank = jnp.cumsum(chosen.astype(jnp.int32), axis=1) - 1
    hit = chosen[:, None, :] & (
        rank[:, None, :] == jnp.arange(moving, dtype=jnp.int32)[None, :, None]
    )
    width = P_SIZE**3
    exact = lax.Precision.HIGHEST
    counts = jnp.concatenate(
        [new_slot[None, :].astype(jnp.float32), orders[None, :].astype(jnp.float32)], axis=0
    )
    hit_values = hit.astype(jnp.float32)
    parcels = jnp.concatenate(
        [
            jnp.einsum("qjr,rc->qjc", hit_values, coefficients, precision=exact),
            jnp.einsum("qjr,rc->qjc", hit_values, diffusion, precision=exact),
            jnp.einsum("qjr,rc->qjc", hit_values, velocity, precision=exact),
            jnp.einsum("qjr,cr->qjc", hit_values, counts, precision=exact),
            jnp.zeros(hit.shape[:2] + (128 - side_width,), jnp.float32),
        ],
        axis=2,
    )
    arrivals = []
    got_slot = [jnp.where(destination == here, new_slot, element_count)]
    for index, shift in enumerate(shifts):
        pairs = [(i, (i + shift) % blocks_all) for i in range(blocks_all)]
        arrived = lax.ppermute(parcels[index], ("dom", "face"), pairs)
        arrivals.append(arrived)
        got_slot.append(arrived[:, width + 6].astype(jnp.int32))
    arrivals = jnp.concatenate(arrivals, axis=0)
    got_slot = jnp.concatenate(got_slot, axis=0)
    placing = (got_slot[None, :] == jnp.arange(element_count, dtype=jnp.int32)[:, None]).astype(
        jnp.float32
    )
    staying, coming = placing[:, :element_count], placing[:, element_count:]
    placed = jnp.dot(
        placing, jnp.concatenate([coefficients, arrivals[:, :width]], axis=0), precision=exact
    )
    placed_side = jnp.concatenate(
        [
            jnp.dot(staying, diffusion, precision=exact),
            jnp.dot(staying, velocity, precision=exact),
            jnp.einsum("sr,cr->sc", staying, counts, precision=exact),
        ],
        axis=1,
    ) + jnp.dot(coming, arrivals[:, width : width + side_width], precision=exact)
    weight = placed_side
    top = jnp.asarray(top_modes().astype(np.float32))
    tables = kernel_tables()
    neighbours = jnp.concatenate([local_faces[0], partner_faces[0]], axis=0)
    picks = (
        neighbours[:, :, None] == jnp.arange(element_count, dtype=jnp.int32)[None, None, :]
    ).astype(jnp.bfloat16)
    codes = partner_turns[0].T
    spread_hi, spread_lo, lift, flip = tables
    field = jnp.where(top <= weight[:, 7:8], placed, 0.0)
    slabs = [field[:, a * PLANE : (a + 1) * PLANE] for a in range(P_SIZE)]
    even, total = end_traces(slabs)
    first_step = 0.5 * TIME_STEP
    lower, upper = exchange(even, total)
    pre, even, total = inner(
        (field, weight, top, picks, spread_hi, spread_lo, lift), first_step, None
    )
    below, above, even, total = faces(
        lower, upper, picks, codes, flip, top, weight, even, total, first_step
    )
    lower, upper = exchange(even, total)
    advanced = inner(
        (pre, below, above, field, weight, top, picks, spread_hi, spread_lo, lift)
        + (lower, upper, codes, flip),
        TIME_STEP,
        first_step,
        final=True,
    )
    return advanced


def solution(mesh):
    in_specs = (
        P(("dom", "face"), None),
        P(("dom", "face"), None),
        P(("dom", "face"), None),
        P(("dom", "face")),
        P(("dom", "face")),
        P(("dom", "face"), None, None),
        P(("dom", "face"), None, None),
        P(("dom", "face"), None, None),
    )
    out_specs = P(("dom", "face"), None)
    return jax.shard_map(shards, mesh=mesh, in_specs=in_specs, out_specs=out_specs, check_vma=False)
```

```python
import functools
import jax
import jax.numpy as jnp
import numpy as np
from jax import lax
from jax.experimental import pallas as pl
from jax.experimental.pallas import tpu as pltpu
from jax.sharding import PartitionSpec as P

P_SIZE = 16
PLANE = P_SIZE * P_SIZE
TIME_STEP = 0.25


def mode_tables():
    ladder = np.arange(P_SIZE)
    spacing = ladder[None, :] - ladder[:, None]
    derivative = np.where(
        (spacing > 0) & (spacing % 2 == 1), (2.0 * ladder[:, None] + 1.0) / P_SIZE, 0.0
    )
    second = derivative @ derivative / P_SIZE
    side_signs = np.stack([(-1.0) ** ladder, np.ones(P_SIZE)])
    weights = (2.0 * ladder + 1.0) / (2.0 * P_SIZE)
    return (derivative, second, side_signs, weights)


def side_table(values_pair):
    identity = np.eye(P_SIZE)
    return np.concatenate(
        [
            np.kron(values_pair[0][:, None], identity),
            np.kron(values_pair[1][:, None], identity),
            np.kron(identity, values_pair[0][:, None]),
            np.kron(identity, values_pair[1][:, None]),
        ],
        axis=1,
    )


def kernel_tables():
    derivative, second, side_signs, weights = mode_tables()
    derivative = derivative.astype(np.float32).astype(np.float64)
    second = second.astype(np.float32).astype(np.float64)
    identity = np.eye(P_SIZE)
    traces = side_table(side_signs)
    swapped = traces[:, [16 * g + j for g in (1, 0, 3, 2) for j in range(P_SIZE)]]
    pad = np.zeros((PLANE, 64))
    spread = np.concatenate(
        [
            np.kron(identity, second.T),
            np.kron(second.T, identity),
            np.kron(identity, derivative.T),
            np.kron(derivative.T, identity),
            traces, pad, swapped, pad,
        ],
        axis=1,
    ).astype(np.float32)
    spread_hi = spread.astype(jnp.bfloat16)
    spread_lo = (spread[:, : 2 * PLANE] - spread_hi[:, : 2 * PLANE].astype(np.float32)).astype(jnp.bfloat16)
    lift_signs = side_signs * weights[None, :]
    lift = np.concatenate([side_table(lift_signs).T, np.zeros((64, PLANE))], axis=0)
    lanes = np.arange(PLANE)
    flip = np.zeros((PLANE, PLANE))
    flip[lanes, (lanes % P_SIZE) * P_SIZE + lanes // P_SIZE] = 1.0
    return (
        jnp.asarray(spread_hi),
        jnp.asarray(spread_lo),
        jnp.asarray(lift, jnp.bfloat16),
        jnp.asarray(flip, jnp.bfloat16),
    )


def top_modes():
    ladder = np.arange(P_SIZE)
    first_idx, second_idx, third_idx = np.meshgrid(ladder, ladder, ladder, indexing="ij")
    return np.maximum(np.maximum(first_idx, second_idx), third_idx).reshape(1, -1).astype(np.int32)


def split_two(x):
    hi = x.astype(jnp.bfloat16)
    lo = (x - hi.astype(jnp.float32)).astype(jnp.bfloat16)
    return hi, lo


def mxu(a, b):
    return jnp.dot(a, b, preferred_element_type=jnp.float32)


def split_three(x):
    hi = x.astype(jnp.bfloat16)
    rest = x - hi.astype(jnp.float32)
    mid = rest.astype(jnp.bfloat16)
    lo = (rest - mid.astype(jnp.float32)).astype(jnp.bfloat16)
    return hi, mid, lo


def exact_pick(onehot, x):
    width = x.shape[1]
    joined = mxu(onehot, jnp.concatenate(split_three(x), axis=1))
    return joined[:, :width] + joined[:, width : 2 * width] + joined[:, 2 * width :]


def exact_rows(x, onehot):
    count = x.shape[0]
    joined = mxu(jnp.concatenate(split_three(x), axis=0), onehot)
    return joined[:count] + joined[count : 2 * count] + joined[2 * count :]


def end_traces(slabs):
    total = slabs[0] + slabs[1]
    even = slabs[0] - slabs[1]
    for a in range(2, P_SIZE):
        total = total + slabs[a]
        even = even + slabs[a] if a % 2 == 0 else even - slabs[a]
    return even, total


def turn_pair(lower, upper, picks, codes, flip):
    count = lower.shape[0]
    picked = jnp.concatenate([exact_pick(picks[4], lower), exact_pick(picks[5], upper)], axis=0)
    swapped = exact_rows(picked, flip)
    lane = lax.broadcasted_iota(jnp.int32, (1, PLANE), 1)
    row_odd = (lane // P_SIZE) % 2 == 1
    col_odd = lane % 2 == 1
    sides = []
    for side in range(2):
        rows = slice(side * count, (side + 1) * count)
        code = codes[:, side : side + 1]
        chosen = jnp.where(code % 2 == 1, swapped[rows], picked[rows])
        negate = ((code // 2) % 2 == 1) & row_odd
        negate = negate != (((code // 4) % 2 == 1) & col_odd)
        sides.append(jnp.where(negate, -chosen, chosen))
    return sides


def face_lift(below, above, live, a, scale):
    derivative, second, side_signs, weights = mode_tables()
    lift_signs = (side_signs * weights[None, :]).astype(np.float32)
    update = float(lift_signs[0, a]) * below + float(lift_signs[1, a]) * above
    return scale * jnp.where(live, update, 0.0)


def inner_body(*refs, scale, carried, final):
    if carried is None:
        v_ref, weight_ref, top_ref, pick_ref, spread_hi_ref, spread_lo_ref, lift_ref = refs[:7]
        base_ref = v_ref
    else:
        v_ref, below_ref, above_ref, base_ref, weight_ref, top_ref, pick_ref = refs[:7]
        spread_hi_ref, spread_lo_ref, lift_ref = refs[7:10]
    if final:
        lower_ref, upper_ref, turn_ref, flip_ref = refs[10:14]
        partial_ref = refs[-1]
    else:
        partial_ref, even_ref, total_ref = refs[-3:]
    count = v_ref.shape[0]
    derivative, second, side_signs, weights = mode_tables()
    second = second.astype(np.float32)
    derivative = derivative.astype(np.float32)
    lift_signs = (side_signs * weights[None, :]).astype(np.float32)
    weight = weight_ref[...]
    top = top_ref[...]
    order = weight[:, 7:8]
    slabs = [v_ref[:, a * PLANE : (a + 1) * PLANE] for a in range(P_SIZE)]
    if carried is not None:
        below = below_ref[...]
        above = above_ref[...]
        slabs = [
            slabs[a] + face_lift(below, above, top[:, a * PLANE : (a + 1) * PLANE] <= order, a, carried)
            for a in range(P_SIZE)
        ]
    diff0 = jnp.broadcast_to(weight[:, 0:1], (count, PLANE))
    vel0 = jnp.broadcast_to(weight[:, 3:4], (count, PLANE))
    half = count // 2
    low = P_SIZE // 2

    def kept(a, x):
        return x if a < low else x[half:]

    def start(a):
        return a * count if a < low else low * count + (a - low) * half

    upper_slabs = [s[half:] for s in slabs]
    first = []
    for k in range(P_SIZE):
        parts = []
        for rows, source in ((slice(0, half), slabs), (slice(half, count), upper_slabs)):
            if rows.start == 0 and k >= low:
                continue
            acc_s = None
            acc_d = None
            top_n = low if rows.start == 0 else P_SIZE
            for n in range(k + 1, top_n):
                piece = source[n] if rows.start else source[n][:half]
                if second[k, n] != 0.0:
                    term = float(second[k, n]) * piece
                    acc_s = term if acc_s is None else acc_s + term
                if derivative[k, n] != 0.0:
                    term = float(derivative[k, n]) * piece
                    acc_d = term if acc_d is None else acc_d + term
            part = jnp.zeros((half, PLANE), jnp.float32)
            if acc_s is not None:
                part = part + diff0[rows] * acc_s
            if acc_d is not None:
                part = part - vel0[rows] * acc_d
            parts.append(part)
        first.append(parts[0] if len(parts) == 1 else jnp.concatenate(parts, axis=0))
    stacked = jnp.concatenate([kept(a, slabs[a]) for a in range(P_SIZE)], axis=0)
    hi, lo = split_two(stacked)
    spread_hi = spread_hi_ref[...]
    wide = mxu(hi, spread_hi) + mxu(lo, spread_hi)
    fine = mxu(hi, spread_lo_ref[...])
    weight_rows = jnp.concatenate([kept(a, weight) for a in range(P_SIZE)], axis=0)
    inner = (
        weight_rows[:, 2:3] * (wide[:, 0:PLANE] + fine[:, 0:PLANE])
        + weight_rows[:, 1:2] * (wide[:, PLANE : 2 * PLANE] + fine[:, PLANE : 2 * PLANE])
        - weight_rows[:, 5:6] * wide[:, 2 * PLANE : 3 * PLANE]
        - weight_rows[:, 4:5] * wide[:, 3 * PLANE : 4 * PLANE]
    )
    blank = jnp.zeros((half, 128), jnp.float32)

    def trace_block(a, offset):
        rows = wide[start(a) : start(a) + (count if a < low else half), offset : offset + 128]
        return rows if a < low else jnp.concatenate([blank, rows], axis=0)

    own = jnp.concatenate([trace_block(a, 4 * PLANE) for a in range(P_SIZE)], axis=1)
    other = jnp.concatenate([trace_block(a, 4 * PLANE + 128) for a in range(P_SIZE)], axis=1)
    lane = lax.broadcasted_iota(jnp.int32, (1, P_SIZE * 128), 1) % 128
    across = jnp.zeros_like(own)
    for face in range(4):
        gathered = exact_pick(pick_ref[face], other)
        across = jnp.where(lane // P_SIZE == face, gathered, across)
    jump = own - across
    jump_rows = jnp.concatenate(
        [kept(a, jump[:, a * 128 : (a + 1) * 128]) for a in range(P_SIZE)], axis=0
    )
    jhi, jlo = split_two(jump_rows)
    lift_mat = lift_ref[...]
    lifted = mxu(jhi, lift_mat) + mxu(jlo, lift_mat)
    even, total = end_traces(slabs)
    if final:
        below, above = turn_pair(
            lower_ref[...], upper_ref[...], pick_ref, turn_ref[...], flip_ref[...]
        )
    news = []
    for a in range(P_SIZE):
        rows = slice(start(a), start(a) + (count if a < low else half))
        lanes = slice(a * PLANE, (a + 1) * PLANE)
        own_lift = lifted[rows] + float(lift_signs[0, a]) * kept(a, even)
        own_lift = own_lift + float(lift_signs[1, a]) * kept(a, total)
        if final:
            own_lift = own_lift - float(lift_signs[0, a]) * kept(a, below)
            own_lift = own_lift - float(lift_signs[1, a]) * kept(a, above)
        live = kept(a, top[:, lanes] <= order)
        update = jnp.where(live, first[a] + inner[rows] - own_lift, 0.0)
        if a < low:
            new = base_ref[:, lanes] + scale * update
        else:
            new = jnp.concatenate(
                [base_ref[:half, lanes] + 0.0, base_ref[half:, lanes] + scale * update], axis=0
            )
        partial_ref[:, lanes] = new
        news.append(new)
    if not final:
        even, total = end_traces(news)
        even_ref[...] = even
        total_ref[...] = total


def faces_body(
    lower_ref, upper_ref, pick_ref, turn_ref, flip_ref, top_ref, weight_ref, even_ref, total_ref,
    below_ref, above_ref, new_even_ref, new_total_ref, *, scale
):
    below, above = turn_pair(lower_ref[...], upper_ref[...], pick_ref, turn_ref[...], flip_ref[...])
    below_ref[...] = below
    above_ref[...] = above
    top = top_ref[...]
    order = weight_ref[:, 7:8]
    parts = [
        face_lift(below, above, top[:, a * PLANE : (a + 1) * PLANE] <= order, a, scale)
        for a in range(P_SIZE)
    ]
    even, total = end_traces(parts)
    new_even_ref[...] = even_ref[...] + even
    new_total_ref[...] = total_ref[...] + total


def outer_body(
    pre_ref, top_ref, weight_ref, lower_ref, upper_ref, pick_ref, turn_ref, flip_ref,
    out_ref, even_ref, total_ref, *, scale
):
    derivative, second, side_signs, weights = mode_tables()
    lift_signs = (side_signs * weights[None, :]).astype(np.float32)
    below, above = turn_pair(lower_ref[...], upper_ref[...], pick_ref, turn_ref[...], flip_ref[...])
    top = top_ref[...]
    order = weight_ref[:, 7:8]
    news = []
    for a in range(P_SIZE):
        lanes = slice(a * PLANE, (a + 1) * PLANE)
        update = float(lift_signs[0, a]) * below + float(lift_signs[1, a]) * above
        live = top[:, lanes] <= order
        new = pre_ref[:, lanes] + scale * jnp.where(live, update, 0.0)
        out_ref[:, lanes] = new
        news.append(new)
    even, total = end_traces(news)
    even_ref[...] = even
    total_ref[...] = total


def inner(operands, scale, carried, final=False):
    count = operands[0].shape[0]
    spec = pl.BlockSpec(memory_space=pltpu.VMEM)
    square = jax.ShapeDtypeStruct((count, PLANE), jnp.float32)
    field = jax.ShapeDtypeStruct(operands[0].shape, jnp.float32)
    return pl.pallas_call(
        functools.partial(inner_body, scale=scale, carried=carried, final=final),
        out_shape=field if final else (field, square, square),
        in_specs=[spec] * len(operands),
        out_specs=spec if final else (spec, spec, spec),
        compiler_params=pltpu.CompilerParams(vmem_limit_bytes=60 * 1024 * 1024),
        cost_estimate=pl.CostEstimate(
            flops=2_500_000_000, transcendentals=0, bytes_accessed=4_000_000
        ),
    )(*operands)


def faces(lower, upper, picks, codes, flip, top, weight, even, total, scale):
    count = lower.shape[0]
    spec = pl.BlockSpec(memory_space=pltpu.VMEM)
    square = jax.ShapeDtypeStruct((count, PLANE), jnp.float32)
    return pl.pallas_call(
        functools.partial(faces_body, scale=scale),
        out_shape=(square,) * 4,
        in_specs=[spec] * 9,
        out_specs=(spec,) * 4,
        input_output_aliases={7: 2, 8: 3},
    )(lower, upper, picks, codes, flip, top, weight, even, total)


def outer(pre, top, weight, lower, upper, picks, codes, flip, scale):
    count = pre.shape[0]
    spec = pl.BlockSpec(memory_space=pltpu.VMEM)
    return pl.pallas_call(
        functools.partial(outer_body, scale=scale),
        out_shape=(
            jax.ShapeDtypeStruct(pre.shape, jnp.float32),
            jax.ShapeDtypeStruct((count, PLANE), jnp.float32),
            jax.ShapeDtypeStruct((count, PLANE), jnp.float32),
        ),
        in_specs=[spec] * 8,
        out_specs=(spec, spec, spec),
    )(pre, top, weight, lower, upper, picks, codes, flip)


def prep_body(placed_ref, top_ref, weight_ref, field_ref, even_ref, total_ref):
    news = []
    for a in range(P_SIZE):
        lanes = slice(a * PLANE, (a + 1) * PLANE)
        live = top_ref[:, lanes] <= weight_ref[:, 7:8]
        new = jnp.where(live, placed_ref[:, lanes], 0.0)
        field_ref[:, lanes] = new
        news.append(new)
    even, total = end_traces(news)
    even_ref[...] = even
    total_ref[...] = total


def prep(placed, top, weight):
    count = placed.shape[0]
    spec = pl.BlockSpec(memory_space=pltpu.VMEM)
    return pl.pallas_call(
        prep_body,
        out_shape=(
            jax.ShapeDtypeStruct(placed.shape, jnp.float32),
            jax.ShapeDtypeStruct((count, PLANE), jnp.float32),
            jax.ShapeDtypeStruct((count, PLANE), jnp.float32),
        ),
        in_specs=[spec] * 3,
        out_specs=(spec, spec, spec),
    )(placed, top, weight)


def exchange(even, total):
    size = lax.axis_size("dom")
    up = [(i, (i + 1) % size) for i in range(size)]
    down = [((i + 1) % size, i) for i in range(size)]
    return lax.ppermute(total, "dom", up), lax.ppermute(even, "dom", down)


def shards(
    coefficients, diffusion, velocity, orders, target, local_faces, partner_faces, partner_turns
):
    element_count = coefficients.shape[0]
    blocks_all = lax.axis_size(("dom", "face"))
    moving = element_count // 16
    destination = target // element_count
    new_slot = target % element_count
    here = lax.axis_index(("dom", "face"))
    side_info = jnp.concatenate(
        [
            diffusion,
            velocity,
            new_slot[:, None].astype(jnp.float32),
            orders[:, None].astype(jnp.float32),
        ],
        axis=1,
    )
    side_width = side_info.shape[1]
    shifts = (1, blocks_all - 1, blocks_all // 2)
    goal = (here + jnp.asarray(shifts, jnp.int32)) % blocks_all
    chosen = destination[None, :] == goal[:, None]
    rank = jnp.cumsum(chosen.astype(jnp.int32), axis=1) - 1
    hit = chosen[:, None, :] & (
        rank[:, None, :] == jnp.arange(moving, dtype=jnp.int32)[None, :, None]
    )
    width = P_SIZE**3
    exact = lax.Precision.HIGHEST
    counts = jnp.concatenate(
        [new_slot[None, :].astype(jnp.float32), orders[None, :].astype(jnp.float32)], axis=0
    )
    hit_values = hit.astype(jnp.float32)
    parcels = jnp.concatenate(
        [
            jnp.einsum("qjr,rc->qjc", hit_values, coefficients, precision=exact),
            jnp.einsum("qjr,rc->qjc", hit_values, diffusion, precision=exact),
            jnp.einsum("qjr,rc->qjc", hit_values, velocity, precision=exact),
            jnp.einsum("qjr,cr->qjc", hit_values, counts, precision=exact),
            jnp.zeros(hit.shape[:2] + (128 - side_width,), jnp.float32),
        ],
        axis=2,
    )
    arrivals = []
    got_slot = [jnp.where(destination == here, new_slot, element_count)]
    for index, shift in enumerate(shifts):
        pairs = [(i, (i + shift) % blocks_all) for i in range(blocks_all)]
        arrived = lax.ppermute(parcels[index], ("dom", "face"), pairs)
        arrivals.append(arrived)
        got_slot.append(arrived[:, width + 6].astype(jnp.int32))
    arrivals = jnp.concatenate(arrivals, axis=0)
    got_slot = jnp.concatenate(got_slot, axis=0)
    placing = (got_slot[None, :] == jnp.arange(element_count, dtype=jnp.int32)[:, None]).astype(
        jnp.float32
    )
    staying, coming = placing[:, :element_count], placing[:, element_count:]
    placed = jnp.dot(
        placing, jnp.concatenate([coefficients, arrivals[:, :width]], axis=0), precision=exact
    )
    placed_side = jnp.concatenate(
        [
            jnp.dot(staying, diffusion, precision=exact),
            jnp.dot(staying, velocity, precision=exact),
            jnp.einsum("sr,cr->sc", staying, counts, precision=exact),
        ],
        axis=1,
    ) + jnp.dot(coming, arrivals[:, width : width + side_width], precision=exact)
    weight = placed_side
    top = jnp.asarray(top_modes().astype(np.float32))
    tables = kernel_tables()
    neighbours = jnp.concatenate([local_faces[0], partner_faces[0]], axis=0)
    picks = (
        neighbours[:, :, None] == jnp.arange(element_count, dtype=jnp.int32)[None, None, :]
    ).astype(jnp.bfloat16)
    codes = partner_turns[0].T
    spread_hi, spread_lo, lift, flip = tables
    field = jnp.where(top <= weight[:, 7:8], placed, 0.0)
    slabs = [field[:, a * PLANE : (a + 1) * PLANE] for a in range(P_SIZE)]
    even, total = end_traces(slabs)
    first_step = 0.5 * TIME_STEP
    lower, upper = exchange(even, total)
    pre, even, total = inner(
        (field, weight, top, picks, spread_hi, spread_lo, lift), first_step, None
    )
    below, above, even, total = faces(
        lower, upper, picks, codes, flip, top, weight, even, total, first_step
    )
    lower, upper = exchange(even, total)
    advanced = inner(
        (pre, below, above, field, weight, top, picks, spread_hi, spread_lo, lift)
        + (lower, upper, codes, flip),
        TIME_STEP,
        first_step,
        final=True,
    )
    return advanced


def solution(mesh):
    in_specs = (
        P(("dom", "face"), None),
        P(("dom", "face"), None),
        P(("dom", "face"), None),
        P(("dom", "face")),
        P(("dom", "face")),
        P(("dom", "face"), None, None),
        P(("dom", "face"), None, None),
        P(("dom", "face"), None, None),
    )
    out_specs = P(("dom", "face"), None)
    return jax.shard_map(shards, mesh=mesh, in_specs=in_specs, out_specs=out_specs, check_vma=False)
```
